32 devices in a mesh: dp: 8 (over z, x), head: 4 (over y, core).
Axes of the slice: x: 2, y: 2, z: 4, core: 2. Of those that a mesh axis runs over, the one named last changes fastest.
Arguments:
- tokens: bfloat16 [8192, 1024], P(('dp', 'head'))
- doc_ids: int32 [8, 1024], P('dp'), may hold values from 0 to 7, never falling along the last dimension, each value on 1 to 512 neighbouring positions
- gain_attn: float32 [1024], replicated, may hold values from 0.1 to 1.9
- a_weight: bfloat16 [1024, 160], P(None, 'head'), may hold values from -0.4375 to 0.4375
- b_weight: bfloat16 [1024, 640], replicated, may hold values from -0.1875 to 0.1875
- out_weight: bfloat16 [1024, 1024], P('head'), may hold values from -0.5 to 0.5
- gain_ffn: float32 [1024], replicated, may hold values from 0.1 to 1.9
- gate_weight: bfloat16 [1024, 2816], P(None, 'head'), may hold values from -0.1875 to 0.1875
- up_weight: bfloat16 [1024, 2816], P(None, 'head'), may hold values from -0.1875 to 0.1875
- down_weight: bfloat16 [2816, 1024], P('head'), may hold values from -0.109375 to 0.109375
- cotangent: bfloat16 [8192, 1024], P(('dp', 'head'))
Outputs:
- output: bfloat16 [8192, 1024], P(('dp', 'head'))
- input_grad: float32 [8192, 1024], P(('dp', 'head'))
- grad_gain_attn: float32 [1024], replicated
- grad_a: float32 [1024, 160], P(None, 'head')
- grad_b: float32 [1024, 640], replicated
- grad_out: float32 [1024, 1024], P('head')
- grad_gain_ffn: float32 [1024], replicated
- grad_gate: float32 [1024, 2816], P(None, 'head')
- grad_up: float32 [1024, 2816], P(None, 'head')
- grad_down: float32 [2816, 1024], P('head')
The draws below stay inside these ranges and needn't reach their ends.
Inputs may be any that keep to these rules, and one draw needn't show every extreme that they name: `doc_ids`: within a row the document number never falls; a document holds 1 to 512 positions.
All inputs are finite; a program needn't handle non-finite values.
Results may differ from the reference program's by a relative error of at most 0.019.
The reference program's roundings to bfloat16 on the way count: a program that leaves them out, or rounds other values in their place, can miss the bound.
Values may be sent and summed in bfloat16 or wider, within the bound.
No kernel may reach another device: no remote copies, remote signals or barrier semaphores. Data moves between devices by JAX's collectives and lax.ppermute only.
A program may use at most 192 MiB of HBM per device.

```python
import math
import jax
import jax.numpy as jnp
import numpy as np
from jax import lax

D = 1024
H = 16
DH = 64
RQ = 6
RK = 2
FF = 2816
LEN = 1024
DOCS = 8
DOC_MOST = 512
ROWS = 8
TOKENS = 8192


def draw_tokens(key, part):
    subkeys = jax.random.split(key, 3)
    row_scale = jnp.exp(jax.random.uniform(subkeys[1], (TOKENS, 1), jnp.float32, -0.7, 0.7))
    col_scale = jnp.exp(jax.random.uniform(subkeys[2], (1, D), jnp.float32, -0.7, 0.7))
    base = jax.random.normal(subkeys[0], (TOKENS, D), jnp.float32)
    return (base * row_scale * col_scale).astype(jnp.bfloat16)


def draw_cotangent(key, part):
    subkeys = jax.random.split(key, 1)
    rising = 1.0 + 2.0 * jnp.arange(TOKENS, dtype=jnp.float32)[:, None] / TOKENS
    base = jax.random.normal(subkeys[0], (TOKENS, D), jnp.float32)
    return (base * rising).astype(jnp.bfloat16)


def block_levels(key, dims, pieces, smallest, top_value):
    def one(dim, parts):
        heights = jax.random.uniform(jax.random.fold_in(jax.random.fold_in(key, 6), dim), (parts,), jnp.float32, smallest / len(pieces), top_value / len(pieces))
        return jnp.repeat(jnp.exp(heights), dims[dim] // parts).reshape((-1,) + (1,) * (len(dims) - dim - 1))

    factor_of = one(*pieces[0])
    for cut in pieces[1:]:
        factor_of = factor_of * one(*cut)
    return factor_of


def split_up(count, total, bound, lean):
    weights = [(1 << 20) // math.isqrt(grade ** lean) + 1 for grade in range(2, count + 1)]
    spare, holding = total - bound - (count - 1), [1] * (count - 1)
    while spare > 0:
        candidates = [i for i in range(count - 1) if holding[i] < bound]
        pool, left = sum([weights[i] for i in candidates]), spare
        for i in candidates:
            more = min(bound - holding[i], max(1, left * weights[i] // pool), spare)
            holding[i] = holding[i] + more
            spare = spare - more
    return np.array([bound] + holding)


def uneven_parts(stream_key, amount, total, limit, slope):
    if amount == 2:
        one = jax.random.randint(stream_key, (), max(1, total - limit), min(limit, total - 1) + 1)
        return jnp.stack([one, total - one])
    sizes = jnp.asarray(split_up(amount, total, limit, slope), jnp.int32)
    couples = (amount - 1) // 2
    donor, taker = sizes[1:1 + 2 * couples:2], sizes[2:2 + 2 * couples:2]
    slack = jnp.minimum(donor - 1, limit - taker)
    moved = jax.random.randint(jax.random.fold_in(stream_key, 1), (couples,), 0, 1 << 20) % (slack + 1)
    sizes = sizes.at[1:1 + 2 * couples:2].set(donor - moved).at[2:2 + 2 * couples:2].set(taker + moved)
    return sizes[jax.random.permutation(jax.random.fold_in(stream_key, 2), amount)]


def normal_values(stream_key, dims, spread, reach, cuts=(), held_as=jnp.bfloat16):
    values = spread * jax.random.normal(stream_key, dims, jnp.float32)
    if cuts:
        values = values * block_levels(stream_key, dims, cuts, -0.22, 0.18)
    return jnp.clip(values, -reach, reach).astype(held_as)


def setup_inputs(seed: int = 0) -> dict:
    splits = jax.random.split(jax.random.key(seed), 12)
    return {
        "tokens": draw_tokens(jax.random.fold_in(splits[11], 71), 0),
        "doc_ids": jax.vmap(lambda own: jnp.searchsorted(jnp.cumsum(uneven_parts(own, DOCS, LEN, DOC_MOST, 2)), jnp.arange(LEN), side="right"))(jax.random.split(splits[1], ROWS)).reshape((ROWS, LEN)).astype(jnp.int32),
        "gain_attn": jnp.clip(1.0 + 0.18 * jax.random.normal(splits[2], (D,), jnp.float32), 0.1, 1.9),
        "a_weight": normal_values(splits[3], (D, H * (RQ + 2 * RK)), (D // 6) ** -0.5, 0.4375, ((1, 4),)),
        "b_weight": normal_values(splits[4], (D, (RQ + 2 * RK) * DH), D ** -0.5, 0.1875),
        "out_weight": normal_values(splits[5], (H * DH, D), (H * DH // 8) ** -0.5, 0.5, ((0, 4),)),
        "gain_ffn": jnp.clip(1.0 + 0.18 * jax.random.normal(splits[6], (D,), jnp.float32), 0.1, 1.9),
        "gate_weight": normal_values(splits[7], (D, FF), D ** -0.5, 0.1875, ((1, 4),)),
        "up_weight": normal_values(splits[8], (D, FF), D ** -0.5, 0.1875, ((1, 4),)),
        "down_weight": normal_values(splits[9], (FF, D), FF ** -0.5, 0.109375, ((0, 4),)),
        "cotangent": draw_cotangent(jax.random.fold_in(splits[11], 71), 0),
    }


EPSILON = 1e-06
MASKED = -1e+30
PRECISE = lax.Precision.HIGHEST

@jax.custom_vjp
def low(v):
    return lax.optimization_barrier(v.astype(jnp.bfloat16)).astype(jnp.float32)

@jax.custom_vjp
def low_back(v):
    return v

def low_keep(v):
    return (low(v), None)

def low_pass(kept, grad):
    return (grad,)

def back_keep(v):
    return (v, None)

def back_low(kept, grad):
    return (low(grad),)
low.defvjp(low_keep, low_pass)
low_back.defvjp(back_keep, back_low)

def rope_tables(length):
    half_depth = DH // 2
    position = jnp.arange(length, dtype=jnp.float32)
    frequency = jnp.exp(jnp.arange(half_depth, dtype=jnp.float32) * (-2.0 * math.log(10000.0) / DH))
    angle = position[:, None] * frequency[None, :]
    return (jnp.cos(angle), jnp.sin(angle))

def rotate(basis, cosine, sine):
    half_depth = basis.shape[-1] // 2
    first_half = basis[..., :half_depth]
    second_half = basis[..., half_depth:]
    cosine_row = cosine[:, None, :]
    sine_row = sine[:, None, :]
    return jnp.concatenate([first_half * cosine_row - second_half * sine_row, second_half * cosine_row + first_half * sine_row], axis=-1)

def layer_row(x_row, doc_row, gain_one, weight_a, weight_b, weight_out, gain_two, weight_gate, weight_up, weight_down):
    length = x_row.shape[0]
    rank_all = RQ + 2 * RK
    score_scale = 1.0 / math.sqrt(DH)
    inv_one = lax.rsqrt(lax.optimization_barrier(jnp.mean(x_row * x_row, axis=-1, keepdims=True)) + EPSILON)
    normed_one = low(x_row * inv_one * gain_one)
    factor_a = low_back(jnp.dot(normed_one, weight_a, precision=PRECISE)).reshape(length, H, rank_all)
    factor_b = low_back(jnp.dot(normed_one, weight_b, precision=PRECISE))
    cosine, sine = rope_tables(length)
    basis_query = rotate(factor_b[:, :RQ * DH].reshape(length, RQ, DH), cosine, sine)
    basis_key = rotate(factor_b[:, RQ * DH:(RQ + RK) * DH].reshape(length, RK, DH), cosine, sine)
    basis_value = factor_b[:, (RQ + RK) * DH:].reshape(length, RK, DH)
    queries = jnp.einsum('thr,trd->thd', factor_a[:, :, :RQ], basis_query, precision=PRECISE) / RQ
    key_rows = jnp.einsum('thr,trd->thd', factor_a[:, :, RQ:RQ + RK], basis_key, precision=PRECISE) / RK
    value_rows = jnp.einsum('thr,trd->thd', factor_a[:, :, RQ + RK:], basis_value, precision=PRECISE) / RK
    queries = low_back(low(queries))
    key_rows = low_back(low(key_rows))
    value_rows = low_back(low(value_rows))
    scores = low_back(jnp.einsum('qhd,khd->hqk', queries, key_rows, precision=PRECISE) * score_scale)
    position = jnp.arange(length, dtype=jnp.int32)
    allowed = (doc_row[:, None] == doc_row[None, :]) & (position[None, :] <= position[:, None])
    scores = jnp.where(allowed[None], scores, MASKED)
    row_peak = lax.optimization_barrier(jnp.max(scores, axis=-1, keepdims=True))
    exponent = jnp.exp(scores - row_peak)
    weights = low(exponent / lax.optimization_barrier(jnp.sum(exponent, axis=-1, keepdims=True)))
    mixed = jnp.einsum('hqk,khd->qhd', weights, value_rows, precision=PRECISE)
    mixed = low_back(low(mixed)).reshape(length, H * DH)
    branch = low_back(jnp.dot(mixed, weight_out, precision=PRECISE))
    resid = x_row + branch
    inv_two = lax.rsqrt(lax.optimization_barrier(jnp.mean(resid * resid, axis=-1, keepdims=True)) + EPSILON)
    normed_two = low(resid * inv_two * gain_two)
    gate_act = low_back(jnp.dot(normed_two, weight_gate, precision=PRECISE))
    up_act = low_back(jnp.dot(normed_two, weight_up, precision=PRECISE))
    hidden = low(jax.nn.sigmoid(gate_act) * gate_act * up_act)
    return resid + jnp.dot(hidden, weight_down, precision=PRECISE)

def reference(tokens, doc_ids, gain_attn, a_weight, b_weight, out_weight, gain_ffn, gate_weight, up_weight, down_weight, cotangent):
    layer_step = jax.checkpoint(layer_row)

    def forward(inputs, gain_one, weight_a, weight_b, weight_out, gain_two, weight_gate, weight_up, weight_down):

        def scan_step(state_in, row_item):
            return (state_in, layer_step(row_item[0], row_item[1], gain_one, weight_a, weight_b, weight_out, gain_two, weight_gate, weight_up, weight_down))
        unused, outputs = lax.scan(scan_step, jnp.zeros((), jnp.float32), (inputs.reshape(-1, LEN, D), doc_ids))
        return outputs.reshape(-1, D)
    result, pullback = jax.vjp(forward, tokens.astype(jnp.float32), gain_attn.astype(jnp.float32), a_weight.astype(jnp.float32), b_weight.astype(jnp.float32), out_weight.astype(jnp.float32), gain_ffn.astype(jnp.float32), gate_weight.astype(jnp.float32), up_weight.astype(jnp.float32), down_weight.astype(jnp.float32))
    grads = pullback(cotangent.astype(jnp.float32))
    return (result.astype(jnp.bfloat16), grads[0], grads[1], grads[2], grads[3], grads[4], grads[5], grads[6], grads[7], grads[8])
```

```python
import math

import jax
import jax.numpy as jnp
from jax import lax
from jax.sharding import PartitionSpec as P

DH = 64
RQ = 6
RK = 2


EPSILON = 1e-06
MASKED = -1e30
PRECISE = lax.Precision.HIGHEST


def rope_tables(total_rows, length):
    half_depth = DH // 2
    position = (jnp.arange(total_rows, dtype=jnp.int32) % length).astype(jnp.float32)
    frequency = jnp.exp(jnp.arange(half_depth, dtype=jnp.float32) * (-2.0 * math.log(10000.0) / DH))
    angle = position[:, None] * frequency[None, :]
    return (jnp.cos(angle), jnp.sin(angle))


def rotate(basis, cosine, sine):
    half_depth = basis.shape[-1] // 2
    first_half = basis[..., :half_depth]
    second_half = basis[..., half_depth:]
    cosine_row = cosine[:, None, :]
    sine_row = sine[:, None, :]
    return jnp.concatenate(
        [
            first_half * cosine_row - second_half * sine_row,
            second_half * cosine_row + first_half * sine_row,
        ],
        axis=-1,
    )


def unrotate(grad_basis, cosine, sine):
    half_depth = grad_basis.shape[-1] // 2
    first_half = grad_basis[..., :half_depth]
    second_half = grad_basis[..., half_depth:]
    cosine_row = cosine[:, None, :]
    sine_row = sine[:, None, :]
    return jnp.concatenate(
        [
            first_half * cosine_row + second_half * sine_row,
            second_half * cosine_row - first_half * sine_row,
        ],
        axis=-1,
    )


def dot_last(left, right):
    return lax.dot_general(
        left, right, (((1,), (1,)), ((), ())), preferred_element_type=jnp.float32
    )


def dot_first(left, right):
    return lax.dot_general(
        left, right, (((0,), (0,)), ((), ())), preferred_element_type=jnp.float32
    )


def norm_backward(inputs, inverse, gain, grad_normed):
    scaled = gain * grad_normed
    inner = jnp.mean(scaled * inputs, axis=-1, keepdims=True)
    grad_inputs = inverse * scaled - inputs * (inverse * inverse * inverse) * inner
    grad_gain = jnp.sum(grad_normed * inputs * inverse, axis=0)
    return (grad_inputs, grad_gain)


def block_scores(queries, key_rows, doc_row, first_row, last_row):
    position = jnp.arange(last_row, dtype=jnp.int32)
    allowed = (doc_row[first_row:last_row, None] == doc_row[None, :last_row]) & (
        position[None, :] <= position[first_row:last_row, None]
    )
    score_scale = 1.0 / math.sqrt(queries.shape[2])
    scores = (
        jnp.einsum(
            "qhd,khd->hqk",
            queries[first_row:last_row],
            key_rows[:last_row],
            preferred_element_type=jnp.float32,
        )
        * score_scale
    )
    return jnp.where(allowed[None], scores, MASKED)


def attend_row(row_item):
    queries, key_rows, value_rows, doc_row = row_item
    length = queries.shape[0]
    block_rows = min(512, length)
    mixed_parts = []
    total_parts = []
    for first_row in range(0, length, block_rows):
        last_row = first_row + block_rows
        scores = block_scores(queries, key_rows, doc_row, first_row, last_row)
        row_peak = jnp.max(scores, axis=-1, keepdims=True)
        exponent = jnp.exp(scores - row_peak)
        row_total = jnp.sum(exponent, axis=-1, keepdims=True)
        weights = (exponent / row_total).astype(jnp.bfloat16)
        mixed_parts.append(
            jnp.einsum(
                "hqk,khd->qhd", weights, value_rows[:last_row], preferred_element_type=jnp.float32
            ).astype(jnp.bfloat16)
        )
        total_parts.append(row_peak[..., 0] + jnp.log(row_total[..., 0]))
    return (jnp.concatenate(mixed_parts, axis=0), jnp.concatenate(total_parts, axis=1))


def attend_back(row_item):
    queries, key_rows, value_rows, doc_row, log_total, grad_mixed = row_item
    length = queries.shape[0]
    block_rows = min(512, length)
    score_scale = 1.0 / math.sqrt(queries.shape[2])
    grad_query_parts = []
    grad_keys = jnp.zeros(key_rows.shape, jnp.float32)
    grad_values = jnp.zeros(value_rows.shape, jnp.float32)
    for first_row in range(0, length, block_rows):
        last_row = first_row + block_rows
        scores = block_scores(queries, key_rows, doc_row, first_row, last_row)
        weights = jnp.exp(scores - log_total[:, first_row:last_row, None])
        grad_weights = jnp.einsum(
            "qhd,khd->hqk",
            grad_mixed[first_row:last_row],
            value_rows[:last_row],
            preferred_element_type=jnp.float32,
        )
        inner = jnp.sum(weights * grad_weights, axis=-1, keepdims=True)
        grad_scores = (weights * (grad_weights - inner)).astype(jnp.bfloat16)
        grad_query_parts.append(
            jnp.einsum(
                "hqk,khd->qhd", grad_scores, key_rows[:last_row], preferred_element_type=jnp.float32
            )
            * score_scale
        )
        padding = ((0, length - last_row), (0, 0), (0, 0))
        key_part = (
            jnp.einsum(
                "hqk,qhd->khd",
                grad_scores,
                queries[first_row:last_row],
                preferred_element_type=jnp.float32,
            )
            * score_scale
        )
        value_part = jnp.einsum(
            "hqk,qhd->khd",
            weights.astype(jnp.bfloat16),
            grad_mixed[first_row:last_row],
            preferred_element_type=jnp.float32,
        )
        grad_keys = grad_keys + jnp.pad(key_part, padding)
        grad_values = grad_values + jnp.pad(value_part, padding)
    return (jnp.concatenate(grad_query_parts, axis=0), grad_keys, grad_values)


def rounded(values_in):
    return lax.optimization_barrier(values_in.astype(jnp.bfloat16)).astype(jnp.float32)


def local(
    tokens,
    doc_ids,
    gain_attn,
    a_weight,
    b_weight,
    out_weight,
    gain_ffn,
    gate_weight,
    up_weight,
    down_weight,
    cotangent,
):
    rows_dev, length = doc_ids.shape
    total_rows = rows_dev * length
    own_rows = tokens.shape[0]
    local_heads = out_weight.shape[0] // DH
    rank_all = RQ + 2 * RK
    x_own = tokens.astype(jnp.float32)
    inv_one = lax.rsqrt(jnp.mean(x_own * x_own, axis=-1, keepdims=True) + EPSILON)
    normed_one = (x_own * inv_one * gain_attn).astype(jnp.bfloat16)
    normed_all, grad_out_all = (
        lax.all_gather(normed_one, "head", axis=0, tiled=True),
        lax.all_gather(cotangent, "head", axis=0, tiled=True),
    )
    factor_a = jnp.dot(normed_all, a_weight, preferred_element_type=jnp.float32).reshape(
        total_rows, local_heads, rank_all
    )
    factor_b = jnp.dot(normed_all, b_weight, preferred_element_type=jnp.float32)
    cosine, sine = rope_tables(total_rows, length)
    basis_query = rotate(factor_b[:, : RQ * DH].reshape(total_rows, RQ, DH), cosine, sine)
    basis_key = rotate(
        factor_b[:, RQ * DH : (RQ + RK) * DH].reshape(total_rows, RK, DH), cosine, sine
    )
    basis_value = factor_b[:, (RQ + RK) * DH :].reshape(total_rows, RK, DH)
    coef_query = factor_a[:, :, :RQ]
    coef_key = factor_a[:, :, RQ : RQ + RK]
    coef_value = factor_a[:, :, RQ + RK :]
    queries = (jnp.einsum("thr,trd->thd", coef_query, basis_query, precision=PRECISE) / RQ).astype(
        jnp.bfloat16
    )
    key_rows = (jnp.einsum("thr,trd->thd", coef_key, basis_key, precision=PRECISE) / RK).astype(
        jnp.bfloat16
    )
    value_rows = (
        jnp.einsum("thr,trd->thd", coef_value, basis_value, precision=PRECISE) / RK
    ).astype(jnp.bfloat16)
    row_shape = (rows_dev, length, local_heads, DH)
    query_rows = queries.reshape(row_shape)
    keys_rows = key_rows.reshape(row_shape)
    values_rows = value_rows.reshape(row_shape)
    mixed_rows, log_total = lax.map(attend_row, (query_rows, keys_rows, values_rows, doc_ids))
    mixed = mixed_rows.reshape(total_rows, local_heads * DH)
    piece = lax.slice_in_dim(mixed, 0, lax.axis_size("head") * own_rows, axis=0)
    resid_own = x_own + lax.psum_scatter(
        jnp.dot(piece, out_weight, preferred_element_type=jnp.float32),
        "head",
        scatter_dimension=0,
        tiled=True,
    )
    inv_two = lax.rsqrt(jnp.mean(resid_own * resid_own, axis=-1, keepdims=True) + EPSILON)
    normed_two = (resid_own * inv_two * gain_ffn).astype(jnp.bfloat16)
    normed_two_all = lax.all_gather(normed_two, "head", axis=0, tiled=True)
    gate_act = jnp.dot(normed_two_all, gate_weight, preferred_element_type=jnp.float32)
    up_act = jnp.dot(normed_two_all, up_weight, preferred_element_type=jnp.float32)
    sigmoid_gate = jax.nn.sigmoid(gate_act)
    silu_gate = sigmoid_gate * gate_act
    hidden = (silu_gate * up_act).astype(jnp.bfloat16)
    piece = lax.slice_in_dim(hidden, 0, lax.axis_size("head") * own_rows, axis=0)
    output = (
        resid_own
        + lax.psum_scatter(
            jnp.dot(piece, down_weight, preferred_element_type=jnp.float32).astype(jnp.bfloat16),
            "head",
            scatter_dimension=0,
            tiled=True,
        ).astype(jnp.float32)
    ).astype(jnp.bfloat16)
    grad_down = dot_first(hidden, grad_out_all)
    grad_hidden = dot_last(grad_out_all, down_weight)
    grad_gate_act = (
        grad_hidden * up_act * (sigmoid_gate * (1.0 + gate_act * (1.0 - sigmoid_gate)))
    ).astype(jnp.bfloat16)
    grad_up_act = (grad_hidden * silu_gate).astype(jnp.bfloat16)
    grad_gate = dot_first(normed_two_all, grad_gate_act)
    grad_up = dot_first(normed_two_all, grad_up_act)
    gate_piece = lax.slice_in_dim(grad_gate_act, 0, lax.axis_size("head") * own_rows, axis=0)
    up_piece = lax.slice_in_dim(grad_up_act, 0, lax.axis_size("head") * own_rows, axis=0)
    grad_normed_two = lax.psum_scatter(
        dot_last(gate_piece, gate_weight) + dot_last(up_piece, up_weight),
        "head",
        scatter_dimension=0,
        tiled=True,
    )
    resid_part, grad_gain_ffn_own = norm_backward(resid_own, inv_two, gain_ffn, grad_normed_two)
    grad_resid = cotangent.astype(jnp.float32) + resid_part
    grad_branch = lax.all_gather(grad_resid.astype(jnp.bfloat16), "head", axis=0, tiled=True)
    grad_mixed = dot_last(grad_branch, out_weight).astype(jnp.bfloat16)
    grad_out = dot_first(mixed, grad_branch)
    grad_query_rows, grad_key_rows, grad_value_rows = lax.map(
        attend_back,
        (query_rows, keys_rows, values_rows, doc_ids, log_total, grad_mixed.reshape(row_shape)),
    )
    head_shape = (total_rows, local_heads, DH)
    grad_query = rounded(grad_query_rows.reshape(head_shape))
    grad_key = rounded(grad_key_rows.reshape(head_shape))
    grad_value = rounded(grad_value_rows.reshape(head_shape))
    grad_coef_query = jnp.einsum("thd,trd->thr", grad_query, basis_query, precision=PRECISE) / RQ
    grad_coef_key = jnp.einsum("thd,trd->thr", grad_key, basis_key, precision=PRECISE) / RK
    grad_coef_value = jnp.einsum("thd,trd->thr", grad_value, basis_value, precision=PRECISE) / RK
    grad_basis_query = unrotate(
        jnp.einsum("thr,thd->trd", coef_query, grad_query, precision=PRECISE) / RQ, cosine, sine
    )
    grad_basis_key = unrotate(
        jnp.einsum("thr,thd->trd", coef_key, grad_key, precision=PRECISE) / RK, cosine, sine
    )
    grad_basis_value = jnp.einsum("thr,thd->trd", coef_value, grad_value, precision=PRECISE) / RK
    grad_factor_a = (
        jnp.concatenate([grad_coef_query, grad_coef_key, grad_coef_value], axis=-1)
        .reshape(total_rows, local_heads * rank_all)
        .astype(jnp.bfloat16)
    )
    grad_factor_b = jnp.concatenate(
        [
            grad_basis_query.reshape(total_rows, RQ * DH),
            grad_basis_key.reshape(total_rows, RK * DH),
            grad_basis_value.reshape(total_rows, RK * DH),
        ],
        axis=-1,
    )
    head_count = lax.axis_size("head")
    basis_cols = grad_factor_b.shape[1] // head_count
    factor_cols = lax.psum_scatter(
        grad_factor_b.astype(jnp.bfloat16), "head", scatter_dimension=1, tiled=True
    )
    weight_cols = lax.dynamic_slice_in_dim(
        b_weight, lax.axis_index("head") * basis_cols, basis_cols, axis=1
    )
    piece = grad_factor_a
    grad_normed_one = lax.psum_scatter(
        (dot_last(piece, a_weight) + dot_last(factor_cols, weight_cols)).astype(jnp.bfloat16),
        "head",
        scatter_dimension=0,
        tiled=True,
    ).astype(jnp.float32)
    input_part, grad_gain_attn_own = norm_backward(x_own, inv_one, gain_attn, grad_normed_one)
    input_grad = grad_resid + input_part
    grad_a = dot_first(normed_all, grad_factor_a)
    grad_b_cols = dot_first(normed_all, factor_cols)

    def dp_sum(values):
        return lax.all_gather(
            lax.psum_scatter(values.astype(jnp.bfloat16), "dp", scatter_dimension=1, tiled=True),
            "dp",
            axis=1,
            tiled=True,
        ).astype(jnp.float32)

    grad_gate, grad_up, grad_down = dp_sum(grad_gate), dp_sum(grad_up), dp_sum(grad_down)
    grad_out = lax.psum(grad_out.astype(jnp.bfloat16), "dp").astype(jnp.float32)
    features = grad_gain_attn_own.shape[0]
    gain_rows = -(-2 * features // basis_cols)
    gains = jnp.pad(
        jnp.concatenate([grad_gain_attn_own, grad_gain_ffn_own]),
        (0, gain_rows * basis_cols - 2 * features),
    ).reshape(gain_rows, basis_cols)
    grad_a, packed = lax.psum(
        (grad_a.astype(jnp.bfloat16), jnp.concatenate([grad_b_cols, gains], axis=0)), "dp"
    )
    grad_a = grad_a.astype(jnp.float32)
    packed = lax.all_gather(packed, "head", axis=1, tiled=True)
    grad_b = packed[: grad_b_cols.shape[0]]
    gains = jnp.sum(
        packed[grad_b_cols.shape[0] :].reshape(gain_rows, head_count, basis_cols), axis=1
    ).reshape(-1)
    grad_gain_attn, grad_gain_ffn = gains[:features], gains[features : 2 * features]
    return (
        output,
        input_grad,
        grad_gain_attn,
        grad_a,
        grad_b,
        grad_out,
        grad_gain_ffn,
        grad_gate,
        grad_up,
        grad_down,
    )


def solution(mesh):
    return jax.shard_map(
        local,
        mesh=mesh,
        in_specs=(
            P(("dp", "head"), None),
            P("dp", None),
            P(),
            P(None, "head"),
            P(),
            P("head", None),
            P(),
            P(None, "head"),
            P(None, "head"),
            P("head", None),
            P(("dp", "head"), None),
        ),
        out_specs=(
            P(("dp", "head"), None),
            P(("dp", "head"), None),
            P(),
            P(None, "head"),
            P(),
            P("head", None),
            P(),
            P(None, "head"),
            P(None, "head"),
            P("head", None),
        ),
        check_vma=False,
    )
```

```python
import math

import jax
import jax.numpy as jnp
from jax import lax
from jax.sharding import PartitionSpec as P

DH = 64
RQ = 6
RK = 2


EPSILON = 1e-06
MASKED = -1e30
PRECISE = lax.Precision.HIGHEST


def rope_tables(total_rows, length):
    half_depth = DH // 2
    position = (jnp.arange(total_rows, dtype=jnp.int32) % length).astype(jnp.float32)
    frequency = jnp.exp(jnp.arange(half_depth, dtype=jnp.float32) * (-2.0 * math.log(10000.0) / DH))
    angle = position[:, None] * frequency[None, :]
    return (jnp.cos(angle), jnp.sin(angle))


def rotate(basis, cosine, sine):
    half_depth = basis.shape[-1] // 2
    first_half = basis[..., :half_depth]
    second_half = basis[..., half_depth:]
    cosine_row = cosine[:, None, :]
    sine_row = sine[:, None, :]
    return jnp.concatenate(
        [
            first_half * cosine_row - second_half * sine_row,
            second_half * cosine_row + first_half * sine_row,
        ],
        axis=-1,
    )


def unrotate(grad_basis, cosine, sine):
    half_depth = grad_basis.shape[-1] // 2
    first_half = grad_basis[..., :half_depth]
    second_half = grad_basis[..., half_depth:]
    cosine_row = cosine[:, None, :]
    sine_row = sine[:, None, :]
    return jnp.concatenate(
        [
            first_half * cosine_row + second_half * sine_row,
            second_half * cosine_row - first_half * sine_row,
        ],
        axis=-1,
    )


def dot_last(left, right):
    return lax.dot_general(
        left, right, (((1,), (1,)), ((), ())), preferred_element_type=jnp.float32
    )


def dot_first(left, right):
    return lax.dot_general(
        left, right, (((0,), (0,)), ((), ())), preferred_element_type=jnp.float32
    )


def norm_backward(inputs, inverse, gain, grad_normed):
    scaled = gain * grad_normed
    inner = jnp.mean(scaled * inputs, axis=-1, keepdims=True)
    grad_inputs = inverse * scaled - inputs * (inverse * inverse * inverse) * inner
    grad_gain = jnp.sum(grad_normed * inputs * inverse, axis=0)
    return (grad_inputs, grad_gain)


def block_scores(queries, key_rows, doc_row, first_row, last_row):
    position = jnp.arange(last_row, dtype=jnp.int32)
    allowed = (doc_row[first_row:last_row, None] == doc_row[None, :last_row]) & (
        position[None, :] <= position[first_row:last_row, None]
    )
    score_scale = 1.0 / math.sqrt(queries.shape[2])
    scores = (
        jnp.einsum(
            "qhd,khd->hqk",
            queries[first_row:last_row],
            key_rows[:last_row],
            preferred_element_type=jnp.float32,
        )
        * score_scale
    )
    return jnp.where(allowed[None], scores, MASKED)


def attend_row(row_item):
    queries, key_rows, value_rows, doc_row = row_item
    length = queries.shape[0]
    block_rows = min(512, length)
    mixed_parts = []
    total_parts = []
    for first_row in range(0, length, block_rows):
        last_row = first_row + block_rows
        scores = block_scores(queries, key_rows, doc_row, first_row, last_row)
        row_peak = jnp.max(scores, axis=-1, keepdims=True)
        exponent = jnp.exp(scores - row_peak)
        row_total = jnp.sum(exponent, axis=-1, keepdims=True)
        weights = (exponent / row_total).astype(jnp.bfloat16)
        mixed_parts.append(
            jnp.einsum(
                "hqk,khd->qhd", weights, value_rows[:last_row], preferred_element_type=jnp.float32
            ).astype(jnp.bfloat16)
        )
        total_parts.append(row_peak[..., 0] + jnp.log(row_total[..., 0]))
    return (jnp.concatenate(mixed_parts, axis=0), jnp.concatenate(total_parts, axis=1))


def attend_back(row_item):
    queries, key_rows, value_rows, doc_row, log_total, grad_mixed = row_item
    length = queries.shape[0]
    block_rows = min(512, length)
    score_scale = 1.0 / math.sqrt(queries.shape[2])
    grad_query_parts = []
    grad_keys = jnp.zeros(key_rows.shape, jnp.float32)
    grad_values = jnp.zeros(value_rows.shape, jnp.float32)
    for first_row in range(0, length, block_rows):
        last_row = first_row + block_rows
        scores = block_scores(queries, key_rows, doc_row, first_row, last_row)
        weights = jnp.exp(scores - log_total[:, first_row:last_row, None])
        grad_weights = jnp.einsum(
            "qhd,khd->hqk",
            grad_mixed[first_row:last_row],
            value_rows[:last_row],
            preferred_element_type=jnp.float32,
        )
        inner = jnp.sum(weights * grad_weights, axis=-1, keepdims=True)
        grad_scores = (weights * (grad_weights - inner)).astype(jnp.bfloat16)
        grad_query_parts.append(
            jnp.einsum(
                "hqk,khd->qhd", grad_scores, key_rows[:last_row], preferred_element_type=jnp.float32
            )
            * score_scale
        )
        padding = ((0, length - last_row), (0, 0), (0, 0))
        key_part = (
            jnp.einsum(
                "hqk,qhd->khd",
                grad_scores,
                queries[first_row:last_row],
                preferred_element_type=jnp.float32,
            )
            * score_scale
        )
        value_part = jnp.einsum(
            "hqk,qhd->khd",
            weights.astype(jnp.bfloat16),
            grad_mixed[first_row:last_row],
            preferred_element_type=jnp.float32,
        )
        grad_keys = grad_keys + jnp.pad(key_part, padding)
        grad_values = grad_values + jnp.pad(value_part, padding)
    return (jnp.concatenate(grad_query_parts, axis=0), grad_keys, grad_values)


def rounded(values_in):
    return lax.optimization_barrier(values_in.astype(jnp.bfloat16)).astype(jnp.float32)


def local(
    tokens,
    doc_ids,
    gain_attn,
    a_weight,
    b_weight,
    out_weight,
    gain_ffn,
    gate_weight,
    up_weight,
    down_weight,
    cotangent,
):
    rows_dev, length = doc_ids.shape
    total_rows = rows_dev * length
    own_rows = tokens.shape[0]
    local_heads = out_weight.shape[0] // DH
    rank_all = RQ + 2 * RK
    x_own = tokens.astype(jnp.float32)
    inv_one = lax.rsqrt(jnp.mean(x_own * x_own, axis=-1, keepdims=True) + EPSILON)
    normed_one = (x_own * inv_one * gain_attn).astype(jnp.bfloat16)
    normed_all, grad_out_all = (
        lax.all_gather(normed_one, "head", axis=0, tiled=True),
        lax.all_gather(cotangent, "head", axis=0, tiled=True),
    )
    factor_a = jnp.dot(normed_all, a_weight, preferred_element_type=jnp.float32).reshape(
        total_rows, local_heads, rank_all
    )
    factor_b = jnp.dot(normed_all, b_weight, preferred_element_type=jnp.float32)
    cosine, sine = rope_tables(total_rows, length)
    basis_query = rotate(factor_b[:, : RQ * DH].reshape(total_rows, RQ, DH), cosine, sine)
    basis_key = rotate(
        factor_b[:, RQ * DH : (RQ + RK) * DH].reshape(total_rows, RK, DH), cosine, sine
    )
    basis_value = factor_b[:, (RQ + RK) * DH :].reshape(total_rows, RK, DH)
    coef_query = factor_a[:, :, :RQ]
    coef_key = factor_a[:, :, RQ : RQ + RK]
    coef_value = factor_a[:, :, RQ + RK :]
    queries = (jnp.einsum("thr,trd->thd", coef_query, basis_query, precision=PRECISE) / RQ).astype(
        jnp.bfloat16
    )
    key_rows = (jnp.einsum("thr,trd->thd", coef_key, basis_key, precision=PRECISE) / RK).astype(
        jnp.bfloat16
    )
    value_rows = (
        jnp.einsum("thr,trd->thd", coef_value, basis_value, precision=PRECISE) / RK
    ).astype(jnp.bfloat16)
    row_shape = (rows_dev, length, local_heads, DH)
    query_rows = queries.reshape(row_shape)
    keys_rows = key_rows.reshape(row_shape)
    values_rows = value_rows.reshape(row_shape)
    mixed_rows, log_total = lax.map(attend_row, (query_rows, keys_rows, values_rows, doc_ids))
    mixed = mixed_rows.reshape(total_rows, local_heads * DH)
    piece = lax.slice_in_dim(mixed, 0, lax.axis_size("head") * own_rows, axis=0)
    resid_own = x_own + lax.psum_scatter(
        jnp.dot(piece, out_weight, preferred_element_type=jnp.float32),
        "head",
        scatter_dimension=0,
        tiled=True,
    )
    inv_two = lax.rsqrt(jnp.mean(resid_own * resid_own, axis=-1, keepdims=True) + EPSILON)
    normed_two = (resid_own * inv_two * gain_ffn).astype(jnp.bfloat16)
    normed_two_all = lax.all_gather(normed_two, "head", axis=0, tiled=True)
    gate_act = jnp.dot(normed_two_all, gate_weight, preferred_element_type=jnp.float32)
    up_act = jnp.dot(normed_two_all, up_weight, preferred_element_type=jnp.float32)
    sigmoid_gate = jax.nn.sigmoid(gate_act)
    silu_gate = sigmoid_gate * gate_act
    hidden = (silu_gate * up_act).astype(jnp.bfloat16)
    piece = lax.slice_in_dim(hidden, 0, lax.axis_size("head") * own_rows, axis=0)
    output = (
        resid_own
        + lax.psum_scatter(
            jnp.dot(piece, down_weight, preferred_element_type=jnp.float32).astype(jnp.bfloat16),
            "head",
            scatter_dimension=0,
            tiled=True,
        ).astype(jnp.float32)
    ).astype(jnp.bfloat16)
    grad_down = dot_first(hidden, grad_out_all)
    grad_hidden = dot_last(grad_out_all, down_weight)
    grad_gate_act = (
        grad_hidden * up_act * (sigmoid_gate * (1.0 + gate_act * (1.0 - sigmoid_gate)))
    ).astype(jnp.bfloat16)
    grad_up_act = (grad_hidden * silu_gate).astype(jnp.bfloat16)
    grad_gate = dot_first(normed_two_all, grad_gate_act)
    grad_up = dot_first(normed_two_all, grad_up_act)
    gate_piece = lax.slice_in_dim(grad_gate_act, 0, lax.axis_size("head") * own_rows, axis=0)
    up_piece = lax.slice_in_dim(grad_up_act, 0, lax.axis_size("head") * own_rows, axis=0)
    grad_normed_two = lax.psum_scatter(
        dot_last(gate_piece, gate_weight) + dot_last(up_piece, up_weight),
        "head",
        scatter_dimension=0,
        tiled=True,
    )
    resid_part, grad_gain_ffn_own = norm_backward(resid_own, inv_two, gain_ffn, grad_normed_two)
    grad_resid = cotangent.astype(jnp.float32) + resid_part
    grad_branch = lax.all_gather(grad_resid.astype(jnp.bfloat16), "head", axis=0, tiled=True)
    grad_mixed = dot_last(grad_branch, out_weight).astype(jnp.bfloat16)
    grad_out = dot_first(mixed, grad_branch)
    grad_query_rows, grad_key_rows, grad_value_rows = lax.map(
        attend_back,
        (query_rows, keys_rows, values_rows, doc_ids, log_total, grad_mixed.reshape(row_shape)),
    )
    head_shape = (total_rows, local_heads, DH)
    grad_query = rounded(grad_query_rows.reshape(head_shape))
    grad_key = rounded(grad_key_rows.reshape(head_shape))
    grad_value = rounded(grad_value_rows.reshape(head_shape))
    grad_coef_query = jnp.einsum("thd,trd->thr", grad_query, basis_query, precision=PRECISE) / RQ
    grad_coef_key = jnp.einsum("thd,trd->thr", grad_key, basis_key, precision=PRECISE) / RK
    grad_coef_value = jnp.einsum("thd,trd->thr", grad_value, basis_value, precision=PRECISE) / RK
    grad_basis_query = unrotate(
        jnp.einsum("thr,thd->trd", coef_query, grad_query, precision=PRECISE) / RQ, cosine, sine
    )
    grad_basis_key = unrotate(
        jnp.einsum("thr,thd->trd", coef_key, grad_key, precision=PRECISE) / RK, cosine, sine
    )
    grad_basis_value = jnp.einsum("thr,thd->trd", coef_value, grad_value, precision=PRECISE) / RK
    grad_factor_a = (
        jnp.concatenate([grad_coef_query, grad_coef_key, grad_coef_value], axis=-1)
        .reshape(total_rows, local_heads * rank_all)
        .astype(jnp.bfloat16)
    )
    grad_factor_b = jnp.concatenate(
        [
            grad_basis_query.reshape(total_rows, RQ * DH),
            grad_basis_key.reshape(total_rows, RK * DH),
            grad_basis_value.reshape(total_rows, RK * DH),
        ],
        axis=-1,
    )
    head_count = lax.axis_size("head")
    basis_cols = grad_factor_b.shape[1] // head_count
    factor_cols = lax.psum_scatter(
        grad_factor_b.astype(jnp.bfloat16), "head", scatter_dimension=1, tiled=True
    )
    weight_cols = lax.dynamic_slice_in_dim(
        b_weight, lax.axis_index("head") * basis_cols, basis_cols, axis=1
    )
    piece = grad_factor_a
    grad_normed_one = lax.psum_scatter(
        (dot_last(piece, a_weight) + dot_last(factor_cols, weight_cols)).astype(jnp.bfloat16),
        "head",
        scatter_dimension=0,
        tiled=True,
    ).astype(jnp.float32)
    input_part, grad_gain_attn_own = norm_backward(x_own, inv_one, gain_attn, grad_normed_one)
    input_grad = grad_resid + input_part
    grad_a = dot_first(normed_all, grad_factor_a)
    grad_b_cols = dot_first(normed_all, factor_cols)

    features = grad_gain_attn_own.shape[0]
    gain_rows = -(-2 * features // basis_cols)
    gains = jnp.pad(
        jnp.concatenate([grad_gain_attn_own, grad_gain_ffn_own]),
        (0, gain_rows * basis_cols - 2 * features),
    ).reshape(gain_rows, basis_cols)
    grad_a, grad_out, grad_gate, grad_up, grad_down, packed = lax.psum(
        (
            grad_a.astype(jnp.bfloat16),
            grad_out.astype(jnp.bfloat16),
            grad_gate.astype(jnp.bfloat16),
            grad_up.astype(jnp.bfloat16),
            grad_down.astype(jnp.bfloat16),
            jnp.concatenate([grad_b_cols, gains], axis=0).astype(jnp.bfloat16),
        ),
        "dp",
    )
    grad_out, grad_gate, grad_up, grad_down = (
        grad_out.astype(jnp.float32),
        grad_gate.astype(jnp.float32),
        grad_up.astype(jnp.float32),
        grad_down.astype(jnp.float32),
    )
    grad_a = grad_a.astype(jnp.float32)
    packed = lax.all_gather(packed, "head", axis=1, tiled=True).astype(jnp.float32)
    grad_b = packed[: grad_b_cols.shape[0]]
    gains = jnp.sum(
        packed[grad_b_cols.shape[0] :].reshape(gain_rows, head_count, basis_cols), axis=1
    ).reshape(-1)
    grad_gain_attn, grad_gain_ffn = gains[:features], gains[features : 2 * features]
    return (
        output,
        input_grad,
        grad_gain_attn,
        grad_a,
        grad_b,
        grad_out,
        grad_gain_ffn,
        grad_gate,
        grad_up,
        grad_down,
    )


def solution(mesh):
    return jax.shard_map(
        local,
        mesh=mesh,
        in_specs=(
            P(("dp", "head"), None),
            P("dp", None),
            P(),
            P(None, "head"),
            P(),
            P("head", None),
            P(),
            P(None, "head"),
            P(None, "head"),
            P("head", None),
            P(("dp", "head"), None),
        ),
        out_specs=(
            P(("dp", "head"), None),
            P(("dp", "head"), None),
            P(),
            P(None, "head"),
            P(),
            P("head", None),
            P(),
            P(None, "head"),
            P(None, "head"),
            P("head", None),
        ),
        check_vma=False,
    )
```

```python
import math

import jax
import jax.numpy as jnp
from jax import lax
from jax.sharding import PartitionSpec as P

DH = 64
RQ = 6
RK = 2


EPSILON = 1e-06
MASKED = -1e30
PRECISE = lax.Precision.HIGHEST


def rope_tables(total_rows, length):
    half_depth = DH // 2
    position = (jnp.arange(total_rows, dtype=jnp.int32) % length).astype(jnp.float32)
    frequency = jnp.exp(jnp.arange(half_depth, dtype=jnp.float32) * (-2.0 * math.log(10000.0) / DH))
    angle = position[:, None] * frequency[None, :]
    return (jnp.cos(angle), jnp.sin(angle))


def rotate(basis, cosine, sine):
    half_depth = basis.shape[-1] // 2
    first_half = basis[..., :half_depth]
    second_half = basis[..., half_depth:]
    cosine_row = cosine[:, None, :]
    sine_row = sine[:, None, :]
    return jnp.concatenate(
        [
            first_half * cosine_row - second_half * sine_row,
            second_half * cosine_row + first_half * sine_row,
        ],
        axis=-1,
    )


def unrotate(grad_basis, cosine, sine):
    half_depth = grad_basis.shape[-1] // 2
    first_half = grad_basis[..., :half_depth]
    second_half = grad_basis[..., half_depth:]
    cosine_row = cosine[:, None, :]
    sine_row = sine[:, None, :]
    return jnp.concatenate(
        [
            first_half * cosine_row + second_half * sine_row,
            second_half * cosine_row - first_half * sine_row,
        ],
        axis=-1,
    )


def dot_last(left, right):
    return lax.dot_general(
        left, right, (((1,), (1,)), ((), ())), preferred_element_type=jnp.float32
    )


def dot_first(left, right):
    return lax.dot_general(
        left, right, (((0,), (0,)), ((), ())), preferred_element_type=jnp.float32
    )


def norm_backward(inputs, inverse, gain, grad_normed):
    scaled = gain * grad_normed
    inner = jnp.mean(scaled * inputs, axis=-1, keepdims=True)
    grad_inputs = inverse * scaled - inputs * (inverse * inverse * inverse) * inner
    grad_gain = jnp.sum(grad_normed * inputs * inverse, axis=0)
    return (grad_inputs, grad_gain)


def block_scores(queries, key_rows, doc_row, first_row, last_row):
    position = jnp.arange(last_row, dtype=jnp.int32)
    allowed = (doc_row[first_row:last_row, None] == doc_row[None, :last_row]) & (
        position[None, :] <= position[first_row:last_row, None]
    )
    score_scale = 1.0 / math.sqrt(queries.shape[2])
    scores = (
        jnp.einsum(
            "qhd,khd->hqk",
            queries[first_row:last_row],
            key_rows[:last_row],
            preferred_element_type=jnp.float32,
        )
        * score_scale
    )
    return jnp.where(allowed[None], scores, MASKED)


def attend_row(row_item):
    queries, key_rows, value_rows, doc_row = row_item
    length = queries.shape[0]
    block_rows = min(512, length)
    mixed_parts = []
    total_parts = []
    for first_row in range(0, length, block_rows):
        last_row = first_row + block_rows
        scores = block_scores(queries, key_rows, doc_row, first_row, last_row)
        row_peak = jnp.max(scores, axis=-1, keepdims=True)
        exponent = jnp.exp(scores - row_peak)
        row_total = jnp.sum(exponent, axis=-1, keepdims=True)
        weights = (exponent / row_total).astype(jnp.bfloat16)
        mixed_parts.append(
            jnp.einsum(
                "hqk,khd->qhd", weights, value_rows[:last_row], preferred_element_type=jnp.float32
            ).astype(jnp.bfloat16)
        )
        total_parts.append(row_peak[..., 0] + jnp.log(row_total[..., 0]))
    return (jnp.concatenate(mixed_parts, axis=0), jnp.concatenate(total_parts, axis=1))


def attend_back(row_item):
    queries, key_rows, value_rows, doc_row, log_total, grad_mixed = row_item
    length = queries.shape[0]
    block_rows = min(512, length)
    score_scale = 1.0 / math.sqrt(queries.shape[2])
    grad_query_parts = []
    grad_keys = jnp.zeros(key_rows.shape, jnp.float32)
    grad_values = jnp.zeros(value_rows.shape, jnp.float32)
    for first_row in range(0, length, block_rows):
        last_row = first_row + block_rows
        scores = block_scores(queries, key_rows, doc_row, first_row, last_row)
        weights = jnp.exp(scores - log_total[:, first_row:last_row, None])
        grad_weights = jnp.einsum(
            "qhd,khd->hqk",
            grad_mixed[first_row:last_row],
            value_rows[:last_row],
            preferred_element_type=jnp.float32,
        )
        inner = jnp.sum(weights * grad_weights, axis=-1, keepdims=True)
        grad_scores = (weights * (grad_weights - inner)).astype(jnp.bfloat16)
        grad_query_parts.append(
            jnp.einsum(
                "hqk,khd->qhd", grad_scores, key_rows[:last_row], preferred_element_type=jnp.float32
            )
            * score_scale
        )
        padding = ((0, length - last_row), (0, 0), (0, 0))
        key_part = (
            jnp.einsum(
                "hqk,qhd->khd",
                grad_scores,
                queries[first_row:last_row],
                preferred_element_type=jnp.float32,
            )
            * score_scale
        )
        value_part = jnp.einsum(
            "hqk,qhd->khd",
            weights.astype(jnp.bfloat16),
            grad_mixed[first_row:last_row],
            preferred_element_type=jnp.float32,
        )
        grad_keys = grad_keys + jnp.pad(key_part, padding)
        grad_values = grad_values + jnp.pad(value_part, padding)
    return (jnp.concatenate(grad_query_parts, axis=0), grad_keys, grad_values)


def rounded(values_in):
    return lax.optimization_barrier(values_in.astype(jnp.bfloat16)).astype(jnp.float32)


def local(
    tokens,
    doc_ids,
    gain_attn,
    a_weight,
    b_weight,
    out_weight,
    gain_ffn,
    gate_weight,
    up_weight,
    down_weight,
    cotangent,
):
    rows_dev, length = doc_ids.shape
    total_rows = rows_dev * length
    own_rows = tokens.shape[0]
    local_heads = out_weight.shape[0] // DH
    rank_all = RQ + 2 * RK
    x_own = tokens.astype(jnp.float32)
    inv_one = lax.rsqrt(jnp.mean(x_own * x_own, axis=-1, keepdims=True) + EPSILON)
    normed_one = (x_own * inv_one * gain_attn).astype(jnp.bfloat16)
    normed_all, grad_out_all = (
        lax.all_gather(normed_one, "head", axis=0, tiled=True),
        lax.all_gather(cotangent, "head", axis=0, tiled=True),
    )
    factor_a = jnp.dot(normed_all, a_weight, preferred_element_type=jnp.float32).reshape(
        total_rows, local_heads, rank_all
    )
    factor_b = jnp.dot(normed_all, b_weight, preferred_element_type=jnp.float32)
    cosine, sine = rope_tables(total_rows, length)
    basis_query = rotate(factor_b[:, : RQ * DH].reshape(total_rows, RQ, DH), cosine, sine)
    basis_key = rotate(
        factor_b[:, RQ * DH : (RQ + RK) * DH].reshape(total_rows, RK, DH), cosine, sine
    )
    basis_value = factor_b[:, (RQ + RK) * DH :].reshape(total_rows, RK, DH)
    coef_query = factor_a[:, :, :RQ]
    coef_key = factor_a[:, :, RQ : RQ + RK]
    coef_value = factor_a[:, :, RQ + RK :]
    queries = (jnp.einsum("thr,trd->thd", coef_query, basis_query, precision=PRECISE) / RQ).astype(
        jnp.bfloat16
    )
    key_rows = (jnp.einsum("thr,trd->thd", coef_key, basis_key, precision=PRECISE) / RK).astype(
        jnp.bfloat16
    )
    value_rows = (
        jnp.einsum("thr,trd->thd", coef_value, basis_value, precision=PRECISE) / RK
    ).astype(jnp.bfloat16)
    row_shape = (rows_dev, length, local_heads, DH)
    query_rows = queries.reshape(row_shape)
    keys_rows = key_rows.reshape(row_shape)
    values_rows = value_rows.reshape(row_shape)
    mixed_rows, log_total = lax.map(attend_row, (query_rows, keys_rows, values_rows, doc_ids))
    mixed = mixed_rows.reshape(total_rows, local_heads * DH)
    piece = lax.slice_in_dim(mixed, 0, lax.axis_size("head") * own_rows, axis=0)
    resid_own = x_own + lax.psum_scatter(
        jnp.dot(piece, out_weight, preferred_element_type=jnp.float32).astype(jnp.bfloat16),
        "head",
        scatter_dimension=0,
        tiled=True,
    ).astype(jnp.float32)
    inv_two = lax.rsqrt(jnp.mean(resid_own * resid_own, axis=-1, keepdims=True) + EPSILON)
    normed_two = (resid_own * inv_two * gain_ffn).astype(jnp.bfloat16)
    normed_two_all = lax.all_gather(normed_two, "head", axis=0, tiled=True)
    gate_act = jnp.dot(normed_two_all, gate_weight, preferred_element_type=jnp.float32)
    up_act = jnp.dot(normed_two_all, up_weight, preferred_element_type=jnp.float32)
    sigmoid_gate = jax.nn.sigmoid(gate_act)
    silu_gate = sigmoid_gate * gate_act
    hidden = (silu_gate * up_act).astype(jnp.bfloat16)
    piece = lax.slice_in_dim(hidden, 0, lax.axis_size("head") * own_rows, axis=0)
    output = (
        resid_own
        + lax.psum_scatter(
            jnp.dot(piece, down_weight, preferred_element_type=jnp.float32).astype(jnp.bfloat16),
            "head",
            scatter_dimension=0,
            tiled=True,
        ).astype(jnp.float32)
    ).astype(jnp.bfloat16)
    grad_down = dot_first(hidden, grad_out_all)
    grad_hidden = dot_last(grad_out_all, down_weight)
    grad_gate_act = (
        grad_hidden * up_act * (sigmoid_gate * (1.0 + gate_act * (1.0 - sigmoid_gate)))
    ).astype(jnp.bfloat16)
    grad_up_act = (grad_hidden * silu_gate).astype(jnp.bfloat16)
    grad_gate = dot_first(normed_two_all, grad_gate_act)
    grad_up = dot_first(normed_two_all, grad_up_act)
    gate_piece = lax.slice_in_dim(grad_gate_act, 0, lax.axis_size("head") * own_rows, axis=0)
    up_piece = lax.slice_in_dim(grad_up_act, 0, lax.axis_size("head") * own_rows, axis=0)
    grad_normed_two = lax.psum_scatter(
        (dot_last(gate_piece, gate_weight) + dot_last(up_piece, up_weight)).astype(jnp.bfloat16),
        "head",
        scatter_dimension=0,
        tiled=True,
    ).astype(jnp.float32)
    resid_part, grad_gain_ffn_own = norm_backward(resid_own, inv_two, gain_ffn, grad_normed_two)
    grad_resid = cotangent.astype(jnp.float32) + resid_part
    grad_branch = lax.all_gather(grad_resid.astype(jnp.bfloat16), "head", axis=0, tiled=True)
    grad_mixed = dot_last(grad_branch, out_weight).astype(jnp.bfloat16)
    grad_out = dot_first(mixed, grad_branch)
    grad_query_rows, grad_key_rows, grad_value_rows = lax.map(
        attend_back,
        (query_rows, keys_rows, values_rows, doc_ids, log_total, grad_mixed.reshape(row_shape)),
    )
    head_shape = (total_rows, local_heads, DH)
    grad_query = rounded(grad_query_rows.reshape(head_shape))
    grad_key = rounded(grad_key_rows.reshape(head_shape))
    grad_value = rounded(grad_value_rows.reshape(head_shape))
    grad_coef_query = jnp.einsum("thd,trd->thr", grad_query, basis_query, precision=PRECISE) / RQ
    grad_coef_key = jnp.einsum("thd,trd->thr", grad_key, basis_key, precision=PRECISE) / RK
    grad_coef_value = jnp.einsum("thd,trd->thr", grad_value, basis_value, precision=PRECISE) / RK
    grad_basis_query = unrotate(
        jnp.einsum("thr,thd->trd", coef_query, grad_query, precision=PRECISE) / RQ, cosine, sine
    )
    grad_basis_key = unrotate(
        jnp.einsum("thr,thd->trd", coef_key, grad_key, precision=PRECISE) / RK, cosine, sine
    )
    grad_basis_value = jnp.einsum("thr,thd->trd", coef_value, grad_value, precision=PRECISE) / RK
    grad_factor_a = (
        jnp.concatenate([grad_coef_query, grad_coef_key, grad_coef_value], axis=-1)
        .reshape(total_rows, local_heads * rank_all)
        .astype(jnp.bfloat16)
    )
    grad_factor_b = jnp.concatenate(
        [
            grad_basis_query.reshape(total_rows, RQ * DH),
            grad_basis_key.reshape(total_rows, RK * DH),
            grad_basis_value.reshape(total_rows, RK * DH),
        ],
        axis=-1,
    )
    head_count = lax.axis_size("head")
    basis_cols = grad_factor_b.shape[1] // head_count
    factor_cols = lax.psum_scatter(
        grad_factor_b.astype(jnp.bfloat16), "head", scatter_dimension=1, tiled=True
    )
    weight_cols = lax.dynamic_slice_in_dim(
        b_weight, lax.axis_index("head") * basis_cols, basis_cols, axis=1
    )
    piece = grad_factor_a
    grad_normed_one = lax.psum_scatter(
        (dot_last(piece, a_weight) + dot_last(factor_cols, weight_cols)).astype(jnp.bfloat16),
        "head",
        scatter_dimension=0,
        tiled=True,
    ).astype(jnp.float32)
    input_part, grad_gain_attn_own = norm_backward(x_own, inv_one, gain_attn, grad_normed_one)
    input_grad = grad_resid + input_part
    grad_a = dot_first(normed_all, grad_factor_a)
    grad_b_cols = dot_first(normed_all, factor_cols)

    features = grad_gain_attn_own.shape[0]
    gain_rows = -(-2 * features // basis_cols)
    gains = jnp.pad(
        jnp.concatenate([grad_gain_attn_own, grad_gain_ffn_own]),
        (0, gain_rows * basis_cols - 2 * features),
    ).reshape(gain_rows, basis_cols)
    grad_a, grad_out, grad_gate, grad_up, grad_down, packed = lax.psum(
        (
            grad_a.astype(jnp.bfloat16),
            grad_out.astype(jnp.bfloat16),
            grad_gate.astype(jnp.bfloat16),
            grad_up.astype(jnp.bfloat16),
            grad_down.astype(jnp.bfloat16),
            jnp.concatenate([grad_b_cols, gains], axis=0).astype(jnp.bfloat16),
        ),
        "dp",
    )
    grad_out, grad_gate, grad_up, grad_down = (
        grad_out.astype(jnp.float32),
        grad_gate.astype(jnp.float32),
        grad_up.astype(jnp.float32),
        grad_down.astype(jnp.float32),
    )
    grad_a = grad_a.astype(jnp.float32)
    packed = lax.all_gather(packed, "head", axis=1, tiled=True).astype(jnp.float32)
    grad_b = packed[: grad_b_cols.shape[0]]
    gains = jnp.sum(
        packed[grad_b_cols.shape[0] :].reshape(gain_rows, head_count, basis_cols), axis=1
    ).reshape(-1)
    grad_gain_attn, grad_gain_ffn = gains[:features], gains[features : 2 * features]
    return (
        output,
        input_grad,
        grad_gain_attn,
        grad_a,
        grad_b,
        grad_out,
        grad_gain_ffn,
        grad_gate,
        grad_up,
        grad_down,
    )


def solution(mesh):
    return jax.shard_map(
        local,
        mesh=mesh,
        in_specs=(
            P(("dp", "head"), None),
            P("dp", None),
            P(),
            P(None, "head"),
            P(),
            P("head", None),
            P(),
            P(None, "head"),
            P(None, "head"),
            P("head", None),
            P(("dp", "head"), None),
        ),
        out_specs=(
            P(("dp", "head"), None),
            P(("dp", "head"), None),
            P(),
            P(None, "head"),
            P(),
            P("head", None),
            P(),
            P(None, "head"),
            P(None, "head"),
            P("head", None),
        ),
        check_vma=False,
    )
```

```python
import math

import jax
import jax.numpy as jnp
from jax import lax
from jax.sharding import PartitionSpec as P

DH = 64
RQ = 6
RK = 2


EPSILON = 1e-06
MASKED = -1e30
PRECISE = lax.Precision.HIGHEST


def rope_tables(total_rows, length):
    half_depth = DH // 2
    position = (jnp.arange(total_rows, dtype=jnp.int32) % length).astype(jnp.float32)
    frequency = jnp.exp(jnp.arange(half_depth, dtype=jnp.float32) * (-2.0 * math.log(10000.0) / DH))
    angle = position[:, None] * frequency[None, :]
    return (jnp.cos(angle), jnp.sin(angle))


def rotate(basis, cosine, sine):
    half_depth = basis.shape[-1] // 2
    first_half = basis[..., :half_depth]
    second_half = basis[..., half_depth:]
    cosine_row = cosine[:, None, :]
    sine_row = sine[:, None, :]
    return jnp.concatenate(
        [
            first_half * cosine_row - second_half * sine_row,
            second_half * cosine_row + first_half * sine_row,
        ],
        axis=-1,
    )


def unrotate(grad_basis, cosine, sine):
    half_depth = grad_basis.shape[-1] // 2
    first_half = grad_basis[..., :half_depth]
    second_half = grad_basis[..., half_depth:]
    cosine_row = cosine[:, None, :]
    sine_row = sine[:, None, :]
    return jnp.concatenate(
        [
            first_half * cosine_row + second_half * sine_row,
            second_half * cosine_row - first_half * sine_row,
        ],
        axis=-1,
    )


def dot_last(left, right):
    return lax.dot_general(
        left, right, (((1,), (1,)), ((), ())), preferred_element_type=jnp.float32
    )


def dot_first(left, right):
    return lax.dot_general(
        left, right, (((0,), (0,)), ((), ())), preferred_element_type=jnp.float32
    )


def norm_backward(inputs, inverse, gain, grad_normed):
    scaled = gain * grad_normed
    inner = jnp.mean(scaled * inputs, axis=-1, keepdims=True)
    grad_inputs = inverse * scaled - inputs * (inverse * inverse * inverse) * inner
    grad_gain = jnp.sum(grad_normed * inputs * inverse, axis=0)
    return (grad_inputs, grad_gain)


def block_scores(queries, key_rows, doc_row, first_row, last_row):
    position = jnp.arange(last_row, dtype=jnp.int32)
    allowed = (doc_row[first_row:last_row, None] == doc_row[None, :last_row]) & (
        position[None, :] <= position[first_row:last_row, None]
    )
    score_scale = 1.0 / math.sqrt(queries.shape[2])
    scores = (
        jnp.einsum(
            "qhd,khd->hqk",
            queries[first_row:last_row],
            key_rows[:last_row],
            preferred_element_type=jnp.float32,
        )
        * score_scale
    )
    return jnp.where(allowed[None], scores, MASKED)


def attend_row(row_item):
    queries, key_rows, value_rows, doc_row = row_item
    length = queries.shape[0]
    block_rows = min(512, length)
    mixed_parts = []
    total_parts = []
    for first_row in range(0, length, block_rows):
        last_row = first_row + block_rows
        scores = block_scores(queries, key_rows, doc_row, first_row, last_row)
        row_peak = jnp.max(scores, axis=-1, keepdims=True)
        exponent = jnp.exp(scores - row_peak)
        row_total = jnp.sum(exponent, axis=-1, keepdims=True)
        weights = (exponent / row_total).astype(jnp.bfloat16)
        mixed_parts.append(
            jnp.einsum(
                "hqk,khd->qhd", weights, value_rows[:last_row], preferred_element_type=jnp.float32
            ).astype(jnp.bfloat16)
        )
        total_parts.append(row_peak[..., 0] + jnp.log(row_total[..., 0]))
    return (jnp.concatenate(mixed_parts, axis=0), jnp.concatenate(total_parts, axis=1))


def attend_back(row_item):
    queries, key_rows, value_rows, doc_row, log_total, grad_mixed = row_item
    length = queries.shape[0]
    block_rows = min(512, length)
    score_scale = 1.0 / math.sqrt(queries.shape[2])
    grad_query_parts = []
    grad_keys = jnp.zeros(key_rows.shape, jnp.float32)
    grad_values = jnp.zeros(value_rows.shape, jnp.float32)
    for first_row in range(0, length, block_rows):
        last_row = first_row + block_rows
        scores = block_scores(queries, key_rows, doc_row, first_row, last_row)
        weights = jnp.exp(scores - log_total[:, first_row:last_row, None])
        grad_weights = jnp.einsum(
            "qhd,khd->hqk",
            grad_mixed[first_row:last_row],
            value_rows[:last_row],
            preferred_element_type=jnp.float32,
        )
        inner = jnp.sum(weights * grad_weights, axis=-1, keepdims=True)
        grad_scores = (weights * (grad_weights - inner)).astype(jnp.bfloat16)
        grad_query_parts.append(
            jnp.einsum(
                "hqk,khd->qhd", grad_scores, key_rows[:last_row], preferred_element_type=jnp.float32
            )
            * score_scale
        )
        padding = ((0, length - last_row), (0, 0), (0, 0))
        key_part = (
            jnp.einsum(
                "hqk,qhd->khd",
                grad_scores,
                queries[first_row:last_row],
                preferred_element_type=jnp.float32,
            )
            * score_scale
        )
        value_part = jnp.einsum(
            "hqk,qhd->khd",
            weights.astype(jnp.bfloat16),
            grad_mixed[first_row:last_row],
            preferred_element_type=jnp.float32,
        )
        grad_keys = grad_keys + jnp.pad(key_part, padding)
        grad_values = grad_values + jnp.pad(value_part, padding)
    return (jnp.concatenate(grad_query_parts, axis=0), grad_keys, grad_values)


def rounded(values_in):
    return lax.optimization_barrier(values_in.astype(jnp.bfloat16)).astype(jnp.float32)


def head_reduce_scatter(values, axis):
    count = lax.axis_size("head")
    own = lax.axis_index("head")
    width = values.shape[axis] // count
    total = lax.dynamic_slice_in_dim(values, own * width, width, axis=axis).astype(jnp.float32)
    for shift in range(1, count):
        sent = lax.dynamic_slice_in_dim(values, ((own + shift) % count) * width, width, axis=axis)
        total = total + lax.ppermute(
            sent, "head", [(device, (device + shift) % count) for device in range(count)]
        ).astype(jnp.float32)
    return total


def local(
    tokens,
    doc_ids,
    gain_attn,
    a_weight,
    b_weight,
    out_weight,
    gain_ffn,
    gate_weight,
    up_weight,
    down_weight,
    cotangent,
):
    rows_dev, length = doc_ids.shape
    total_rows = rows_dev * length
    own_rows = tokens.shape[0]
    local_heads = out_weight.shape[0] // DH
    rank_all = RQ + 2 * RK
    x_own = tokens.astype(jnp.float32)
    inv_one = lax.rsqrt(jnp.mean(x_own * x_own, axis=-1, keepdims=True) + EPSILON)
    normed_one = (x_own * inv_one * gain_attn).astype(jnp.bfloat16)
    normed_all, grad_out_all = (
        lax.all_gather(normed_one, "head", axis=0, tiled=True),
        lax.all_gather(cotangent, "head", axis=0, tiled=True),
    )
    factor_a = jnp.dot(normed_all, a_weight, preferred_element_type=jnp.float32).reshape(
        total_rows, local_heads, rank_all
    )
    factor_b = jnp.dot(normed_all, b_weight, preferred_element_type=jnp.float32)
    cosine, sine = rope_tables(total_rows, length)
    basis_query = rotate(factor_b[:, : RQ * DH].reshape(total_rows, RQ, DH), cosine, sine)
    basis_key = rotate(
        factor_b[:, RQ * DH : (RQ + RK) * DH].reshape(total_rows, RK, DH), cosine, sine
    )
    basis_value = factor_b[:, (RQ + RK) * DH :].reshape(total_rows, RK, DH)
    coef_query = factor_a[:, :, :RQ]
    coef_key = factor_a[:, :, RQ : RQ + RK]
    coef_value = factor_a[:, :, RQ + RK :]
    queries = (jnp.einsum("thr,trd->thd", coef_query, basis_query, precision=PRECISE) / RQ).astype(
        jnp.bfloat16
    )
    key_rows = (jnp.einsum("thr,trd->thd", coef_key, basis_key, precision=PRECISE) / RK).astype(
        jnp.bfloat16
    )
    value_rows = (
        jnp.einsum("thr,trd->thd", coef_value, basis_value, precision=PRECISE) / RK
    ).astype(jnp.bfloat16)
    row_shape = (rows_dev, length, local_heads, DH)
    query_rows = queries.reshape(row_shape)
    keys_rows = key_rows.reshape(row_shape)
    values_rows = value_rows.reshape(row_shape)
    mixed_rows, log_total = lax.map(attend_row, (query_rows, keys_rows, values_rows, doc_ids))
    mixed = mixed_rows.reshape(total_rows, local_heads * DH)
    piece = lax.slice_in_dim(mixed, 0, lax.axis_size("head") * own_rows, axis=0)
    resid_own = x_own + lax.psum_scatter(
        jnp.dot(piece, out_weight, preferred_element_type=jnp.float32).astype(jnp.bfloat16),
        "head",
        scatter_dimension=0,
        tiled=True,
    ).astype(jnp.float32)
    inv_two = lax.rsqrt(jnp.mean(resid_own * resid_own, axis=-1, keepdims=True) + EPSILON)
    normed_two = (resid_own * inv_two * gain_ffn).astype(jnp.bfloat16)
    normed_two_all = lax.all_gather(normed_two, "head", axis=0, tiled=True)
    gate_act = jnp.dot(normed_two_all, gate_weight, preferred_element_type=jnp.float32)
    up_act = jnp.dot(normed_two_all, up_weight, preferred_element_type=jnp.float32)
    sigmoid_gate = jax.nn.sigmoid(gate_act)
    silu_gate = sigmoid_gate * gate_act
    hidden = (silu_gate * up_act).astype(jnp.bfloat16)
    piece = lax.slice_in_dim(hidden, 0, lax.axis_size("head") * own_rows, axis=0)
    output = (
        resid_own
        + lax.psum_scatter(
            jnp.dot(piece, down_weight, preferred_element_type=jnp.float32).astype(jnp.bfloat16),
            "head",
            scatter_dimension=0,
            tiled=True,
        ).astype(jnp.float32)
    ).astype(jnp.bfloat16)
    grad_down = dot_first(hidden, grad_out_all)
    grad_hidden = dot_last(grad_out_all, down_weight)
    grad_gate_act = (
        grad_hidden * up_act * (sigmoid_gate * (1.0 + gate_act * (1.0 - sigmoid_gate)))
    ).astype(jnp.bfloat16)
    grad_up_act = (grad_hidden * silu_gate).astype(jnp.bfloat16)
    grad_gate = dot_first(normed_two_all, grad_gate_act)
    grad_up = dot_first(normed_two_all, grad_up_act)
    gate_piece = lax.slice_in_dim(grad_gate_act, 0, lax.axis_size("head") * own_rows, axis=0)
    up_piece = lax.slice_in_dim(grad_up_act, 0, lax.axis_size("head") * own_rows, axis=0)
    grad_normed_two = lax.psum_scatter(
        (dot_last(gate_piece, gate_weight) + dot_last(up_piece, up_weight)).astype(jnp.bfloat16),
        "head",
        scatter_dimension=0,
        tiled=True,
    ).astype(jnp.float32)
    resid_part, grad_gain_ffn_own = norm_backward(resid_own, inv_two, gain_ffn, grad_normed_two)
    grad_resid = cotangent.astype(jnp.float32) + resid_part
    output, grad_resid = lax.optimization_barrier((output, grad_resid))
    grad_branch = lax.all_gather(grad_resid.astype(jnp.bfloat16), "head", axis=0, tiled=True)
    grad_mixed = dot_last(grad_branch, out_weight).astype(jnp.bfloat16)
    grad_out = dot_first(mixed, grad_branch)
    grad_query_rows, grad_key_rows, grad_value_rows = lax.map(
        attend_back,
        (query_rows, keys_rows, values_rows, doc_ids, log_total, grad_mixed.reshape(row_shape)),
    )
    head_shape = (total_rows, local_heads, DH)
    grad_query = rounded(grad_query_rows.reshape(head_shape))
    grad_key = rounded(grad_key_rows.reshape(head_shape))
    grad_value = rounded(grad_value_rows.reshape(head_shape))
    grad_coef_query = jnp.einsum("thd,trd->thr", grad_query, basis_query, precision=PRECISE) / RQ
    grad_coef_key = jnp.einsum("thd,trd->thr", grad_key, basis_key, precision=PRECISE) / RK
    grad_coef_value = jnp.einsum("thd,trd->thr", grad_value, basis_value, precision=PRECISE) / RK
    grad_basis_query = unrotate(
        jnp.einsum("thr,thd->trd", coef_query, grad_query, precision=PRECISE) / RQ, cosine, sine
    )
    grad_basis_key = unrotate(
        jnp.einsum("thr,thd->trd", coef_key, grad_key, precision=PRECISE) / RK, cosine, sine
    )
    grad_basis_value = jnp.einsum("thr,thd->trd", coef_value, grad_value, precision=PRECISE) / RK
    grad_factor_a = (
        jnp.concatenate([grad_coef_query, grad_coef_key, grad_coef_value], axis=-1)
        .reshape(total_rows, local_heads * rank_all)
        .astype(jnp.bfloat16)
    )
    grad_factor_b = jnp.concatenate(
        [
            grad_basis_query.reshape(total_rows, RQ * DH),
            grad_basis_key.reshape(total_rows, RK * DH),
            grad_basis_value.reshape(total_rows, RK * DH),
        ],
        axis=-1,
    )
    head_count = lax.axis_size("head")
    basis_cols = grad_factor_b.shape[1] // head_count
    factor_cols = head_reduce_scatter(grad_factor_b.astype(jnp.bfloat16), 1).astype(jnp.bfloat16)
    weight_cols = lax.dynamic_slice_in_dim(
        b_weight, lax.axis_index("head") * basis_cols, basis_cols, axis=1
    )
    piece = grad_factor_a
    grad_normed_one = head_reduce_scatter(
        (dot_last(piece, a_weight) + dot_last(factor_cols, weight_cols)).astype(jnp.bfloat16), 0
    )
    input_part, grad_gain_attn_own = norm_backward(x_own, inv_one, gain_attn, grad_normed_one)
    input_grad = grad_resid + input_part
    grad_a = dot_first(normed_all, grad_factor_a)
    grad_b_cols = dot_first(normed_all, factor_cols)

    features = grad_gain_attn_own.shape[0]
    gain_rows = -(-2 * features // basis_cols)
    gains = jnp.pad(
        jnp.concatenate([grad_gain_attn_own, grad_gain_ffn_own]),
        (0, gain_rows * basis_cols - 2 * features),
    ).reshape(gain_rows, basis_cols)
    grad_out, grad_gate, grad_up, grad_down = lax.psum(
        (
            grad_out.astype(jnp.bfloat16),
            grad_gate.astype(jnp.bfloat16),
            grad_up.astype(jnp.bfloat16),
            grad_down.astype(jnp.bfloat16),
        ),
        "dp",
    )
    tail = (grad_a.astype(jnp.bfloat16), jnp.concatenate([grad_b_cols, gains], axis=0).astype(jnp.bfloat16))
    tail, (grad_out, grad_gate, grad_up, grad_down) = lax.optimization_barrier(
        (tail, (grad_out, grad_gate, grad_up, grad_down))
    )
    grad_a, packed = lax.psum(tail, "dp")
    grad_out, grad_gate, grad_up, grad_down = (
        grad_out.astype(jnp.float32),
        grad_gate.astype(jnp.float32),
        grad_up.astype(jnp.float32),
        grad_down.astype(jnp.float32),
    )
    grad_a = grad_a.astype(jnp.float32)
    packed = lax.all_gather(packed, "head", axis=1, tiled=True).astype(jnp.float32)
    grad_b = packed[: grad_b_cols.shape[0]]
    gains = jnp.sum(
        packed[grad_b_cols.shape[0] :].reshape(gain_rows, head_count, basis_cols), axis=1
    ).reshape(-1)
    grad_gain_attn, grad_gain_ffn = gains[:features], gains[features : 2 * features]
    return (
        output,
        input_grad,
        grad_gain_attn,
        grad_a,
        grad_b,
        grad_out,
        grad_gain_ffn,
        grad_gate,
        grad_up,
        grad_down,
    )


def solution(mesh):
    return jax.shard_map(
        local,
        mesh=mesh,
        in_specs=(
            P(("dp", "head"), None),
            P("dp", None),
            P(),
            P(None, "head"),
            P(),
            P("head", None),
            P(),
            P(None, "head"),
            P(None, "head"),
            P("head", None),
            P(("dp", "head"), None),
        ),
        out_specs=(
            P(("dp", "head"), None),
            P(("dp", "head"), None),
            P(),
            P(None, "head"),
            P(),
            P("head", None),
            P(),
            P(None, "head"),
            P(None, "head"),
            P("head", None),
        ),
        check_vma=False,
    )
```

```python
import math

import jax
import jax.numpy as jnp
from jax import lax
from jax.sharding import PartitionSpec as P

DH = 64
RQ = 6
RK = 2


EPSILON = 1e-06
MASKED = -1e30
PRECISE = lax.Precision.HIGHEST


def rope_tables(total_rows, length):
    half_depth = DH // 2
    position = (jnp.arange(total_rows, dtype=jnp.int32) % length).astype(jnp.float32)
    frequency = jnp.exp(jnp.arange(half_depth, dtype=jnp.float32) * (-2.0 * math.log(10000.0) / DH))
    angle = position[:, None] * frequency[None, :]
    return (jnp.cos(angle), jnp.sin(angle))


def rotate(basis, cosine, sine):
    half_depth = basis.shape[-1] // 2
    first_half = basis[..., :half_depth]
    second_half = basis[..., half_depth:]
    cosine_row = cosine[:, None, :]
    sine_row = sine[:, None, :]
    return jnp.concatenate(
        [
            first_half * cosine_row - second_half * sine_row,
            second_half * cosine_row + first_half * sine_row,
        ],
        axis=-1,
    )


def unrotate(grad_basis, cosine, sine):
    half_depth = grad_basis.shape[-1] // 2
    first_half = grad_basis[..., :half_depth]
    second_half = grad_basis[..., half_depth:]
    cosine_row = cosine[:, None, :]
    sine_row = sine[:, None, :]
    return jnp.concatenate(
        [
            first_half * cosine_row + second_half * sine_row,
            second_half * cosine_row - first_half * sine_row,
        ],
        axis=-1,
    )


def dot_last(left, right):
    return lax.dot_general(
        left, right, (((1,), (1,)), ((), ())), preferred_element_type=jnp.float32
    )


def dot_first(left, right):
    return lax.dot_general(
        left, right, (((0,), (0,)), ((), ())), preferred_element_type=jnp.float32
    )


def norm_backward(inputs, inverse, gain, grad_normed):
    scaled = gain * grad_normed
    inner = jnp.mean(scaled * inputs, axis=-1, keepdims=True)
    grad_inputs = inverse * scaled - inputs * (inverse * inverse * inverse) * inner
    grad_gain = jnp.sum(grad_normed * inputs * inverse, axis=0)
    return (grad_inputs, grad_gain)


def block_scores(queries, key_rows, doc_row, first_row, last_row):
    position = jnp.arange(last_row, dtype=jnp.int32)
    allowed = (doc_row[first_row:last_row, None] == doc_row[None, :last_row]) & (
        position[None, :] <= position[first_row:last_row, None]
    )
    score_scale = 1.0 / math.sqrt(queries.shape[2])
    scores = (
        jnp.einsum(
            "qhd,khd->hqk",
            queries[first_row:last_row],
            key_rows[:last_row],
            preferred_element_type=jnp.float32,
        )
        * score_scale
    )
    return jnp.where(allowed[None], scores, MASKED)


def attend_row(row_item):
    queries, key_rows, value_rows, doc_row = row_item
    length = queries.shape[0]
    block_rows = min(512, length)
    mixed_parts = []
    total_parts = []
    for first_row in range(0, length, block_rows):
        last_row = first_row + block_rows
        scores = block_scores(queries, key_rows, doc_row, first_row, last_row)
        row_peak = jnp.max(scores, axis=-1, keepdims=True)
        exponent = jnp.exp(scores - row_peak)
        row_total = jnp.sum(exponent, axis=-1, keepdims=True)
        weights = (exponent / row_total).astype(jnp.bfloat16)
        mixed_parts.append(
            jnp.einsum(
                "hqk,khd->qhd", weights, value_rows[:last_row], preferred_element_type=jnp.float32
            ).astype(jnp.bfloat16)
        )
        total_parts.append(row_peak[..., 0] + jnp.log(row_total[..., 0]))
    return (jnp.concatenate(mixed_parts, axis=0), jnp.concatenate(total_parts, axis=1))


def attend_back(row_item):
    queries, key_rows, value_rows, doc_row, log_total, grad_mixed = row_item
    length = queries.shape[0]
    block_rows = min(512, length)
    score_scale = 1.0 / math.sqrt(queries.shape[2])
    grad_query_parts = []
    grad_keys = jnp.zeros(key_rows.shape, jnp.float32)
    grad_values = jnp.zeros(value_rows.shape, jnp.float32)
    for first_row in range(0, length, block_rows):
        last_row = first_row + block_rows
        scores = block_scores(queries, key_rows, doc_row, first_row, last_row)
        weights = jnp.exp(scores - log_total[:, first_row:last_row, None])
        grad_weights = jnp.einsum(
            "qhd,khd->hqk",
            grad_mixed[first_row:last_row],
            value_rows[:last_row],
            preferred_element_type=jnp.float32,
        )
        inner = jnp.sum(weights * grad_weights, axis=-1, keepdims=True)
        grad_scores = (weights * (grad_weights - inner)).astype(jnp.bfloat16)
        grad_query_parts.append(
            jnp.einsum(
                "hqk,khd->qhd", grad_scores, key_rows[:last_row], preferred_element_type=jnp.float32
            )
            * score_scale
        )
        padding = ((0, length - last_row), (0, 0), (0, 0))
        key_part = (
            jnp.einsum(
                "hqk,qhd->khd",
                grad_scores,
                queries[first_row:last_row],
                preferred_element_type=jnp.float32,
            )
            * score_scale
        )
        value_part = jnp.einsum(
            "hqk,qhd->khd",
            weights.astype(jnp.bfloat16),
            grad_mixed[first_row:last_row],
            preferred_element_type=jnp.float32,
        )
        grad_keys = grad_keys + jnp.pad(key_part, padding)
        grad_values = grad_values + jnp.pad(value_part, padding)
    return (jnp.concatenate(grad_query_parts, axis=0), grad_keys, grad_values)


def rounded(values_in):
    return lax.optimization_barrier(values_in.astype(jnp.bfloat16)).astype(jnp.float32)


def head_reduce_scatter(values, axis):
    count = lax.axis_size("head")
    own = lax.axis_index("head")
    width = values.shape[axis] // count
    total = lax.dynamic_slice_in_dim(values, own * width, width, axis=axis).astype(jnp.float32)
    for shift in range(1, count):
        sent = lax.dynamic_slice_in_dim(values, ((own + shift) % count) * width, width, axis=axis)
        total = total + lax.ppermute(
            sent, "head", [(device, (device + shift) % count) for device in range(count)]
        ).astype(jnp.float32)
    return total


def head_all_gather(values, axis):
    count = lax.axis_size("head")
    own = lax.axis_index("head")
    width = values.shape[axis]
    shape = list(values.shape)
    shape[axis] = width * count
    gathered = lax.dynamic_update_slice_in_dim(
        jnp.zeros(shape, values.dtype), values, own * width, axis=axis
    )
    for shift in range(1, count):
        arrived = lax.ppermute(
            values, "head", [(device, (device + shift) % count) for device in range(count)]
        )
        gathered = lax.dynamic_update_slice_in_dim(
            gathered, arrived, ((own - shift) % count) * width, axis=axis
        )
    return gathered


def local(
    tokens,
    doc_ids,
    gain_attn,
    a_weight,
    b_weight,
    out_weight,
    gain_ffn,
    gate_weight,
    up_weight,
    down_weight,
    cotangent,
):
    rows_dev, length = doc_ids.shape
    total_rows = rows_dev * length
    own_rows = tokens.shape[0]
    local_heads = out_weight.shape[0] // DH
    rank_all = RQ + 2 * RK
    x_own = tokens.astype(jnp.float32)
    inv_one = lax.rsqrt(jnp.mean(x_own * x_own, axis=-1, keepdims=True) + EPSILON)
    normed_one = (x_own * inv_one * gain_attn).astype(jnp.bfloat16)
    normed_all, grad_out_all = (
        lax.all_gather(normed_one, "head", axis=0, tiled=True),
        lax.all_gather(cotangent, "head", axis=0, tiled=True),
    )
    factor_a = jnp.dot(normed_all, a_weight, preferred_element_type=jnp.float32).reshape(
        total_rows, local_heads, rank_all
    )
    factor_b = jnp.dot(normed_all, b_weight, preferred_element_type=jnp.float32)
    cosine, sine = rope_tables(total_rows, length)
    basis_query = rotate(factor_b[:, : RQ * DH].reshape(total_rows, RQ, DH), cosine, sine)
    basis_key = rotate(
        factor_b[:, RQ * DH : (RQ + RK) * DH].reshape(total_rows, RK, DH), cosine, sine
    )
    basis_value = factor_b[:, (RQ + RK) * DH :].reshape(total_rows, RK, DH)
    coef_query = factor_a[:, :, :RQ]
    coef_key = factor_a[:, :, RQ : RQ + RK]
    coef_value = factor_a[:, :, RQ + RK :]
    queries = (jnp.einsum("thr,trd->thd", coef_query, basis_query, precision=PRECISE) / RQ).astype(
        jnp.bfloat16
    )
    key_rows = (jnp.einsum("thr,trd->thd", coef_key, basis_key, precision=PRECISE) / RK).astype(
        jnp.bfloat16
    )
    value_rows = (
        jnp.einsum("thr,trd->thd", coef_value, basis_value, precision=PRECISE) / RK
    ).astype(jnp.bfloat16)
    row_shape = (rows_dev, length, local_heads, DH)
    query_rows = queries.reshape(row_shape)
    keys_rows = key_rows.reshape(row_shape)
    values_rows = value_rows.reshape(row_shape)
    mixed_rows, log_total = lax.map(attend_row, (query_rows, keys_rows, values_rows, doc_ids))
    mixed = mixed_rows.reshape(total_rows, local_heads * DH)
    piece = lax.slice_in_dim(mixed, 0, lax.axis_size("head") * own_rows, axis=0)
    resid_own = x_own + lax.psum_scatter(
        jnp.dot(piece, out_weight, preferred_element_type=jnp.float32).astype(jnp.bfloat16),
        "head",
        scatter_dimension=0,
        tiled=True,
    ).astype(jnp.float32)
    inv_two = lax.rsqrt(jnp.mean(resid_own * resid_own, axis=-1, keepdims=True) + EPSILON)
    normed_two = (resid_own * inv_two * gain_ffn).astype(jnp.bfloat16)
    normed_two_all = lax.all_gather(normed_two, "head", axis=0, tiled=True)
    gate_act = jnp.dot(normed_two_all, gate_weight, preferred_element_type=jnp.float32)
    up_act = jnp.dot(normed_two_all, up_weight, preferred_element_type=jnp.float32)
    sigmoid_gate = jax.nn.sigmoid(gate_act)
    silu_gate = sigmoid_gate * gate_act
    hidden = (silu_gate * up_act).astype(jnp.bfloat16)
    piece = lax.slice_in_dim(hidden, 0, lax.axis_size("head") * own_rows, axis=0)
    output = (
        resid_own
        + head_reduce_scatter(
            jnp.dot(piece, down_weight, preferred_element_type=jnp.float32).astype(jnp.bfloat16), 0
        )
    ).astype(jnp.bfloat16)
    grad_down = dot_first(hidden, grad_out_all)
    grad_hidden = dot_last(grad_out_all, down_weight)
    grad_gate_act = (
        grad_hidden * up_act * (sigmoid_gate * (1.0 + gate_act * (1.0 - sigmoid_gate)))
    ).astype(jnp.bfloat16)
    grad_up_act = (grad_hidden * silu_gate).astype(jnp.bfloat16)
    grad_gate = dot_first(normed_two_all, grad_gate_act)
    grad_up = dot_first(normed_two_all, grad_up_act)
    gate_piece = lax.slice_in_dim(grad_gate_act, 0, lax.axis_size("head") * own_rows, axis=0)
    up_piece = lax.slice_in_dim(grad_up_act, 0, lax.axis_size("head") * own_rows, axis=0)
    grad_normed_two = lax.psum_scatter(
        (dot_last(gate_piece, gate_weight) + dot_last(up_piece, up_weight)).astype(jnp.bfloat16),
        "head",
        scatter_dimension=0,
        tiled=True,
    ).astype(jnp.float32)
    ffn_grads = (grad_gate.astype(jnp.bfloat16), grad_up.astype(jnp.bfloat16), grad_down.astype(jnp.bfloat16))
    ffn_grads, grad_normed_two = lax.optimization_barrier((ffn_grads, grad_normed_two))
    grad_gate, grad_up, grad_down = lax.psum(ffn_grads, "dp")
    resid_part, grad_gain_ffn_own = norm_backward(resid_own, inv_two, gain_ffn, grad_normed_two)
    grad_resid = cotangent.astype(jnp.float32) + resid_part
    output, grad_resid = lax.optimization_barrier((output, grad_resid))
    grad_branch = head_all_gather(grad_resid.astype(jnp.bfloat16), 0)
    grad_mixed = dot_last(grad_branch, out_weight).astype(jnp.bfloat16)
    grad_out = dot_first(mixed, grad_branch)
    grad_query_rows, grad_key_rows, grad_value_rows = lax.map(
        attend_back,
        (query_rows, keys_rows, values_rows, doc_ids, log_total, grad_mixed.reshape(row_shape)),
    )
    head_shape = (total_rows, local_heads, DH)
    grad_query = rounded(grad_query_rows.reshape(head_shape))
    grad_key = rounded(grad_key_rows.reshape(head_shape))
    grad_value = rounded(grad_value_rows.reshape(head_shape))
    grad_coef_query = jnp.einsum("thd,trd->thr", grad_query, basis_query, precision=PRECISE) / RQ
    grad_coef_key = jnp.einsum("thd,trd->thr", grad_key, basis_key, precision=PRECISE) / RK
    grad_coef_value = jnp.einsum("thd,trd->thr", grad_value, basis_value, precision=PRECISE) / RK
    grad_basis_query = unrotate(
        jnp.einsum("thr,thd->trd", coef_query, grad_query, precision=PRECISE) / RQ, cosine, sine
    )
    grad_basis_key = unrotate(
        jnp.einsum("thr,thd->trd", coef_key, grad_key, precision=PRECISE) / RK, cosine, sine
    )
    grad_basis_value = jnp.einsum("thr,thd->trd", coef_value, grad_value, precision=PRECISE) / RK
    grad_factor_a = (
        jnp.concatenate([grad_coef_query, grad_coef_key, grad_coef_value], axis=-1)
        .reshape(total_rows, local_heads * rank_all)
        .astype(jnp.bfloat16)
    )
    grad_factor_b = jnp.concatenate(
        [
            grad_basis_query.reshape(total_rows, RQ * DH),
            grad_basis_key.reshape(total_rows, RK * DH),
            grad_basis_value.reshape(total_rows, RK * DH),
        ],
        axis=-1,
    )
    head_count = lax.axis_size("head")
    basis_cols = grad_factor_b.shape[1] // head_count
    factor_cols = head_reduce_scatter(grad_factor_b.astype(jnp.bfloat16), 1).astype(jnp.bfloat16)
    weight_cols = lax.dynamic_slice_in_dim(
        b_weight, lax.axis_index("head") * basis_cols, basis_cols, axis=1
    )
    piece = grad_factor_a
    grad_normed_one = head_reduce_scatter(
        (dot_last(piece, a_weight) + dot_last(factor_cols, weight_cols)).astype(jnp.bfloat16), 0
    )
    input_part, grad_gain_attn_own = norm_backward(x_own, inv_one, gain_attn, grad_normed_one)
    input_grad = grad_resid + input_part
    grad_a = dot_first(normed_all, grad_factor_a)
    grad_b_cols = dot_first(normed_all, factor_cols)

    features = grad_gain_attn_own.shape[0]
    gain_rows = -(-2 * features // basis_cols)
    gains = jnp.pad(
        jnp.concatenate([grad_gain_attn_own, grad_gain_ffn_own]),
        (0, gain_rows * basis_cols - 2 * features),
    ).reshape(gain_rows, basis_cols)
    tail = (
        grad_a.astype(jnp.bfloat16),
        grad_out.astype(jnp.bfloat16),
        jnp.concatenate([grad_b_cols, gains], axis=0).astype(jnp.bfloat16),
    )
    tail, (grad_gate, grad_up, grad_down) = lax.optimization_barrier(
        (tail, (grad_gate, grad_up, grad_down))
    )
    grad_a, grad_out, packed = lax.psum(tail, "dp")
    grad_out, grad_gate, grad_up, grad_down = (
        grad_out.astype(jnp.float32),
        grad_gate.astype(jnp.float32),
        grad_up.astype(jnp.float32),
        grad_down.astype(jnp.float32),
    )
    grad_a = grad_a.astype(jnp.float32)
    packed = lax.all_gather(packed, "head", axis=1, tiled=True).astype(jnp.float32)
    grad_b = packed[: grad_b_cols.shape[0]]
    gains = jnp.sum(
        packed[grad_b_cols.shape[0] :].reshape(gain_rows, head_count, basis_cols), axis=1
    ).reshape(-1)
    grad_gain_attn, grad_gain_ffn = gains[:features], gains[features : 2 * features]
    return (
        output,
        input_grad,
        grad_gain_attn,
        grad_a,
        grad_b,
        grad_out,
        grad_gain_ffn,
        grad_gate,
        grad_up,
        grad_down,
    )


def solution(mesh):
    return jax.shard_map(
        local,
        mesh=mesh,
        in_specs=(
            P(("dp", "head"), None),
            P("dp", None),
            P(),
            P(None, "head"),
            P(),
            P("head", None),
            P(),
            P(None, "head"),
            P(None, "head"),
            P("head", None),
            P(("dp", "head"), None),
        ),
        out_specs=(
            P(("dp", "head"), None),
            P(("dp", "head"), None),
            P(),
            P(None, "head"),
            P(),
            P("head", None),
            P(),
            P(None, "head"),
            P(None, "head"),
            P("head", None),
        ),
        check_vma=False,
    )
```

```python
import math

import jax
import jax.numpy as jnp
from jax import lax
from jax.sharding import PartitionSpec as P

DH = 64
RQ = 6
RK = 2


EPSILON = 1e-06
MASKED = -1e30
PRECISE = lax.Precision.HIGHEST


def rope_tables(total_rows, length):
    half_depth = DH // 2
    position = (jnp.arange(total_rows, dtype=jnp.int32) % length).astype(jnp.float32)
    frequency = jnp.exp(jnp.arange(half_depth, dtype=jnp.float32) * (-2.0 * math.log(10000.0) / DH))
    angle = position[:, None] * frequency[None, :]
    return (jnp.cos(angle), jnp.sin(angle))


def rotate(basis, cosine, sine):
    half_depth = basis.shape[-1] // 2
    first_half = basis[..., :half_depth]
    second_half = basis[..., half_depth:]
    cosine_row = cosine[:, None, :]
    sine_row = sine[:, None, :]
    return jnp.concatenate(
        [
            first_half * cosine_row - second_half * sine_row,
            second_half * cosine_row + first_half * sine_row,
        ],
        axis=-1,
    )


def unrotate(grad_basis, cosine, sine):
    half_depth = grad_basis.shape[-1] // 2
    first_half = grad_basis[..., :half_depth]
    second_half = grad_basis[..., half_depth:]
    cosine_row = cosine[:, None, :]
    sine_row = sine[:, None, :]
    return jnp.concatenate(
        [
            first_half * cosine_row + second_half * sine_row,
            second_half * cosine_row - first_half * sine_row,
        ],
        axis=-1,
    )


def dot_last(left, right):
    return lax.dot_general(
        left, right, (((1,), (1,)), ((), ())), preferred_element_type=jnp.float32
    )


def dot_first(left, right):
    return lax.dot_general(
        left, right, (((0,), (0,)), ((), ())), preferred_element_type=jnp.float32
    )


def norm_backward(inputs, inverse, gain, grad_normed):
    scaled = gain * grad_normed
    inner = jnp.mean(scaled * inputs, axis=-1, keepdims=True)
    grad_inputs = inverse * scaled - inputs * (inverse * inverse * inverse) * inner
    grad_gain = jnp.sum(grad_normed * inputs * inverse, axis=0)
    return (grad_inputs, grad_gain)


def block_scores(queries, key_rows, doc_row, first_row, last_row):
    position = jnp.arange(last_row, dtype=jnp.int32)
    allowed = (doc_row[first_row:last_row, None] == doc_row[None, :last_row]) & (
        position[None, :] <= position[first_row:last_row, None]
    )
    score_scale = 1.0 / math.sqrt(queries.shape[2])
    scores = (
        jnp.einsum(
            "qhd,khd->hqk",
            queries[first_row:last_row],
            key_rows[:last_row],
            preferred_element_type=jnp.float32,
        )
        * score_scale
    )
    return jnp.where(allowed[None], scores, MASKED)


def attend_row(row_item):
    queries, key_rows, value_rows, doc_row = row_item
    length = queries.shape[0]
    block_rows = min(512, length)
    mixed_parts = []
    total_parts = []
    for first_row in range(0, length, block_rows):
        last_row = first_row + block_rows
        scores = block_scores(queries, key_rows, doc_row, first_row, last_row)
        row_peak = jnp.max(scores, axis=-1, keepdims=True)
        exponent = jnp.exp(scores - row_peak)
        row_total = jnp.sum(exponent, axis=-1, keepdims=True)
        weights = (exponent / row_total).astype(jnp.bfloat16)
        mixed_parts.append(
            jnp.einsum(
                "hqk,khd->qhd", weights, value_rows[:last_row], preferred_element_type=jnp.float32
            ).astype(jnp.bfloat16)
        )
        total_parts.append(row_peak[..., 0] + jnp.log(row_total[..., 0]))
    return (jnp.concatenate(mixed_parts, axis=0), jnp.concatenate(total_parts, axis=1))


def attend_back(row_item):
    queries, key_rows, value_rows, doc_row, log_total, grad_mixed = row_item
    length = queries.shape[0]
    block_rows = min(512, length)
    score_scale = 1.0 / math.sqrt(queries.shape[2])
    grad_query_parts = []
    grad_keys = jnp.zeros(key_rows.shape, jnp.float32)
    grad_values = jnp.zeros(value_rows.shape, jnp.float32)
    for first_row in range(0, length, block_rows):
        last_row = first_row + block_rows
        scores = block_scores(queries, key_rows, doc_row, first_row, last_row)
        weights = jnp.exp(scores - log_total[:, first_row:last_row, None])
        grad_weights = jnp.einsum(
            "qhd,khd->hqk",
            grad_mixed[first_row:last_row],
            value_rows[:last_row],
            preferred_element_type=jnp.float32,
        )
        inner = jnp.sum(weights * grad_weights, axis=-1, keepdims=True)
        grad_scores = (weights * (grad_weights - inner)).astype(jnp.bfloat16)
        grad_query_parts.append(
            jnp.einsum(
                "hqk,khd->qhd", grad_scores, key_rows[:last_row], preferred_element_type=jnp.float32
            )
            * score_scale
        )
        padding = ((0, length - last_row), (0, 0), (0, 0))
        key_part = (
            jnp.einsum(
                "hqk,qhd->khd",
                grad_scores,
                queries[first_row:last_row],
                preferred_element_type=jnp.float32,
            )
            * score_scale
        )
        value_part = jnp.einsum(
            "hqk,qhd->khd",
            weights.astype(jnp.bfloat16),
            grad_mixed[first_row:last_row],
            preferred_element_type=jnp.float32,
        )
        grad_keys = grad_keys + jnp.pad(key_part, padding)
        grad_values = grad_values + jnp.pad(value_part, padding)
    return (jnp.concatenate(grad_query_parts, axis=0), grad_keys, grad_values)


def rounded(values_in):
    return lax.optimization_barrier(values_in.astype(jnp.bfloat16)).astype(jnp.float32)


def head_reduce_scatter(values, axis):
    count = lax.axis_size("head")
    own = lax.axis_index("head")
    width = values.shape[axis] // count
    total = lax.dynamic_slice_in_dim(values, own * width, width, axis=axis).astype(jnp.float32)
    for shift in range(1, count):
        sent = lax.dynamic_slice_in_dim(values, ((own + shift) % count) * width, width, axis=axis)
        total = total + lax.ppermute(
            sent, "head", [(device, (device + shift) % count) for device in range(count)]
        ).astype(jnp.float32)
    return total


def head_all_gather(values, axis):
    count = lax.axis_size("head")
    own = lax.axis_index("head")
    width = values.shape[axis]
    shape = list(values.shape)
    shape[axis] = width * count
    gathered = lax.dynamic_update_slice_in_dim(
        jnp.zeros(shape, values.dtype), values, own * width, axis=axis
    )
    for shift in range(1, count):
        arrived = lax.ppermute(
            values, "head", [(device, (device + shift) % count) for device in range(count)]
        )
        gathered = lax.dynamic_update_slice_in_dim(
            gathered, arrived, ((own - shift) % count) * width, axis=axis
        )
    return gathered


def local(
    tokens,
    doc_ids,
    gain_attn,
    a_weight,
    b_weight,
    out_weight,
    gain_ffn,
    gate_weight,
    up_weight,
    down_weight,
    cotangent,
):
    rows_dev, length = doc_ids.shape
    total_rows = rows_dev * length
    own_rows = tokens.shape[0]
    local_heads = out_weight.shape[0] // DH
    rank_all = RQ + 2 * RK
    x_own = tokens.astype(jnp.float32)
    inv_one = lax.rsqrt(jnp.mean(x_own * x_own, axis=-1, keepdims=True) + EPSILON)
    normed_one = (x_own * inv_one * gain_attn).astype(jnp.bfloat16)
    normed_all, grad_out_all = (
        head_all_gather(normed_one, 0),
        head_all_gather(cotangent, 0),
    )
    factor_a = jnp.dot(normed_all, a_weight, preferred_element_type=jnp.float32).reshape(
        total_rows, local_heads, rank_all
    )
    factor_b = jnp.dot(normed_all, b_weight, preferred_element_type=jnp.float32)
    cosine, sine = rope_tables(total_rows, length)
    basis_query = rotate(factor_b[:, : RQ * DH].reshape(total_rows, RQ, DH), cosine, sine)
    basis_key = rotate(
        factor_b[:, RQ * DH : (RQ + RK) * DH].reshape(total_rows, RK, DH), cosine, sine
    )
    basis_value = factor_b[:, (RQ + RK) * DH :].reshape(total_rows, RK, DH)
    coef_query = factor_a[:, :, :RQ]
    coef_key = factor_a[:, :, RQ : RQ + RK]
    coef_value = factor_a[:, :, RQ + RK :]
    queries = (jnp.einsum("thr,trd->thd", coef_query, basis_query, precision=PRECISE) / RQ).astype(
        jnp.bfloat16
    )
    key_rows = (jnp.einsum("thr,trd->thd", coef_key, basis_key, precision=PRECISE) / RK).astype(
        jnp.bfloat16
    )
    value_rows = (
        jnp.einsum("thr,trd->thd", coef_value, basis_value, precision=PRECISE) / RK
    ).astype(jnp.bfloat16)
    row_shape = (rows_dev, length, local_heads, DH)
    query_rows = queries.reshape(row_shape)
    keys_rows = key_rows.reshape(row_shape)
    values_rows = value_rows.reshape(row_shape)
    mixed_rows, log_total = lax.map(attend_row, (query_rows, keys_rows, values_rows, doc_ids))
    mixed = mixed_rows.reshape(total_rows, local_heads * DH)
    piece = lax.slice_in_dim(mixed, 0, lax.axis_size("head") * own_rows, axis=0)
    resid_own = x_own + head_reduce_scatter(
        jnp.dot(piece, out_weight, preferred_element_type=jnp.float32).astype(jnp.bfloat16), 0
    )
    inv_two = lax.rsqrt(jnp.mean(resid_own * resid_own, axis=-1, keepdims=True) + EPSILON)
    normed_two = (resid_own * inv_two * gain_ffn).astype(jnp.bfloat16)
    normed_two_all = head_all_gather(normed_two, 0)
    gate_act = jnp.dot(normed_two_all, gate_weight, preferred_element_type=jnp.float32)
    up_act = jnp.dot(normed_two_all, up_weight, preferred_element_type=jnp.float32)
    sigmoid_gate = jax.nn.sigmoid(gate_act)
    silu_gate = sigmoid_gate * gate_act
    hidden = (silu_gate * up_act).astype(jnp.bfloat16)
    piece = lax.slice_in_dim(hidden, 0, lax.axis_size("head") * own_rows, axis=0)
    output = (
        resid_own
        + head_reduce_scatter(
            jnp.dot(piece, down_weight, preferred_element_type=jnp.float32).astype(jnp.bfloat16), 0
        )
    ).astype(jnp.bfloat16)
    grad_down = dot_first(hidden, grad_out_all)
    grad_hidden = dot_last(grad_out_all, down_weight)
    grad_gate_act = (
        grad_hidden * up_act * (sigmoid_gate * (1.0 + gate_act * (1.0 - sigmoid_gate)))
    ).astype(jnp.bfloat16)
    grad_up_act = (grad_hidden * silu_gate).astype(jnp.bfloat16)
    grad_gate = dot_first(normed_two_all, grad_gate_act)
    grad_up = dot_first(normed_two_all, grad_up_act)
    gate_piece = lax.slice_in_dim(grad_gate_act, 0, lax.axis_size("head") * own_rows, axis=0)
    up_piece = lax.slice_in_dim(grad_up_act, 0, lax.axis_size("head") * own_rows, axis=0)
    grad_normed_two = head_reduce_scatter(
        (dot_last(gate_piece, gate_weight) + dot_last(up_piece, up_weight)).astype(jnp.bfloat16), 0
    )
    ffn_grads = (grad_gate.astype(jnp.bfloat16), grad_up.astype(jnp.bfloat16), grad_down.astype(jnp.bfloat16))
    ffn_grads, grad_normed_two = lax.optimization_barrier((ffn_grads, grad_normed_two))
    grad_gate, grad_up, grad_down = lax.psum(ffn_grads, "dp")
    resid_part, grad_gain_ffn_own = norm_backward(resid_own, inv_two, gain_ffn, grad_normed_two)
    grad_resid = cotangent.astype(jnp.float32) + resid_part
    output, grad_resid = lax.optimization_barrier((output, grad_resid))
    grad_branch = head_all_gather(grad_resid.astype(jnp.bfloat16), 0)
    grad_mixed = dot_last(grad_branch, out_weight).astype(jnp.bfloat16)
    grad_out = dot_first(mixed, grad_branch)
    grad_query_rows, grad_key_rows, grad_value_rows = lax.map(
        attend_back,
        (query_rows, keys_rows, values_rows, doc_ids, log_total, grad_mixed.reshape(row_shape)),
    )
    head_shape = (total_rows, local_heads, DH)
    grad_query = rounded(grad_query_rows.reshape(head_shape))
    grad_key = rounded(grad_key_rows.reshape(head_shape))
    grad_value = rounded(grad_value_rows.reshape(head_shape))
    grad_coef_query = jnp.einsum("thd,trd->thr", grad_query, basis_query, precision=PRECISE) / RQ
    grad_coef_key = jnp.einsum("thd,trd->thr", grad_key, basis_key, precision=PRECISE) / RK
    grad_coef_value = jnp.einsum("thd,trd->thr", grad_value, basis_value, precision=PRECISE) / RK
    grad_basis_query = unrotate(
        jnp.einsum("thr,thd->trd", coef_query, grad_query, precision=PRECISE) / RQ, cosine, sine
    )
    grad_basis_key = unrotate(
        jnp.einsum("thr,thd->trd", coef_key, grad_key, precision=PRECISE) / RK, cosine, sine
    )
    grad_basis_value = jnp.einsum("thr,thd->trd", coef_value, grad_value, precision=PRECISE) / RK
    grad_factor_a = (
        jnp.concatenate([grad_coef_query, grad_coef_key, grad_coef_value], axis=-1)
        .reshape(total_rows, local_heads * rank_all)
        .astype(jnp.bfloat16)
    )
    grad_factor_b = jnp.concatenate(
        [
            grad_basis_query.reshape(total_rows, RQ * DH),
            grad_basis_key.reshape(total_rows, RK * DH),
            grad_basis_value.reshape(total_rows, RK * DH),
        ],
        axis=-1,
    )
    head_count = lax.axis_size("head")
    basis_cols = grad_factor_b.shape[1] // head_count
    factor_cols = head_reduce_scatter(grad_factor_b.astype(jnp.bfloat16), 1).astype(jnp.bfloat16)
    weight_cols = lax.dynamic_slice_in_dim(
        b_weight, lax.axis_index("head") * basis_cols, basis_cols, axis=1
    )
    piece = grad_factor_a
    grad_normed_one = head_reduce_scatter(
        (dot_last(piece, a_weight) + dot_last(factor_cols, weight_cols)).astype(jnp.bfloat16), 0
    )
    input_part, grad_gain_attn_own = norm_backward(x_own, inv_one, gain_attn, grad_normed_one)
    input_grad = grad_resid + input_part
    grad_a = dot_first(normed_all, grad_factor_a)
    grad_b_cols = dot_first(normed_all, factor_cols)

    features = grad_gain_attn_own.shape[0]
    gain_rows = -(-2 * features // basis_cols)
    gains = jnp.pad(
        jnp.concatenate([grad_gain_attn_own, grad_gain_ffn_own]),
        (0, gain_rows * basis_cols - 2 * features),
    ).reshape(gain_rows, basis_cols)
    tail = (
        grad_a.astype(jnp.bfloat16),
        grad_out.astype(jnp.bfloat16),
        jnp.concatenate([grad_b_cols, gains], axis=0).astype(jnp.bfloat16),
    )
    tail, (grad_gate, grad_up, grad_down) = lax.optimization_barrier(
        (tail, (grad_gate, grad_up, grad_down))
    )
    grad_a, grad_out, packed = lax.psum(tail, "dp")
    grad_out, grad_gate, grad_up, grad_down = (
        grad_out.astype(jnp.float32),
        grad_gate.astype(jnp.float32),
        grad_up.astype(jnp.float32),
        grad_down.astype(jnp.float32),
    )
    grad_a = grad_a.astype(jnp.float32)
    packed = lax.all_gather(packed, "head", axis=1, tiled=True).astype(jnp.float32)
    grad_b = packed[: grad_b_cols.shape[0]]
    gains = jnp.sum(
        packed[grad_b_cols.shape[0] :].reshape(gain_rows, head_count, basis_cols), axis=1
    ).reshape(-1)
    grad_gain_attn, grad_gain_ffn = gains[:features], gains[features : 2 * features]
    return (
        output,
        input_grad,
        grad_gain_attn,
        grad_a,
        grad_b,
        grad_out,
        grad_gain_ffn,
        grad_gate,
        grad_up,
        grad_down,
    )


def solution(mesh):
    return jax.shard_map(
        local,
        mesh=mesh,
        in_specs=(
            P(("dp", "head"), None),
            P("dp", None),
            P(),
            P(None, "head"),
            P(),
            P("head", None),
            P(),
            P(None, "head"),
            P(None, "head"),
            P("head", None),
            P(("dp", "head"), None),
        ),
        out_specs=(
            P(("dp", "head"), None),
            P(("dp", "head"), None),
            P(),
            P(None, "head"),
            P(),
            P("head", None),
            P(),
            P(None, "head"),
            P(None, "head"),
            P("head", None),
        ),
        check_vma=False,
    )
```

```python
import math

import jax
import jax.numpy as jnp
from jax import lax
from jax.sharding import PartitionSpec as P

DH = 64
RQ = 6
RK = 2


EPSILON = 1e-06
MASKED = -1e30
PRECISE = lax.Precision.HIGHEST


def rope_tables(total_rows, length):
    half_depth = DH // 2
    position = (jnp.arange(total_rows, dtype=jnp.int32) % length).astype(jnp.float32)
    frequency = jnp.exp(jnp.arange(half_depth, dtype=jnp.float32) * (-2.0 * math.log(10000.0) / DH))
    angle = position[:, None] * frequency[None, :]
    return (jnp.cos(angle), jnp.sin(angle))


def rotate(basis, cosine, sine):
    half_depth = basis.shape[-1] // 2
    first_half = basis[..., :half_depth]
    second_half = basis[..., half_depth:]
    cosine_row = cosine[:, None, :]
    sine_row = sine[:, None, :]
    return jnp.concatenate(
        [
            first_half * cosine_row - second_half * sine_row,
            second_half * cosine_row + first_half * sine_row,
        ],
        axis=-1,
    )


def unrotate(grad_basis, cosine, sine):
    half_depth = grad_basis.shape[-1] // 2
    first_half = grad_basis[..., :half_depth]
    second_half = grad_basis[..., half_depth:]
    cosine_row = cosine[:, None, :]
    sine_row = sine[:, None, :]
    return jnp.concatenate(
        [
            first_half * cosine_row + second_half * sine_row,
            second_half * cosine_row - first_half * sine_row,
        ],
        axis=-1,
    )


def dot_last(left, right):
    return lax.dot_general(
        left, right, (((1,), (1,)), ((), ())), preferred_element_type=jnp.float32
    )


def dot_first(left, right):
    return lax.dot_general(
        left, right, (((0,), (0,)), ((), ())), preferred_element_type=jnp.float32
    )


def norm_backward(inputs, inverse, gain, grad_normed):
    scaled = gain * grad_normed
    inner = jnp.mean(scaled * inputs, axis=-1, keepdims=True)
    grad_inputs = inverse * scaled - inputs * (inverse * inverse * inverse) * inner
    grad_gain = jnp.sum(grad_normed * inputs * inverse, axis=0)
    return (grad_inputs, grad_gain)


def block_scores(queries, key_rows, doc_row, first_row, last_row):
    position = jnp.arange(last_row, dtype=jnp.int32)
    allowed = (doc_row[first_row:last_row, None] == doc_row[None, :last_row]) & (
        position[None, :] <= position[first_row:last_row, None]
    )
    score_scale = 1.0 / math.sqrt(queries.shape[2])
    scores = (
        jnp.einsum(
            "qhd,khd->hqk",
            queries[first_row:last_row],
            key_rows[:last_row],
            preferred_element_type=jnp.float32,
        )
        * score_scale
    )
    return jnp.where(allowed[None], scores, MASKED)


def attend_row(row_item):
    queries, key_rows, value_rows, doc_row = row_item
    length = queries.shape[0]
    block_rows = min(512, length)
    mixed_parts = []
    total_parts = []
    for first_row in range(0, length, block_rows):
        last_row = first_row + block_rows
        scores = block_scores(queries, key_rows, doc_row, first_row, last_row)
        row_peak = jnp.max(scores, axis=-1, keepdims=True)
        exponent = jnp.exp(scores - row_peak)
        row_total = jnp.sum(exponent, axis=-1, keepdims=True)
        weights = (exponent / row_total).astype(jnp.bfloat16)
        mixed_parts.append(
            jnp.einsum(
                "hqk,khd->qhd", weights, value_rows[:last_row], preferred_element_type=jnp.float32
            ).astype(jnp.bfloat16)
        )
        total_parts.append(row_peak[..., 0] + jnp.log(row_total[..., 0]))
    return (jnp.concatenate(mixed_parts, axis=0), jnp.concatenate(total_parts, axis=1))


def attend_back(row_item):
    queries, key_rows, value_rows, doc_row, log_total, grad_mixed = row_item
    length = queries.shape[0]
    block_rows = min(512, length)
    score_scale = 1.0 / math.sqrt(queries.shape[2])
    grad_query_parts = []
    grad_keys = jnp.zeros(key_rows.shape, jnp.float32)
    grad_values = jnp.zeros(value_rows.shape, jnp.float32)
    for first_row in range(0, length, block_rows):
        last_row = first_row + block_rows
        scores = block_scores(queries, key_rows, doc_row, first_row, last_row)
        weights = jnp.exp(scores - log_total[:, first_row:last_row, None])
        grad_weights = jnp.einsum(
            "qhd,khd->hqk",
            grad_mixed[first_row:last_row],
            value_rows[:last_row],
            preferred_element_type=jnp.float32,
        )
        inner = jnp.sum(weights * grad_weights, axis=-1, keepdims=True)
        grad_scores = (weights * (grad_weights - inner)).astype(jnp.bfloat16)
        grad_query_parts.append(
            jnp.einsum(
                "hqk,khd->qhd", grad_scores, key_rows[:last_row], preferred_element_type=jnp.float32
            )
            * score_scale
        )
        padding = ((0, length - last_row), (0, 0), (0, 0))
        key_part = (
            jnp.einsum(
                "hqk,qhd->khd",
                grad_scores,
                queries[first_row:last_row],
                preferred_element_type=jnp.float32,
            )
            * score_scale
        )
        value_part = jnp.einsum(
            "hqk,qhd->khd",
            weights.astype(jnp.bfloat16),
            grad_mixed[first_row:last_row],
            preferred_element_type=jnp.float32,
        )
        grad_keys = grad_keys + jnp.pad(key_part, padding)
        grad_values = grad_values + jnp.pad(value_part, padding)
    return (jnp.concatenate(grad_query_parts, axis=0), grad_keys, grad_values)


def rounded(values_in):
    return lax.optimization_barrier(values_in.astype(jnp.bfloat16)).astype(jnp.float32)


def head_reduce_scatter(values, axis):
    count = lax.axis_size("head")
    own = lax.axis_index("head")
    width = values.shape[axis] // count
    total = lax.dynamic_slice_in_dim(values, own * width, width, axis=axis).astype(jnp.float32)
    for shift in range(1, count):
        sent = lax.dynamic_slice_in_dim(values, ((own + shift) % count) * width, width, axis=axis)
        total = total + lax.ppermute(
            sent, "head", [(device, (device + shift) % count) for device in range(count)]
        ).astype(jnp.float32)
    return total


def head_all_gather(values, axis):
    count = lax.axis_size("head")
    own = lax.axis_index("head")
    width = values.shape[axis]
    shape = list(values.shape)
    shape[axis] = width * count
    gathered = lax.dynamic_update_slice_in_dim(
        jnp.zeros(shape, values.dtype), values, own * width, axis=axis
    )
    for shift in range(1, count):
        arrived = lax.ppermute(
            values, "head", [(device, (device + shift) % count) for device in range(count)]
        )
        gathered = lax.dynamic_update_slice_in_dim(
            gathered, arrived, ((own - shift) % count) * width, axis=axis
        )
    return gathered


def dp_all_reduce(flat):
    count = lax.axis_size("dp")
    own = lax.axis_index("dp")
    steps = count.bit_length() - 1
    assert count == 1 << steps
    width = -(-flat.shape[0] // (count * 128)) * 128
    blocks = jnp.pad(flat, (0, count * width - flat.shape[0])).reshape((2,) * steps + (width,))
    kept = blocks.astype(jnp.float32)
    for step in range(steps):
        axis = steps - 1 - step
        bit = (own >> step) & 1
        sent = lax.dynamic_index_in_dim(kept, 1 - bit, axis, keepdims=False)
        kept = lax.dynamic_index_in_dim(kept, bit, axis, keepdims=False)
        pairs = [(device, device ^ (1 << step)) for device in range(count)]
        kept = kept + lax.ppermute(sent.astype(jnp.bfloat16), "dp", pairs).astype(jnp.float32)
    whole = kept.astype(jnp.bfloat16)[None]
    for step in reversed(range(steps)):
        bit = (own >> step) & 1
        pairs = [(device, device ^ (1 << step)) for device in range(count)]
        arrived = lax.ppermute(whole, "dp", pairs)
        low_half = jnp.where(bit == 0, whole, arrived)
        high_half = jnp.where(bit == 0, arrived, whole)
        whole = jnp.stack([low_half, high_half], axis=1).reshape((-1,) + whole.shape[1:])
    return whole.reshape(-1)[: flat.shape[0]]


def local(
    tokens,
    doc_ids,
    gain_attn,
    a_weight,
    b_weight,
    out_weight,
    gain_ffn,
    gate_weight,
    up_weight,
    down_weight,
    cotangent,
):
    rows_dev, length = doc_ids.shape
    total_rows = rows_dev * length
    own_rows = tokens.shape[0]
    local_heads = out_weight.shape[0] // DH
    rank_all = RQ + 2 * RK
    x_own = tokens.astype(jnp.float32)
    inv_one = lax.rsqrt(jnp.mean(x_own * x_own, axis=-1, keepdims=True) + EPSILON)
    normed_one = (x_own * inv_one * gain_attn).astype(jnp.bfloat16)
    normed_all, grad_out_all = (
        head_all_gather(normed_one, 0),
        head_all_gather(cotangent, 0),
    )
    factor_a = jnp.dot(normed_all, a_weight, preferred_element_type=jnp.float32).reshape(
        total_rows, local_heads, rank_all
    )
    factor_b = jnp.dot(normed_all, b_weight, preferred_element_type=jnp.float32)
    cosine, sine = rope_tables(total_rows, length)
    basis_query = rotate(factor_b[:, : RQ * DH].reshape(total_rows, RQ, DH), cosine, sine)
    basis_key = rotate(
        factor_b[:, RQ * DH : (RQ + RK) * DH].reshape(total_rows, RK, DH), cosine, sine
    )
    basis_value = factor_b[:, (RQ + RK) * DH :].reshape(total_rows, RK, DH)
    coef_query = factor_a[:, :, :RQ]
    coef_key = factor_a[:, :, RQ : RQ + RK]
    coef_value = factor_a[:, :, RQ + RK :]
    queries = (jnp.einsum("thr,trd->thd", coef_query, basis_query, precision=PRECISE) / RQ).astype(
        jnp.bfloat16
    )
    key_rows = (jnp.einsum("thr,trd->thd", coef_key, basis_key, precision=PRECISE) / RK).astype(
        jnp.bfloat16
    )
    value_rows = (
        jnp.einsum("thr,trd->thd", coef_value, basis_value, precision=PRECISE) / RK
    ).astype(jnp.bfloat16)
    row_shape = (rows_dev, length, local_heads, DH)
    query_rows = queries.reshape(row_shape)
    keys_rows = key_rows.reshape(row_shape)
    values_rows = value_rows.reshape(row_shape)
    mixed_rows, log_total = lax.map(attend_row, (query_rows, keys_rows, values_rows, doc_ids))
    mixed = mixed_rows.reshape(total_rows, local_heads * DH)
    piece = lax.slice_in_dim(mixed, 0, lax.axis_size("head") * own_rows, axis=0)
    resid_own = x_own + head_reduce_scatter(
        jnp.dot(piece, out_weight, preferred_element_type=jnp.float32).astype(jnp.bfloat16), 0
    )
    inv_two = lax.rsqrt(jnp.mean(resid_own * resid_own, axis=-1, keepdims=True) + EPSILON)
    normed_two = (resid_own * inv_two * gain_ffn).astype(jnp.bfloat16)
    normed_two_all = head_all_gather(normed_two, 0)
    gate_act = jnp.dot(normed_two_all, gate_weight, preferred_element_type=jnp.float32)
    up_act = jnp.dot(normed_two_all, up_weight, preferred_element_type=jnp.float32)
    sigmoid_gate = jax.nn.sigmoid(gate_act)
    silu_gate = sigmoid_gate * gate_act
    hidden = (silu_gate * up_act).astype(jnp.bfloat16)
    piece = lax.slice_in_dim(hidden, 0, lax.axis_size("head") * own_rows, axis=0)
    output = (
        resid_own
        + head_reduce_scatter(
            jnp.dot(piece, down_weight, preferred_element_type=jnp.float32).astype(jnp.bfloat16), 0
        )
    ).astype(jnp.bfloat16)
    grad_down = dot_first(hidden, grad_out_all)
    grad_hidden = dot_last(grad_out_all, down_weight)
    grad_gate_act = (
        grad_hidden * up_act * (sigmoid_gate * (1.0 + gate_act * (1.0 - sigmoid_gate)))
    ).astype(jnp.bfloat16)
    grad_up_act = (grad_hidden * silu_gate).astype(jnp.bfloat16)
    grad_gate = dot_first(normed_two_all, grad_gate_act)
    grad_up = dot_first(normed_two_all, grad_up_act)
    gate_piece = lax.slice_in_dim(grad_gate_act, 0, lax.axis_size("head") * own_rows, axis=0)
    up_piece = lax.slice_in_dim(grad_up_act, 0, lax.axis_size("head") * own_rows, axis=0)
    grad_normed_two = head_reduce_scatter(
        (dot_last(gate_piece, gate_weight) + dot_last(up_piece, up_weight)).astype(jnp.bfloat16), 0
    )
    ffn_grads = (grad_gate.astype(jnp.bfloat16), grad_up.astype(jnp.bfloat16), grad_down.astype(jnp.bfloat16))
    ffn_grads, grad_normed_two = lax.optimization_barrier((ffn_grads, grad_normed_two))
    grad_gate, grad_up, grad_down = lax.psum(ffn_grads, "dp")
    resid_part, grad_gain_ffn_own = norm_backward(resid_own, inv_two, gain_ffn, grad_normed_two)
    grad_resid = cotangent.astype(jnp.float32) + resid_part
    output, grad_resid = lax.optimization_barrier((output, grad_resid))
    grad_branch = head_all_gather(grad_resid.astype(jnp.bfloat16), 0)
    grad_mixed = dot_last(grad_branch, out_weight).astype(jnp.bfloat16)
    grad_out = dot_first(mixed, grad_branch)
    grad_query_rows, grad_key_rows, grad_value_rows = lax.map(
        attend_back,
        (query_rows, keys_rows, values_rows, doc_ids, log_total, grad_mixed.reshape(row_shape)),
    )
    head_shape = (total_rows, local_heads, DH)
    grad_query = rounded(grad_query_rows.reshape(head_shape))
    grad_key = rounded(grad_key_rows.reshape(head_shape))
    grad_value = rounded(grad_value_rows.reshape(head_shape))
    grad_coef_query = jnp.einsum("thd,trd->thr", grad_query, basis_query, precision=PRECISE) / RQ
    grad_coef_key = jnp.einsum("thd,trd->thr", grad_key, basis_key, precision=PRECISE) / RK
    grad_coef_value = jnp.einsum("thd,trd->thr", grad_value, basis_value, precision=PRECISE) / RK
    grad_basis_query = unrotate(
        jnp.einsum("thr,thd->trd", coef_query, grad_query, precision=PRECISE) / RQ, cosine, sine
    )
    grad_basis_key = unrotate(
        jnp.einsum("thr,thd->trd", coef_key, grad_key, precision=PRECISE) / RK, cosine, sine
    )
    grad_basis_value = jnp.einsum("thr,thd->trd", coef_value, grad_value, precision=PRECISE) / RK
    grad_factor_a = (
        jnp.concatenate([grad_coef_query, grad_coef_key, grad_coef_value], axis=-1)
        .reshape(total_rows, local_heads * rank_all)
        .astype(jnp.bfloat16)
    )
    grad_factor_b = jnp.concatenate(
        [
            grad_basis_query.reshape(total_rows, RQ * DH),
            grad_basis_key.reshape(total_rows, RK * DH),
            grad_basis_value.reshape(total_rows, RK * DH),
        ],
        axis=-1,
    )
    head_count = lax.axis_size("head")
    basis_cols = grad_factor_b.shape[1] // head_count
    factor_cols = head_reduce_scatter(grad_factor_b.astype(jnp.bfloat16), 1).astype(jnp.bfloat16)
    weight_cols = lax.dynamic_slice_in_dim(
        b_weight, lax.axis_index("head") * basis_cols, basis_cols, axis=1
    )
    piece = grad_factor_a
    grad_normed_one = head_reduce_scatter(
        (dot_last(piece, a_weight) + dot_last(factor_cols, weight_cols)).astype(jnp.bfloat16), 0
    )
    input_part, grad_gain_attn_own = norm_backward(x_own, inv_one, gain_attn, grad_normed_one)
    input_grad = grad_resid + input_part
    grad_a = dot_first(normed_all, grad_factor_a)
    grad_b_cols = dot_first(normed_all, factor_cols)

    features = grad_gain_attn_own.shape[0]
    gain_rows = -(-2 * features // basis_cols)
    gains = jnp.pad(
        jnp.concatenate([grad_gain_attn_own, grad_gain_ffn_own]),
        (0, gain_rows * basis_cols - 2 * features),
    ).reshape(gain_rows, basis_cols)
    tail = (
        grad_a.astype(jnp.bfloat16),
        grad_out.astype(jnp.bfloat16),
        jnp.concatenate([grad_b_cols, gains], axis=0).astype(jnp.bfloat16),
    )
    tail, (grad_gate, grad_up, grad_down) = lax.optimization_barrier(
        (tail, (grad_gate, grad_up, grad_down))
    )
    sizes = [part.size for part in tail]
    summed = dp_all_reduce(jnp.concatenate([part.reshape(-1) for part in tail]))
    grad_a, grad_out, packed = (
        summed[sum(sizes[:index]) : sum(sizes[: index + 1])].reshape(part.shape)
        for index, part in enumerate(tail)
    )
    grad_out, grad_gate, grad_up, grad_down = (
        grad_out.astype(jnp.float32),
        grad_gate.astype(jnp.float32),
        grad_up.astype(jnp.float32),
        grad_down.astype(jnp.float32),
    )
    grad_a = grad_a.astype(jnp.float32)
    packed = head_all_gather(packed, 1).astype(jnp.float32)
    grad_b = packed[: grad_b_cols.shape[0]]
    gains = jnp.sum(
        packed[grad_b_cols.shape[0] :].reshape(gain_rows, head_count, basis_cols), axis=1
    ).reshape(-1)
    grad_gain_attn, grad_gain_ffn = gains[:features], gains[features : 2 * features]
    return (
        output,
        input_grad,
        grad_gain_attn,
        grad_a,
        grad_b,
        grad_out,
        grad_gain_ffn,
        grad_gate,
        grad_up,
        grad_down,
    )


def solution(mesh):
    return jax.shard_map(
        local,
        mesh=mesh,
        in_specs=(
            P(("dp", "head"), None),
            P("dp", None),
            P(),
            P(None, "head"),
            P(),
            P("head", None),
            P(),
            P(None, "head"),
            P(None, "head"),
            P("head", None),
            P(("dp", "head"), None),
        ),
        out_specs=(
            P(("dp", "head"), None),
            P(("dp", "head"), None),
            P(),
            P(None, "head"),
            P(),
            P("head", None),
            P(),
            P(None, "head"),
            P(None, "head"),
            P("head", None),
        ),
        check_vma=False,
    )
```

```python
import math

import jax
import jax.numpy as jnp
from jax import lax
from jax.sharding import PartitionSpec as P

DH = 64
RQ = 6
RK = 2


EPSILON = 1e-06
MASKED = -1e30
PRECISE = lax.Precision.HIGHEST


def rope_tables(total_rows, length):
    half_depth = DH // 2
    position = (jnp.arange(total_rows, dtype=jnp.int32) % length).astype(jnp.float32)
    frequency = jnp.exp(jnp.arange(half_depth, dtype=jnp.float32) * (-2.0 * math.log(10000.0) / DH))
    angle = position[:, None] * frequency[None, :]
    return (jnp.cos(angle), jnp.sin(angle))


def rotate(basis, cosine, sine):
    half_depth = basis.shape[-1] // 2
    first_half = basis[..., :half_depth]
    second_half = basis[..., half_depth:]
    cosine_row = cosine[:, None, :]
    sine_row = sine[:, None, :]
    return jnp.concatenate(
        [
            first_half * cosine_row - second_half * sine_row,
            second_half * cosine_row + first_half * sine_row,
        ],
        axis=-1,
    )


def unrotate(grad_basis, cosine, sine):
    half_depth = grad_basis.shape[-1] // 2
    first_half = grad_basis[..., :half_depth]
    second_half = grad_basis[..., half_depth:]
    cosine_row = cosine[:, None, :]
    sine_row = sine[:, None, :]
    return jnp.concatenate(
        [
            first_half * cosine_row + second_half * sine_row,
            second_half * cosine_row - first_half * sine_row,
        ],
        axis=-1,
    )


def dot_last(left, right):
    return lax.dot_general(
        left, right, (((1,), (1,)), ((), ())), preferred_element_type=jnp.float32
    )


def dot_first(left, right):
    return lax.dot_general(
        left, right, (((0,), (0,)), ((), ())), preferred_element_type=jnp.float32
    )


def norm_backward(inputs, inverse, gain, grad_normed):
    scaled = gain * grad_normed
    inner = jnp.mean(scaled * inputs, axis=-1, keepdims=True)
    grad_inputs = inverse * scaled - inputs * (inverse * inverse * inverse) * inner
    grad_gain = jnp.sum(grad_normed * inputs * inverse, axis=0)
    return (grad_inputs, grad_gain)


def block_scores(queries, key_rows, doc_row, first_row, last_row):
    position = jnp.arange(last_row, dtype=jnp.int32)
    allowed = (doc_row[first_row:last_row, None] == doc_row[None, :last_row]) & (
        position[None, :] <= position[first_row:last_row, None]
    )
    score_scale = 1.0 / math.sqrt(queries.shape[2])
    scores = (
        jnp.einsum(
            "qhd,khd->hqk",
            queries[first_row:last_row],
            key_rows[:last_row],
            preferred_element_type=jnp.float32,
        )
        * score_scale
    )
    return jnp.where(allowed[None], scores, MASKED)


def attend_row(row_item):
    queries, key_rows, value_rows, doc_row = row_item
    length = queries.shape[0]
    block_rows = min(512, length)
    mixed_parts = []
    total_parts = []
    for first_row in range(0, length, block_rows):
        last_row = first_row + block_rows
        scores = block_scores(queries, key_rows, doc_row, first_row, last_row)
        row_peak = jnp.max(scores, axis=-1, keepdims=True)
        exponent = jnp.exp(scores - row_peak)
        row_total = jnp.sum(exponent, axis=-1, keepdims=True)
        weights = (exponent / row_total).astype(jnp.bfloat16)
        mixed_parts.append(
            jnp.einsum(
                "hqk,khd->qhd", weights, value_rows[:last_row], preferred_element_type=jnp.float32
            ).astype(jnp.bfloat16)
        )
        total_parts.append(row_peak[..., 0] + jnp.log(row_total[..., 0]))
    return (jnp.concatenate(mixed_parts, axis=0), jnp.concatenate(total_parts, axis=1))


def attend_back(row_item):
    queries, key_rows, value_rows, doc_row, log_total, grad_mixed = row_item
    length = queries.shape[0]
    block_rows = min(512, length)
    score_scale = 1.0 / math.sqrt(queries.shape[2])
    grad_query_parts = []
    grad_keys = jnp.zeros(key_rows.shape, jnp.float32)
    grad_values = jnp.zeros(value_rows.shape, jnp.float32)
    for first_row in range(0, length, block_rows):
        last_row = first_row + block_rows
        scores = block_scores(queries, key_rows, doc_row, first_row, last_row)
        weights = jnp.exp(scores - log_total[:, first_row:last_row, None])
        grad_weights = jnp.einsum(
            "qhd,khd->hqk",
            grad_mixed[first_row:last_row],
            value_rows[:last_row],
            preferred_element_type=jnp.float32,
        )
        inner = jnp.sum(weights * grad_weights, axis=-1, keepdims=True)
        grad_scores = (weights * (grad_weights - inner)).astype(jnp.bfloat16)
        grad_query_parts.append(
            jnp.einsum(
                "hqk,khd->qhd", grad_scores, key_rows[:last_row], preferred_element_type=jnp.float32
            )
            * score_scale
        )
        padding = ((0, length - last_row), (0, 0), (0, 0))
        key_part = (
            jnp.einsum(
                "hqk,qhd->khd",
                grad_scores,
                queries[first_row:last_row],
                preferred_element_type=jnp.float32,
            )
            * score_scale
        )
        value_part = jnp.einsum(
            "hqk,qhd->khd",
            weights.astype(jnp.bfloat16),
            grad_mixed[first_row:last_row],
            preferred_element_type=jnp.float32,
        )
        grad_keys = grad_keys + jnp.pad(key_part, padding)
        grad_values = grad_values + jnp.pad(value_part, padding)
    return (jnp.concatenate(grad_query_parts, axis=0), grad_keys, grad_values)


def rounded(values_in):
    return lax.optimization_barrier(values_in.astype(jnp.bfloat16)).astype(jnp.float32)


def head_reduce_scatter(values, axis):
    count = lax.axis_size("head")
    own = lax.axis_index("head")
    width = values.shape[axis] // count
    total = lax.dynamic_slice_in_dim(values, own * width, width, axis=axis).astype(jnp.float32)
    for shift in range(1, count):
        sent = lax.dynamic_slice_in_dim(values, ((own + shift) % count) * width, width, axis=axis)
        total = total + lax.ppermute(
            sent, "head", [(device, (device + shift) % count) for device in range(count)]
        ).astype(jnp.float32)
    return total


def head_all_gather(values, axis):
    count = lax.axis_size("head")
    own = lax.axis_index("head")
    width = values.shape[axis]
    shape = list(values.shape)
    shape[axis] = width * count
    gathered = lax.dynamic_update_slice_in_dim(
        jnp.zeros(shape, values.dtype), values, own * width, axis=axis
    )
    for shift in range(1, count):
        arrived = lax.ppermute(
            values, "head", [(device, (device + shift) % count) for device in range(count)]
        )
        gathered = lax.dynamic_update_slice_in_dim(
            gathered, arrived, ((own - shift) % count) * width, axis=axis
        )
    return gathered


def dp_all_reduce(flat):
    count = lax.axis_size("dp")
    own = lax.axis_index("dp")
    steps = count.bit_length() - 1
    assert count == 1 << steps
    width = -(-flat.shape[0] // (count * 128)) * 128
    blocks = jnp.pad(flat, (0, count * width - flat.shape[0])).reshape((2,) * steps + (width,))
    kept = blocks.astype(jnp.float32)
    for step in range(steps):
        axis = steps - 1 - step
        bit = (own >> step) & 1
        sent = lax.dynamic_index_in_dim(kept, 1 - bit, axis, keepdims=False)
        kept = lax.dynamic_index_in_dim(kept, bit, axis, keepdims=False)
        pairs = [(device, device ^ (1 << step)) for device in range(count)]
        kept = kept + lax.ppermute(sent.astype(jnp.bfloat16), "dp", pairs).astype(jnp.float32)
    whole = kept.astype(jnp.bfloat16)[None]
    for step in reversed(range(steps)):
        bit = (own >> step) & 1
        pairs = [(device, device ^ (1 << step)) for device in range(count)]
        arrived = lax.ppermute(whole, "dp", pairs)
        low_half = jnp.where(bit == 0, whole, arrived)
        high_half = jnp.where(bit == 0, arrived, whole)
        whole = jnp.stack([low_half, high_half], axis=1).reshape((-1,) + whole.shape[1:])
    return whole.reshape(-1)[: flat.shape[0]]


def head_gather_relative(values):
    count = lax.axis_size("head")
    parts = [values]
    for shift in range(1, count):
        parts.append(
            lax.ppermute(values, "head", [(device, (device + shift) % count) for device in range(count)])
        )
    return jnp.concatenate(parts, axis=0)


def head_scatter_relative(values):
    count = lax.axis_size("head")
    width = values.shape[0] // count
    total = values[:width].astype(jnp.float32)
    for shift in range(1, count):
        sent = values[(count - shift) * width : (count - shift + 1) * width]
        total = total + lax.ppermute(
            sent, "head", [(device, (device + shift) % count) for device in range(count)]
        ).astype(jnp.float32)
    return total


def local(
    tokens,
    doc_ids,
    gain_attn,
    a_weight,
    b_weight,
    out_weight,
    gain_ffn,
    gate_weight,
    up_weight,
    down_weight,
    cotangent,
):
    rows_dev, length = doc_ids.shape
    total_rows = rows_dev * length
    own_rows = tokens.shape[0]
    local_heads = out_weight.shape[0] // DH
    rank_all = RQ + 2 * RK
    x_own = tokens.astype(jnp.float32)
    inv_one = lax.rsqrt(jnp.mean(x_own * x_own, axis=-1, keepdims=True) + EPSILON)
    normed_one = (x_own * inv_one * gain_attn).astype(jnp.bfloat16)
    normed_all, grad_out_all = (
        head_all_gather(normed_one, 0),
        head_gather_relative(cotangent),
    )
    factor_a = jnp.dot(normed_all, a_weight, preferred_element_type=jnp.float32).reshape(
        total_rows, local_heads, rank_all
    )
    factor_b = jnp.dot(normed_all, b_weight, preferred_element_type=jnp.float32)
    cosine, sine = rope_tables(total_rows, length)
    basis_query = rotate(factor_b[:, : RQ * DH].reshape(total_rows, RQ, DH), cosine, sine)
    basis_key = rotate(
        factor_b[:, RQ * DH : (RQ + RK) * DH].reshape(total_rows, RK, DH), cosine, sine
    )
    basis_value = factor_b[:, (RQ + RK) * DH :].reshape(total_rows, RK, DH)
    coef_query = factor_a[:, :, :RQ]
    coef_key = factor_a[:, :, RQ : RQ + RK]
    coef_value = factor_a[:, :, RQ + RK :]
    queries = (jnp.einsum("thr,trd->thd", coef_query, basis_query, precision=PRECISE) / RQ).astype(
        jnp.bfloat16
    )
    key_rows = (jnp.einsum("thr,trd->thd", coef_key, basis_key, precision=PRECISE) / RK).astype(
        jnp.bfloat16
    )
    value_rows = (
        jnp.einsum("thr,trd->thd", coef_value, basis_value, precision=PRECISE) / RK
    ).astype(jnp.bfloat16)
    row_shape = (rows_dev, length, local_heads, DH)
    query_rows = queries.reshape(row_shape)
    keys_rows = key_rows.reshape(row_shape)
    values_rows = value_rows.reshape(row_shape)
    mixed_rows, log_total = lax.map(attend_row, (query_rows, keys_rows, values_rows, doc_ids))
    mixed = mixed_rows.reshape(total_rows, local_heads * DH)
    piece = lax.slice_in_dim(mixed, 0, lax.axis_size("head") * own_rows, axis=0)
    resid_own = x_own + head_reduce_scatter(
        jnp.dot(piece, out_weight, preferred_element_type=jnp.float32).astype(jnp.bfloat16), 0
    )
    inv_two = lax.rsqrt(jnp.mean(resid_own * resid_own, axis=-1, keepdims=True) + EPSILON)
    normed_two = (resid_own * inv_two * gain_ffn).astype(jnp.bfloat16)
    normed_two_all = head_gather_relative(normed_two)
    gate_act = jnp.dot(normed_two_all, gate_weight, preferred_element_type=jnp.float32)
    up_act = jnp.dot(normed_two_all, up_weight, preferred_element_type=jnp.float32)
    sigmoid_gate = jax.nn.sigmoid(gate_act)
    silu_gate = sigmoid_gate * gate_act
    hidden = (silu_gate * up_act).astype(jnp.bfloat16)
    piece = lax.slice_in_dim(hidden, 0, lax.axis_size("head") * own_rows, axis=0)
    output = (
        resid_own
        + head_scatter_relative(
            jnp.dot(piece, down_weight, preferred_element_type=jnp.float32).astype(jnp.bfloat16)
        )
    ).astype(jnp.bfloat16)
    grad_down = dot_first(hidden, grad_out_all)
    grad_hidden = dot_last(grad_out_all, down_weight)
    grad_gate_act = (
        grad_hidden * up_act * (sigmoid_gate * (1.0 + gate_act * (1.0 - sigmoid_gate)))
    ).astype(jnp.bfloat16)
    grad_up_act = (grad_hidden * silu_gate).astype(jnp.bfloat16)
    grad_gate = dot_first(normed_two_all, grad_gate_act)
    grad_up = dot_first(normed_two_all, grad_up_act)
    gate_piece = lax.slice_in_dim(grad_gate_act, 0, lax.axis_size("head") * own_rows, axis=0)
    up_piece = lax.slice_in_dim(grad_up_act, 0, lax.axis_size("head") * own_rows, axis=0)
    grad_normed_two = head_scatter_relative(
        (dot_last(gate_piece, gate_weight) + dot_last(up_piece, up_weight)).astype(jnp.bfloat16)
    )
    ffn_grads = (grad_gate.astype(jnp.bfloat16), grad_up.astype(jnp.bfloat16), grad_down.astype(jnp.bfloat16))
    ffn_grads, grad_normed_two = lax.optimization_barrier((ffn_grads, grad_normed_two))
    grad_gate, grad_up, grad_down = lax.psum(ffn_grads, "dp")
    resid_part, grad_gain_ffn_own = norm_backward(resid_own, inv_two, gain_ffn, grad_normed_two)
    grad_resid = cotangent.astype(jnp.float32) + resid_part
    output, grad_resid = lax.optimization_barrier((output, grad_resid))
    grad_branch = head_all_gather(grad_resid.astype(jnp.bfloat16), 0)
    grad_mixed = dot_last(grad_branch, out_weight).astype(jnp.bfloat16)
    grad_out = dot_first(mixed, grad_branch)
    grad_query_rows, grad_key_rows, grad_value_rows = lax.map(
        attend_back,
        (query_rows, keys_rows, values_rows, doc_ids, log_total, grad_mixed.reshape(row_shape)),
    )
    head_shape = (total_rows, local_heads, DH)
    grad_query = rounded(grad_query_rows.reshape(head_shape))
    grad_key = rounded(grad_key_rows.reshape(head_shape))
    grad_value = rounded(grad_value_rows.reshape(head_shape))
    grad_coef_query = jnp.einsum("thd,trd->thr", grad_query, basis_query, precision=PRECISE) / RQ
    grad_coef_key = jnp.einsum("thd,trd->thr", grad_key, basis_key, precision=PRECISE) / RK
    grad_coef_value = jnp.einsum("thd,trd->thr", grad_value, basis_value, precision=PRECISE) / RK
    grad_basis_query = unrotate(
        jnp.einsum("thr,thd->trd", coef_query, grad_query, precision=PRECISE) / RQ, cosine, sine
    )
    grad_basis_key = unrotate(
        jnp.einsum("thr,thd->trd", coef_key, grad_key, precision=PRECISE) / RK, cosine, sine
    )
    grad_basis_value = jnp.einsum("thr,thd->trd", coef_value, grad_value, precision=PRECISE) / RK
    grad_factor_a = (
        jnp.concatenate([grad_coef_query, grad_coef_key, grad_coef_value], axis=-1)
        .reshape(total_rows, local_heads * rank_all)
        .astype(jnp.bfloat16)
    )
    grad_factor_b = jnp.concatenate(
        [
            grad_basis_query.reshape(total_rows, RQ * DH),
            grad_basis_key.reshape(total_rows, RK * DH),
            grad_basis_value.reshape(total_rows, RK * DH),
        ],
        axis=-1,
    )
    head_count = lax.axis_size("head")
    basis_cols = grad_factor_b.shape[1] // head_count
    factor_cols = head_reduce_scatter(grad_factor_b.astype(jnp.bfloat16), 1).astype(jnp.bfloat16)
    weight_cols = lax.dynamic_slice_in_dim(
        b_weight, lax.axis_index("head") * basis_cols, basis_cols, axis=1
    )
    piece = grad_factor_a
    grad_normed_one = head_reduce_scatter(
        (dot_last(piece, a_weight) + dot_last(factor_cols, weight_cols)).astype(jnp.bfloat16), 0
    )
    input_part, grad_gain_attn_own = norm_backward(x_own, inv_one, gain_attn, grad_normed_one)
    input_grad = grad_resid + input_part
    grad_a = dot_first(normed_all, grad_factor_a)
    grad_b_cols = dot_first(normed_all, factor_cols)

    features = grad_gain_attn_own.shape[0]
    gain_rows = -(-2 * features // basis_cols)
    gains = jnp.pad(
        jnp.concatenate([grad_gain_attn_own, grad_gain_ffn_own]),
        (0, gain_rows * basis_cols - 2 * features),
    ).reshape(gain_rows, basis_cols)
    tail = (
        grad_a.astype(jnp.bfloat16),
        grad_out.astype(jnp.bfloat16),
        jnp.concatenate([grad_b_cols, gains], axis=0).astype(jnp.bfloat16),
    )
    tail, (grad_gate, grad_up, grad_down) = lax.optimization_barrier(
        (tail, (grad_gate, grad_up, grad_down))
    )
    sizes = [part.size for part in tail]
    summed = dp_all_reduce(jnp.concatenate([part.reshape(-1) for part in tail]))
    grad_a, grad_out, packed = (
        summed[sum(sizes[:index]) : sum(sizes[: index + 1])].reshape(part.shape)
        for index, part in enumerate(tail)
    )
    grad_out, grad_gate, grad_up, grad_down = (
        grad_out.astype(jnp.float32),
        grad_gate.astype(jnp.float32),
        grad_up.astype(jnp.float32),
        grad_down.astype(jnp.float32),
    )
    grad_a = grad_a.astype(jnp.float32)
    packed = lax.all_gather(packed, "head", axis=1, tiled=True).astype(jnp.float32)
    grad_b = packed[: grad_b_cols.shape[0]]
    gains = jnp.sum(
        packed[grad_b_cols.shape[0] :].reshape(gain_rows, head_count, basis_cols), axis=1
    ).reshape(-1)
    grad_gain_attn, grad_gain_ffn = gains[:features], gains[features : 2 * features]
    return (
        output,
        input_grad,
        grad_gain_attn,
        grad_a,
        grad_b,
        grad_out,
        grad_gain_ffn,
        grad_gate,
        grad_up,
        grad_down,
    )


def solution(mesh):
    return jax.shard_map(
        local,
        mesh=mesh,
        in_specs=(
            P(("dp", "head"), None),
            P("dp", None),
            P(),
            P(None, "head"),
            P(),
            P("head", None),
            P(),
            P(None, "head"),
            P(None, "head"),
            P("head", None),
            P(("dp", "head"), None),
        ),
        out_specs=(
            P(("dp", "head"), None),
            P(("dp", "head"), None),
            P(),
            P(None, "head"),
            P(),
            P("head", None),
            P(),
            P(None, "head"),
            P(None, "head"),
            P("head", None),
        ),
        check_vma=False,
    )
```

```python
import math

import jax
import jax.numpy as jnp
from jax import lax
from jax.sharding import PartitionSpec as P

DH = 64
RQ = 6
RK = 2


EPSILON = 1e-06
MASKED = -1e30
PRECISE = lax.Precision.HIGHEST


def rope_tables(total_rows, length):
    half_depth = DH // 2
    position = (jnp.arange(total_rows, dtype=jnp.int32) % length).astype(jnp.float32)
    frequency = jnp.exp(jnp.arange(half_depth, dtype=jnp.float32) * (-2.0 * math.log(10000.0) / DH))
    angle = position[:, None] * frequency[None, :]
    return (jnp.cos(angle), jnp.sin(angle))


def rotate(basis, cosine, sine):
    half_depth = basis.shape[-1] // 2
    first_half = basis[..., :half_depth]
    second_half = basis[..., half_depth:]
    cosine_row = cosine[:, None, :]
    sine_row = sine[:, None, :]
    return jnp.concatenate(
        [
            first_half * cosine_row - second_half * sine_row,
            second_half * cosine_row + first_half * sine_row,
        ],
        axis=-1,
    )


def unrotate(grad_basis, cosine, sine):
    half_depth = grad_basis.shape[-1] // 2
    first_half = grad_basis[..., :half_depth]
    second_half = grad_basis[..., half_depth:]
    cosine_row = cosine[:, None, :]
    sine_row = sine[:, None, :]
    return jnp.concatenate(
        [
            first_half * cosine_row + second_half * sine_row,
            second_half * cosine_row - first_half * sine_row,
        ],
        axis=-1,
    )


def dot_last(left, right):
    return lax.dot_general(
        left, right, (((1,), (1,)), ((), ())), preferred_element_type=jnp.float32
    )


def dot_first(left, right):
    return lax.dot_general(
        left, right, (((0,), (0,)), ((), ())), preferred_element_type=jnp.float32
    )


def norm_backward(inputs, inverse, gain, grad_normed):
    scaled = gain * grad_normed
    inner = jnp.mean(scaled * inputs, axis=-1, keepdims=True)
    grad_inputs = inverse * scaled - inputs * (inverse * inverse * inverse) * inner
    grad_gain = jnp.sum(grad_normed * inputs * inverse, axis=0)
    return (grad_inputs, grad_gain)


def block_scores(queries, key_rows, doc_row, first_row, last_row):
    position = jnp.arange(last_row, dtype=jnp.int32)
    allowed = (doc_row[first_row:last_row, None] == doc_row[None, :last_row]) & (
        position[None, :] <= position[first_row:last_row, None]
    )
    score_scale = 1.0 / math.sqrt(queries.shape[2])
    scores = (
        jnp.einsum(
            "qhd,khd->hqk",
            queries[first_row:last_row],
            key_rows[:last_row],
            preferred_element_type=jnp.float32,
        )
        * score_scale
    )
    return jnp.where(allowed[None], scores, MASKED)


def attend_row(row_item):
    queries, key_rows, value_rows, doc_row = row_item
    length = queries.shape[0]
    block_rows = min(512, length)
    mixed_parts = []
    total_parts = []
    for first_row in range(0, length, block_rows):
        last_row = first_row + block_rows
        scores = block_scores(queries, key_rows, doc_row, first_row, last_row)
        row_peak = jnp.max(scores, axis=-1, keepdims=True)
        exponent = jnp.exp(scores - row_peak)
        row_total = jnp.sum(exponent, axis=-1, keepdims=True)
        weights = (exponent / row_total).astype(jnp.bfloat16)
        mixed_parts.append(
            jnp.einsum(
                "hqk,khd->qhd", weights, value_rows[:last_row], preferred_element_type=jnp.float32
            ).astype(jnp.bfloat16)
        )
        total_parts.append(row_peak[..., 0] + jnp.log(row_total[..., 0]))
    return (jnp.concatenate(mixed_parts, axis=0), jnp.concatenate(total_parts, axis=1))


def attend_back(row_item):
    queries, key_rows, value_rows, doc_row, log_total, grad_mixed = row_item
    length = queries.shape[0]
    block_rows = min(512, length)
    score_scale = 1.0 / math.sqrt(queries.shape[2])
    grad_query_parts = []
    grad_keys = jnp.zeros(key_rows.shape, jnp.float32)
    grad_values = jnp.zeros(value_rows.shape, jnp.float32)
    for first_row in range(0, length, block_rows):
        last_row = first_row + block_rows
        scores = block_scores(queries, key_rows, doc_row, first_row, last_row)
        weights = jnp.exp(scores - log_total[:, first_row:last_row, None])
        grad_weights = jnp.einsum(
            "qhd,khd->hqk",
            grad_mixed[first_row:last_row],
            value_rows[:last_row],
            preferred_element_type=jnp.float32,
        )
        inner = jnp.sum(weights * grad_weights, axis=-1, keepdims=True)
        grad_scores = (weights * (grad_weights - inner)).astype(jnp.bfloat16)
        grad_query_parts.append(
            jnp.einsum(
                "hqk,khd->qhd", grad_scores, key_rows[:last_row], preferred_element_type=jnp.float32
            )
            * score_scale
        )
        padding = ((0, length - last_row), (0, 0), (0, 0))
        key_part = (
            jnp.einsum(
                "hqk,qhd->khd",
                grad_scores,
                queries[first_row:last_row],
                preferred_element_type=jnp.float32,
            )
            * score_scale
        )
        value_part = jnp.einsum(
            "hqk,qhd->khd",
            weights.astype(jnp.bfloat16),
            grad_mixed[first_row:last_row],
            preferred_element_type=jnp.float32,
        )
        grad_keys = grad_keys + jnp.pad(key_part, padding)
        grad_values = grad_values + jnp.pad(value_part, padding)
    return (jnp.concatenate(grad_query_parts, axis=0), grad_keys, grad_values)


def rounded(values_in):
    return lax.optimization_barrier(values_in.astype(jnp.bfloat16)).astype(jnp.float32)


def head_reduce_scatter(values, axis):
    count = lax.axis_size("head")
    own = lax.axis_index("head")
    width = values.shape[axis] // count
    total = lax.dynamic_slice_in_dim(values, own * width, width, axis=axis).astype(jnp.float32)
    for shift in range(1, count):
        sent = lax.dynamic_slice_in_dim(values, ((own + shift) % count) * width, width, axis=axis)
        total = total + lax.ppermute(
            sent, "head", [(device, (device + shift) % count) for device in range(count)]
        ).astype(jnp.float32)
    return total


def head_all_gather(values, axis):
    count = lax.axis_size("head")
    own = lax.axis_index("head")
    width = values.shape[axis]
    shape = list(values.shape)
    shape[axis] = width * count
    gathered = lax.dynamic_update_slice_in_dim(
        jnp.zeros(shape, values.dtype), values, own * width, axis=axis
    )
    for shift in range(1, count):
        arrived = lax.ppermute(
            values, "head", [(device, (device + shift) % count) for device in range(count)]
        )
        gathered = lax.dynamic_update_slice_in_dim(
            gathered, arrived, ((own - shift) % count) * width, axis=axis
        )
    return gathered


def dp_all_reduce(flat):
    count = lax.axis_size("dp")
    own = lax.axis_index("dp")
    steps = count.bit_length() - 1
    assert count == 1 << steps
    width = -(-flat.shape[0] // (count * 128)) * 128
    blocks = jnp.pad(flat, (0, count * width - flat.shape[0])).reshape((2,) * steps + (width,))
    kept = blocks.astype(jnp.float32)
    for step in range(steps):
        axis = steps - 1 - step
        bit = (own >> step) & 1
        sent = lax.dynamic_index_in_dim(kept, 1 - bit, axis, keepdims=False)
        kept = lax.dynamic_index_in_dim(kept, bit, axis, keepdims=False)
        pairs = [(device, device ^ (1 << step)) for device in range(count)]
        kept = kept + lax.ppermute(sent.astype(jnp.bfloat16), "dp", pairs).astype(jnp.float32)
    whole = kept.astype(jnp.bfloat16)[None]
    for step in reversed(range(steps)):
        bit = (own >> step) & 1
        pairs = [(device, device ^ (1 << step)) for device in range(count)]
        arrived = lax.ppermute(whole, "dp", pairs)
        low_half = jnp.where(bit == 0, whole, arrived)
        high_half = jnp.where(bit == 0, arrived, whole)
        whole = jnp.stack([low_half, high_half], axis=1).reshape((-1,) + whole.shape[1:])
    return whole.reshape(-1)[: flat.shape[0]]


def head_gather_relative(values):
    count = lax.axis_size("head")
    parts = [values]
    for shift in range(1, count):
        parts.append(
            lax.ppermute(values, "head", [(device, (device + shift) % count) for device in range(count)])
        )
    return jnp.concatenate(parts, axis=0)


def head_scatter_relative(values):
    count = lax.axis_size("head")
    width = values.shape[0] // count
    total = values[:width].astype(jnp.float32)
    for shift in range(1, count):
        sent = values[(count - shift) * width : (count - shift + 1) * width]
        total = total + lax.ppermute(
            sent, "head", [(device, (device + shift) % count) for device in range(count)]
        ).astype(jnp.float32)
    return total


def map_rows(step, items):
    outs = [step(tuple(item[row] for item in items)) for row in range(items[0].shape[0])]
    return tuple(jnp.stack(parts) for parts in zip(*outs))


def local(
    tokens,
    doc_ids,
    gain_attn,
    a_weight,
    b_weight,
    out_weight,
    gain_ffn,
    gate_weight,
    up_weight,
    down_weight,
    cotangent,
):
    rows_dev, length = doc_ids.shape
    total_rows = rows_dev * length
    own_rows = tokens.shape[0]
    local_heads = out_weight.shape[0] // DH
    rank_all = RQ + 2 * RK
    x_own = tokens.astype(jnp.float32)
    inv_one = lax.rsqrt(jnp.mean(x_own * x_own, axis=-1, keepdims=True) + EPSILON)
    normed_one = (x_own * inv_one * gain_attn).astype(jnp.bfloat16)
    normed_all, grad_out_all = (
        head_all_gather(normed_one, 0),
        head_gather_relative(cotangent),
    )
    factor_a = jnp.dot(normed_all, a_weight, preferred_element_type=jnp.float32).reshape(
        total_rows, local_heads, rank_all
    )
    factor_b = jnp.dot(normed_all, b_weight, preferred_element_type=jnp.float32)
    cosine, sine = rope_tables(total_rows, length)
    basis_query = rotate(factor_b[:, : RQ * DH].reshape(total_rows, RQ, DH), cosine, sine)
    basis_key = rotate(
        factor_b[:, RQ * DH : (RQ + RK) * DH].reshape(total_rows, RK, DH), cosine, sine
    )
    basis_value = factor_b[:, (RQ + RK) * DH :].reshape(total_rows, RK, DH)
    coef_query = factor_a[:, :, :RQ]
    coef_key = factor_a[:, :, RQ : RQ + RK]
    coef_value = factor_a[:, :, RQ + RK :]
    queries = (jnp.einsum("thr,trd->thd", coef_query, basis_query, precision=PRECISE) / RQ).astype(
        jnp.bfloat16
    )
    key_rows = (jnp.einsum("thr,trd->thd", coef_key, basis_key, precision=PRECISE) / RK).astype(
        jnp.bfloat16
    )
    value_rows = (
        jnp.einsum("thr,trd->thd", coef_value, basis_value, precision=PRECISE) / RK
    ).astype(jnp.bfloat16)
    row_shape = (rows_dev, length, local_heads, DH)
    query_rows = queries.reshape(row_shape)
    keys_rows = key_rows.reshape(row_shape)
    values_rows = value_rows.reshape(row_shape)
    mixed_rows, log_total = map_rows(attend_row, (query_rows, keys_rows, values_rows, doc_ids))
    mixed = mixed_rows.reshape(total_rows, local_heads * DH)
    piece = lax.slice_in_dim(mixed, 0, lax.axis_size("head") * own_rows, axis=0)
    resid_own = x_own + head_reduce_scatter(
        jnp.dot(piece, out_weight, preferred_element_type=jnp.float32).astype(jnp.bfloat16), 0
    )
    inv_two = lax.rsqrt(jnp.mean(resid_own * resid_own, axis=-1, keepdims=True) + EPSILON)
    normed_two = (resid_own * inv_two * gain_ffn).astype(jnp.bfloat16)
    normed_two_all = head_gather_relative(normed_two)
    gate_act = jnp.dot(normed_two_all, gate_weight, preferred_element_type=jnp.float32)
    up_act = jnp.dot(normed_two_all, up_weight, preferred_element_type=jnp.float32)
    sigmoid_gate = jax.nn.sigmoid(gate_act)
    silu_gate = sigmoid_gate * gate_act
    hidden = (silu_gate * up_act).astype(jnp.bfloat16)
    piece = lax.slice_in_dim(hidden, 0, lax.axis_size("head") * own_rows, axis=0)
    output = (
        resid_own
        + head_scatter_relative(
            jnp.dot(piece, down_weight, preferred_element_type=jnp.float32).astype(jnp.bfloat16)
        )
    ).astype(jnp.bfloat16)
    grad_down = dot_first(hidden, grad_out_all)
    grad_hidden = dot_last(grad_out_all, down_weight)
    grad_gate_act = (
        grad_hidden * up_act * (sigmoid_gate * (1.0 + gate_act * (1.0 - sigmoid_gate)))
    ).astype(jnp.bfloat16)
    grad_up_act = (grad_hidden * silu_gate).astype(jnp.bfloat16)
    grad_gate = dot_first(normed_two_all, grad_gate_act)
    grad_up = dot_first(normed_two_all, grad_up_act)
    gate_piece = lax.slice_in_dim(grad_gate_act, 0, lax.axis_size("head") * own_rows, axis=0)
    up_piece = lax.slice_in_dim(grad_up_act, 0, lax.axis_size("head") * own_rows, axis=0)
    grad_normed_two = head_scatter_relative(
        (dot_last(gate_piece, gate_weight) + dot_last(up_piece, up_weight)).astype(jnp.bfloat16)
    )
    ffn_grads = (grad_gate.astype(jnp.bfloat16), grad_up.astype(jnp.bfloat16), grad_down.astype(jnp.bfloat16))
    ffn_grads, grad_normed_two = lax.optimization_barrier((ffn_grads, grad_normed_two))
    grad_gate, grad_up, grad_down = lax.psum(ffn_grads, "dp")
    resid_part, grad_gain_ffn_own = norm_backward(resid_own, inv_two, gain_ffn, grad_normed_two)
    grad_resid = cotangent.astype(jnp.float32) + resid_part
    output, grad_resid = lax.optimization_barrier((output, grad_resid))
    grad_branch = head_all_gather(grad_resid.astype(jnp.bfloat16), 0)
    grad_mixed = dot_last(grad_branch, out_weight).astype(jnp.bfloat16)
    grad_out = dp_all_reduce(dot_first(mixed, grad_branch).astype(jnp.bfloat16).reshape(-1))
    grad_query_rows, grad_key_rows, grad_value_rows = map_rows(
        attend_back,
        (query_rows, keys_rows, values_rows, doc_ids, log_total, grad_mixed.reshape(row_shape)),
    )
    head_shape = (total_rows, local_heads, DH)
    grad_query = rounded(grad_query_rows.reshape(head_shape))
    grad_key = rounded(grad_key_rows.reshape(head_shape))
    grad_value = rounded(grad_value_rows.reshape(head_shape))
    grad_coef_query = jnp.einsum("thd,trd->thr", grad_query, basis_query, precision=PRECISE) / RQ
    grad_coef_key = jnp.einsum("thd,trd->thr", grad_key, basis_key, precision=PRECISE) / RK
    grad_coef_value = jnp.einsum("thd,trd->thr", grad_value, basis_value, precision=PRECISE) / RK
    grad_basis_query = unrotate(
        jnp.einsum("thr,thd->trd", coef_query, grad_query, precision=PRECISE) / RQ, cosine, sine
    )
    grad_basis_key = unrotate(
        jnp.einsum("thr,thd->trd", coef_key, grad_key, precision=PRECISE) / RK, cosine, sine
    )
    grad_basis_value = jnp.einsum("thr,thd->trd", coef_value, grad_value, precision=PRECISE) / RK
    grad_factor_a = (
        jnp.concatenate([grad_coef_query, grad_coef_key, grad_coef_value], axis=-1)
        .reshape(total_rows, local_heads * rank_all)
        .astype(jnp.bfloat16)
    )
    grad_factor_b = jnp.concatenate(
        [
            grad_basis_query.reshape(total_rows, RQ * DH),
            grad_basis_key.reshape(total_rows, RK * DH),
            grad_basis_value.reshape(total_rows, RK * DH),
        ],
        axis=-1,
    )
    head_count = lax.axis_size("head")
    basis_cols = grad_factor_b.shape[1] // head_count
    factor_cols = head_reduce_scatter(grad_factor_b.astype(jnp.bfloat16), 1).astype(jnp.bfloat16)
    weight_cols = lax.dynamic_slice_in_dim(
        b_weight, lax.axis_index("head") * basis_cols, basis_cols, axis=1
    )
    piece = grad_factor_a
    grad_normed_one = head_reduce_scatter(
        (dot_last(piece, a_weight) + dot_last(factor_cols, weight_cols)).astype(jnp.bfloat16), 0
    )
    input_part, grad_gain_attn_own = norm_backward(x_own, inv_one, gain_attn, grad_normed_one)
    input_grad = grad_resid + input_part
    grad_a = dot_first(normed_all, grad_factor_a)
    grad_b_cols = dot_first(normed_all, factor_cols)

    features = grad_gain_attn_own.shape[0]
    gain_rows = -(-2 * features // basis_cols)
    gains = jnp.pad(
        jnp.concatenate([grad_gain_attn_own, grad_gain_ffn_own]),
        (0, gain_rows * basis_cols - 2 * features),
    ).reshape(gain_rows, basis_cols)
    grad_out = grad_out.reshape(out_weight.shape)
    tail = (
        grad_a.astype(jnp.bfloat16),
        jnp.concatenate([grad_b_cols, gains], axis=0).astype(jnp.bfloat16),
    )
    tail, (grad_gate, grad_up, grad_down) = lax.optimization_barrier(
        (tail, (grad_gate, grad_up, grad_down))
    )
    sizes = [part.size for part in tail]
    summed = dp_all_reduce(jnp.concatenate([part.reshape(-1) for part in tail]))
    grad_a, packed = (
        summed[sum(sizes[:index]) : sum(sizes[: index + 1])].reshape(part.shape)
        for index, part in enumerate(tail)
    )
    grad_out, grad_gate, grad_up, grad_down = (
        grad_out.astype(jnp.float32),
        grad_gate.astype(jnp.float32),
        grad_up.astype(jnp.float32),
        grad_down.astype(jnp.float32),
    )
    grad_a = grad_a.astype(jnp.float32)
    packed = lax.all_gather(packed, "head", axis=1, tiled=True).astype(jnp.float32)
    grad_b = packed[: grad_b_cols.shape[0]]
    gains = jnp.sum(
        packed[grad_b_cols.shape[0] :].reshape(gain_rows, head_count, basis_cols), axis=1
    ).reshape(-1)
    grad_gain_attn, grad_gain_ffn = gains[:features], gains[features : 2 * features]
    return (
        output,
        input_grad,
        grad_gain_attn,
        grad_a,
        grad_b,
        grad_out,
        grad_gain_ffn,
        grad_gate,
        grad_up,
        grad_down,
    )


def solution(mesh):
    return jax.shard_map(
        local,
        mesh=mesh,
        in_specs=(
            P(("dp", "head"), None),
            P("dp", None),
            P(),
            P(None, "head"),
            P(),
            P("head", None),
            P(),
            P(None, "head"),
            P(None, "head"),
            P("head", None),
            P(("dp", "head"), None),
        ),
        out_specs=(
            P(("dp", "head"), None),
            P(("dp", "head"), None),
            P(),
            P(None, "head"),
            P(),
            P("head", None),
            P(),
            P(None, "head"),
            P(None, "head"),
            P("head", None),
        ),
        check_vma=False,
    )
```

```python
import math

import jax
import jax.numpy as jnp
from jax import lax
from jax.sharding import PartitionSpec as P

DH = 64
RQ = 6
RK = 2


EPSILON = 1e-06
MASKED = -1e30
PRECISE = lax.Precision.HIGHEST


def rope_tables(total_rows, length):
    half_depth = DH // 2
    position = (jnp.arange(total_rows, dtype=jnp.int32) % length).astype(jnp.float32)
    frequency = jnp.exp(jnp.arange(half_depth, dtype=jnp.float32) * (-2.0 * math.log(10000.0) / DH))
    angle = position[:, None] * frequency[None, :]
    return (jnp.cos(angle), jnp.sin(angle))


def rotate(basis, cosine, sine):
    half_depth = basis.shape[-1] // 2
    first_half = basis[..., :half_depth]
    second_half = basis[..., half_depth:]
    cosine_row = cosine[:, None, :]
    sine_row = sine[:, None, :]
    return jnp.concatenate(
        [
            first_half * cosine_row - second_half * sine_row,
            second_half * cosine_row + first_half * sine_row,
        ],
        axis=-1,
    )


def unrotate(grad_basis, cosine, sine):
    half_depth = grad_basis.shape[-1] // 2
    first_half = grad_basis[..., :half_depth]
    second_half = grad_basis[..., half_depth:]
    cosine_row = cosine[:, None, :]
    sine_row = sine[:, None, :]
    return jnp.concatenate(
        [
            first_half * cosine_row + second_half * sine_row,
            second_half * cosine_row - first_half * sine_row,
        ],
        axis=-1,
    )


def dot_last(left, right):
    return lax.dot_general(
        left, right, (((1,), (1,)), ((), ())), preferred_element_type=jnp.float32
    )


def dot_first(left, right):
    return lax.dot_general(
        left, right, (((0,), (0,)), ((), ())), preferred_element_type=jnp.float32
    )


def norm_backward(inputs, inverse, gain, grad_normed):
    scaled = gain * grad_normed
    inner = jnp.mean(scaled * inputs, axis=-1, keepdims=True)
    grad_inputs = inverse * scaled - inputs * (inverse * inverse * inverse) * inner
    grad_gain = jnp.sum(grad_normed * inputs * inverse, axis=0)
    return (grad_inputs, grad_gain)


def block_scores(queries, key_rows, doc_row, first_row, last_row):
    position = jnp.arange(last_row, dtype=jnp.int32)
    allowed = (doc_row[first_row:last_row, None] == doc_row[None, :last_row]) & (
        position[None, :] <= position[first_row:last_row, None]
    )
    score_scale = 1.0 / math.sqrt(queries.shape[2])
    scores = (
        jnp.einsum(
            "qhd,khd->hqk",
            queries[first_row:last_row],
            key_rows[:last_row],
            preferred_element_type=jnp.float32,
        )
        * score_scale
    )
    return jnp.where(allowed[None], scores, MASKED)


def attend_row(row_item):
    queries, key_rows, value_rows, doc_row = row_item
    length = queries.shape[0]
    block_rows = min(512, length)
    mixed_parts = []
    total_parts = []
    for first_row in range(0, length, block_rows):
        last_row = first_row + block_rows
        scores = block_scores(queries, key_rows, doc_row, first_row, last_row)
        row_peak = jnp.max(scores, axis=-1, keepdims=True)
        exponent = jnp.exp(scores - row_peak)
        row_total = jnp.sum(exponent, axis=-1, keepdims=True)
        weights = (exponent / row_total).astype(jnp.bfloat16)
        mixed_parts.append(
            jnp.einsum(
                "hqk,khd->qhd", weights, value_rows[:last_row], preferred_element_type=jnp.float32
            ).astype(jnp.bfloat16)
        )
        total_parts.append(row_peak[..., 0] + jnp.log(row_total[..., 0]))
    return (jnp.concatenate(mixed_parts, axis=0), jnp.concatenate(total_parts, axis=1))


def attend_back(row_item):
    queries, key_rows, value_rows, doc_row, log_total, grad_mixed = row_item
    length = queries.shape[0]
    block_rows = min(512, length)
    score_scale = 1.0 / math.sqrt(queries.shape[2])
    grad_query_parts = []
    grad_keys = jnp.zeros(key_rows.shape, jnp.float32)
    grad_values = jnp.zeros(value_rows.shape, jnp.float32)
    for first_row in range(0, length, block_rows):
        last_row = first_row + block_rows
        scores = block_scores(queries, key_rows, doc_row, first_row, last_row)
        weights = jnp.exp(scores - log_total[:, first_row:last_row, None])
        grad_weights = jnp.einsum(
            "qhd,khd->hqk",
            grad_mixed[first_row:last_row],
            value_rows[:last_row],
            preferred_element_type=jnp.float32,
        )
        inner = jnp.sum(weights * grad_weights, axis=-1, keepdims=True)
        grad_scores = (weights * (grad_weights - inner)).astype(jnp.bfloat16)
        grad_query_parts.append(
            jnp.einsum(
                "hqk,khd->qhd", grad_scores, key_rows[:last_row], preferred_element_type=jnp.float32
            )
            * score_scale
        )
        padding = ((0, length - last_row), (0, 0), (0, 0))
        key_part = (
            jnp.einsum(
                "hqk,qhd->khd",
                grad_scores,
                queries[first_row:last_row],
                preferred_element_type=jnp.float32,
            )
            * score_scale
        )
        value_part = jnp.einsum(
            "hqk,qhd->khd",
            weights.astype(jnp.bfloat16),
            grad_mixed[first_row:last_row],
            preferred_element_type=jnp.float32,
        )
        grad_keys = grad_keys + jnp.pad(key_part, padding)
        grad_values = grad_values + jnp.pad(value_part, padding)
    return (jnp.concatenate(grad_query_parts, axis=0), grad_keys, grad_values)


def rounded(values_in):
    return lax.optimization_barrier(values_in.astype(jnp.bfloat16)).astype(jnp.float32)


def head_reduce_scatter(values, axis):
    count = lax.axis_size("head")
    own = lax.axis_index("head")
    width = values.shape[axis] // count
    total = lax.dynamic_slice_in_dim(values, own * width, width, axis=axis).astype(jnp.float32)
    for shift in range(1, count):
        sent = lax.dynamic_slice_in_dim(values, ((own + shift) % count) * width, width, axis=axis)
        total = total + lax.ppermute(
            sent, "head", [(device, (device + shift) % count) for device in range(count)]
        ).astype(jnp.float32)
    return total


def head_all_gather(values, axis):
    count = lax.axis_size("head")
    own = lax.axis_index("head")
    width = values.shape[axis]
    shape = list(values.shape)
    shape[axis] = width * count
    gathered = lax.dynamic_update_slice_in_dim(
        jnp.zeros(shape, values.dtype), values, own * width, axis=axis
    )
    for shift in range(1, count):
        arrived = lax.ppermute(
            values, "head", [(device, (device + shift) % count) for device in range(count)]
        )
        gathered = lax.dynamic_update_slice_in_dim(
            gathered, arrived, ((own - shift) % count) * width, axis=axis
        )
    return gathered


def dp_all_reduce(flat):
    count = lax.axis_size("dp")
    own = lax.axis_index("dp")
    steps = count.bit_length() - 1
    assert count == 1 << steps
    width = -(-flat.shape[0] // (count * 128)) * 128
    blocks = jnp.pad(flat, (0, count * width - flat.shape[0])).reshape((2,) * steps + (width,))
    kept = blocks.astype(jnp.float32)
    for step in range(steps):
        axis = steps - 1 - step
        bit = (own >> step) & 1
        sent = lax.dynamic_index_in_dim(kept, 1 - bit, axis, keepdims=False)
        kept = lax.dynamic_index_in_dim(kept, bit, axis, keepdims=False)
        pairs = [(device, device ^ (1 << step)) for device in range(count)]
        kept = kept + lax.ppermute(sent.astype(jnp.bfloat16), "dp", pairs).astype(jnp.float32)
    whole = kept.astype(jnp.bfloat16)[None]
    for step in reversed(range(steps)):
        bit = (own >> step) & 1
        pairs = [(device, device ^ (1 << step)) for device in range(count)]
        arrived = lax.ppermute(whole, "dp", pairs)
        low_half = jnp.where(bit == 0, whole, arrived)
        high_half = jnp.where(bit == 0, arrived, whole)
        whole = jnp.stack([low_half, high_half], axis=1).reshape((-1,) + whole.shape[1:])
    return whole.reshape(-1)[: flat.shape[0]]


def head_gather_relative(values):
    count = lax.axis_size("head")
    parts = [values]
    for shift in range(1, count):
        parts.append(
            lax.ppermute(values, "head", [(device, (device + shift) % count) for device in range(count)])
        )
    return jnp.concatenate(parts, axis=0)


def head_scatter_relative(values):
    count = lax.axis_size("head")
    width = values.shape[0] // count
    total = values[:width].astype(jnp.float32)
    for shift in range(1, count):
        sent = values[(count - shift) * width : (count - shift + 1) * width]
        total = total + lax.ppermute(
            sent, "head", [(device, (device + shift) % count) for device in range(count)]
        ).astype(jnp.float32)
    return total


def map_rows(step, items):
    outs = [step(tuple(item[row] for item in items)) for row in range(items[0].shape[0])]
    return tuple(jnp.stack(parts) for parts in zip(*outs))


def turn(block, cosine, sine):
    half_depth = block.shape[-1] // 2
    first_half, second_half = block[:, :half_depth], block[:, half_depth:]
    return jnp.concatenate(
        [first_half * cosine - second_half * sine, second_half * cosine + first_half * sine], axis=1
    )


def unturn(block, cosine, sine):
    half_depth = block.shape[-1] // 2
    first_half, second_half = block[:, :half_depth], block[:, half_depth:]
    return jnp.concatenate(
        [first_half * cosine + second_half * sine, second_half * cosine - first_half * sine], axis=1
    )


def local(
    tokens,
    doc_ids,
    gain_attn,
    a_weight,
    b_weight,
    out_weight,
    gain_ffn,
    gate_weight,
    up_weight,
    down_weight,
    cotangent,
):
    rows_dev, length = doc_ids.shape
    total_rows = rows_dev * length
    own_rows = tokens.shape[0]
    local_heads = out_weight.shape[0] // DH
    rank_all = RQ + 2 * RK
    x_own = tokens.astype(jnp.float32)
    inv_one = lax.rsqrt(jnp.mean(x_own * x_own, axis=-1, keepdims=True) + EPSILON)
    normed_one = (x_own * inv_one * gain_attn).astype(jnp.bfloat16)
    normed_all, grad_out_all = (
        head_all_gather(normed_one, 0),
        head_gather_relative(cotangent),
    )
    factor_a = jnp.dot(normed_all, a_weight, preferred_element_type=jnp.float32)
    factor_b = jnp.dot(normed_all, b_weight, preferred_element_type=jnp.float32)
    cosine, sine = rope_tables(total_rows, length)
    basis_query = [
        turn(factor_b[:, rank * DH : (rank + 1) * DH], cosine, sine) for rank in range(RQ)
    ]
    basis_key = [
        turn(factor_b[:, (RQ + rank) * DH : (RQ + rank + 1) * DH], cosine, sine)
        for rank in range(RK)
    ]
    basis_value = [
        factor_b[:, (RQ + RK + rank) * DH : (RQ + RK + rank + 1) * DH] for rank in range(RK)
    ]
    coef = [
        [factor_a[:, head * rank_all + column] [:, None] for column in range(rank_all)]
        for head in range(local_heads)
    ]

    def combine(bases, offset):
        return jnp.stack(
            [
                sum(coef[head][offset + rank] * bases[rank] for rank in range(len(bases)))
                / len(bases)
                for head in range(local_heads)
            ],
            axis=1,
        ).astype(jnp.bfloat16)

    queries = combine(basis_query, 0)
    key_rows = combine(basis_key, RQ)
    value_rows = combine(basis_value, RQ + RK)
    row_shape = (rows_dev, length, local_heads, DH)
    query_rows = queries.reshape(row_shape)
    keys_rows = key_rows.reshape(row_shape)
    values_rows = value_rows.reshape(row_shape)
    mixed_rows, log_total = map_rows(attend_row, (query_rows, keys_rows, values_rows, doc_ids))
    mixed = mixed_rows.reshape(total_rows, local_heads * DH)
    piece = lax.slice_in_dim(mixed, 0, lax.axis_size("head") * own_rows, axis=0)
    resid_own = x_own + head_reduce_scatter(
        jnp.dot(piece, out_weight, preferred_element_type=jnp.float32).astype(jnp.bfloat16), 0
    )
    inv_two = lax.rsqrt(jnp.mean(resid_own * resid_own, axis=-1, keepdims=True) + EPSILON)
    normed_two = (resid_own * inv_two * gain_ffn).astype(jnp.bfloat16)
    normed_two_all = head_gather_relative(normed_two)
    gate_act = jnp.dot(normed_two_all, gate_weight, preferred_element_type=jnp.float32)
    up_act = jnp.dot(normed_two_all, up_weight, preferred_element_type=jnp.float32)
    sigmoid_gate = jax.nn.sigmoid(gate_act)
    silu_gate = sigmoid_gate * gate_act
    hidden = (silu_gate * up_act).astype(jnp.bfloat16)
    piece = lax.slice_in_dim(hidden, 0, lax.axis_size("head") * own_rows, axis=0)
    output = (
        resid_own
        + head_scatter_relative(
            jnp.dot(piece, down_weight, preferred_element_type=jnp.float32).astype(jnp.bfloat16)
        )
    ).astype(jnp.bfloat16)
    grad_down = dot_first(hidden, grad_out_all)
    grad_hidden = dot_last(grad_out_all, down_weight)
    grad_gate_act = (
        grad_hidden * up_act * (sigmoid_gate * (1.0 + gate_act * (1.0 - sigmoid_gate)))
    ).astype(jnp.bfloat16)
    grad_up_act = (grad_hidden * silu_gate).astype(jnp.bfloat16)
    grad_gate = dot_first(normed_two_all, grad_gate_act)
    grad_up = dot_first(normed_two_all, grad_up_act)
    gate_piece = lax.slice_in_dim(grad_gate_act, 0, lax.axis_size("head") * own_rows, axis=0)
    up_piece = lax.slice_in_dim(grad_up_act, 0, lax.axis_size("head") * own_rows, axis=0)
    grad_normed_two = head_scatter_relative(
        (dot_last(gate_piece, gate_weight) + dot_last(up_piece, up_weight)).astype(jnp.bfloat16)
    )
    ffn_grads = (grad_gate.astype(jnp.bfloat16), grad_up.astype(jnp.bfloat16), grad_down.astype(jnp.bfloat16))
    ffn_grads, grad_normed_two = lax.optimization_barrier((ffn_grads, grad_normed_two))
    grad_gate, grad_up, grad_down = lax.psum(ffn_grads, "dp")
    resid_part, grad_gain_ffn_own = norm_backward(resid_own, inv_two, gain_ffn, grad_normed_two)
    grad_resid = cotangent.astype(jnp.float32) + resid_part
    output, grad_resid = lax.optimization_barrier((output, grad_resid))
    grad_branch = head_all_gather(grad_resid.astype(jnp.bfloat16), 0)
    grad_mixed = dot_last(grad_branch, out_weight).astype(jnp.bfloat16)
    grad_out = dot_first(mixed, grad_branch)
    grad_query_rows, grad_key_rows, grad_value_rows = map_rows(
        attend_back,
        (query_rows, keys_rows, values_rows, doc_ids, log_total, grad_mixed.reshape(row_shape)),
    )
    head_shape = (total_rows, local_heads, DH)
    grad_query = rounded(grad_query_rows.reshape(head_shape))
    grad_key = rounded(grad_key_rows.reshape(head_shape))
    grad_value = rounded(grad_value_rows.reshape(head_shape))
    grads_by_part = ((grad_query, basis_query, 0), (grad_key, basis_key, RQ), (grad_value, basis_value, RQ + RK))
    coef_columns = [None] * (local_heads * rank_all)
    basis_grads = []
    for grad_part, bases, offset in grads_by_part:
        for rank, basis in enumerate(bases):
            for head in range(local_heads):
                coef_columns[head * rank_all + offset + rank] = jnp.sum(
                    grad_part[:, head, :] * basis, axis=1
                ) / len(bases)
            basis_grad = sum(
                coef[head][offset + rank] * grad_part[:, head, :] for head in range(local_heads)
            ) / len(bases)
            basis_grads.append(basis_grad if offset == RQ + RK else unturn(basis_grad, cosine, sine))
    grad_factor_a = jnp.stack(coef_columns, axis=1).astype(jnp.bfloat16)
    grad_factor_b = jnp.concatenate(basis_grads, axis=1)
    head_count = lax.axis_size("head")
    basis_cols = grad_factor_b.shape[1] // head_count
    factor_cols = head_reduce_scatter(grad_factor_b.astype(jnp.bfloat16), 1).astype(jnp.bfloat16)
    weight_cols = lax.dynamic_slice_in_dim(
        b_weight, lax.axis_index("head") * basis_cols, basis_cols, axis=1
    )
    piece = grad_factor_a
    grad_normed_one = head_reduce_scatter(
        (dot_last(piece, a_weight) + dot_last(factor_cols, weight_cols)).astype(jnp.bfloat16), 0
    )
    input_part, grad_gain_attn_own = norm_backward(x_own, inv_one, gain_attn, grad_normed_one)
    input_grad = grad_resid + input_part
    grad_a = dot_first(normed_all, grad_factor_a)
    grad_b_cols = dot_first(normed_all, factor_cols)

    features = grad_gain_attn_own.shape[0]
    gain_rows = -(-2 * features // basis_cols)
    gains = jnp.pad(
        jnp.concatenate([grad_gain_attn_own, grad_gain_ffn_own]),
        (0, gain_rows * basis_cols - 2 * features),
    ).reshape(gain_rows, basis_cols)
    tail = (
        grad_a.astype(jnp.bfloat16),
        grad_out.astype(jnp.bfloat16),
        jnp.concatenate([grad_b_cols, gains], axis=0).astype(jnp.bfloat16),
    )
    tail, (grad_gate, grad_up, grad_down) = lax.optimization_barrier(
        (tail, (grad_gate, grad_up, grad_down))
    )
    sizes = [part.size for part in tail]
    summed = dp_all_reduce(jnp.concatenate([part.reshape(-1) for part in tail]))
    grad_a, grad_out, packed = (
        summed[sum(sizes[:index]) : sum(sizes[: index + 1])].reshape(part.shape)
        for index, part in enumerate(tail)
    )
    grad_out, grad_gate, grad_up, grad_down = (
        grad_out.astype(jnp.float32),
        grad_gate.astype(jnp.float32),
        grad_up.astype(jnp.float32),
        grad_down.astype(jnp.float32),
    )
    grad_a = grad_a.astype(jnp.float32)
    packed = lax.all_gather(packed, "head", axis=1, tiled=True).astype(jnp.float32)
    grad_b = packed[: grad_b_cols.shape[0]]
    gains = jnp.sum(
        packed[grad_b_cols.shape[0] :].reshape(gain_rows, head_count, basis_cols), axis=1
    ).reshape(-1)
    grad_gain_attn, grad_gain_ffn = gains[:features], gains[features : 2 * features]
    return (
        output,
        input_grad,
        grad_gain_attn,
        grad_a,
        grad_b,
        grad_out,
        grad_gain_ffn,
        grad_gate,
        grad_up,
        grad_down,
    )


def solution(mesh):
    return jax.shard_map(
        local,
        mesh=mesh,
        in_specs=(
            P(("dp", "head"), None),
            P("dp", None),
            P(),
            P(None, "head"),
            P(),
            P("head", None),
            P(),
            P(None, "head"),
            P(None, "head"),
            P("head", None),
            P(("dp", "head"), None),
        ),
        out_specs=(
            P(("dp", "head"), None),
            P(("dp", "head"), None),
            P(),
            P(None, "head"),
            P(),
            P("head", None),
            P(),
            P(None, "head"),
            P(None, "head"),
            P("head", None),
        ),
        check_vma=False,
    )
```

```python
import math

import jax
import jax.numpy as jnp
from jax import lax
from jax.sharding import PartitionSpec as P

DH = 64
RQ = 6
RK = 2


EPSILON = 1e-06
MASKED = -1e30
PRECISE = lax.Precision.HIGHEST


def rope_tables(total_rows, length):
    half_depth = DH // 2
    position = (jnp.arange(total_rows, dtype=jnp.int32) % length).astype(jnp.float32)
    frequency = jnp.exp(jnp.arange(half_depth, dtype=jnp.float32) * (-2.0 * math.log(10000.0) / DH))
    angle = position[:, None] * frequency[None, :]
    return (jnp.cos(angle), jnp.sin(angle))


def rotate(basis, cosine, sine):
    half_depth = basis.shape[-1] // 2
    first_half = basis[..., :half_depth]
    second_half = basis[..., half_depth:]
    cosine_row = cosine[:, None, :]
    sine_row = sine[:, None, :]
    return jnp.concatenate(
        [
            first_half * cosine_row - second_half * sine_row,
            second_half * cosine_row + first_half * sine_row,
        ],
        axis=-1,
    )


def unrotate(grad_basis, cosine, sine):
    half_depth = grad_basis.shape[-1] // 2
    first_half = grad_basis[..., :half_depth]
    second_half = grad_basis[..., half_depth:]
    cosine_row = cosine[:, None, :]
    sine_row = sine[:, None, :]
    return jnp.concatenate(
        [
            first_half * cosine_row + second_half * sine_row,
            second_half * cosine_row - first_half * sine_row,
        ],
        axis=-1,
    )


def dot_last(left, right):
    return lax.dot_general(
        left, right, (((1,), (1,)), ((), ())), preferred_element_type=jnp.float32
    )


def dot_first(left, right):
    return lax.dot_general(
        left, right, (((0,), (0,)), ((), ())), preferred_element_type=jnp.float32
    )


def norm_backward(inputs, inverse, gain, grad_normed):
    scaled = gain * grad_normed
    inner = jnp.mean(scaled * inputs, axis=-1, keepdims=True)
    grad_inputs = inverse * scaled - inputs * (inverse * inverse * inverse) * inner
    grad_gain = jnp.sum(grad_normed * inputs * inverse, axis=0)
    return (grad_inputs, grad_gain)


def block_scores(queries, key_rows, doc_row, first_row, last_row):
    position = jnp.arange(last_row, dtype=jnp.int32)
    allowed = (doc_row[first_row:last_row, None] == doc_row[None, :last_row]) & (
        position[None, :] <= position[first_row:last_row, None]
    )
    score_scale = 1.0 / math.sqrt(queries.shape[2])
    scores = (
        jnp.einsum(
            "qhd,khd->hqk",
            queries[first_row:last_row],
            key_rows[:last_row],
            preferred_element_type=jnp.float32,
        )
        * score_scale
    )
    return jnp.where(allowed[None], scores, MASKED)


def attend_row(row_item):
    queries, key_rows, value_rows, doc_row = row_item
    length = queries.shape[0]
    block_rows = min(512, length)
    mixed_parts = []
    total_parts = []
    for first_row in range(0, length, block_rows):
        last_row = first_row + block_rows
        scores = block_scores(queries, key_rows, doc_row, first_row, last_row)
        row_peak = jnp.max(scores, axis=-1, keepdims=True)
        exponent = jnp.exp(scores - row_peak)
        row_total = jnp.sum(exponent, axis=-1, keepdims=True)
        weights = (exponent / row_total).astype(jnp.bfloat16)
        mixed_parts.append(
            jnp.einsum(
                "hqk,khd->qhd", weights, value_rows[:last_row], preferred_element_type=jnp.float32
            ).astype(jnp.bfloat16)
        )
        total_parts.append(row_peak[..., 0] + jnp.log(row_total[..., 0]))
    return (jnp.concatenate(mixed_parts, axis=0), jnp.concatenate(total_parts, axis=1))


def attend_back(row_item):
    queries, key_rows, value_rows, doc_row, log_total, grad_mixed = row_item
    length = queries.shape[0]
    block_rows = min(512, length)
    score_scale = 1.0 / math.sqrt(queries.shape[2])
    grad_query_parts = []
    grad_keys = jnp.zeros(key_rows.shape, jnp.float32)
    grad_values = jnp.zeros(value_rows.shape, jnp.float32)
    for first_row in range(0, length, block_rows):
        last_row = first_row + block_rows
        scores = block_scores(queries, key_rows, doc_row, first_row, last_row)
        weights = jnp.exp(scores - log_total[:, first_row:last_row, None])
        grad_weights = jnp.einsum(
            "qhd,khd->hqk",
            grad_mixed[first_row:last_row],
            value_rows[:last_row],
            preferred_element_type=jnp.float32,
        )
        inner = jnp.sum(weights * grad_weights, axis=-1, keepdims=True)
        grad_scores = (weights * (grad_weights - inner)).astype(jnp.bfloat16)
        grad_query_parts.append(
            jnp.einsum(
                "hqk,khd->qhd", grad_scores, key_rows[:last_row], preferred_element_type=jnp.float32
            )
            * score_scale
        )
        padding = ((0, length - last_row), (0, 0), (0, 0))
        key_part = (
            jnp.einsum(
                "hqk,qhd->khd",
                grad_scores,
                queries[first_row:last_row],
                preferred_element_type=jnp.float32,
            )
            * score_scale
        )
        value_part = jnp.einsum(
            "hqk,qhd->khd",
            weights.astype(jnp.bfloat16),
            grad_mixed[first_row:last_row],
            preferred_element_type=jnp.float32,
        )
        grad_keys = grad_keys + jnp.pad(key_part, padding)
        grad_values = grad_values + jnp.pad(value_part, padding)
    return (jnp.concatenate(grad_query_parts, axis=0), grad_keys, grad_values)


def rounded(values_in):
    return lax.optimization_barrier(values_in.astype(jnp.bfloat16)).astype(jnp.float32)


def head_reduce_scatter(values, axis):
    count = lax.axis_size("head")
    own = lax.axis_index("head")
    width = values.shape[axis] // count
    total = lax.dynamic_slice_in_dim(values, own * width, width, axis=axis).astype(jnp.float32)
    for shift in range(1, count):
        sent = lax.dynamic_slice_in_dim(values, ((own + shift) % count) * width, width, axis=axis)
        total = total + lax.ppermute(
            sent, "head", [(device, (device + shift) % count) for device in range(count)]
        ).astype(jnp.float32)
    return total


def head_all_gather(values, axis):
    count = lax.axis_size("head")
    own = lax.axis_index("head")
    width = values.shape[axis]
    shape = list(values.shape)
    shape[axis] = width * count
    gathered = lax.dynamic_update_slice_in_dim(
        jnp.zeros(shape, values.dtype), values, own * width, axis=axis
    )
    for shift in range(1, count):
        arrived = lax.ppermute(
            values, "head", [(device, (device + shift) % count) for device in range(count)]
        )
        gathered = lax.dynamic_update_slice_in_dim(
            gathered, arrived, ((own - shift) % count) * width, axis=axis
        )
    return gathered


def dp_all_reduce(flat):
    count = lax.axis_size("dp")
    own = lax.axis_index("dp")
    steps = count.bit_length() - 1
    assert count == 1 << steps
    width = -(-flat.shape[0] // (count * 128)) * 128
    blocks = jnp.pad(flat, (0, count * width - flat.shape[0])).reshape((2,) * steps + (width,))
    kept = blocks.astype(jnp.float32)
    for step in range(steps):
        axis = steps - 1 - step
        bit = (own >> step) & 1
        sent = lax.dynamic_index_in_dim(kept, 1 - bit, axis, keepdims=False)
        kept = lax.dynamic_index_in_dim(kept, bit, axis, keepdims=False)
        pairs = [(device, device ^ (1 << step)) for device in range(count)]
        kept = kept + lax.ppermute(sent.astype(jnp.bfloat16), "dp", pairs).astype(jnp.float32)
    whole = kept.astype(jnp.bfloat16)[None]
    for step in reversed(range(steps)):
        bit = (own >> step) & 1
        pairs = [(device, device ^ (1 << step)) for device in range(count)]
        arrived = lax.ppermute(whole, "dp", pairs)
        low_half = jnp.where(bit == 0, whole, arrived)
        high_half = jnp.where(bit == 0, arrived, whole)
        whole = jnp.stack([low_half, high_half], axis=1).reshape((-1,) + whole.shape[1:])
    return whole.reshape(-1)[: flat.shape[0]]


def head_gather_relative(values):
    count = lax.axis_size("head")
    parts = [values]
    for shift in range(1, count):
        parts.append(
            lax.ppermute(values, "head", [(device, (device + shift) % count) for device in range(count)])
        )
    return jnp.concatenate(parts, axis=0)


def head_scatter_relative(values):
    count = lax.axis_size("head")
    width = values.shape[0] // count
    total = values[:width].astype(jnp.float32)
    for shift in range(1, count):
        sent = values[(count - shift) * width : (count - shift + 1) * width]
        total = total + lax.ppermute(
            sent, "head", [(device, (device + shift) % count) for device in range(count)]
        ).astype(jnp.float32)
    return total


def map_rows(step, items):
    outs = [step(tuple(item[row] for item in items)) for row in range(items[0].shape[0])]
    return tuple(jnp.stack(parts) for parts in zip(*outs))


def turn(block, cosine, sine):
    half_depth = block.shape[-1] // 2
    first_half, second_half = block[:, :half_depth], block[:, half_depth:]
    return jnp.concatenate(
        [first_half * cosine - second_half * sine, second_half * cosine + first_half * sine], axis=1
    )


def unturn(block, cosine, sine):
    half_depth = block.shape[-1] // 2
    first_half, second_half = block[:, :half_depth], block[:, half_depth:]
    return jnp.concatenate(
        [first_half * cosine + second_half * sine, second_half * cosine - first_half * sine], axis=1
    )


def local(
    tokens,
    doc_ids,
    gain_attn,
    a_weight,
    b_weight,
    out_weight,
    gain_ffn,
    gate_weight,
    up_weight,
    down_weight,
    cotangent,
):
    rows_dev, length = doc_ids.shape
    total_rows = rows_dev * length
    own_rows = tokens.shape[0]
    local_heads = out_weight.shape[0] // DH
    rank_all = RQ + 2 * RK
    x_own = tokens.astype(jnp.float32)
    inv_one = lax.rsqrt(jnp.mean(x_own * x_own, axis=-1, keepdims=True) + EPSILON)
    normed_one = (x_own * inv_one * gain_attn).astype(jnp.bfloat16)
    normed_all, grad_out_all = (
        head_all_gather(normed_one, 0),
        head_gather_relative(cotangent),
    )
    factor_a = jnp.dot(normed_all, a_weight, preferred_element_type=jnp.float32)
    factor_b = jnp.dot(normed_all, b_weight, preferred_element_type=jnp.float32)
    cosine, sine = rope_tables(total_rows, length)
    basis_query = [
        turn(factor_b[:, rank * DH : (rank + 1) * DH], cosine, sine) for rank in range(RQ)
    ]
    basis_key = [
        turn(factor_b[:, (RQ + rank) * DH : (RQ + rank + 1) * DH], cosine, sine)
        for rank in range(RK)
    ]
    basis_value = [
        factor_b[:, (RQ + RK + rank) * DH : (RQ + RK + rank + 1) * DH] for rank in range(RK)
    ]
    coef = [
        [factor_a[:, head * rank_all + column] [:, None] for column in range(rank_all)]
        for head in range(local_heads)
    ]

    def combine(bases, offset):
        return jnp.stack(
            [
                sum(coef[head][offset + rank] * bases[rank] for rank in range(len(bases)))
                / len(bases)
                for head in range(local_heads)
            ],
            axis=1,
        ).astype(jnp.bfloat16)

    queries = combine(basis_query, 0)
    key_rows = combine(basis_key, RQ)
    value_rows = combine(basis_value, RQ + RK)
    row_shape = (rows_dev, length, local_heads, DH)
    query_rows = queries.reshape(row_shape)
    keys_rows = key_rows.reshape(row_shape)
    values_rows = value_rows.reshape(row_shape)
    mixed_rows, log_total = map_rows(attend_row, (query_rows, keys_rows, values_rows, doc_ids))
    mixed = mixed_rows.reshape(total_rows, local_heads * DH)
    piece = lax.slice_in_dim(mixed, 0, lax.axis_size("head") * own_rows, axis=0)
    resid_own = x_own + head_reduce_scatter(
        jnp.dot(piece, out_weight, preferred_element_type=jnp.float32).astype(jnp.bfloat16), 0
    )
    inv_two = lax.rsqrt(jnp.mean(resid_own * resid_own, axis=-1, keepdims=True) + EPSILON)
    normed_two = (resid_own * inv_two * gain_ffn).astype(jnp.bfloat16)
    normed_two_all = head_gather_relative(normed_two)
    gate_act = jnp.dot(normed_two_all, gate_weight, preferred_element_type=jnp.float32)
    up_act = jnp.dot(normed_two_all, up_weight, preferred_element_type=jnp.float32)
    sigmoid_gate = jax.nn.sigmoid(gate_act)
    silu_gate = sigmoid_gate * gate_act
    hidden = (silu_gate * up_act).astype(jnp.bfloat16)
    piece = lax.slice_in_dim(hidden, 0, lax.axis_size("head") * own_rows, axis=0)
    output = (
        resid_own
        + head_scatter_relative(
            jnp.dot(piece, down_weight, preferred_element_type=jnp.float32).astype(jnp.bfloat16)
        )
    ).astype(jnp.bfloat16)
    grad_down = dot_first(hidden, grad_out_all)
    grad_hidden = dot_last(grad_out_all, down_weight)
    grad_gate_act = (
        grad_hidden * up_act * (sigmoid_gate * (1.0 + gate_act * (1.0 - sigmoid_gate)))
    ).astype(jnp.bfloat16)
    grad_up_act = (grad_hidden * silu_gate).astype(jnp.bfloat16)
    grad_gate = dot_first(normed_two_all, grad_gate_act)
    grad_up = dot_first(normed_two_all, grad_up_act)
    gate_piece = lax.slice_in_dim(grad_gate_act, 0, lax.axis_size("head") * own_rows, axis=0)
    up_piece = lax.slice_in_dim(grad_up_act, 0, lax.axis_size("head") * own_rows, axis=0)
    grad_normed_two = head_scatter_relative(
        (dot_last(gate_piece, gate_weight) + dot_last(up_piece, up_weight)).astype(jnp.bfloat16)
    )
    ffn_grads = (grad_gate.astype(jnp.bfloat16), grad_up.astype(jnp.bfloat16), grad_down.astype(jnp.bfloat16))
    ffn_grads, grad_normed_two = lax.optimization_barrier((ffn_grads, grad_normed_two))
    grad_gate, grad_up, grad_down = lax.psum(ffn_grads, "dp")
    resid_part, grad_gain_ffn_own = norm_backward(resid_own, inv_two, gain_ffn, grad_normed_two)
    grad_resid = cotangent.astype(jnp.float32) + resid_part
    output, grad_resid = lax.optimization_barrier((output, grad_resid))
    grad_branch = head_all_gather(grad_resid.astype(jnp.bfloat16), 0)
    grad_mixed = dot_last(grad_branch, out_weight).astype(jnp.bfloat16)
    grad_out = dot_first(mixed, grad_branch)
    grad_query_rows, grad_key_rows, grad_value_rows = map_rows(
        attend_back,
        (query_rows, keys_rows, values_rows, doc_ids, log_total, grad_mixed.reshape(row_shape)),
    )
    head_shape = (total_rows, local_heads, DH)
    grad_query = rounded(grad_query_rows.reshape(head_shape))
    grad_key = rounded(grad_key_rows.reshape(head_shape))
    grad_value = rounded(grad_value_rows.reshape(head_shape))
    grads_by_part = ((grad_query, basis_query, 0), (grad_key, basis_key, RQ), (grad_value, basis_value, RQ + RK))
    coef_columns = [None] * (local_heads * rank_all)
    basis_grads = []
    for grad_part, bases, offset in grads_by_part:
        for rank, basis in enumerate(bases):
            for head in range(local_heads):
                coef_columns[head * rank_all + offset + rank] = jnp.sum(
                    grad_part[:, head, :] * basis, axis=1
                )
            basis_grad = sum(
                coef[head][offset + rank] * grad_part[:, head, :] for head in range(local_heads)
            ) / len(bases)
            basis_grads.append(basis_grad if offset == RQ + RK else unturn(basis_grad, cosine, sine))
    rank_of = jnp.array([RQ] * RQ + [RK] * (2 * RK) * 1, jnp.float32)
    grad_factor_a = (
        jnp.stack(coef_columns, axis=1) / jnp.tile(rank_of, local_heads)[None, :]
    ).astype(jnp.bfloat16)
    grad_factor_b = jnp.concatenate(basis_grads, axis=1)
    head_count = lax.axis_size("head")
    basis_cols = grad_factor_b.shape[1] // head_count
    factor_cols = head_reduce_scatter(grad_factor_b.astype(jnp.bfloat16), 1).astype(jnp.bfloat16)
    weight_cols = lax.dynamic_slice_in_dim(
        b_weight, lax.axis_index("head") * basis_cols, basis_cols, axis=1
    )
    piece = grad_factor_a
    grad_normed_one = head_reduce_scatter(
        (dot_last(piece, a_weight) + dot_last(factor_cols, weight_cols)).astype(jnp.bfloat16), 0
    )
    input_part, grad_gain_attn_own = norm_backward(x_own, inv_one, gain_attn, grad_normed_one)
    input_grad = grad_resid + input_part
    grad_a = dot_first(normed_all, grad_factor_a)
    grad_b_cols = dot_first(normed_all, factor_cols)

    features = grad_gain_attn_own.shape[0]
    gain_rows = -(-2 * features // basis_cols)
    gains = jnp.pad(
        jnp.concatenate([grad_gain_attn_own, grad_gain_ffn_own]),
        (0, gain_rows * basis_cols - 2 * features),
    ).reshape(gain_rows, basis_cols)
    tail = (
        grad_a.astype(jnp.bfloat16),
        grad_out.astype(jnp.bfloat16),
        jnp.concatenate([grad_b_cols, gains], axis=0).astype(jnp.bfloat16),
    )
    sizes = [part.size for part in tail]
    summed = dp_all_reduce(jnp.concatenate([part.reshape(-1) for part in tail]))
    grad_a, grad_out, packed = (
        summed[sum(sizes[:index]) : sum(sizes[: index + 1])].reshape(part.shape)
        for index, part in enumerate(tail)
    )
    grad_out, grad_gate, grad_up, grad_down = (
        grad_out.astype(jnp.float32),
        grad_gate.astype(jnp.float32),
        grad_up.astype(jnp.float32),
        grad_down.astype(jnp.float32),
    )
    grad_a = grad_a.astype(jnp.float32)
    packed = lax.all_gather(packed, "head", axis=1, tiled=True).astype(jnp.float32)
    grad_b = packed[: grad_b_cols.shape[0]]
    gains = jnp.sum(
        packed[grad_b_cols.shape[0] :].reshape(gain_rows, head_count, basis_cols), axis=1
    ).reshape(-1)
    grad_gain_attn, grad_gain_ffn = gains[:features], gains[features : 2 * features]
    return (
        output,
        input_grad,
        grad_gain_attn,
        grad_a,
        grad_b,
        grad_out,
        grad_gain_ffn,
        grad_gate,
        grad_up,
        grad_down,
    )


def solution(mesh):
    return jax.shard_map(
        local,
        mesh=mesh,
        in_specs=(
            P(("dp", "head"), None),
            P("dp", None),
            P(),
            P(None, "head"),
            P(),
            P("head", None),
            P(),
            P(None, "head"),
            P(None, "head"),
            P("head", None),
            P(("dp", "head"), None),
        ),
        out_specs=(
            P(("dp", "head"), None),
            P(("dp", "head"), None),
            P(),
            P(None, "head"),
            P(),
            P("head", None),
            P(),
            P(None, "head"),
            P(None, "head"),
            P("head", None),
        ),
        check_vma=False,
    )
```

```python
import math

import jax
import jax.numpy as jnp
from jax import lax
from jax.sharding import PartitionSpec as P

DH = 64
RQ = 6
RK = 2


EPSILON = 1e-06
MASKED = -1e30
PRECISE = lax.Precision.HIGHEST


def rope_tables(total_rows, length):
    half_depth = DH // 2
    position = (jnp.arange(total_rows, dtype=jnp.int32) % length).astype(jnp.float32)
    frequency = jnp.exp(jnp.arange(half_depth, dtype=jnp.float32) * (-2.0 * math.log(10000.0) / DH))
    angle = position[:, None] * frequency[None, :]
    return (jnp.cos(angle), jnp.sin(angle))


def rotate(basis, cosine, sine):
    half_depth = basis.shape[-1] // 2
    first_half = basis[..., :half_depth]
    second_half = basis[..., half_depth:]
    cosine_row = cosine[:, None, :]
    sine_row = sine[:, None, :]
    return jnp.concatenate(
        [
            first_half * cosine_row - second_half * sine_row,
            second_half * cosine_row + first_half * sine_row,
        ],
        axis=-1,
    )


def unrotate(grad_basis, cosine, sine):
    half_depth = grad_basis.shape[-1] // 2
    first_half = grad_basis[..., :half_depth]
    second_half = grad_basis[..., half_depth:]
    cosine_row = cosine[:, None, :]
    sine_row = sine[:, None, :]
    return jnp.concatenate(
        [
            first_half * cosine_row + second_half * sine_row,
            second_half * cosine_row - first_half * sine_row,
        ],
        axis=-1,
    )


def dot_last(left, right):
    return lax.dot_general(
        left, right, (((1,), (1,)), ((), ())), preferred_element_type=jnp.float32
    )


def dot_first(left, right):
    return lax.dot_general(
        left, right, (((0,), (0,)), ((), ())), preferred_element_type=jnp.float32
    )


def norm_backward(inputs, inverse, gain, grad_normed):
    scaled = gain * grad_normed
    inner = jnp.mean(scaled * inputs, axis=-1, keepdims=True)
    grad_inputs = inverse * scaled - inputs * (inverse * inverse * inverse) * inner
    grad_gain = jnp.sum(grad_normed * inputs * inverse, axis=0)
    return (grad_inputs, grad_gain)


def block_scores(queries, key_rows, doc_row, first_row, last_row):
    position = jnp.arange(last_row, dtype=jnp.int32)
    allowed = (doc_row[first_row:last_row, None] == doc_row[None, :last_row]) & (
        position[None, :] <= position[first_row:last_row, None]
    )
    score_scale = 1.0 / math.sqrt(queries.shape[2])
    scores = (
        jnp.einsum(
            "qhd,khd->hqk",
            queries[first_row:last_row],
            key_rows[:last_row],
            preferred_element_type=jnp.float32,
        )
        * score_scale
    )
    return jnp.where(allowed[None], scores, MASKED)


def attend_row(row_item):
    queries, key_rows, value_rows, doc_row = row_item
    length = queries.shape[0]
    block_rows = min(512, length)
    mixed_parts = []
    total_parts = []
    for first_row in range(0, length, block_rows):
        last_row = first_row + block_rows
        scores = block_scores(queries, key_rows, doc_row, first_row, last_row)
        row_peak = jnp.max(scores, axis=-1, keepdims=True)
        exponent = jnp.exp(scores - row_peak)
        row_total = jnp.sum(exponent, axis=-1, keepdims=True)
        weights = (exponent / row_total).astype(jnp.bfloat16)
        mixed_parts.append(
            jnp.einsum(
                "hqk,khd->qhd", weights, value_rows[:last_row], preferred_element_type=jnp.float32
            ).astype(jnp.bfloat16)
        )
        total_parts.append(row_peak[..., 0] + jnp.log(row_total[..., 0]))
    return (jnp.concatenate(mixed_parts, axis=0), jnp.concatenate(total_parts, axis=1))


def attend_back(row_item):
    queries, key_rows, value_rows, doc_row, log_total, grad_mixed = row_item
    length = queries.shape[0]
    block_rows = min(512, length)
    score_scale = 1.0 / math.sqrt(queries.shape[2])
    grad_query_parts = []
    grad_keys = jnp.zeros(key_rows.shape, jnp.float32)
    grad_values = jnp.zeros(value_rows.shape, jnp.float32)
    for first_row in range(0, length, block_rows):
        last_row = first_row + block_rows
        scores = block_scores(queries, key_rows, doc_row, first_row, last_row)
        weights = jnp.exp(scores - log_total[:, first_row:last_row, None])
        grad_weights = jnp.einsum(
            "qhd,khd->hqk",
            grad_mixed[first_row:last_row],
            value_rows[:last_row],
            preferred_element_type=jnp.float32,
        )
        inner = jnp.sum(weights * grad_weights, axis=-1, keepdims=True)
        grad_scores = (weights * (grad_weights - inner)).astype(jnp.bfloat16)
        grad_query_parts.append(
            jnp.einsum(
                "hqk,khd->qhd", grad_scores, key_rows[:last_row], preferred_element_type=jnp.float32
            )
            * score_scale
        )
        padding = ((0, length - last_row), (0, 0), (0, 0))
        key_part = (
            jnp.einsum(
                "hqk,qhd->khd",
                grad_scores,
                queries[first_row:last_row],
                preferred_element_type=jnp.float32,
            )
            * score_scale
        )
        value_part = jnp.einsum(
            "hqk,qhd->khd",
            weights.astype(jnp.bfloat16),
            grad_mixed[first_row:last_row],
            preferred_element_type=jnp.float32,
        )
        grad_keys = grad_keys + jnp.pad(key_part, padding)
        grad_values = grad_values + jnp.pad(value_part, padding)
    return (jnp.concatenate(grad_query_parts, axis=0), grad_keys, grad_values)


def rounded(values_in):
    return lax.optimization_barrier(values_in.astype(jnp.bfloat16)).astype(jnp.float32)


def head_reduce_scatter(values, axis):
    count = lax.axis_size("head")
    own = lax.axis_index("head")
    width = values.shape[axis] // count
    total = lax.dynamic_slice_in_dim(values, own * width, width, axis=axis).astype(jnp.float32)
    for shift in range(1, count):
        sent = lax.dynamic_slice_in_dim(values, ((own + shift) % count) * width, width, axis=axis)
        total = total + lax.ppermute(
            sent, "head", [(device, (device + shift) % count) for device in range(count)]
        ).astype(jnp.float32)
    return total


def head_all_gather(values, axis):
    count = lax.axis_size("head")
    own = lax.axis_index("head")
    width = values.shape[axis]
    shape = list(values.shape)
    shape[axis] = width * count
    gathered = lax.dynamic_update_slice_in_dim(
        jnp.zeros(shape, values.dtype), values, own * width, axis=axis
    )
    for shift in range(1, count):
        arrived = lax.ppermute(
            values, "head", [(device, (device + shift) % count) for device in range(count)]
        )
        gathered = lax.dynamic_update_slice_in_dim(
            gathered, arrived, ((own - shift) % count) * width, axis=axis
        )
    return gathered


def dp_all_reduce(flat):
    count = lax.axis_size("dp")
    own = lax.axis_index("dp")
    steps = count.bit_length() - 1
    assert count == 1 << steps
    width = -(-flat.shape[0] // (count * 128)) * 128
    blocks = jnp.pad(flat, (0, count * width - flat.shape[0])).reshape((2,) * steps + (width,))
    kept = blocks.astype(jnp.float32)
    for step in range(steps):
        axis = steps - 1 - step
        bit = (own >> step) & 1
        sent = lax.dynamic_index_in_dim(kept, 1 - bit, axis, keepdims=False)
        kept = lax.dynamic_index_in_dim(kept, bit, axis, keepdims=False)
        pairs = [(device, device ^ (1 << step)) for device in range(count)]
        kept = kept + lax.ppermute(sent.astype(jnp.bfloat16), "dp", pairs).astype(jnp.float32)
    whole = kept.astype(jnp.bfloat16)[None]
    for step in reversed(range(steps)):
        bit = (own >> step) & 1
        pairs = [(device, device ^ (1 << step)) for device in range(count)]
        arrived = lax.ppermute(whole, "dp", pairs)
        low_half = jnp.where(bit == 0, whole, arrived)
        high_half = jnp.where(bit == 0, arrived, whole)
        whole = jnp.stack([low_half, high_half], axis=1).reshape((-1,) + whole.shape[1:])
    return whole.reshape(-1)[: flat.shape[0]]


def head_gather_relative(values):
    count = lax.axis_size("head")
    parts = [values]
    for shift in range(1, count):
        parts.append(
            lax.ppermute(values, "head", [(device, (device + shift) % count) for device in range(count)])
        )
    return jnp.concatenate(parts, axis=0)


def head_scatter_relative(values):
    count = lax.axis_size("head")
    width = values.shape[0] // count
    total = values[:width].astype(jnp.float32)
    for shift in range(1, count):
        sent = values[(count - shift) * width : (count - shift + 1) * width]
        total = total + lax.ppermute(
            sent, "head", [(device, (device + shift) % count) for device in range(count)]
        ).astype(jnp.float32)
    return total


def map_rows(step, items):
    outs = [step(tuple(item[row] for item in items)) for row in range(items[0].shape[0])]
    return tuple(jnp.stack(parts) for parts in zip(*outs))


def turn(block, cosine, sine):
    half_depth = block.shape[-1] // 2
    first_half, second_half = block[:, :half_depth], block[:, half_depth:]
    return jnp.concatenate(
        [first_half * cosine - second_half * sine, second_half * cosine + first_half * sine], axis=1
    )


def unturn(block, cosine, sine):
    half_depth = block.shape[-1] // 2
    first_half, second_half = block[:, :half_depth], block[:, half_depth:]
    return jnp.concatenate(
        [first_half * cosine + second_half * sine, second_half * cosine - first_half * sine], axis=1
    )


def local(
    tokens,
    doc_ids,
    gain_attn,
    a_weight,
    b_weight,
    out_weight,
    gain_ffn,
    gate_weight,
    up_weight,
    down_weight,
    cotangent,
):
    rows_dev, length = doc_ids.shape
    total_rows = rows_dev * length
    own_rows = tokens.shape[0]
    local_heads = out_weight.shape[0] // DH
    rank_all = RQ + 2 * RK
    x_own = tokens.astype(jnp.float32)
    inv_one = lax.rsqrt(jnp.mean(x_own * x_own, axis=-1, keepdims=True) + EPSILON)
    normed_one = (x_own * inv_one * gain_attn).astype(jnp.bfloat16)
    normed_all, grad_out_all = (
        head_all_gather(normed_one, 0),
        head_gather_relative(cotangent),
    )
    factor_a = jnp.dot(normed_all, a_weight, preferred_element_type=jnp.float32)
    factor_b = jnp.dot(normed_all, b_weight, preferred_element_type=jnp.float32)
    cosine, sine = rope_tables(total_rows, length)
    basis_query = [
        turn(factor_b[:, rank * DH : (rank + 1) * DH], cosine, sine) for rank in range(RQ)
    ]
    basis_key = [
        turn(factor_b[:, (RQ + rank) * DH : (RQ + rank + 1) * DH], cosine, sine)
        for rank in range(RK)
    ]
    basis_value = [
        factor_b[:, (RQ + RK + rank) * DH : (RQ + RK + rank + 1) * DH] for rank in range(RK)
    ]
    coef = [
        [factor_a[:, head * rank_all + column] [:, None] for column in range(rank_all)]
        for head in range(local_heads)
    ]

    def combine(bases, offset):
        return jnp.stack(
            [
                sum(coef[head][offset + rank] * bases[rank] for rank in range(len(bases)))
                / len(bases)
                for head in range(local_heads)
            ],
            axis=1,
        ).astype(jnp.bfloat16)

    queries = combine(basis_query, 0)
    key_rows = combine(basis_key, RQ)
    value_rows = combine(basis_value, RQ + RK)
    row_shape = (rows_dev, length, local_heads, DH)
    query_rows = queries.reshape(row_shape)
    keys_rows = key_rows.reshape(row_shape)
    values_rows = value_rows.reshape(row_shape)
    mixed_rows, log_total = map_rows(attend_row, (query_rows, keys_rows, values_rows, doc_ids))
    mixed = mixed_rows.reshape(total_rows, local_heads * DH)
    piece = lax.slice_in_dim(mixed, 0, lax.axis_size("head") * own_rows, axis=0)
    resid_own = x_own + head_reduce_scatter(
        jnp.dot(piece, out_weight, preferred_element_type=jnp.float32).astype(jnp.bfloat16), 0
    )
    inv_two = lax.rsqrt(jnp.mean(resid_own * resid_own, axis=-1, keepdims=True) + EPSILON)
    normed_two = (resid_own * inv_two * gain_ffn).astype(jnp.bfloat16)
    normed_two_all = head_gather_relative(normed_two)
    gate_act = jnp.dot(normed_two_all, gate_weight, preferred_element_type=jnp.float32)
    up_act = jnp.dot(normed_two_all, up_weight, preferred_element_type=jnp.float32)
    sigmoid_gate = jax.nn.sigmoid(gate_act)
    silu_gate = sigmoid_gate * gate_act
    hidden = (silu_gate * up_act).astype(jnp.bfloat16)
    piece = lax.slice_in_dim(hidden, 0, lax.axis_size("head") * own_rows, axis=0)
    output = (
        resid_own
        + head_scatter_relative(
            jnp.dot(piece, down_weight, preferred_element_type=jnp.float32).astype(jnp.bfloat16)
        )
    ).astype(jnp.bfloat16)
    grad_down = dot_first(hidden, grad_out_all)
    grad_hidden = dot_last(grad_out_all, down_weight)
    grad_gate_act = (
        grad_hidden * up_act * (sigmoid_gate * (1.0 + gate_act * (1.0 - sigmoid_gate)))
    ).astype(jnp.bfloat16)
    grad_up_act = (grad_hidden * silu_gate).astype(jnp.bfloat16)
    grad_gate = dot_first(normed_two_all, grad_gate_act)
    grad_up = dot_first(normed_two_all, grad_up_act)
    gate_piece = lax.slice_in_dim(grad_gate_act, 0, lax.axis_size("head") * own_rows, axis=0)
    up_piece = lax.slice_in_dim(grad_up_act, 0, lax.axis_size("head") * own_rows, axis=0)
    normed_two_part = (dot_last(gate_piece, gate_weight) + dot_last(up_piece, up_weight)).astype(
        jnp.bfloat16
    )
    ffn_grads = (grad_gate.astype(jnp.bfloat16), grad_up.astype(jnp.bfloat16), grad_down.astype(jnp.bfloat16))
    ffn_grads, normed_two_part = lax.optimization_barrier((ffn_grads, normed_two_part))
    grad_normed_two = head_scatter_relative(normed_two_part)
    grad_gate, grad_up, grad_down = lax.psum(ffn_grads, "dp")
    resid_part, grad_gain_ffn_own = norm_backward(resid_own, inv_two, gain_ffn, grad_normed_two)
    grad_resid = cotangent.astype(jnp.float32) + resid_part
    output, grad_resid = lax.optimization_barrier((output, grad_resid))
    grad_branch = head_all_gather(grad_resid.astype(jnp.bfloat16), 0)
    grad_mixed = dot_last(grad_branch, out_weight).astype(jnp.bfloat16)
    grad_out = dot_first(mixed, grad_branch)
    grad_query_rows, grad_key_rows, grad_value_rows = map_rows(
        attend_back,
        (query_rows, keys_rows, values_rows, doc_ids, log_total, grad_mixed.reshape(row_shape)),
    )
    head_shape = (total_rows, local_heads, DH)
    grad_query = rounded(grad_query_rows.reshape(head_shape))
    grad_key = rounded(grad_key_rows.reshape(head_shape))
    grad_value = rounded(grad_value_rows.reshape(head_shape))
    grads_by_part = ((grad_query, basis_query, 0), (grad_key, basis_key, RQ), (grad_value, basis_value, RQ + RK))
    coef_columns = [None] * (local_heads * rank_all)
    basis_grads = []
    for grad_part, bases, offset in grads_by_part:
        for rank, basis in enumerate(bases):
            for head in range(local_heads):
                coef_columns[head * rank_all + offset + rank] = jnp.sum(
                    grad_part[:, head, :] * basis, axis=1
                )
            basis_grad = sum(
                coef[head][offset + rank] * grad_part[:, head, :] for head in range(local_heads)
            ) / len(bases)
            basis_grads.append(basis_grad if offset == RQ + RK else unturn(basis_grad, cosine, sine))
    rank_of = jnp.array([RQ] * RQ + [RK] * (2 * RK) * 1, jnp.float32)
    grad_factor_a = (
        jnp.stack(coef_columns, axis=1) / jnp.tile(rank_of, local_heads)[None, :]
    ).astype(jnp.bfloat16)
    grad_factor_b = jnp.concatenate(basis_grads, axis=1)
    head_count = lax.axis_size("head")
    basis_cols = grad_factor_b.shape[1] // head_count
    factor_cols = head_reduce_scatter(grad_factor_b.astype(jnp.bfloat16), 1).astype(jnp.bfloat16)
    weight_cols = lax.dynamic_slice_in_dim(
        b_weight, lax.axis_index("head") * basis_cols, basis_cols, axis=1
    )
    piece = grad_factor_a
    grad_normed_one = head_reduce_scatter(
        (dot_last(piece, a_weight) + dot_last(factor_cols, weight_cols)).astype(jnp.bfloat16), 0
    )
    input_part, grad_gain_attn_own = norm_backward(x_own, inv_one, gain_attn, grad_normed_one)
    input_grad = grad_resid + input_part
    grad_a = dot_first(normed_all, grad_factor_a)
    grad_b_cols = dot_first(normed_all, factor_cols)

    features = grad_gain_attn_own.shape[0]
    gain_rows = -(-2 * features // basis_cols)
    gains = jnp.pad(
        jnp.concatenate([grad_gain_attn_own, grad_gain_ffn_own]),
        (0, gain_rows * basis_cols - 2 * features),
    ).reshape(gain_rows, basis_cols)
    tail = (
        grad_a.astype(jnp.bfloat16),
        grad_out.astype(jnp.bfloat16),
        jnp.concatenate([grad_b_cols, gains], axis=0).astype(jnp.bfloat16),
    )
    sizes = [part.size for part in tail]
    tail, (grad_gate, grad_up, grad_down) = lax.optimization_barrier(
        (tail, (grad_gate, grad_up, grad_down))
    )
    summed = dp_all_reduce(jnp.concatenate([part.reshape(-1) for part in tail]))
    grad_a, grad_out, packed = (
        summed[sum(sizes[:index]) : sum(sizes[: index + 1])].reshape(part.shape)
        for index, part in enumerate(tail)
    )
    grad_out, grad_gate, grad_up, grad_down = (
        grad_out.astype(jnp.float32),
        grad_gate.astype(jnp.float32),
        grad_up.astype(jnp.float32),
        grad_down.astype(jnp.float32),
    )
    grad_a = grad_a.astype(jnp.float32)
    packed = lax.all_gather(packed, "head", axis=1, tiled=True).astype(jnp.float32)
    grad_b = packed[: grad_b_cols.shape[0]]
    gains = jnp.sum(
        packed[grad_b_cols.shape[0] :].reshape(gain_rows, head_count, basis_cols), axis=1
    ).reshape(-1)
    grad_gain_attn, grad_gain_ffn = gains[:features], gains[features : 2 * features]
    return (
        output,
        input_grad,
        grad_gain_attn,
        grad_a,
        grad_b,
        grad_out,
        grad_gain_ffn,
        grad_gate,
        grad_up,
        grad_down,
    )


def solution(mesh):
    return jax.shard_map(
        local,
        mesh=mesh,
        in_specs=(
            P(("dp", "head"), None),
            P("dp", None),
            P(),
            P(None, "head"),
            P(),
            P("head", None),
            P(),
            P(None, "head"),
            P(None, "head"),
            P("head", None),
            P(("dp", "head"), None),
        ),
        out_specs=(
            P(("dp", "head"), None),
            P(("dp", "head"), None),
            P(),
            P(None, "head"),
            P(),
            P("head", None),
            P(),
            P(None, "head"),
            P(None, "head"),
            P("head", None),
        ),
        check_vma=False,
    )
```

```python
import math

import jax
import jax.numpy as jnp
from jax import lax
from jax.sharding import PartitionSpec as P

DH = 64
RQ = 6
RK = 2


EPSILON = 1e-06
MASKED = -1e30
PRECISE = lax.Precision.HIGHEST


def rope_tables(total_rows, length):
    half_depth = DH // 2
    position = (jnp.arange(total_rows, dtype=jnp.int32) % length).astype(jnp.float32)
    frequency = jnp.exp(jnp.arange(half_depth, dtype=jnp.float32) * (-2.0 * math.log(10000.0) / DH))
    angle = position[:, None] * frequency[None, :]
    return (jnp.cos(angle), jnp.sin(angle))


def rotate(basis, cosine, sine):
    half_depth = basis.shape[-1] // 2
    first_half = basis[..., :half_depth]
    second_half = basis[..., half_depth:]
    cosine_row = cosine[:, None, :]
    sine_row = sine[:, None, :]
    return jnp.concatenate(
        [
            first_half * cosine_row - second_half * sine_row,
            second_half * cosine_row + first_half * sine_row,
        ],
        axis=-1,
    )


def unrotate(grad_basis, cosine, sine):
    half_depth = grad_basis.shape[-1] // 2
    first_half = grad_basis[..., :half_depth]
    second_half = grad_basis[..., half_depth:]
    cosine_row = cosine[:, None, :]
    sine_row = sine[:, None, :]
    return jnp.concatenate(
        [
            first_half * cosine_row + second_half * sine_row,
            second_half * cosine_row - first_half * sine_row,
        ],
        axis=-1,
    )


def dot_last(left, right):
    return lax.dot_general(
        left, right, (((1,), (1,)), ((), ())), preferred_element_type=jnp.float32
    )


def dot_first(left, right):
    return lax.dot_general(
        left, right, (((0,), (0,)), ((), ())), preferred_element_type=jnp.float32
    )


def norm_backward(inputs, inverse, gain, grad_normed):
    scaled = gain * grad_normed
    inner = jnp.mean(scaled * inputs, axis=-1, keepdims=True)
    grad_inputs = inverse * scaled - inputs * (inverse * inverse * inverse) * inner
    grad_gain = jnp.sum(grad_normed * inputs * inverse, axis=0)
    return (grad_inputs, grad_gain)


def block_scores(queries, key_rows, doc_row, first_row, last_row):
    position = jnp.arange(last_row, dtype=jnp.int32)
    allowed = (doc_row[first_row:last_row, None] == doc_row[None, :last_row]) & (
        position[None, :] <= position[first_row:last_row, None]
    )
    score_scale = 1.0 / math.sqrt(queries.shape[2])
    scores = (
        jnp.einsum(
            "qhd,khd->hqk",
            queries[first_row:last_row],
            key_rows[:last_row],
            preferred_element_type=jnp.float32,
        )
        * score_scale
    )
    return jnp.where(allowed[None], scores, MASKED)


def attend_row(row_item):
    queries, key_rows, value_rows, doc_row = row_item
    length = queries.shape[0]
    block_rows = min(512, length)
    mixed_parts = []
    total_parts = []
    for first_row in range(0, length, block_rows):
        last_row = first_row + block_rows
        scores = block_scores(queries, key_rows, doc_row, first_row, last_row)
        row_peak = jnp.max(scores, axis=-1, keepdims=True)
        exponent = jnp.exp(scores - row_peak)
        row_total = jnp.sum(exponent, axis=-1, keepdims=True)
        weights = (exponent / row_total).astype(jnp.bfloat16)
        mixed_parts.append(
            jnp.einsum(
                "hqk,khd->qhd", weights, value_rows[:last_row], preferred_element_type=jnp.float32
            ).astype(jnp.bfloat16)
        )
        total_parts.append(row_peak[..., 0] + jnp.log(row_total[..., 0]))
    return (jnp.concatenate(mixed_parts, axis=0), jnp.concatenate(total_parts, axis=1))


def attend_back(row_item):
    queries, key_rows, value_rows, doc_row, log_total, grad_mixed = row_item
    length = queries.shape[0]
    block_rows = min(512, length)
    score_scale = 1.0 / math.sqrt(queries.shape[2])
    grad_query_parts = []
    grad_keys = jnp.zeros(key_rows.shape, jnp.float32)
    grad_values = jnp.zeros(value_rows.shape, jnp.float32)
    for first_row in range(0, length, block_rows):
        last_row = first_row + block_rows
        scores = block_scores(queries, key_rows, doc_row, first_row, last_row)
        weights = jnp.exp(scores - log_total[:, first_row:last_row, None])
        grad_weights = jnp.einsum(
            "qhd,khd->hqk",
            grad_mixed[first_row:last_row],
            value_rows[:last_row],
            preferred_element_type=jnp.float32,
        )
        inner = jnp.sum(weights * grad_weights, axis=-1, keepdims=True)
        grad_scores = (weights * (grad_weights - inner)).astype(jnp.bfloat16)
        grad_query_parts.append(
            jnp.einsum(
                "hqk,khd->qhd", grad_scores, key_rows[:last_row], preferred_element_type=jnp.float32
            )
            * score_scale
        )
        padding = ((0, length - last_row), (0, 0), (0, 0))
        key_part = (
            jnp.einsum(
                "hqk,qhd->khd",
                grad_scores,
                queries[first_row:last_row],
                preferred_element_type=jnp.float32,
            )
            * score_scale
        )
        value_part = jnp.einsum(
            "hqk,qhd->khd",
            weights.astype(jnp.bfloat16),
            grad_mixed[first_row:last_row],
            preferred_element_type=jnp.float32,
        )
        grad_keys = grad_keys + jnp.pad(key_part, padding)
        grad_values = grad_values + jnp.pad(value_part, padding)
    return (jnp.concatenate(grad_query_parts, axis=0), grad_keys, grad_values)


def rounded(values_in):
    return lax.optimization_barrier(values_in.astype(jnp.bfloat16)).astype(jnp.float32)


def head_reduce_scatter(values, axis):
    count = lax.axis_size("head")
    own = lax.axis_index("head")
    width = values.shape[axis] // count
    total = lax.dynamic_slice_in_dim(values, own * width, width, axis=axis).astype(jnp.float32)
    for shift in range(1, count):
        sent = lax.dynamic_slice_in_dim(values, ((own + shift) % count) * width, width, axis=axis)
        total = total + lax.ppermute(
            sent, "head", [(device, (device + shift) % count) for device in range(count)]
        ).astype(jnp.float32)
    return total


def head_all_gather(values, axis):
    count = lax.axis_size("head")
    own = lax.axis_index("head")
    width = values.shape[axis]
    shape = list(values.shape)
    shape[axis] = width * count
    gathered = lax.dynamic_update_slice_in_dim(
        jnp.zeros(shape, values.dtype), values, own * width, axis=axis
    )
    for shift in range(1, count):
        arrived = lax.ppermute(
            values, "head", [(device, (device + shift) % count) for device in range(count)]
        )
        gathered = lax.dynamic_update_slice_in_dim(
            gathered, arrived, ((own - shift) % count) * width, axis=axis
        )
    return gathered


def dp_all_reduce(flat):
    count = lax.axis_size("dp")
    own = lax.axis_index("dp")
    steps = count.bit_length() - 1
    assert count == 1 << steps
    width = -(-flat.shape[0] // (count * 128)) * 128
    blocks = jnp.pad(flat, (0, count * width - flat.shape[0])).reshape((2,) * steps + (width,))
    kept = blocks.astype(jnp.float32)
    for step in range(steps):
        axis = steps - 1 - step
        bit = (own >> step) & 1
        sent = lax.dynamic_index_in_dim(kept, 1 - bit, axis, keepdims=False)
        kept = lax.dynamic_index_in_dim(kept, bit, axis, keepdims=False)
        pairs = [(device, device ^ (1 << step)) for device in range(count)]
        kept = kept + lax.ppermute(sent.astype(jnp.bfloat16), "dp", pairs).astype(jnp.float32)
    whole = kept.astype(jnp.bfloat16)[None]
    for step in reversed(range(steps)):
        bit = (own >> step) & 1
        pairs = [(device, device ^ (1 << step)) for device in range(count)]
        arrived = lax.ppermute(whole, "dp", pairs)
        low_half = jnp.where(bit == 0, whole, arrived)
        high_half = jnp.where(bit == 0, arrived, whole)
        whole = jnp.stack([low_half, high_half], axis=1).reshape((-1,) + whole.shape[1:])
    return whole.reshape(-1)[: flat.shape[0]]


def head_gather_relative(values):
    count = lax.axis_size("head")
    parts = [values]
    for shift in range(1, count):
        parts.append(
            lax.ppermute(values, "head", [(device, (device + shift) % count) for device in range(count)])
        )
    return jnp.concatenate(parts, axis=0)


def head_scatter_relative(values):
    count = lax.axis_size("head")
    width = values.shape[0] // count
    total = values[:width].astype(jnp.float32)
    for shift in range(1, count):
        sent = values[(count - shift) * width : (count - shift + 1) * width]
        total = total + lax.ppermute(
            sent, "head", [(device, (device + shift) % count) for device in range(count)]
        ).astype(jnp.float32)
    return total


def map_rows(step, items):
    outs = [step(tuple(item[row] for item in items)) for row in range(items[0].shape[0])]
    return tuple(jnp.stack(parts) for parts in zip(*outs))


def turn(block, cosine, sine):
    half_depth = block.shape[-1] // 2
    first_half, second_half = block[:, :half_depth], block[:, half_depth:]
    return jnp.concatenate(
        [first_half * cosine - second_half * sine, second_half * cosine + first_half * sine], axis=1
    )


def unturn(block, cosine, sine):
    half_depth = block.shape[-1] // 2
    first_half, second_half = block[:, :half_depth], block[:, half_depth:]
    return jnp.concatenate(
        [first_half * cosine + second_half * sine, second_half * cosine - first_half * sine], axis=1
    )


def local(
    tokens,
    doc_ids,
    gain_attn,
    a_weight,
    b_weight,
    out_weight,
    gain_ffn,
    gate_weight,
    up_weight,
    down_weight,
    cotangent,
):
    rows_dev, length = doc_ids.shape
    total_rows = rows_dev * length
    own_rows = tokens.shape[0]
    local_heads = out_weight.shape[0] // DH
    rank_all = RQ + 2 * RK
    x_own = tokens.astype(jnp.float32)
    inv_one = lax.rsqrt(jnp.mean(x_own * x_own, axis=-1, keepdims=True) + EPSILON)
    normed_one = (x_own * inv_one * gain_attn).astype(jnp.bfloat16)
    normed_all, grad_out_all = (
        head_all_gather(normed_one, 0),
        head_gather_relative(cotangent),
    )
    factor_a = jnp.dot(normed_all, a_weight, preferred_element_type=jnp.float32)
    factor_b = jnp.dot(normed_all, b_weight, preferred_element_type=jnp.float32)
    cosine, sine = rope_tables(total_rows, length)
    basis_query = [
        turn(factor_b[:, rank * DH : (rank + 1) * DH], cosine, sine) for rank in range(RQ)
    ]
    basis_key = [
        turn(factor_b[:, (RQ + rank) * DH : (RQ + rank + 1) * DH], cosine, sine)
        for rank in range(RK)
    ]
    basis_value = [
        factor_b[:, (RQ + RK + rank) * DH : (RQ + RK + rank + 1) * DH] for rank in range(RK)
    ]
    coef = [
        [factor_a[:, head * rank_all + column] [:, None] for column in range(rank_all)]
        for head in range(local_heads)
    ]

    def combine(bases, offset):
        return jnp.stack(
            [
                sum(coef[head][offset + rank] * bases[rank] for rank in range(len(bases)))
                / len(bases)
                for head in range(local_heads)
            ],
            axis=1,
        ).astype(jnp.bfloat16)

    queries = combine(basis_query, 0)
    key_rows = combine(basis_key, RQ)
    value_rows = combine(basis_value, RQ + RK)
    row_shape = (rows_dev, length, local_heads, DH)
    query_rows = queries.reshape(row_shape)
    keys_rows = key_rows.reshape(row_shape)
    values_rows = value_rows.reshape(row_shape)
    mixed_rows, log_total = map_rows(attend_row, (query_rows, keys_rows, values_rows, doc_ids))
    mixed = mixed_rows.reshape(total_rows, local_heads * DH)
    mixed, grad_out_all = lax.optimization_barrier((mixed, grad_out_all))
    piece = lax.slice_in_dim(mixed, 0, lax.axis_size("head") * own_rows, axis=0)
    resid_own = x_own + head_reduce_scatter(
        jnp.dot(piece, out_weight, preferred_element_type=jnp.float32).astype(jnp.bfloat16), 0
    )
    inv_two = lax.rsqrt(jnp.mean(resid_own * resid_own, axis=-1, keepdims=True) + EPSILON)
    normed_two = (resid_own * inv_two * gain_ffn).astype(jnp.bfloat16)
    normed_two_all = head_gather_relative(normed_two)
    gate_act = jnp.dot(normed_two_all, gate_weight, preferred_element_type=jnp.float32)
    up_act = jnp.dot(normed_two_all, up_weight, preferred_element_type=jnp.float32)
    sigmoid_gate = jax.nn.sigmoid(gate_act)
    silu_gate = sigmoid_gate * gate_act
    hidden = (silu_gate * up_act).astype(jnp.bfloat16)
    piece = lax.slice_in_dim(hidden, 0, lax.axis_size("head") * own_rows, axis=0)
    output = (
        resid_own
        + head_scatter_relative(
            jnp.dot(piece, down_weight, preferred_element_type=jnp.float32).astype(jnp.bfloat16)
        )
    ).astype(jnp.bfloat16)
    grad_down = dot_first(hidden, grad_out_all)
    grad_hidden = dot_last(grad_out_all, down_weight)
    grad_gate_act = (
        grad_hidden * up_act * (sigmoid_gate * (1.0 + gate_act * (1.0 - sigmoid_gate)))
    ).astype(jnp.bfloat16)
    grad_up_act = (grad_hidden * silu_gate).astype(jnp.bfloat16)
    grad_gate = dot_first(normed_two_all, grad_gate_act)
    grad_up = dot_first(normed_two_all, grad_up_act)
    gate_piece = lax.slice_in_dim(grad_gate_act, 0, lax.axis_size("head") * own_rows, axis=0)
    up_piece = lax.slice_in_dim(grad_up_act, 0, lax.axis_size("head") * own_rows, axis=0)
    grad_normed_two = head_scatter_relative(
        (dot_last(gate_piece, gate_weight) + dot_last(up_piece, up_weight)).astype(jnp.bfloat16)
    )
    ffn_grads = (grad_gate.astype(jnp.bfloat16), grad_up.astype(jnp.bfloat16), grad_down.astype(jnp.bfloat16))
    ffn_grads, grad_normed_two = lax.optimization_barrier((ffn_grads, grad_normed_two))
    grad_gate, grad_up, grad_down = lax.psum(ffn_grads, "dp")
    resid_part, grad_gain_ffn_own = norm_backward(resid_own, inv_two, gain_ffn, grad_normed_two)
    grad_resid = cotangent.astype(jnp.float32) + resid_part
    output, grad_resid = lax.optimization_barrier((output, grad_resid))
    grad_branch = head_all_gather(grad_resid.astype(jnp.bfloat16), 0)
    grad_mixed = dot_last(grad_branch, out_weight).astype(jnp.bfloat16)
    grad_out = dot_first(mixed, grad_branch)
    grad_query_rows, grad_key_rows, grad_value_rows = map_rows(
        attend_back,
        (query_rows, keys_rows, values_rows, doc_ids, log_total, grad_mixed.reshape(row_shape)),
    )
    head_shape = (total_rows, local_heads, DH)
    grad_query = rounded(grad_query_rows.reshape(head_shape))
    grad_key = rounded(grad_key_rows.reshape(head_shape))
    grad_value = rounded(grad_value_rows.reshape(head_shape))
    grads_by_part = ((grad_query, basis_query, 0), (grad_key, basis_key, RQ), (grad_value, basis_value, RQ + RK))
    coef_columns = [None] * (local_heads * rank_all)
    basis_grads = []
    for grad_part, bases, offset in grads_by_part:
        for rank, basis in enumerate(bases):
            for head in range(local_heads):
                coef_columns[head * rank_all + offset + rank] = jnp.sum(
                    grad_part[:, head, :] * basis, axis=1
                ) / len(bases)
            basis_grad = sum(
                coef[head][offset + rank] * grad_part[:, head, :] for head in range(local_heads)
            ) / len(bases)
            basis_grads.append(basis_grad if offset == RQ + RK else unturn(basis_grad, cosine, sine))
    grad_factor_a = jnp.stack(coef_columns, axis=1).astype(jnp.bfloat16)
    grad_factor_b = jnp.concatenate(basis_grads, axis=1)
    head_count = lax.axis_size("head")
    basis_cols = grad_factor_b.shape[1] // head_count
    factor_cols = head_reduce_scatter(grad_factor_b.astype(jnp.bfloat16), 1).astype(jnp.bfloat16)
    weight_cols = lax.dynamic_slice_in_dim(
        b_weight, lax.axis_index("head") * basis_cols, basis_cols, axis=1
    )
    piece = grad_factor_a
    grad_normed_one = head_reduce_scatter(
        (dot_last(piece, a_weight) + dot_last(factor_cols, weight_cols)).astype(jnp.bfloat16), 0
    )
    input_part, grad_gain_attn_own = norm_backward(x_own, inv_one, gain_attn, grad_normed_one)
    input_grad = grad_resid + input_part
    grad_a = dot_first(normed_all, grad_factor_a)
    grad_b_cols = dot_first(normed_all, factor_cols)

    features = grad_gain_attn_own.shape[0]
    gain_rows = -(-2 * features // basis_cols)
    gains = jnp.pad(
        jnp.concatenate([grad_gain_attn_own, grad_gain_ffn_own]),
        (0, gain_rows * basis_cols - 2 * features),
    ).reshape(gain_rows, basis_cols)
    tail = (
        grad_a.astype(jnp.bfloat16),
        grad_out.astype(jnp.bfloat16),
        jnp.concatenate([grad_b_cols, gains], axis=0).astype(jnp.bfloat16),
    )
    tail, (grad_gate, grad_up, grad_down) = lax.optimization_barrier(
        (tail, (grad_gate, grad_up, grad_down))
    )
    sizes = [part.size for part in tail]
    summed = dp_all_reduce(jnp.concatenate([part.reshape(-1) for part in tail]))
    grad_a, grad_out, packed = (
        summed[sum(sizes[:index]) : sum(sizes[: index + 1])].reshape(part.shape)
        for index, part in enumerate(tail)
    )
    grad_out, grad_gate, grad_up, grad_down = (
        grad_out.astype(jnp.float32),
        grad_gate.astype(jnp.float32),
        grad_up.astype(jnp.float32),
        grad_down.astype(jnp.float32),
    )
    grad_a = grad_a.astype(jnp.float32)
    packed = lax.all_gather(packed, "head", axis=1, tiled=True).astype(jnp.float32)
    grad_b = packed[: grad_b_cols.shape[0]]
    gains = jnp.sum(
        packed[grad_b_cols.shape[0] :].reshape(gain_rows, head_count, basis_cols), axis=1
    ).reshape(-1)
    grad_gain_attn, grad_gain_ffn = gains[:features], gains[features : 2 * features]
    return (
        output,
        input_grad,
        grad_gain_attn,
        grad_a,
        grad_b,
        grad_out,
        grad_gain_ffn,
        grad_gate,
        grad_up,
        grad_down,
    )


def solution(mesh):
    return jax.shard_map(
        local,
        mesh=mesh,
        in_specs=(
            P(("dp", "head"), None),
            P("dp", None),
            P(),
            P(None, "head"),
            P(),
            P("head", None),
            P(),
            P(None, "head"),
            P(None, "head"),
            P("head", None),
            P(("dp", "head"), None),
        ),
        out_specs=(
            P(("dp", "head"), None),
            P(("dp", "head"), None),
            P(),
            P(None, "head"),
            P(),
            P("head", None),
            P(),
            P(None, "head"),
            P(None, "head"),
            P("head", None),
        ),
        check_vma=False,
    )
```

```python
import math

import jax
import jax.numpy as jnp
from jax import lax
from jax.sharding import PartitionSpec as P

DH = 64
RQ = 6
RK = 2


EPSILON = 1e-06
MASKED = -1e30
PRECISE = lax.Precision.HIGHEST


def rope_tables(total_rows, length):
    half_depth = DH // 2
    position = (jnp.arange(total_rows, dtype=jnp.int32) % length).astype(jnp.float32)
    frequency = jnp.exp(jnp.arange(half_depth, dtype=jnp.float32) * (-2.0 * math.log(10000.0) / DH))
    angle = position[:, None] * frequency[None, :]
    return (jnp.cos(angle), jnp.sin(angle))


def rotate(basis, cosine, sine):
    half_depth = basis.shape[-1] // 2
    first_half = basis[..., :half_depth]
    second_half = basis[..., half_depth:]
    cosine_row = cosine[:, None, :]
    sine_row = sine[:, None, :]
    return jnp.concatenate(
        [
            first_half * cosine_row - second_half * sine_row,
            second_half * cosine_row + first_half * sine_row,
        ],
        axis=-1,
    )


def unrotate(grad_basis, cosine, sine):
    half_depth = grad_basis.shape[-1] // 2
    first_half = grad_basis[..., :half_depth]
    second_half = grad_basis[..., half_depth:]
    cosine_row = cosine[:, None, :]
    sine_row = sine[:, None, :]
    return jnp.concatenate(
        [
            first_half * cosine_row + second_half * sine_row,
            second_half * cosine_row - first_half * sine_row,
        ],
        axis=-1,
    )


def dot_last(left, right):
    return lax.dot_general(
        left, right, (((1,), (1,)), ((), ())), preferred_element_type=jnp.float32
    )


def dot_first(left, right):
    return lax.dot_general(
        left, right, (((0,), (0,)), ((), ())), preferred_element_type=jnp.float32
    )


def norm_backward(inputs, inverse, gain, grad_normed):
    scaled = gain * grad_normed
    inner = jnp.mean(scaled * inputs, axis=-1, keepdims=True)
    grad_inputs = inverse * scaled - inputs * (inverse * inverse * inverse) * inner
    grad_gain = jnp.sum(grad_normed * inputs * inverse, axis=0)
    return (grad_inputs, grad_gain)


def block_scores(queries, key_rows, doc_row, first_row, last_row):
    position = jnp.arange(last_row, dtype=jnp.int32)
    allowed = (doc_row[first_row:last_row, None] == doc_row[None, :last_row]) & (
        position[None, :] <= position[first_row:last_row, None]
    )
    score_scale = 1.0 / math.sqrt(queries.shape[2])
    scores = (
        jnp.einsum(
            "qhd,khd->hqk",
            queries[first_row:last_row],
            key_rows[:last_row],
            preferred_element_type=jnp.float32,
        )
        * score_scale
    )
    return jnp.where(allowed[None], scores, MASKED)


def attend_row(row_item):
    queries, key_rows, value_rows, doc_row = row_item
    length = queries.shape[0]
    block_rows = min(512, length)
    mixed_parts = []
    total_parts = []
    for first_row in range(0, length, block_rows):
        last_row = first_row + block_rows
        scores = block_scores(queries, key_rows, doc_row, first_row, last_row)
        row_peak = jnp.max(scores, axis=-1, keepdims=True)
        exponent = jnp.exp(scores - row_peak)
        row_total = jnp.sum(exponent, axis=-1, keepdims=True)
        weights = (exponent / row_total).astype(jnp.bfloat16)
        mixed_parts.append(
            jnp.einsum(
                "hqk,khd->qhd", weights, value_rows[:last_row], preferred_element_type=jnp.float32
            ).astype(jnp.bfloat16)
        )
        total_parts.append(row_peak[..., 0] + jnp.log(row_total[..., 0]))
    return (jnp.concatenate(mixed_parts, axis=0), jnp.concatenate(total_parts, axis=1))


def attend_back(row_item):
    queries, key_rows, value_rows, doc_row, log_total, grad_mixed = row_item
    length = queries.shape[0]
    block_rows = min(512, length)
    score_scale = 1.0 / math.sqrt(queries.shape[2])
    grad_query_parts = []
    grad_keys = jnp.zeros(key_rows.shape, jnp.float32)
    grad_values = jnp.zeros(value_rows.shape, jnp.float32)
    for first_row in range(0, length, block_rows):
        last_row = first_row + block_rows
        scores = block_scores(queries, key_rows, doc_row, first_row, last_row)
        weights = jnp.exp(scores - log_total[:, first_row:last_row, None])
        grad_weights = jnp.einsum(
            "qhd,khd->hqk",
            grad_mixed[first_row:last_row],
            value_rows[:last_row],
            preferred_element_type=jnp.float32,
        )
        inner = jnp.sum(weights * grad_weights, axis=-1, keepdims=True)
        grad_scores = (weights * (grad_weights - inner)).astype(jnp.bfloat16)
        grad_query_parts.append(
            jnp.einsum(
                "hqk,khd->qhd", grad_scores, key_rows[:last_row], preferred_element_type=jnp.float32
            )
            * score_scale
        )
        padding = ((0, length - last_row), (0, 0), (0, 0))
        key_part = (
            jnp.einsum(
                "hqk,qhd->khd",
                grad_scores,
                queries[first_row:last_row],
                preferred_element_type=jnp.float32,
            )
            * score_scale
        )
        value_part = jnp.einsum(
            "hqk,qhd->khd",
            weights.astype(jnp.bfloat16),
            grad_mixed[first_row:last_row],
            preferred_element_type=jnp.float32,
        )
        grad_keys = grad_keys + jnp.pad(key_part, padding)
        grad_values = grad_values + jnp.pad(value_part, padding)
    return (jnp.concatenate(grad_query_parts, axis=0), grad_keys, grad_values)


def rounded(values_in):
    return lax.optimization_barrier(values_in.astype(jnp.bfloat16)).astype(jnp.float32)


def head_reduce_scatter(values, axis):
    count = lax.axis_size("head")
    own = lax.axis_index("head")
    width = values.shape[axis] // count
    total = lax.dynamic_slice_in_dim(values, own * width, width, axis=axis).astype(jnp.float32)
    for shift in range(1, count):
        sent = lax.dynamic_slice_in_dim(values, ((own + shift) % count) * width, width, axis=axis)
        total = total + lax.ppermute(
            sent, "head", [(device, (device + shift) % count) for device in range(count)]
        ).astype(jnp.float32)
    return total


def head_all_gather(values, axis):
    count = lax.axis_size("head")
    own = lax.axis_index("head")
    width = values.shape[axis]
    shape = list(values.shape)
    shape[axis] = width * count
    gathered = lax.dynamic_update_slice_in_dim(
        jnp.zeros(shape, values.dtype), values, own * width, axis=axis
    )
    for shift in range(1, count):
        arrived = lax.ppermute(
            values, "head", [(device, (device + shift) % count) for device in range(count)]
        )
        gathered = lax.dynamic_update_slice_in_dim(
            gathered, arrived, ((own - shift) % count) * width, axis=axis
        )
    return gathered


def dp_all_reduce(flat):
    count = lax.axis_size("dp")
    own = lax.axis_index("dp")
    steps = count.bit_length() - 1
    assert count == 1 << steps
    width = -(-flat.shape[0] // (count * 128)) * 128
    blocks = jnp.pad(flat, (0, count * width - flat.shape[0])).reshape((2,) * steps + (width,))
    kept = blocks.astype(jnp.float32)
    for step in range(steps):
        axis = steps - 1 - step
        bit = (own >> step) & 1
        sent = lax.dynamic_index_in_dim(kept, 1 - bit, axis, keepdims=False)
        kept = lax.dynamic_index_in_dim(kept, bit, axis, keepdims=False)
        pairs = [(device, device ^ (1 << step)) for device in range(count)]
        kept = kept + lax.ppermute(sent.astype(jnp.bfloat16), "dp", pairs).astype(jnp.float32)
    whole = kept.astype(jnp.bfloat16)[None]
    for step in reversed(range(steps)):
        bit = (own >> step) & 1
        pairs = [(device, device ^ (1 << step)) for device in range(count)]
        arrived = lax.ppermute(whole, "dp", pairs)
        low_half = jnp.where(bit == 0, whole, arrived)
        high_half = jnp.where(bit == 0, arrived, whole)
        whole = jnp.stack([low_half, high_half], axis=1).reshape((-1,) + whole.shape[1:])
    return whole.reshape(-1)[: flat.shape[0]]


def head_gather_relative(values):
    count = lax.axis_size("head")
    parts = [values]
    for shift in range(1, count):
        parts.append(
            lax.ppermute(values, "head", [(device, (device + shift) % count) for device in range(count)])
        )
    return jnp.concatenate(parts, axis=0)


def head_scatter_relative(values):
    count = lax.axis_size("head")
    width = values.shape[0] // count
    total = values[:width].astype(jnp.float32)
    for shift in range(1, count):
        sent = values[(count - shift) * width : (count - shift + 1) * width]
        total = total + lax.ppermute(
            sent, "head", [(device, (device + shift) % count) for device in range(count)]
        ).astype(jnp.float32)
    return total


def map_rows(step, items):
    outs = [step(tuple(item[row] for item in items)) for row in range(items[0].shape[0])]
    return tuple(jnp.stack(parts) for parts in zip(*outs))


def turn(block, cosine, sine):
    half_depth = block.shape[-1] // 2
    first_half, second_half = block[:, :half_depth], block[:, half_depth:]
    return jnp.concatenate(
        [first_half * cosine - second_half * sine, second_half * cosine + first_half * sine], axis=1
    )


def unturn(block, cosine, sine):
    half_depth = block.shape[-1] // 2
    first_half, second_half = block[:, :half_depth], block[:, half_depth:]
    return jnp.concatenate(
        [first_half * cosine + second_half * sine, second_half * cosine - first_half * sine], axis=1
    )


def local(
    tokens,
    doc_ids,
    gain_attn,
    a_weight,
    b_weight,
    out_weight,
    gain_ffn,
    gate_weight,
    up_weight,
    down_weight,
    cotangent,
):
    rows_dev, length = doc_ids.shape
    total_rows = rows_dev * length
    own_rows = tokens.shape[0]
    local_heads = out_weight.shape[0] // DH
    rank_all = RQ + 2 * RK
    x_own = tokens.astype(jnp.float32)
    inv_one = lax.rsqrt(jnp.mean(x_own * x_own, axis=-1, keepdims=True) + EPSILON)
    normed_one = (x_own * inv_one * gain_attn).astype(jnp.bfloat16)
    normed_all, grad_out_all = (
        head_all_gather(normed_one, 0),
        head_gather_relative(cotangent),
    )
    factor_a = jnp.dot(normed_all, a_weight, preferred_element_type=jnp.float32)
    factor_b = jnp.dot(normed_all, b_weight, preferred_element_type=jnp.float32)
    cosine, sine = rope_tables(total_rows, length)
    basis_query = [
        turn(factor_b[:, rank * DH : (rank + 1) * DH], cosine, sine) for rank in range(RQ)
    ]
    basis_key = [
        turn(factor_b[:, (RQ + rank) * DH : (RQ + rank + 1) * DH], cosine, sine)
        for rank in range(RK)
    ]
    basis_value = [
        factor_b[:, (RQ + RK + rank) * DH : (RQ + RK + rank + 1) * DH] for rank in range(RK)
    ]
    coef = [
        [factor_a[:, head * rank_all + column] [:, None] for column in range(rank_all)]
        for head in range(local_heads)
    ]

    def combine(bases, offset):
        return jnp.stack(
            [
                sum(coef[head][offset + rank] * bases[rank] for rank in range(len(bases)))
                / len(bases)
                for head in range(local_heads)
            ],
            axis=1,
        ).astype(jnp.bfloat16)

    queries = combine(basis_query, 0)
    key_rows = combine(basis_key, RQ)
    value_rows = combine(basis_value, RQ + RK)
    row_shape = (rows_dev, length, local_heads, DH)
    query_rows = queries.reshape(row_shape)
    keys_rows = key_rows.reshape(row_shape)
    values_rows = value_rows.reshape(row_shape)
    mixed_rows, log_total = map_rows(attend_row, (query_rows, keys_rows, values_rows, doc_ids))
    mixed = mixed_rows.reshape(total_rows, local_heads * DH)
    mixed, grad_out_all = lax.optimization_barrier((mixed, grad_out_all))
    piece = lax.slice_in_dim(mixed, 0, lax.axis_size("head") * own_rows, axis=0)
    resid_own = x_own + head_reduce_scatter(
        jnp.dot(piece, out_weight, preferred_element_type=jnp.float32).astype(jnp.bfloat16), 0
    )
    inv_two = lax.rsqrt(jnp.mean(resid_own * resid_own, axis=-1, keepdims=True) + EPSILON)
    normed_two = (resid_own * inv_two * gain_ffn).astype(jnp.bfloat16)
    normed_two_all = head_gather_relative(normed_two)
    gate_act = jnp.dot(normed_two_all, gate_weight, preferred_element_type=jnp.float32)
    up_act = jnp.dot(normed_two_all, up_weight, preferred_element_type=jnp.float32)
    sigmoid_gate = jax.nn.sigmoid(gate_act)
    silu_gate = sigmoid_gate * gate_act
    hidden = (silu_gate * up_act).astype(jnp.bfloat16)
    piece = lax.slice_in_dim(hidden, 0, lax.axis_size("head") * own_rows, axis=0)
    output = (
        resid_own
        + head_scatter_relative(
            jnp.dot(piece, down_weight, preferred_element_type=jnp.float32).astype(jnp.bfloat16)
        )
    ).astype(jnp.bfloat16)
    grad_down = dot_first(hidden, grad_out_all)
    grad_hidden = dot_last(grad_out_all, down_weight)
    grad_gate_act = (
        grad_hidden * up_act * (sigmoid_gate * (1.0 + gate_act * (1.0 - sigmoid_gate)))
    ).astype(jnp.bfloat16)
    grad_up_act = (grad_hidden * silu_gate).astype(jnp.bfloat16)
    grad_gate = dot_first(normed_two_all, grad_gate_act)
    grad_up = dot_first(normed_two_all, grad_up_act)
    gate_piece = lax.slice_in_dim(grad_gate_act, 0, lax.axis_size("head") * own_rows, axis=0)
    up_piece = lax.slice_in_dim(grad_up_act, 0, lax.axis_size("head") * own_rows, axis=0)
    grad_normed_two = head_scatter_relative(
        (dot_last(gate_piece, gate_weight) + dot_last(up_piece, up_weight)).astype(jnp.bfloat16)
    )
    ffn_grads = (grad_gate.astype(jnp.bfloat16), grad_up, grad_down.astype(jnp.bfloat16))
    ffn_grads, grad_normed_two = lax.optimization_barrier((ffn_grads, grad_normed_two))
    grad_up = ffn_grads[1]
    grad_gate, grad_down = lax.psum((ffn_grads[0], ffn_grads[2]), "dp")
    grad_up = lax.psum(grad_up, "dp")
    resid_part, grad_gain_ffn_own = norm_backward(resid_own, inv_two, gain_ffn, grad_normed_two)
    grad_resid = cotangent.astype(jnp.float32) + resid_part
    output, grad_resid = lax.optimization_barrier((output, grad_resid))
    grad_branch = head_all_gather(grad_resid.astype(jnp.bfloat16), 0)
    grad_mixed = dot_last(grad_branch, out_weight).astype(jnp.bfloat16)
    grad_out = dot_first(mixed, grad_branch)
    grad_query_rows, grad_key_rows, grad_value_rows = map_rows(
        attend_back,
        (query_rows, keys_rows, values_rows, doc_ids, log_total, grad_mixed.reshape(row_shape)),
    )
    head_shape = (total_rows, local_heads, DH)
    grad_query = rounded(grad_query_rows.reshape(head_shape))
    grad_key = rounded(grad_key_rows.reshape(head_shape))
    grad_value = rounded(grad_value_rows.reshape(head_shape))
    grads_by_part = ((grad_query, basis_query, 0), (grad_key, basis_key, RQ), (grad_value, basis_value, RQ + RK))
    coef_columns = [None] * (local_heads * rank_all)
    basis_grads = []
    for grad_part, bases, offset in grads_by_part:
        for rank, basis in enumerate(bases):
            for head in range(local_heads):
                coef_columns[head * rank_all + offset + rank] = jnp.sum(
                    grad_part[:, head, :] * basis, axis=1
                ) / len(bases)
            basis_grad = sum(
                coef[head][offset + rank] * grad_part[:, head, :] for head in range(local_heads)
            ) / len(bases)
            basis_grads.append(basis_grad if offset == RQ + RK else unturn(basis_grad, cosine, sine))
    grad_factor_a = jnp.stack(coef_columns, axis=1).astype(jnp.bfloat16)
    grad_factor_b = jnp.concatenate(basis_grads, axis=1)
    head_count = lax.axis_size("head")
    basis_cols = grad_factor_b.shape[1] // head_count
    factor_cols = head_reduce_scatter(grad_factor_b.astype(jnp.bfloat16), 1).astype(jnp.bfloat16)
    weight_cols = lax.dynamic_slice_in_dim(
        b_weight, lax.axis_index("head") * basis_cols, basis_cols, axis=1
    )
    piece = grad_factor_a
    grad_normed_one = head_reduce_scatter(
        (dot_last(piece, a_weight) + dot_last(factor_cols, weight_cols)).astype(jnp.bfloat16), 0
    )
    input_part, grad_gain_attn_own = norm_backward(x_own, inv_one, gain_attn, grad_normed_one)
    input_grad = grad_resid + input_part
    grad_a = dot_first(normed_all, grad_factor_a)
    grad_b_cols = dot_first(normed_all, factor_cols)

    features = grad_gain_attn_own.shape[0]
    gain_rows = -(-2 * features // basis_cols)
    gains = jnp.pad(
        jnp.concatenate([grad_gain_attn_own, grad_gain_ffn_own]),
        (0, gain_rows * basis_cols - 2 * features),
    ).reshape(gain_rows, basis_cols)
    tail = (
        grad_a.astype(jnp.bfloat16),
        grad_out.astype(jnp.bfloat16),
        jnp.concatenate([grad_b_cols, gains], axis=0).astype(jnp.bfloat16),
    )
    tail, (grad_gate, grad_up, grad_down) = lax.optimization_barrier(
        (tail, (grad_gate, grad_up, grad_down))
    )
    sizes = [part.size for part in tail]
    summed = dp_all_reduce(jnp.concatenate([part.reshape(-1) for part in tail]))
    grad_a, grad_out, packed = (
        summed[sum(sizes[:index]) : sum(sizes[: index + 1])].reshape(part.shape)
        for index, part in enumerate(tail)
    )
    grad_out, grad_gate, grad_up, grad_down = (
        grad_out.astype(jnp.float32),
        grad_gate.astype(jnp.float32),
        grad_up.astype(jnp.float32),
        grad_down.astype(jnp.float32),
    )
    grad_a = grad_a.astype(jnp.float32)
    packed = lax.all_gather(packed, "head", axis=1, tiled=True).astype(jnp.float32)
    grad_b = packed[: grad_b_cols.shape[0]]
    gains = jnp.sum(
        packed[grad_b_cols.shape[0] :].reshape(gain_rows, head_count, basis_cols), axis=1
    ).reshape(-1)
    grad_gain_attn, grad_gain_ffn = gains[:features], gains[features : 2 * features]
    return (
        output,
        input_grad,
        grad_gain_attn,
        grad_a,
        grad_b,
        grad_out,
        grad_gain_ffn,
        grad_gate,
        grad_up,
        grad_down,
    )


def solution(mesh):
    return jax.shard_map(
        local,
        mesh=mesh,
        in_specs=(
            P(("dp", "head"), None),
            P("dp", None),
            P(),
            P(None, "head"),
            P(),
            P("head", None),
            P(),
            P(None, "head"),
            P(None, "head"),
            P("head", None),
            P(("dp", "head"), None),
        ),
        out_specs=(
            P(("dp", "head"), None),
            P(("dp", "head"), None),
            P(),
            P(None, "head"),
            P(),
            P("head", None),
            P(),
            P(None, "head"),
            P(None, "head"),
            P("head", None),
        ),
        check_vma=False,
    )
```

```python
import math

import jax
import jax.numpy as jnp
from jax import lax
from jax.sharding import PartitionSpec as P

DH = 64
RQ = 6
RK = 2


EPSILON = 1e-06
MASKED = -1e30
PRECISE = lax.Precision.HIGHEST


def rope_tables(total_rows, length):
    half_depth = DH // 2
    position = (jnp.arange(total_rows, dtype=jnp.int32) % length).astype(jnp.float32)
    frequency = jnp.exp(jnp.arange(half_depth, dtype=jnp.float32) * (-2.0 * math.log(10000.0) / DH))
    angle = position[:, None] * frequency[None, :]
    return (jnp.cos(angle), jnp.sin(angle))


def rotate(basis, cosine, sine):
    half_depth = basis.shape[-1] // 2
    first_half = basis[..., :half_depth]
    second_half = basis[..., half_depth:]
    cosine_row = cosine[:, None, :]
    sine_row = sine[:, None, :]
    return jnp.concatenate(
        [
            first_half * cosine_row - second_half * sine_row,
            second_half * cosine_row + first_half * sine_row,
        ],
        axis=-1,
    )


def unrotate(grad_basis, cosine, sine):
    half_depth = grad_basis.shape[-1] // 2
    first_half = grad_basis[..., :half_depth]
    second_half = grad_basis[..., half_depth:]
    cosine_row = cosine[:, None, :]
    sine_row = sine[:, None, :]
    return jnp.concatenate(
        [
            first_half * cosine_row + second_half * sine_row,
            second_half * cosine_row - first_half * sine_row,
        ],
        axis=-1,
    )


def dot_last(left, right):
    return lax.dot_general(
        left, right, (((1,), (1,)), ((), ())), preferred_element_type=jnp.float32
    )


def dot_first(left, right):
    return lax.dot_general(
        left, right, (((0,), (0,)), ((), ())), preferred_element_type=jnp.float32
    )


def norm_backward(inputs, inverse, gain, grad_normed):
    scaled = gain * grad_normed
    inner = jnp.mean(scaled * inputs, axis=-1, keepdims=True)
    grad_inputs = inverse * scaled - inputs * (inverse * inverse * inverse) * inner
    grad_gain = jnp.sum(grad_normed * inputs * inverse, axis=0)
    return (grad_inputs, grad_gain)


def block_scores(queries, key_rows, doc_row, first_row, last_row):
    position = jnp.arange(last_row, dtype=jnp.int32)
    allowed = (doc_row[first_row:last_row, None] == doc_row[None, :last_row]) & (
        position[None, :] <= position[first_row:last_row, None]
    )
    score_scale = 1.0 / math.sqrt(queries.shape[2])
    scores = (
        jnp.einsum(
            "qhd,khd->hqk",
            queries[first_row:last_row],
            key_rows[:last_row],
            preferred_element_type=jnp.float32,
        )
        * score_scale
    )
    return jnp.where(allowed[None], scores, MASKED)


def attend_row(row_item):
    queries, key_rows, value_rows, doc_row = row_item
    length = queries.shape[0]
    block_rows = min(512, length)
    mixed_parts = []
    total_parts = []
    for first_row in range(0, length, block_rows):
        last_row = first_row + block_rows
        scores = block_scores(queries, key_rows, doc_row, first_row, last_row)
        row_peak = jnp.max(scores, axis=-1, keepdims=True)
        exponent = jnp.exp(scores - row_peak)
        row_total = jnp.sum(exponent, axis=-1, keepdims=True)
        weights = (exponent / row_total).astype(jnp.bfloat16)
        mixed_parts.append(
            jnp.einsum(
                "hqk,khd->qhd", weights, value_rows[:last_row], preferred_element_type=jnp.float32
            ).astype(jnp.bfloat16)
        )
        total_parts.append(row_peak[..., 0] + jnp.log(row_total[..., 0]))
    return (jnp.concatenate(mixed_parts, axis=0), jnp.concatenate(total_parts, axis=1))


def attend_back(row_item):
    queries, key_rows, value_rows, doc_row, log_total, grad_mixed = row_item
    length = queries.shape[0]
    block_rows = min(512, length)
    score_scale = 1.0 / math.sqrt(queries.shape[2])
    grad_query_parts = []
    grad_keys = jnp.zeros(key_rows.shape, jnp.float32)
    grad_values = jnp.zeros(value_rows.shape, jnp.float32)
    for first_row in range(0, length, block_rows):
        last_row = first_row + block_rows
        scores = block_scores(queries, key_rows, doc_row, first_row, last_row)
        weights = jnp.exp(scores - log_total[:, first_row:last_row, None])
        grad_weights = jnp.einsum(
            "qhd,khd->hqk",
            grad_mixed[first_row:last_row],
            value_rows[:last_row],
            preferred_element_type=jnp.float32,
        )
        inner = jnp.sum(weights * grad_weights, axis=-1, keepdims=True)
        grad_scores = (weights * (grad_weights - inner)).astype(jnp.bfloat16)
        grad_query_parts.append(
            jnp.einsum(
                "hqk,khd->qhd", grad_scores, key_rows[:last_row], preferred_element_type=jnp.float32
            )
            * score_scale
        )
        padding = ((0, length - last_row), (0, 0), (0, 0))
        key_part = (
            jnp.einsum(
                "hqk,qhd->khd",
                grad_scores,
                queries[first_row:last_row],
                preferred_element_type=jnp.float32,
            )
            * score_scale
        )
        value_part = jnp.einsum(
            "hqk,qhd->khd",
            weights.astype(jnp.bfloat16),
            grad_mixed[first_row:last_row],
            preferred_element_type=jnp.float32,
        )
        grad_keys = grad_keys + jnp.pad(key_part, padding)
        grad_values = grad_values + jnp.pad(value_part, padding)
    return (jnp.concatenate(grad_query_parts, axis=0), grad_keys, grad_values)


def rounded(values_in):
    return lax.optimization_barrier(values_in.astype(jnp.bfloat16)).astype(jnp.float32)


def head_reduce_scatter(values, axis):
    count = lax.axis_size("head")
    own = lax.axis_index("head")
    width = values.shape[axis] // count
    total = lax.dynamic_slice_in_dim(values, own * width, width, axis=axis).astype(jnp.float32)
    for shift in range(1, count):
        sent = lax.dynamic_slice_in_dim(values, ((own + shift) % count) * width, width, axis=axis)
        total = total + lax.ppermute(
            sent, "head", [(device, (device + shift) % count) for device in range(count)]
        ).astype(jnp.float32)
    return total


def head_all_gather(values, axis):
    count = lax.axis_size("head")
    own = lax.axis_index("head")
    width = values.shape[axis]
    shape = list(values.shape)
    shape[axis] = width * count
    gathered = lax.dynamic_update_slice_in_dim(
        jnp.zeros(shape, values.dtype), values, own * width, axis=axis
    )
    for shift in range(1, count):
        arrived = lax.ppermute(
            values, "head", [(device, (device + shift) % count) for device in range(count)]
        )
        gathered = lax.dynamic_update_slice_in_dim(
            gathered, arrived, ((own - shift) % count) * width, axis=axis
        )
    return gathered


def dp_all_reduce(flat):
    count = lax.axis_size("dp")
    own = lax.axis_index("dp")
    steps = count.bit_length() - 1
    assert count == 1 << steps
    width = -(-flat.shape[0] // (count * 128)) * 128
    blocks = jnp.pad(flat, (0, count * width - flat.shape[0])).reshape((2,) * steps + (width,))
    kept = blocks.astype(jnp.float32)
    for step in range(steps):
        axis = steps - 1 - step
        bit = (own >> step) & 1
        sent = lax.dynamic_index_in_dim(kept, 1 - bit, axis, keepdims=False)
        kept = lax.dynamic_index_in_dim(kept, bit, axis, keepdims=False)
        pairs = [(device, device ^ (1 << step)) for device in range(count)]
        kept = kept + lax.ppermute(sent.astype(jnp.bfloat16), "dp", pairs).astype(jnp.float32)
    whole = kept.astype(jnp.bfloat16)[None]
    for step in reversed(range(steps)):
        bit = (own >> step) & 1
        pairs = [(device, device ^ (1 << step)) for device in range(count)]
        arrived = lax.ppermute(whole, "dp", pairs)
        low_half = jnp.where(bit == 0, whole, arrived)
        high_half = jnp.where(bit == 0, arrived, whole)
        whole = jnp.stack([low_half, high_half], axis=1).reshape((-1,) + whole.shape[1:])
    return whole.reshape(-1)[: flat.shape[0]]


def head_gather_relative(values):
    count = lax.axis_size("head")
    parts = [values]
    for shift in range(1, count):
        parts.append(
            lax.ppermute(values, "head", [(device, (device + shift) % count) for device in range(count)])
        )
    return jnp.concatenate(parts, axis=0)


def head_scatter_relative(values):
    count = lax.axis_size("head")
    width = values.shape[0] // count
    total = values[:width].astype(jnp.float32)
    for shift in range(1, count):
        sent = values[(count - shift) * width : (count - shift + 1) * width]
        total = total + lax.ppermute(
            sent, "head", [(device, (device + shift) % count) for device in range(count)]
        ).astype(jnp.float32)
    return total


def map_rows(step, items):
    outs = [step(tuple(item[row] for item in items)) for row in range(items[0].shape[0])]
    return tuple(jnp.stack(parts) for parts in zip(*outs))


def turn(block, cosine, sine):
    half_depth = block.shape[-1] // 2
    first_half, second_half = block[:, :half_depth], block[:, half_depth:]
    return jnp.concatenate(
        [first_half * cosine - second_half * sine, second_half * cosine + first_half * sine], axis=1
    )


def unturn(block, cosine, sine):
    half_depth = block.shape[-1] // 2
    first_half, second_half = block[:, :half_depth], block[:, half_depth:]
    return jnp.concatenate(
        [first_half * cosine + second_half * sine, second_half * cosine - first_half * sine], axis=1
    )


def local(
    tokens,
    doc_ids,
    gain_attn,
    a_weight,
    b_weight,
    out_weight,
    gain_ffn,
    gate_weight,
    up_weight,
    down_weight,
    cotangent,
):
    rows_dev, length = doc_ids.shape
    total_rows = rows_dev * length
    own_rows = tokens.shape[0]
    local_heads = out_weight.shape[0] // DH
    rank_all = RQ + 2 * RK
    x_own = tokens.astype(jnp.float32)
    inv_one = lax.rsqrt(jnp.mean(x_own * x_own, axis=-1, keepdims=True) + EPSILON)
    normed_one = (x_own * inv_one * gain_attn).astype(jnp.bfloat16)
    normed_all = head_all_gather(normed_one, 0)
    normed_all, cotangent_late = lax.optimization_barrier((normed_all, cotangent))
    grad_out_all = head_gather_relative(cotangent_late)
    factor_a = jnp.dot(normed_all, a_weight, preferred_element_type=jnp.float32)
    factor_b = jnp.dot(normed_all, b_weight, preferred_element_type=jnp.float32)
    cosine, sine = rope_tables(total_rows, length)
    basis_query = [
        turn(factor_b[:, rank * DH : (rank + 1) * DH], cosine, sine) for rank in range(RQ)
    ]
    basis_key = [
        turn(factor_b[:, (RQ + rank) * DH : (RQ + rank + 1) * DH], cosine, sine)
        for rank in range(RK)
    ]
    basis_value = [
        factor_b[:, (RQ + RK + rank) * DH : (RQ + RK + rank + 1) * DH] for rank in range(RK)
    ]
    coef = [
        [factor_a[:, head * rank_all + column] [:, None] for column in range(rank_all)]
        for head in range(local_heads)
    ]

    def combine(bases, offset):
        return jnp.stack(
            [
                sum(coef[head][offset + rank] * bases[rank] for rank in range(len(bases)))
                / len(bases)
                for head in range(local_heads)
            ],
            axis=1,
        ).astype(jnp.bfloat16)

    queries = combine(basis_query, 0)
    key_rows = combine(basis_key, RQ)
    value_rows = combine(basis_value, RQ + RK)
    row_shape = (rows_dev, length, local_heads, DH)
    query_rows = queries.reshape(row_shape)
    keys_rows = key_rows.reshape(row_shape)
    values_rows = value_rows.reshape(row_shape)
    mixed_rows, log_total = map_rows(attend_row, (query_rows, keys_rows, values_rows, doc_ids))
    mixed = mixed_rows.reshape(total_rows, local_heads * DH)
    mixed, grad_out_all = lax.optimization_barrier((mixed, grad_out_all))
    piece = lax.slice_in_dim(mixed, 0, lax.axis_size("head") * own_rows, axis=0)
    resid_own = x_own + head_reduce_scatter(
        jnp.dot(piece, out_weight, preferred_element_type=jnp.float32).astype(jnp.bfloat16), 0
    )
    inv_two = lax.rsqrt(jnp.mean(resid_own * resid_own, axis=-1, keepdims=True) + EPSILON)
    normed_two = (resid_own * inv_two * gain_ffn).astype(jnp.bfloat16)
    normed_two_all = head_gather_relative(normed_two)
    gate_act = jnp.dot(normed_two_all, gate_weight, preferred_element_type=jnp.float32)
    up_act = jnp.dot(normed_two_all, up_weight, preferred_element_type=jnp.float32)
    sigmoid_gate = jax.nn.sigmoid(gate_act)
    silu_gate = sigmoid_gate * gate_act
    hidden = (silu_gate * up_act).astype(jnp.bfloat16)
    piece = lax.slice_in_dim(hidden, 0, lax.axis_size("head") * own_rows, axis=0)
    output = (
        resid_own
        + head_scatter_relative(
            jnp.dot(piece, down_weight, preferred_element_type=jnp.float32).astype(jnp.bfloat16)
        )
    ).astype(jnp.bfloat16)
    grad_down = dot_first(hidden, grad_out_all)
    grad_hidden = dot_last(grad_out_all, down_weight)
    grad_gate_act = (
        grad_hidden * up_act * (sigmoid_gate * (1.0 + gate_act * (1.0 - sigmoid_gate)))
    ).astype(jnp.bfloat16)
    grad_up_act = (grad_hidden * silu_gate).astype(jnp.bfloat16)
    grad_gate = dot_first(normed_two_all, grad_gate_act)
    grad_up = dot_first(normed_two_all, grad_up_act)
    gate_piece = lax.slice_in_dim(grad_gate_act, 0, lax.axis_size("head") * own_rows, axis=0)
    up_piece = lax.slice_in_dim(grad_up_act, 0, lax.axis_size("head") * own_rows, axis=0)
    grad_normed_two = head_scatter_relative(
        (dot_last(gate_piece, gate_weight) + dot_last(up_piece, up_weight)).astype(jnp.bfloat16)
    )
    ffn_grads = (grad_gate.astype(jnp.bfloat16), grad_up.astype(jnp.bfloat16), grad_down.astype(jnp.bfloat16))
    ffn_grads, grad_normed_two = lax.optimization_barrier((ffn_grads, grad_normed_two))
    grad_gate, grad_up, grad_down = lax.psum(ffn_grads, "dp")
    resid_part, grad_gain_ffn_own = norm_backward(resid_own, inv_two, gain_ffn, grad_normed_two)
    grad_resid = cotangent.astype(jnp.float32) + resid_part
    output, grad_resid = lax.optimization_barrier((output, grad_resid))
    grad_branch = head_all_gather(grad_resid.astype(jnp.bfloat16), 0)
    grad_mixed = dot_last(grad_branch, out_weight).astype(jnp.bfloat16)
    grad_out = dot_first(mixed, grad_branch)
    grad_query_rows, grad_key_rows, grad_value_rows = map_rows(
        attend_back,
        (query_rows, keys_rows, values_rows, doc_ids, log_total, grad_mixed.reshape(row_shape)),
    )
    head_shape = (total_rows, local_heads, DH)
    grad_query = rounded(grad_query_rows.reshape(head_shape))
    grad_key = rounded(grad_key_rows.reshape(head_shape))
    grad_value = rounded(grad_value_rows.reshape(head_shape))
    grads_by_part = ((grad_query, basis_query, 0), (grad_key, basis_key, RQ), (grad_value, basis_value, RQ + RK))
    coef_columns = [None] * (local_heads * rank_all)
    basis_grads = []
    for grad_part, bases, offset in grads_by_part:
        for rank, basis in enumerate(bases):
            for head in range(local_heads):
                coef_columns[head * rank_all + offset + rank] = jnp.sum(
                    grad_part[:, head, :] * basis, axis=1
                ) / len(bases)
            basis_grad = sum(
                coef[head][offset + rank] * grad_part[:, head, :] for head in range(local_heads)
            ) / len(bases)
            basis_grads.append(basis_grad if offset == RQ + RK else unturn(basis_grad, cosine, sine))
    grad_factor_a = jnp.stack(coef_columns, axis=1).astype(jnp.bfloat16)
    grad_factor_b = jnp.concatenate(basis_grads, axis=1)
    head_count = lax.axis_size("head")
    basis_cols = grad_factor_b.shape[1] // head_count
    factor_cols = head_reduce_scatter(grad_factor_b.astype(jnp.bfloat16), 1).astype(jnp.bfloat16)
    weight_cols = lax.dynamic_slice_in_dim(
        b_weight, lax.axis_index("head") * basis_cols, basis_cols, axis=1
    )
    piece = grad_factor_a
    grad_normed_one = head_reduce_scatter(
        (dot_last(piece, a_weight) + dot_last(factor_cols, weight_cols)).astype(jnp.bfloat16), 0
    )
    input_part, grad_gain_attn_own = norm_backward(x_own, inv_one, gain_attn, grad_normed_one)
    input_grad = grad_resid + input_part
    grad_a = dot_first(normed_all, grad_factor_a)
    grad_b_cols = dot_first(normed_all, factor_cols)

    features = grad_gain_attn_own.shape[0]
    gain_rows = -(-2 * features // basis_cols)
    gains = jnp.pad(
        jnp.concatenate([grad_gain_attn_own, grad_gain_ffn_own]),
        (0, gain_rows * basis_cols - 2 * features),
    ).reshape(gain_rows, basis_cols)
    tail = (
        grad_a.astype(jnp.bfloat16),
        grad_out.astype(jnp.bfloat16),
        jnp.concatenate([grad_b_cols, gains], axis=0).astype(jnp.bfloat16),
    )
    tail, (grad_gate, grad_up, grad_down) = lax.optimization_barrier(
        (tail, (grad_gate, grad_up, grad_down))
    )
    sizes = [part.size for part in tail]
    summed = dp_all_reduce(jnp.concatenate([part.reshape(-1) for part in tail]))
    grad_a, grad_out, packed = (
        summed[sum(sizes[:index]) : sum(sizes[: index + 1])].reshape(part.shape)
        for index, part in enumerate(tail)
    )
    grad_out, grad_gate, grad_up, grad_down = (
        grad_out.astype(jnp.float32),
        grad_gate.astype(jnp.float32),
        grad_up.astype(jnp.float32),
        grad_down.astype(jnp.float32),
    )
    grad_a = grad_a.astype(jnp.float32)
    packed = lax.all_gather(packed, "head", axis=1, tiled=True).astype(jnp.float32)
    grad_b = packed[: grad_b_cols.shape[0]]
    gains = jnp.sum(
        packed[grad_b_cols.shape[0] :].reshape(gain_rows, head_count, basis_cols), axis=1
    ).reshape(-1)
    grad_gain_attn, grad_gain_ffn = gains[:features], gains[features : 2 * features]
    return (
        output,
        input_grad,
        grad_gain_attn,
        grad_a,
        grad_b,
        grad_out,
        grad_gain_ffn,
        grad_gate,
        grad_up,
        grad_down,
    )


def solution(mesh):
    return jax.shard_map(
        local,
        mesh=mesh,
        in_specs=(
            P(("dp", "head"), None),
            P("dp", None),
            P(),
            P(None, "head"),
            P(),
            P("head", None),
            P(),
            P(None, "head"),
            P(None, "head"),
            P("head", None),
            P(("dp", "head"), None),
        ),
        out_specs=(
            P(("dp", "head"), None),
            P(("dp", "head"), None),
            P(),
            P(None, "head"),
            P(),
            P("head", None),
            P(),
            P(None, "head"),
            P(None, "head"),
            P("head", None),
        ),
        check_vma=False,
    )
```

```python
import math

import jax
import jax.numpy as jnp
from jax import lax
from jax.sharding import PartitionSpec as P

DH = 64
RQ = 6
RK = 2


EPSILON = 1e-06
MASKED = -1e30
PRECISE = lax.Precision.HIGHEST


def rope_tables(total_rows, length):
    half_depth = DH // 2
    position = (jnp.arange(total_rows, dtype=jnp.int32) % length).astype(jnp.float32)
    frequency = jnp.exp(jnp.arange(half_depth, dtype=jnp.float32) * (-2.0 * math.log(10000.0) / DH))
    angle = position[:, None] * frequency[None, :]
    return (jnp.cos(angle), jnp.sin(angle))


def rotate(basis, cosine, sine):
    half_depth = basis.shape[-1] // 2
    first_half = basis[..., :half_depth]
    second_half = basis[..., half_depth:]
    cosine_row = cosine[:, None, :]
    sine_row = sine[:, None, :]
    return jnp.concatenate(
        [
            first_half * cosine_row - second_half * sine_row,
            second_half * cosine_row + first_half * sine_row,
        ],
        axis=-1,
    )


def unrotate(grad_basis, cosine, sine):
    half_depth = grad_basis.shape[-1] // 2
    first_half = grad_basis[..., :half_depth]
    second_half = grad_basis[..., half_depth:]
    cosine_row = cosine[:, None, :]
    sine_row = sine[:, None, :]
    return jnp.concatenate(
        [
            first_half * cosine_row + second_half * sine_row,
            second_half * cosine_row - first_half * sine_row,
        ],
        axis=-1,
    )


def dot_last(left, right):
    return lax.dot_general(
        left, right, (((1,), (1,)), ((), ())), preferred_element_type=jnp.float32
    )


def dot_first(left, right):
    return lax.dot_general(
        left, right, (((0,), (0,)), ((), ())), preferred_element_type=jnp.float32
    )


def norm_backward(inputs, inverse, gain, grad_normed):
    scaled = gain * grad_normed
    inner = jnp.mean(scaled * inputs, axis=-1, keepdims=True)
    grad_inputs = inverse * scaled - inputs * (inverse * inverse * inverse) * inner
    grad_gain = jnp.sum(grad_normed * inputs * inverse, axis=0)
    return (grad_inputs, grad_gain)


def block_scores(queries, key_rows, doc_row, first_row, last_row):
    position = jnp.arange(last_row, dtype=jnp.int32)
    allowed = (doc_row[first_row:last_row, None] == doc_row[None, :last_row]) & (
        position[None, :] <= position[first_row:last_row, None]
    )
    score_scale = 1.0 / math.sqrt(queries.shape[2])
    scores = (
        jnp.einsum(
            "qhd,khd->hqk",
            queries[first_row:last_row],
            key_rows[:last_row],
            preferred_element_type=jnp.float32,
        )
        * score_scale
    )
    return jnp.where(allowed[None], scores, MASKED)


def attend_row(row_item):
    queries, key_rows, value_rows, doc_row = row_item
    length = queries.shape[0]
    block_rows = min(512, length)
    mixed_parts = []
    total_parts = []
    for first_row in range(0, length, block_rows):
        last_row = first_row + block_rows
        scores = block_scores(queries, key_rows, doc_row, first_row, last_row)
        row_peak = jnp.max(scores, axis=-1, keepdims=True)
        exponent = jnp.exp(scores - row_peak)
        row_total = jnp.sum(exponent, axis=-1, keepdims=True)
        weights = (exponent / row_total).astype(jnp.bfloat16)
        mixed_parts.append(
            jnp.einsum(
                "hqk,khd->qhd", weights, value_rows[:last_row], preferred_element_type=jnp.float32
            ).astype(jnp.bfloat16)
        )
        total_parts.append(row_peak[..., 0] + jnp.log(row_total[..., 0]))
    return (jnp.concatenate(mixed_parts, axis=0), jnp.concatenate(total_parts, axis=1))


def attend_back(row_item):
    queries, key_rows, value_rows, doc_row, log_total, grad_mixed = row_item
    length = queries.shape[0]
    block_rows = min(512, length)
    score_scale = 1.0 / math.sqrt(queries.shape[2])
    grad_query_parts = []
    grad_keys = jnp.zeros(key_rows.shape, jnp.float32)
    grad_values = jnp.zeros(value_rows.shape, jnp.float32)
    for first_row in range(0, length, block_rows):
        last_row = first_row + block_rows
        scores = block_scores(queries, key_rows, doc_row, first_row, last_row)
        weights = jnp.exp(scores - log_total[:, first_row:last_row, None])
        grad_weights = jnp.einsum(
            "qhd,khd->hqk",
            grad_mixed[first_row:last_row],
            value_rows[:last_row],
            preferred_element_type=jnp.float32,
        )
        inner = jnp.sum(weights * grad_weights, axis=-1, keepdims=True)
        grad_scores = (weights * (grad_weights - inner)).astype(jnp.bfloat16)
        grad_query_parts.append(
            jnp.einsum(
                "hqk,khd->qhd", grad_scores, key_rows[:last_row], preferred_element_type=jnp.float32
            )
            * score_scale
        )
        padding = ((0, length - last_row), (0, 0), (0, 0))
        key_part = (
            jnp.einsum(
                "hqk,qhd->khd",
                grad_scores,
                queries[first_row:last_row],
                preferred_element_type=jnp.float32,
            )
            * score_scale
        )
        value_part = jnp.einsum(
            "hqk,qhd->khd",
            weights.astype(jnp.bfloat16),
            grad_mixed[first_row:last_row],
            preferred_element_type=jnp.float32,
        )
        grad_keys = grad_keys + jnp.pad(key_part, padding)
        grad_values = grad_values + jnp.pad(value_part, padding)
    return (jnp.concatenate(grad_query_parts, axis=0), grad_keys, grad_values)


def rounded(values_in):
    return lax.optimization_barrier(values_in.astype(jnp.bfloat16)).astype(jnp.float32)


def head_reduce_scatter(values, axis):
    count = lax.axis_size("head")
    own = lax.axis_index("head")
    width = values.shape[axis] // count
    total = lax.dynamic_slice_in_dim(values, own * width, width, axis=axis).astype(jnp.float32)
    for shift in range(1, count):
        sent = lax.dynamic_slice_in_dim(values, ((own + shift) % count) * width, width, axis=axis)
        total = total + lax.ppermute(
            sent, "head", [(device, (device + shift) % count) for device in range(count)]
        ).astype(jnp.float32)
    return total


def head_all_gather(values, axis):
    count = lax.axis_size("head")
    own = lax.axis_index("head")
    width = values.shape[axis]
    shape = list(values.shape)
    shape[axis] = width * count
    gathered = lax.dynamic_update_slice_in_dim(
        jnp.zeros(shape, values.dtype), values, own * width, axis=axis
    )
    for shift in range(1, count):
        arrived = lax.ppermute(
            values, "head", [(device, (device + shift) % count) for device in range(count)]
        )
        gathered = lax.dynamic_update_slice_in_dim(
            gathered, arrived, ((own - shift) % count) * width, axis=axis
        )
    return gathered


def dp_all_reduce(flat):
    count = lax.axis_size("dp")
    own = lax.axis_index("dp")
    steps = count.bit_length() - 1
    assert count == 1 << steps
    width = -(-flat.shape[0] // (count * 128)) * 128
    blocks = jnp.pad(flat, (0, count * width - flat.shape[0])).reshape((2,) * steps + (width,))
    kept = blocks.astype(jnp.float32)
    for step in range(steps):
        axis = steps - 1 - step
        bit = (own >> step) & 1
        sent = lax.dynamic_index_in_dim(kept, 1 - bit, axis, keepdims=False)
        kept = lax.dynamic_index_in_dim(kept, bit, axis, keepdims=False)
        pairs = [(device, device ^ (1 << step)) for device in range(count)]
        kept = kept + lax.ppermute(sent.astype(jnp.bfloat16), "dp", pairs).astype(jnp.float32)
    whole = kept.astype(jnp.bfloat16)[None]
    for step in reversed(range(steps)):
        bit = (own >> step) & 1
        pairs = [(device, device ^ (1 << step)) for device in range(count)]
        arrived = lax.ppermute(whole, "dp", pairs)
        low_half = jnp.where(bit == 0, whole, arrived)
        high_half = jnp.where(bit == 0, arrived, whole)
        whole = jnp.stack([low_half, high_half], axis=1).reshape((-1,) + whole.shape[1:])
    return whole.reshape(-1)[: flat.shape[0]]


def head_gather_relative(values):
    count = lax.axis_size("head")
    parts = [values]
    for shift in range(1, count):
        parts.append(
            lax.ppermute(values, "head", [(device, (device + shift) % count) for device in range(count)])
        )
    return jnp.concatenate(parts, axis=0)


def head_scatter_relative(values):
    count = lax.axis_size("head")
    width = values.shape[0] // count
    total = values[:width].astype(jnp.float32)
    for shift in range(1, count):
        sent = values[(count - shift) * width : (count - shift + 1) * width]
        total = total + lax.ppermute(
            sent, "head", [(device, (device + shift) % count) for device in range(count)]
        ).astype(jnp.float32)
    return total


def map_rows(step, items):
    outs = [step(tuple(item[row] for item in items)) for row in range(items[0].shape[0])]
    return tuple(jnp.stack(parts) for parts in zip(*outs))


def turn(block, cosine, sine):
    half_depth = block.shape[-1] // 2
    first_half, second_half = block[:, :half_depth], block[:, half_depth:]
    return jnp.concatenate(
        [first_half * cosine - second_half * sine, second_half * cosine + first_half * sine], axis=1
    )


def unturn(block, cosine, sine):
    half_depth = block.shape[-1] // 2
    first_half, second_half = block[:, :half_depth], block[:, half_depth:]
    return jnp.concatenate(
        [first_half * cosine + second_half * sine, second_half * cosine - first_half * sine], axis=1
    )


def dp_all_reduce_direct(flat):
    count = lax.axis_size("dp")
    own = lax.axis_index("dp")
    width = -(-flat.shape[0] // (count * 128)) * 128
    blocks = jnp.pad(flat, (0, count * width - flat.shape[0])).reshape(count, width)
    total = lax.dynamic_index_in_dim(blocks, own, 0, keepdims=False).astype(jnp.float32)
    for shift in range(1, count):
        sent = lax.dynamic_index_in_dim(blocks, (own + shift) % count, 0, keepdims=False)
        total = total + lax.ppermute(
            sent, "dp", [(device, (device + shift) % count) for device in range(count)]
        ).astype(jnp.float32)
    mine = total.astype(jnp.bfloat16)
    parts = [mine]
    for shift in range(1, count):
        parts.append(
            lax.ppermute(mine, "dp", [(device, (device + shift) % count) for device in range(count)])
        )
    backward = jnp.stack(parts[::-1], axis=0)
    doubled = jnp.concatenate([backward, backward], axis=0)
    ordered = lax.dynamic_slice_in_dim(doubled, (count - 1 - own) % count, count, axis=0)
    return ordered.reshape(-1)[: flat.shape[0]]


def local(
    tokens,
    doc_ids,
    gain_attn,
    a_weight,
    b_weight,
    out_weight,
    gain_ffn,
    gate_weight,
    up_weight,
    down_weight,
    cotangent,
):
    rows_dev, length = doc_ids.shape
    total_rows = rows_dev * length
    own_rows = tokens.shape[0]
    local_heads = out_weight.shape[0] // DH
    rank_all = RQ + 2 * RK
    x_own = tokens.astype(jnp.float32)
    inv_one = lax.rsqrt(jnp.mean(x_own * x_own, axis=-1, keepdims=True) + EPSILON)
    normed_one = (x_own * inv_one * gain_attn).astype(jnp.bfloat16)
    normed_all = head_all_gather(normed_one, 0)
    normed_all, cotangent_late = lax.optimization_barrier((normed_all, cotangent))
    grad_out_all = head_gather_relative(cotangent_late)
    factor_a = jnp.dot(normed_all, a_weight, preferred_element_type=jnp.float32)
    factor_b = jnp.dot(normed_all, b_weight, preferred_element_type=jnp.float32)
    cosine, sine = rope_tables(total_rows, length)
    basis_query = [
        turn(factor_b[:, rank * DH : (rank + 1) * DH], cosine, sine) for rank in range(RQ)
    ]
    basis_key = [
        turn(factor_b[:, (RQ + rank) * DH : (RQ + rank + 1) * DH], cosine, sine)
        for rank in range(RK)
    ]
    basis_value = [
        factor_b[:, (RQ + RK + rank) * DH : (RQ + RK + rank + 1) * DH] for rank in range(RK)
    ]
    coef = [
        [factor_a[:, head * rank_all + column] [:, None] for column in range(rank_all)]
        for head in range(local_heads)
    ]

    def combine(bases, offset):
        return jnp.stack(
            [
                sum(coef[head][offset + rank] * bases[rank] for rank in range(len(bases)))
                / len(bases)
                for head in range(local_heads)
            ],
            axis=1,
        ).astype(jnp.bfloat16)

    queries = combine(basis_query, 0)
    key_rows = combine(basis_key, RQ)
    value_rows = combine(basis_value, RQ + RK)
    row_shape = (rows_dev, length, local_heads, DH)
    query_rows = queries.reshape(row_shape)
    keys_rows = key_rows.reshape(row_shape)
    values_rows = value_rows.reshape(row_shape)
    mixed_rows, log_total = map_rows(attend_row, (query_rows, keys_rows, values_rows, doc_ids))
    mixed = mixed_rows.reshape(total_rows, local_heads * DH)
    mixed, grad_out_all = lax.optimization_barrier((mixed, grad_out_all))
    piece = lax.slice_in_dim(mixed, 0, lax.axis_size("head") * own_rows, axis=0)
    resid_own = x_own + head_reduce_scatter(
        jnp.dot(piece, out_weight, preferred_element_type=jnp.float32).astype(jnp.bfloat16), 0
    )
    inv_two = lax.rsqrt(jnp.mean(resid_own * resid_own, axis=-1, keepdims=True) + EPSILON)
    normed_two = (resid_own * inv_two * gain_ffn).astype(jnp.bfloat16)
    normed_two_all = head_gather_relative(normed_two)
    gate_act = jnp.dot(normed_two_all, gate_weight, preferred_element_type=jnp.float32)
    up_act = jnp.dot(normed_two_all, up_weight, preferred_element_type=jnp.float32)
    sigmoid_gate = jax.nn.sigmoid(gate_act)
    silu_gate = sigmoid_gate * gate_act
    hidden = (silu_gate * up_act).astype(jnp.bfloat16)
    piece = lax.slice_in_dim(hidden, 0, lax.axis_size("head") * own_rows, axis=0)
    output = (
        resid_own
        + head_scatter_relative(
            jnp.dot(piece, down_weight, preferred_element_type=jnp.float32).astype(jnp.bfloat16)
        )
    ).astype(jnp.bfloat16)
    grad_down = dot_first(hidden, grad_out_all)
    grad_hidden = dot_last(grad_out_all, down_weight)
    grad_gate_act = (
        grad_hidden * up_act * (sigmoid_gate * (1.0 + gate_act * (1.0 - sigmoid_gate)))
    ).astype(jnp.bfloat16)
    grad_up_act = (grad_hidden * silu_gate).astype(jnp.bfloat16)
    grad_gate = dot_first(normed_two_all, grad_gate_act)
    grad_up = dot_first(normed_two_all, grad_up_act)
    gate_piece = lax.slice_in_dim(grad_gate_act, 0, lax.axis_size("head") * own_rows, axis=0)
    up_piece = lax.slice_in_dim(grad_up_act, 0, lax.axis_size("head") * own_rows, axis=0)
    grad_normed_two = head_scatter_relative(
        (dot_last(gate_piece, gate_weight) + dot_last(up_piece, up_weight)).astype(jnp.bfloat16)
    )
    ffn_grads = (grad_gate.astype(jnp.bfloat16), grad_up.astype(jnp.bfloat16), grad_down.astype(jnp.bfloat16))
    ffn_grads, grad_normed_two = lax.optimization_barrier((ffn_grads, grad_normed_two))
    grad_gate, grad_up, grad_down = lax.psum(ffn_grads, "dp")
    resid_part, grad_gain_ffn_own = norm_backward(resid_own, inv_two, gain_ffn, grad_normed_two)
    grad_resid = cotangent.astype(jnp.float32) + resid_part
    output, grad_resid = lax.optimization_barrier((output, grad_resid))
    grad_branch = head_all_gather(grad_resid.astype(jnp.bfloat16), 0)
    grad_mixed = dot_last(grad_branch, out_weight).astype(jnp.bfloat16)
    grad_out = dot_first(mixed, grad_branch)
    grad_query_rows, grad_key_rows, grad_value_rows = map_rows(
        attend_back,
        (query_rows, keys_rows, values_rows, doc_ids, log_total, grad_mixed.reshape(row_shape)),
    )
    head_shape = (total_rows, local_heads, DH)
    grad_query = rounded(grad_query_rows.reshape(head_shape))
    grad_key = rounded(grad_key_rows.reshape(head_shape))
    grad_value = rounded(grad_value_rows.reshape(head_shape))
    grads_by_part = ((grad_query, basis_query, 0), (grad_key, basis_key, RQ), (grad_value, basis_value, RQ + RK))
    coef_columns = [None] * (local_heads * rank_all)
    basis_grads = []
    for grad_part, bases, offset in grads_by_part:
        for rank, basis in enumerate(bases):
            for head in range(local_heads):
                coef_columns[head * rank_all + offset + rank] = jnp.sum(
                    grad_part[:, head, :] * basis, axis=1
                ) / len(bases)
            basis_grad = sum(
                coef[head][offset + rank] * grad_part[:, head, :] for head in range(local_heads)
            ) / len(bases)
            basis_grads.append(basis_grad if offset == RQ + RK else unturn(basis_grad, cosine, sine))
    grad_factor_a = jnp.stack(coef_columns, axis=1).astype(jnp.bfloat16)
    grad_factor_b = jnp.concatenate(basis_grads, axis=1)
    head_count = lax.axis_size("head")
    basis_cols = grad_factor_b.shape[1] // head_count
    factor_cols = head_reduce_scatter(grad_factor_b.astype(jnp.bfloat16), 1).astype(jnp.bfloat16)
    weight_cols = lax.dynamic_slice_in_dim(
        b_weight, lax.axis_index("head") * basis_cols, basis_cols, axis=1
    )
    piece = grad_factor_a
    grad_normed_one = head_reduce_scatter(
        (dot_last(piece, a_weight) + dot_last(factor_cols, weight_cols)).astype(jnp.bfloat16), 0
    )
    input_part, grad_gain_attn_own = norm_backward(x_own, inv_one, gain_attn, grad_normed_one)
    input_grad = grad_resid + input_part
    grad_a = dot_first(normed_all, grad_factor_a)
    grad_b_cols = dot_first(normed_all, factor_cols)

    features = grad_gain_attn_own.shape[0]
    gain_rows = -(-2 * features // basis_cols)
    gains = jnp.pad(
        jnp.concatenate([grad_gain_attn_own, grad_gain_ffn_own]),
        (0, gain_rows * basis_cols - 2 * features),
    ).reshape(gain_rows, basis_cols)
    tail = (
        grad_a.astype(jnp.bfloat16),
        grad_out.astype(jnp.bfloat16),
        jnp.concatenate([grad_b_cols, gains], axis=0).astype(jnp.bfloat16),
    )
    tail, (grad_gate, grad_up, grad_down) = lax.optimization_barrier(
        (tail, (grad_gate, grad_up, grad_down))
    )
    sizes = [part.size for part in tail]
    summed = dp_all_reduce_direct(jnp.concatenate([part.reshape(-1) for part in tail]))
    grad_a, grad_out, packed = (
        summed[sum(sizes[:index]) : sum(sizes[: index + 1])].reshape(part.shape)
        for index, part in enumerate(tail)
    )
    grad_out, grad_gate, grad_up, grad_down = (
        grad_out.astype(jnp.float32),
        grad_gate.astype(jnp.float32),
        grad_up.astype(jnp.float32),
        grad_down.astype(jnp.float32),
    )
    grad_a = grad_a.astype(jnp.float32)
    packed = lax.all_gather(packed, "head", axis=1, tiled=True).astype(jnp.float32)
    grad_b = packed[: grad_b_cols.shape[0]]
    gains = jnp.sum(
        packed[grad_b_cols.shape[0] :].reshape(gain_rows, head_count, basis_cols), axis=1
    ).reshape(-1)
    grad_gain_attn, grad_gain_ffn = gains[:features], gains[features : 2 * features]
    return (
        output,
        input_grad,
        grad_gain_attn,
        grad_a,
        grad_b,
        grad_out,
        grad_gain_ffn,
        grad_gate,
        grad_up,
        grad_down,
    )


def solution(mesh):
    return jax.shard_map(
        local,
        mesh=mesh,
        in_specs=(
            P(("dp", "head"), None),
            P("dp", None),
            P(),
            P(None, "head"),
            P(),
            P("head", None),
            P(),
            P(None, "head"),
            P(None, "head"),
            P("head", None),
            P(("dp", "head"), None),
        ),
        out_specs=(
            P(("dp", "head"), None),
            P(("dp", "head"), None),
            P(),
            P(None, "head"),
            P(),
            P("head", None),
            P(),
            P(None, "head"),
            P(None, "head"),
            P("head", None),
        ),
        check_vma=False,
    )
```

```python
import math

import jax
import jax.numpy as jnp
from jax import lax
from jax.sharding import PartitionSpec as P

DH = 64
RQ = 6
RK = 2


EPSILON = 1e-06
MASKED = -1e30
PRECISE = lax.Precision.HIGHEST


def rope_tables(total_rows, length):
    half_depth = DH // 2
    position = (jnp.arange(total_rows, dtype=jnp.int32) % length).astype(jnp.float32)
    frequency = jnp.exp(jnp.arange(half_depth, dtype=jnp.float32) * (-2.0 * math.log(10000.0) / DH))
    angle = position[:, None] * frequency[None, :]
    return (jnp.cos(angle), jnp.sin(angle))


def rotate(basis, cosine, sine):
    half_depth = basis.shape[-1] // 2
    first_half = basis[..., :half_depth]
    second_half = basis[..., half_depth:]
    cosine_row = cosine[:, None, :]
    sine_row = sine[:, None, :]
    return jnp.concatenate(
        [
            first_half * cosine_row - second_half * sine_row,
            second_half * cosine_row + first_half * sine_row,
        ],
        axis=-1,
    )


def unrotate(grad_basis, cosine, sine):
    half_depth = grad_basis.shape[-1] // 2
    first_half = grad_basis[..., :half_depth]
    second_half = grad_basis[..., half_depth:]
    cosine_row = cosine[:, None, :]
    sine_row = sine[:, None, :]
    return jnp.concatenate(
        [
            first_half * cosine_row + second_half * sine_row,
            second_half * cosine_row - first_half * sine_row,
        ],
        axis=-1,
    )


def dot_last(left, right):
    return lax.dot_general(
        left, right, (((1,), (1,)), ((), ())), preferred_element_type=jnp.float32
    )


def dot_first(left, right):
    return lax.dot_general(
        left, right, (((0,), (0,)), ((), ())), preferred_element_type=jnp.float32
    )


def norm_backward(inputs, inverse, gain, grad_normed):
    scaled = gain * grad_normed
    inner = jnp.mean(scaled * inputs, axis=-1, keepdims=True)
    grad_inputs = inverse * scaled - inputs * (inverse * inverse * inverse) * inner
    grad_gain = jnp.sum(grad_normed * inputs * inverse, axis=0)
    return (grad_inputs, grad_gain)


def block_scores(queries, key_rows, doc_row, first_row, last_row):
    position = jnp.arange(last_row, dtype=jnp.int32)
    allowed = (doc_row[first_row:last_row, None] == doc_row[None, :last_row]) & (
        position[None, :] <= position[first_row:last_row, None]
    )
    score_scale = 1.0 / math.sqrt(queries.shape[2])
    scores = (
        jnp.einsum(
            "qhd,khd->hqk",
            queries[first_row:last_row],
            key_rows[:last_row],
            preferred_element_type=jnp.float32,
        )
        * score_scale
    )
    return jnp.where(allowed[None], scores, MASKED)


def attend_row(row_item):
    queries, key_rows, value_rows, doc_row = row_item
    length = queries.shape[0]
    block_rows = min(512, length)
    mixed_parts = []
    total_parts = []
    for first_row in range(0, length, block_rows):
        last_row = first_row + block_rows
        scores = block_scores(queries, key_rows, doc_row, first_row, last_row)
        row_peak = jnp.max(scores, axis=-1, keepdims=True)
        exponent = jnp.exp(scores - row_peak)
        row_total = jnp.sum(exponent, axis=-1, keepdims=True)
        weights = (exponent / row_total).astype(jnp.bfloat16)
        mixed_parts.append(
            jnp.einsum(
                "hqk,khd->qhd", weights, value_rows[:last_row], preferred_element_type=jnp.float32
            ).astype(jnp.bfloat16)
        )
        total_parts.append(row_peak[..., 0] + jnp.log(row_total[..., 0]))
    return (jnp.concatenate(mixed_parts, axis=0), jnp.concatenate(total_parts, axis=1))


def attend_back(row_item):
    queries, key_rows, value_rows, doc_row, log_total, grad_mixed = row_item
    length = queries.shape[0]
    block_rows = min(512, length)
    score_scale = 1.0 / math.sqrt(queries.shape[2])
    grad_query_parts = []
    grad_keys = jnp.zeros(key_rows.shape, jnp.float32)
    grad_values = jnp.zeros(value_rows.shape, jnp.float32)
    for first_row in range(0, length, block_rows):
        last_row = first_row + block_rows
        scores = block_scores(queries, key_rows, doc_row, first_row, last_row)
        weights = jnp.exp(scores - log_total[:, first_row:last_row, None])
        grad_weights = jnp.einsum(
            "qhd,khd->hqk",
            grad_mixed[first_row:last_row],
            value_rows[:last_row],
            preferred_element_type=jnp.float32,
        )
        inner = jnp.sum(weights * grad_weights, axis=-1, keepdims=True)
        grad_scores = (weights * (grad_weights - inner)).astype(jnp.bfloat16)
        grad_query_parts.append(
            jnp.einsum(
                "hqk,khd->qhd", grad_scores, key_rows[:last_row], preferred_element_type=jnp.float32
            )
            * score_scale
        )
        padding = ((0, length - last_row), (0, 0), (0, 0))
        key_part = (
            jnp.einsum(
                "hqk,qhd->khd",
                grad_scores,
                queries[first_row:last_row],
                preferred_element_type=jnp.float32,
            )
            * score_scale
        )
        value_part = jnp.einsum(
            "hqk,qhd->khd",
            weights.astype(jnp.bfloat16),
            grad_mixed[first_row:last_row],
            preferred_element_type=jnp.float32,
        )
        grad_keys = grad_keys + jnp.pad(key_part, padding)
        grad_values = grad_values + jnp.pad(value_part, padding)
    return (jnp.concatenate(grad_query_parts, axis=0), grad_keys, grad_values)


def rounded(values_in):
    return lax.optimization_barrier(values_in.astype(jnp.bfloat16)).astype(jnp.float32)


def head_reduce_scatter(values, axis):
    count = lax.axis_size("head")
    own = lax.axis_index("head")
    width = values.shape[axis] // count
    total = lax.dynamic_slice_in_dim(values, own * width, width, axis=axis).astype(jnp.float32)
    for shift in range(1, count):
        sent = lax.dynamic_slice_in_dim(values, ((own + shift) % count) * width, width, axis=axis)
        total = total + lax.ppermute(
            sent, "head", [(device, (device + shift) % count) for device in range(count)]
        ).astype(jnp.float32)
    return total


def head_all_gather(values, axis):
    count = lax.axis_size("head")
    own = lax.axis_index("head")
    width = values.shape[axis]
    shape = list(values.shape)
    shape[axis] = width * count
    gathered = lax.dynamic_update_slice_in_dim(
        jnp.zeros(shape, values.dtype), values, own * width, axis=axis
    )
    for shift in range(1, count):
        arrived = lax.ppermute(
            values, "head", [(device, (device + shift) % count) for device in range(count)]
        )
        gathered = lax.dynamic_update_slice_in_dim(
            gathered, arrived, ((own - shift) % count) * width, axis=axis
        )
    return gathered


def dp_all_reduce(flat):
    count = lax.axis_size("dp")
    own = lax.axis_index("dp")
    steps = count.bit_length() - 1
    assert count == 1 << steps
    width = -(-flat.shape[0] // (count * 128)) * 128
    blocks = jnp.pad(flat, (0, count * width - flat.shape[0])).reshape((2,) * steps + (width,))
    kept = blocks.astype(jnp.float32)
    for step in range(steps):
        axis = steps - 1 - step
        bit = (own >> step) & 1
        sent = lax.dynamic_index_in_dim(kept, 1 - bit, axis, keepdims=False)
        kept = lax.dynamic_index_in_dim(kept, bit, axis, keepdims=False)
        pairs = [(device, device ^ (1 << step)) for device in range(count)]
        kept = kept + lax.ppermute(sent.astype(jnp.bfloat16), "dp", pairs).astype(jnp.float32)
    whole = kept.astype(jnp.bfloat16)[None]
    for step in reversed(range(steps)):
        bit = (own >> step) & 1
        pairs = [(device, device ^ (1 << step)) for device in range(count)]
        arrived = lax.ppermute(whole, "dp", pairs)
        low_half = jnp.where(bit == 0, whole, arrived)
        high_half = jnp.where(bit == 0, arrived, whole)
        whole = jnp.stack([low_half, high_half], axis=1).reshape((-1,) + whole.shape[1:])
    return whole.reshape(-1)[: flat.shape[0]]


def head_gather_relative(values):
    count = lax.axis_size("head")
    parts = [values]
    for shift in range(1, count):
        parts.append(
            lax.ppermute(values, "head", [(device, (device + shift) % count) for device in range(count)])
        )
    return jnp.concatenate(parts, axis=0)


def head_scatter_relative(values):
    count = lax.axis_size("head")
    width = values.shape[0] // count
    total = values[:width].astype(jnp.float32)
    for shift in range(1, count):
        sent = values[(count - shift) * width : (count - shift + 1) * width]
        total = total + lax.ppermute(
            sent, "head", [(device, (device + shift) % count) for device in range(count)]
        ).astype(jnp.float32)
    return total


def map_rows(step, items):
    outs = [step(tuple(item[row] for item in items)) for row in range(items[0].shape[0])]
    return tuple(jnp.stack(parts) for parts in zip(*outs))


def turn(block, cosine, sine):
    half_depth = block.shape[-1] // 2
    first_half, second_half = block[:, :half_depth], block[:, half_depth:]
    return jnp.concatenate(
        [first_half * cosine - second_half * sine, second_half * cosine + first_half * sine], axis=1
    )


def unturn(block, cosine, sine):
    half_depth = block.shape[-1] // 2
    first_half, second_half = block[:, :half_depth], block[:, half_depth:]
    return jnp.concatenate(
        [first_half * cosine + second_half * sine, second_half * cosine - first_half * sine], axis=1
    )


def local(
    tokens,
    doc_ids,
    gain_attn,
    a_weight,
    b_weight,
    out_weight,
    gain_ffn,
    gate_weight,
    up_weight,
    down_weight,
    cotangent,
):
    rows_dev, length = doc_ids.shape
    total_rows = rows_dev * length
    own_rows = tokens.shape[0]
    local_heads = out_weight.shape[0] // DH
    rank_all = RQ + 2 * RK
    x_own = tokens.astype(jnp.float32)
    inv_one = lax.rsqrt(jnp.mean(x_own * x_own, axis=-1, keepdims=True) + EPSILON)
    normed_one = (x_own * inv_one * gain_attn).astype(jnp.bfloat16)
    normed_all = head_all_gather(normed_one, 0)
    normed_all, cotangent_late = lax.optimization_barrier((normed_all, cotangent))
    grad_out_all = head_gather_relative(cotangent_late)
    factor_a = jnp.dot(normed_all, a_weight, preferred_element_type=jnp.float32)
    factor_b = jnp.dot(normed_all, b_weight, preferred_element_type=jnp.float32)
    cosine, sine = rope_tables(total_rows, length)
    basis_query = [
        turn(factor_b[:, rank * DH : (rank + 1) * DH], cosine, sine) for rank in range(RQ)
    ]
    basis_key = [
        turn(factor_b[:, (RQ + rank) * DH : (RQ + rank + 1) * DH], cosine, sine)
        for rank in range(RK)
    ]
    basis_value = [
        factor_b[:, (RQ + RK + rank) * DH : (RQ + RK + rank + 1) * DH] for rank in range(RK)
    ]
    coef = [
        [factor_a[:, head * rank_all + column] [:, None] for column in range(rank_all)]
        for head in range(local_heads)
    ]

    def combine(bases, offset):
        return jnp.stack(
            [
                sum(coef[head][offset + rank] * bases[rank] for rank in range(len(bases)))
                / len(bases)
                for head in range(local_heads)
            ],
            axis=1,
        ).astype(jnp.bfloat16)

    queries = combine(basis_query, 0)
    key_rows = combine(basis_key, RQ)
    value_rows = combine(basis_value, RQ + RK)
    row_shape = (rows_dev, length, local_heads, DH)
    query_rows = queries.reshape(row_shape)
    keys_rows = key_rows.reshape(row_shape)
    values_rows = value_rows.reshape(row_shape)
    mixed_rows, log_total = map_rows(attend_row, (query_rows, keys_rows, values_rows, doc_ids))
    mixed = mixed_rows.reshape(total_rows, local_heads * DH)
    mixed, grad_out_all = lax.optimization_barrier((mixed, grad_out_all))
    piece = lax.slice_in_dim(mixed, 0, lax.axis_size("head") * own_rows, axis=0)
    resid_own = x_own + head_reduce_scatter(
        jnp.dot(piece, out_weight, preferred_element_type=jnp.float32).astype(jnp.bfloat16), 0
    )
    inv_two = lax.rsqrt(jnp.mean(resid_own * resid_own, axis=-1, keepdims=True) + EPSILON)
    normed_two = (resid_own * inv_two * gain_ffn).astype(jnp.bfloat16)
    normed_two_all = head_gather_relative(normed_two)
    gate_act = jnp.dot(normed_two_all, gate_weight, preferred_element_type=jnp.float32)
    up_act = jnp.dot(normed_two_all, up_weight, preferred_element_type=jnp.float32)
    sigmoid_gate = jax.nn.sigmoid(gate_act)
    silu_gate = sigmoid_gate * gate_act
    hidden = (silu_gate * up_act).astype(jnp.bfloat16)
    piece = lax.slice_in_dim(hidden, 0, lax.axis_size("head") * own_rows, axis=0)
    output = (
        resid_own
        + head_scatter_relative(
            jnp.dot(piece, down_weight, preferred_element_type=jnp.float32).astype(jnp.bfloat16)
        )
    ).astype(jnp.bfloat16)
    grad_down = dot_first(hidden, grad_out_all)
    grad_hidden = dot_last(grad_out_all, down_weight)
    grad_gate_act = (
        grad_hidden * up_act * (sigmoid_gate * (1.0 + gate_act * (1.0 - sigmoid_gate)))
    ).astype(jnp.bfloat16)
    grad_up_act = (grad_hidden * silu_gate).astype(jnp.bfloat16)
    grad_gate = dot_first(normed_two_all, grad_gate_act)
    grad_up = dot_first(normed_two_all, grad_up_act)
    gate_piece = lax.slice_in_dim(grad_gate_act, 0, lax.axis_size("head") * own_rows, axis=0)
    up_piece = lax.slice_in_dim(grad_up_act, 0, lax.axis_size("head") * own_rows, axis=0)
    grad_normed_two = head_scatter_relative(
        (dot_last(gate_piece, gate_weight) + dot_last(up_piece, up_weight)).astype(jnp.bfloat16)
    )
    ffn_grads = (grad_gate.astype(jnp.bfloat16), grad_up.astype(jnp.bfloat16), grad_down.astype(jnp.bfloat16))
    ffn_grads, grad_normed_two = lax.optimization_barrier((ffn_grads, grad_normed_two))
    ffn_summed = dp_all_reduce(jnp.concatenate([part.reshape(-1) for part in ffn_grads]))
    ffn_sizes = [part.size for part in ffn_grads]
    grad_gate, grad_up, grad_down = (
        ffn_summed[sum(ffn_sizes[:index]) : sum(ffn_sizes[: index + 1])].reshape(part.shape)
        for index, part in enumerate(ffn_grads)
    )
    resid_part, grad_gain_ffn_own = norm_backward(resid_own, inv_two, gain_ffn, grad_normed_two)
    grad_resid = cotangent.astype(jnp.float32) + resid_part
    output, grad_resid = lax.optimization_barrier((output, grad_resid))
    grad_branch = head_all_gather(grad_resid.astype(jnp.bfloat16), 0)
    grad_mixed = dot_last(grad_branch, out_weight).astype(jnp.bfloat16)
    grad_out = dot_first(mixed, grad_branch)
    grad_query_rows, grad_key_rows, grad_value_rows = map_rows(
        attend_back,
        (query_rows, keys_rows, values_rows, doc_ids, log_total, grad_mixed.reshape(row_shape)),
    )
    head_shape = (total_rows, local_heads, DH)
    grad_query = rounded(grad_query_rows.reshape(head_shape))
    grad_key = rounded(grad_key_rows.reshape(head_shape))
    grad_value = rounded(grad_value_rows.reshape(head_shape))
    grads_by_part = ((grad_query, basis_query, 0), (grad_key, basis_key, RQ), (grad_value, basis_value, RQ + RK))
    coef_columns = [None] * (local_heads * rank_all)
    basis_grads = []
    for grad_part, bases, offset in grads_by_part:
        for rank, basis in enumerate(bases):
            for head in range(local_heads):
                coef_columns[head * rank_all + offset + rank] = jnp.sum(
                    grad_part[:, head, :] * basis, axis=1
                ) / len(bases)
            basis_grad = sum(
                coef[head][offset + rank] * grad_part[:, head, :] for head in range(local_heads)
            ) / len(bases)
            basis_grads.append(basis_grad if offset == RQ + RK else unturn(basis_grad, cosine, sine))
    grad_factor_a = jnp.stack(coef_columns, axis=1).astype(jnp.bfloat16)
    grad_factor_b = jnp.concatenate(basis_grads, axis=1)
    head_count = lax.axis_size("head")
    basis_cols = grad_factor_b.shape[1] // head_count
    factor_cols = head_reduce_scatter(grad_factor_b.astype(jnp.bfloat16), 1).astype(jnp.bfloat16)
    weight_cols = lax.dynamic_slice_in_dim(
        b_weight, lax.axis_index("head") * basis_cols, basis_cols, axis=1
    )
    piece = grad_factor_a
    grad_normed_one = head_reduce_scatter(
        (dot_last(piece, a_weight) + dot_last(factor_cols, weight_cols)).astype(jnp.bfloat16), 0
    )
    input_part, grad_gain_attn_own = norm_backward(x_own, inv_one, gain_attn, grad_normed_one)
    input_grad = grad_resid + input_part
    grad_a = dot_first(normed_all, grad_factor_a)
    grad_b_cols = dot_first(normed_all, factor_cols)

    features = grad_gain_attn_own.shape[0]
    gain_rows = -(-2 * features // basis_cols)
    gains = jnp.pad(
        jnp.concatenate([grad_gain_attn_own, grad_gain_ffn_own]),
        (0, gain_rows * basis_cols - 2 * features),
    ).reshape(gain_rows, basis_cols)
    tail = (
        grad_a.astype(jnp.bfloat16),
        grad_out.astype(jnp.bfloat16),
        jnp.concatenate([grad_b_cols, gains], axis=0).astype(jnp.bfloat16),
    )
    tail, (grad_gate, grad_up, grad_down) = lax.optimization_barrier(
        (tail, (grad_gate, grad_up, grad_down))
    )
    sizes = [part.size for part in tail]
    summed = dp_all_reduce(jnp.concatenate([part.reshape(-1) for part in tail]))
    grad_a, grad_out, packed = (
        summed[sum(sizes[:index]) : sum(sizes[: index + 1])].reshape(part.shape)
        for index, part in enumerate(tail)
    )
    grad_out, grad_gate, grad_up, grad_down = (
        grad_out.astype(jnp.float32),
        grad_gate.astype(jnp.float32),
        grad_up.astype(jnp.float32),
        grad_down.astype(jnp.float32),
    )
    grad_a = grad_a.astype(jnp.float32)
    packed = lax.all_gather(packed, "head", axis=1, tiled=True).astype(jnp.float32)
    grad_b = packed[: grad_b_cols.shape[0]]
    gains = jnp.sum(
        packed[grad_b_cols.shape[0] :].reshape(gain_rows, head_count, basis_cols), axis=1
    ).reshape(-1)
    grad_gain_attn, grad_gain_ffn = gains[:features], gains[features : 2 * features]
    return (
        output,
        input_grad,
        grad_gain_attn,
        grad_a,
        grad_b,
        grad_out,
        grad_gain_ffn,
        grad_gate,
        grad_up,
        grad_down,
    )


def solution(mesh):
    return jax.shard_map(
        local,
        mesh=mesh,
        in_specs=(
            P(("dp", "head"), None),
            P("dp", None),
            P(),
            P(None, "head"),
            P(),
            P("head", None),
            P(),
            P(None, "head"),
            P(None, "head"),
            P("head", None),
            P(("dp", "head"), None),
        ),
        out_specs=(
            P(("dp", "head"), None),
            P(("dp", "head"), None),
            P(),
            P(None, "head"),
            P(),
            P("head", None),
            P(),
            P(None, "head"),
            P(None, "head"),
            P("head", None),
        ),
        check_vma=False,
    )
```

```python
import math

import jax
import jax.numpy as jnp
from jax import lax
from jax.sharding import PartitionSpec as P

DH = 64
RQ = 6
RK = 2


EPSILON = 1e-06
MASKED = -1e30
PRECISE = lax.Precision.HIGHEST


def rope_tables(total_rows, length):
    half_depth = DH // 2
    position = (jnp.arange(total_rows, dtype=jnp.int32) % length).astype(jnp.float32)
    frequency = jnp.exp(jnp.arange(half_depth, dtype=jnp.float32) * (-2.0 * math.log(10000.0) / DH))
    angle = position[:, None] * frequency[None, :]
    return (jnp.cos(angle), jnp.sin(angle))


def rotate(basis, cosine, sine):
    half_depth = basis.shape[-1] // 2
    first_half = basis[..., :half_depth]
    second_half = basis[..., half_depth:]
    cosine_row = cosine[:, None, :]
    sine_row = sine[:, None, :]
    return jnp.concatenate(
        [
            first_half * cosine_row - second_half * sine_row,
            second_half * cosine_row + first_half * sine_row,
        ],
        axis=-1,
    )


def unrotate(grad_basis, cosine, sine):
    half_depth = grad_basis.shape[-1] // 2
    first_half = grad_basis[..., :half_depth]
    second_half = grad_basis[..., half_depth:]
    cosine_row = cosine[:, None, :]
    sine_row = sine[:, None, :]
    return jnp.concatenate(
        [
            first_half * cosine_row + second_half * sine_row,
            second_half * cosine_row - first_half * sine_row,
        ],
        axis=-1,
    )


def dot_last(left, right):
    return lax.dot_general(
        left, right, (((1,), (1,)), ((), ())), preferred_element_type=jnp.float32
    )


def dot_first(left, right):
    return lax.dot_general(
        left, right, (((0,), (0,)), ((), ())), preferred_element_type=jnp.float32
    )


def norm_backward(inputs, inverse, gain, grad_normed):
    scaled = gain * grad_normed
    inner = jnp.mean(scaled * inputs, axis=-1, keepdims=True)
    grad_inputs = inverse * scaled - inputs * (inverse * inverse * inverse) * inner
    grad_gain = jnp.sum(grad_normed * inputs * inverse, axis=0)
    return (grad_inputs, grad_gain)


def block_scores(queries, key_rows, doc_row, first_row, last_row):
    position = jnp.arange(last_row, dtype=jnp.int32)
    allowed = (doc_row[first_row:last_row, None] == doc_row[None, :last_row]) & (
        position[None, :] <= position[first_row:last_row, None]
    )
    score_scale = 1.0 / math.sqrt(queries.shape[2])
    scores = (
        jnp.einsum(
            "qhd,khd->hqk",
            queries[first_row:last_row],
            key_rows[:last_row],
            preferred_element_type=jnp.float32,
        )
        * score_scale
    )
    return jnp.where(allowed[None], scores, MASKED)


def attend_row(row_item):
    queries, key_rows, value_rows, doc_row = row_item
    length = queries.shape[0]
    block_rows = min(512, length)
    mixed_parts = []
    total_parts = []
    for first_row in range(0, length, block_rows):
        last_row = first_row + block_rows
        scores = block_scores(queries, key_rows, doc_row, first_row, last_row)
        row_peak = jnp.max(scores, axis=-1, keepdims=True)
        exponent = jnp.exp(scores - row_peak)
        row_total = jnp.sum(exponent, axis=-1, keepdims=True)
        weights = (exponent / row_total).astype(jnp.bfloat16)
        mixed_parts.append(
            jnp.einsum(
                "hqk,khd->qhd", weights, value_rows[:last_row], preferred_element_type=jnp.float32
            ).astype(jnp.bfloat16)
        )
        total_parts.append(row_peak[..., 0] + jnp.log(row_total[..., 0]))
    return (jnp.concatenate(mixed_parts, axis=0), jnp.concatenate(total_parts, axis=1))


def attend_back(row_item):
    queries, key_rows, value_rows, doc_row, log_total, grad_mixed = row_item
    length = queries.shape[0]
    block_rows = min(512, length)
    score_scale = 1.0 / math.sqrt(queries.shape[2])
    grad_query_parts = []
    grad_keys = jnp.zeros(key_rows.shape, jnp.float32)
    grad_values = jnp.zeros(value_rows.shape, jnp.float32)
    for first_row in range(0, length, block_rows):
        last_row = first_row + block_rows
        scores = block_scores(queries, key_rows, doc_row, first_row, last_row)
        weights = jnp.exp(scores - log_total[:, first_row:last_row, None])
        grad_weights = jnp.einsum(
            "qhd,khd->hqk",
            grad_mixed[first_row:last_row],
            value_rows[:last_row],
            preferred_element_type=jnp.float32,
        )
        inner = jnp.sum(weights * grad_weights, axis=-1, keepdims=True)
        grad_scores = (weights * (grad_weights - inner)).astype(jnp.bfloat16)
        grad_query_parts.append(
            jnp.einsum(
                "hqk,khd->qhd", grad_scores, key_rows[:last_row], preferred_element_type=jnp.float32
            )
            * score_scale
        )
        padding = ((0, length - last_row), (0, 0), (0, 0))
        key_part = (
            jnp.einsum(
                "hqk,qhd->khd",
                grad_scores,
                queries[first_row:last_row],
                preferred_element_type=jnp.float32,
            )
            * score_scale
        )
        value_part = jnp.einsum(
            "hqk,qhd->khd",
            weights.astype(jnp.bfloat16),
            grad_mixed[first_row:last_row],
            preferred_element_type=jnp.float32,
        )
        grad_keys = grad_keys + jnp.pad(key_part, padding)
        grad_values = grad_values + jnp.pad(value_part, padding)
    return (jnp.concatenate(grad_query_parts, axis=0), grad_keys, grad_values)


def rounded(values_in):
    return lax.optimization_barrier(values_in.astype(jnp.bfloat16)).astype(jnp.float32)


def head_reduce_scatter(values, axis):
    count = lax.axis_size("head")
    own = lax.axis_index("head")
    width = values.shape[axis] // count
    total = lax.dynamic_slice_in_dim(values, own * width, width, axis=axis).astype(jnp.float32)
    for shift in range(1, count):
        sent = lax.dynamic_slice_in_dim(values, ((own + shift) % count) * width, width, axis=axis)
        total = total + lax.ppermute(
            sent, "head", [(device, (device + shift) % count) for device in range(count)]
        ).astype(jnp.float32)
    return total


def head_all_gather(values, axis):
    count = lax.axis_size("head")
    own = lax.axis_index("head")
    width = values.shape[axis]
    shape = list(values.shape)
    shape[axis] = width * count
    gathered = lax.dynamic_update_slice_in_dim(
        jnp.zeros(shape, values.dtype), values, own * width, axis=axis
    )
    for shift in range(1, count):
        arrived = lax.ppermute(
            values, "head", [(device, (device + shift) % count) for device in range(count)]
        )
        gathered = lax.dynamic_update_slice_in_dim(
            gathered, arrived, ((own - shift) % count) * width, axis=axis
        )
    return gathered


def dp_all_reduce(flat):
    count = lax.axis_size("dp")
    own = lax.axis_index("dp")
    steps = count.bit_length() - 1
    assert count == 1 << steps
    width = -(-flat.shape[0] // (count * 128)) * 128
    blocks = jnp.pad(flat, (0, count * width - flat.shape[0])).reshape((2,) * steps + (width,))
    kept = blocks.astype(jnp.float32)
    for step in range(steps):
        axis = steps - 1 - step
        bit = (own >> step) & 1
        sent = lax.dynamic_index_in_dim(kept, 1 - bit, axis, keepdims=False)
        kept = lax.dynamic_index_in_dim(kept, bit, axis, keepdims=False)
        pairs = [(device, device ^ (1 << step)) for device in range(count)]
        kept = kept + lax.ppermute(sent.astype(jnp.bfloat16), "dp", pairs).astype(jnp.float32)
    whole = kept.astype(jnp.bfloat16)[None]
    for step in reversed(range(steps)):
        bit = (own >> step) & 1
        pairs = [(device, device ^ (1 << step)) for device in range(count)]
        arrived = lax.ppermute(whole, "dp", pairs)
        low_half = jnp.where(bit == 0, whole, arrived)
        high_half = jnp.where(bit == 0, arrived, whole)
        whole = jnp.stack([low_half, high_half], axis=1).reshape((-1,) + whole.shape[1:])
    return whole.reshape(-1)[: flat.shape[0]]


def head_gather_relative(values):
    count = lax.axis_size("head")
    parts = [values]
    for shift in range(1, count):
        parts.append(
            lax.ppermute(values, "head", [(device, (device + shift) % count) for device in range(count)])
        )
    return jnp.concatenate(parts, axis=0)


def head_scatter_relative(values):
    count = lax.axis_size("head")
    width = values.shape[0] // count
    total = values[:width].astype(jnp.float32)
    for shift in range(1, count):
        sent = values[(count - shift) * width : (count - shift + 1) * width]
        total = total + lax.ppermute(
            sent, "head", [(device, (device + shift) % count) for device in range(count)]
        ).astype(jnp.float32)
    return total


def map_rows(step, items):
    outs = [step(tuple(item[row] for item in items)) for row in range(items[0].shape[0])]
    return tuple(jnp.stack(parts) for parts in zip(*outs))


def turn(block, cosine, sine):
    half_depth = block.shape[-1] // 2
    first_half, second_half = block[:, :half_depth], block[:, half_depth:]
    return jnp.concatenate(
        [first_half * cosine - second_half * sine, second_half * cosine + first_half * sine], axis=1
    )


def unturn(block, cosine, sine):
    half_depth = block.shape[-1] // 2
    first_half, second_half = block[:, :half_depth], block[:, half_depth:]
    return jnp.concatenate(
        [first_half * cosine + second_half * sine, second_half * cosine - first_half * sine], axis=1
    )


def dp_all_reduce_pairs(flat):
    count = lax.axis_size("dp")
    own = lax.axis_index("dp")
    group = count // 2
    width = -(-flat.shape[0] // (count * 128)) * 128
    blocks = jnp.pad(flat, (0, count * width - flat.shape[0])).reshape(group, 2, width)
    bit = own & 1
    member = own >> 1
    partner = [(device, device ^ 1) for device in range(count)]
    sent = lax.dynamic_index_in_dim(blocks, 1 - bit, 1, keepdims=False)
    kept = lax.dynamic_index_in_dim(blocks, bit, 1, keepdims=False).astype(jnp.float32)
    kept = kept + lax.ppermute(sent, "dp", partner).astype(jnp.float32)
    shifts = [
        [(device, (device & 1) + 2 * (((device >> 1) + shift) % group)) for device in range(count)]
        for shift in range(group)
    ]
    total = lax.dynamic_index_in_dim(kept, member, 0, keepdims=False)
    for shift in range(1, group):
        sent = lax.dynamic_index_in_dim(kept, (member + shift) % group, 0, keepdims=False)
        total = total + lax.ppermute(sent.astype(jnp.bfloat16), "dp", shifts[shift]).astype(
            jnp.float32
        )
    mine = total.astype(jnp.bfloat16)
    parts = [mine] + [lax.ppermute(mine, "dp", shifts[shift]) for shift in range(1, group)]
    backward = jnp.stack(parts[::-1], axis=0)
    doubled = jnp.concatenate([backward, backward], axis=0)
    ordered = lax.dynamic_slice_in_dim(doubled, (group - 1 - member) % group, group, axis=0)
    arrived = lax.ppermute(ordered, "dp", partner)
    low_half = jnp.where(bit == 0, ordered, arrived)
    high_half = jnp.where(bit == 0, arrived, ordered)
    return jnp.stack([low_half, high_half], axis=1).reshape(-1)[: flat.shape[0]]


def local(
    tokens,
    doc_ids,
    gain_attn,
    a_weight,
    b_weight,
    out_weight,
    gain_ffn,
    gate_weight,
    up_weight,
    down_weight,
    cotangent,
):
    rows_dev, length = doc_ids.shape
    total_rows = rows_dev * length
    own_rows = tokens.shape[0]
    local_heads = out_weight.shape[0] // DH
    rank_all = RQ + 2 * RK
    x_own = tokens.astype(jnp.float32)
    inv_one = lax.rsqrt(jnp.mean(x_own * x_own, axis=-1, keepdims=True) + EPSILON)
    normed_one = (x_own * inv_one * gain_attn).astype(jnp.bfloat16)
    normed_all = head_all_gather(normed_one, 0)
    normed_all, cotangent_late = lax.optimization_barrier((normed_all, cotangent))
    grad_out_all = head_gather_relative(cotangent_late)
    factor_a = jnp.dot(normed_all, a_weight, preferred_element_type=jnp.float32)
    factor_b = jnp.dot(normed_all, b_weight, preferred_element_type=jnp.float32)
    cosine, sine = rope_tables(total_rows, length)
    basis_query = [
        turn(factor_b[:, rank * DH : (rank + 1) * DH], cosine, sine) for rank in range(RQ)
    ]
    basis_key = [
        turn(factor_b[:, (RQ + rank) * DH : (RQ + rank + 1) * DH], cosine, sine)
        for rank in range(RK)
    ]
    basis_value = [
        factor_b[:, (RQ + RK + rank) * DH : (RQ + RK + rank + 1) * DH] for rank in range(RK)
    ]
    coef = [
        [factor_a[:, head * rank_all + column] [:, None] for column in range(rank_all)]
        for head in range(local_heads)
    ]

    def combine(bases, offset):
        return jnp.stack(
            [
                sum(coef[head][offset + rank] * bases[rank] for rank in range(len(bases)))
                / len(bases)
                for head in range(local_heads)
            ],
            axis=1,
        ).astype(jnp.bfloat16)

    queries = combine(basis_query, 0)
    key_rows = combine(basis_key, RQ)
    value_rows = combine(basis_value, RQ + RK)
    row_shape = (rows_dev, length, local_heads, DH)
    query_rows = queries.reshape(row_shape)
    keys_rows = key_rows.reshape(row_shape)
    values_rows = value_rows.reshape(row_shape)
    mixed_rows, log_total = map_rows(attend_row, (query_rows, keys_rows, values_rows, doc_ids))
    mixed = mixed_rows.reshape(total_rows, local_heads * DH)
    mixed, grad_out_all = lax.optimization_barrier((mixed, grad_out_all))
    piece = lax.slice_in_dim(mixed, 0, lax.axis_size("head") * own_rows, axis=0)
    resid_own = x_own + head_reduce_scatter(
        jnp.dot(piece, out_weight, preferred_element_type=jnp.float32).astype(jnp.bfloat16), 0
    )
    inv_two = lax.rsqrt(jnp.mean(resid_own * resid_own, axis=-1, keepdims=True) + EPSILON)
    normed_two = (resid_own * inv_two * gain_ffn).astype(jnp.bfloat16)
    normed_two_all = head_gather_relative(normed_two)
    gate_act = jnp.dot(normed_two_all, gate_weight, preferred_element_type=jnp.float32)
    up_act = jnp.dot(normed_two_all, up_weight, preferred_element_type=jnp.float32)
    sigmoid_gate = jax.nn.sigmoid(gate_act)
    silu_gate = sigmoid_gate * gate_act
    hidden = (silu_gate * up_act).astype(jnp.bfloat16)
    piece = lax.slice_in_dim(hidden, 0, lax.axis_size("head") * own_rows, axis=0)
    output = (
        resid_own
        + head_scatter_relative(
            jnp.dot(piece, down_weight, preferred_element_type=jnp.float32).astype(jnp.bfloat16)
        )
    ).astype(jnp.bfloat16)
    grad_down = dot_first(hidden, grad_out_all)
    grad_hidden = dot_last(grad_out_all, down_weight)
    grad_gate_act = (
        grad_hidden * up_act * (sigmoid_gate * (1.0 + gate_act * (1.0 - sigmoid_gate)))
    ).astype(jnp.bfloat16)
    grad_up_act = (grad_hidden * silu_gate).astype(jnp.bfloat16)
    grad_gate = dot_first(normed_two_all, grad_gate_act)
    grad_up = dot_first(normed_two_all, grad_up_act)
    gate_piece = lax.slice_in_dim(grad_gate_act, 0, lax.axis_size("head") * own_rows, axis=0)
    up_piece = lax.slice_in_dim(grad_up_act, 0, lax.axis_size("head") * own_rows, axis=0)
    grad_normed_two = head_scatter_relative(
        (dot_last(gate_piece, gate_weight) + dot_last(up_piece, up_weight)).astype(jnp.bfloat16)
    )
    ffn_grads = (grad_gate.astype(jnp.bfloat16), grad_up.astype(jnp.bfloat16), grad_down.astype(jnp.bfloat16))
    ffn_grads, grad_normed_two = lax.optimization_barrier((ffn_grads, grad_normed_two))
    grad_gate, grad_up, grad_down = lax.psum(ffn_grads, "dp")
    resid_part, grad_gain_ffn_own = norm_backward(resid_own, inv_two, gain_ffn, grad_normed_two)
    grad_resid = cotangent.astype(jnp.float32) + resid_part
    output, grad_resid = lax.optimization_barrier((output, grad_resid))
    grad_branch = head_all_gather(grad_resid.astype(jnp.bfloat16), 0)
    grad_mixed = dot_last(grad_branch, out_weight).astype(jnp.bfloat16)
    grad_out = dot_first(mixed, grad_branch)
    grad_query_rows, grad_key_rows, grad_value_rows = map_rows(
        attend_back,
        (query_rows, keys_rows, values_rows, doc_ids, log_total, grad_mixed.reshape(row_shape)),
    )
    head_shape = (total_rows, local_heads, DH)
    grad_query = rounded(grad_query_rows.reshape(head_shape))
    grad_key = rounded(grad_key_rows.reshape(head_shape))
    grad_value = rounded(grad_value_rows.reshape(head_shape))
    grads_by_part = ((grad_query, basis_query, 0), (grad_key, basis_key, RQ), (grad_value, basis_value, RQ + RK))
    coef_columns = [None] * (local_heads * rank_all)
    basis_grads = []
    for grad_part, bases, offset in grads_by_part:
        for rank, basis in enumerate(bases):
            for head in range(local_heads):
                coef_columns[head * rank_all + offset + rank] = jnp.sum(
                    grad_part[:, head, :] * basis, axis=1
                ) / len(bases)
            basis_grad = sum(
                coef[head][offset + rank] * grad_part[:, head, :] for head in range(local_heads)
            ) / len(bases)
            basis_grads.append(basis_grad if offset == RQ + RK else unturn(basis_grad, cosine, sine))
    grad_factor_a = jnp.stack(coef_columns, axis=1).astype(jnp.bfloat16)
    grad_factor_b = jnp.concatenate(basis_grads, axis=1)
    head_count = lax.axis_size("head")
    basis_cols = grad_factor_b.shape[1] // head_count
    factor_cols = head_reduce_scatter(grad_factor_b.astype(jnp.bfloat16), 1).astype(jnp.bfloat16)
    weight_cols = lax.dynamic_slice_in_dim(
        b_weight, lax.axis_index("head") * basis_cols, basis_cols, axis=1
    )
    piece = grad_factor_a
    grad_normed_one = head_reduce_scatter(
        (dot_last(piece, a_weight) + dot_last(factor_cols, weight_cols)).astype(jnp.bfloat16), 0
    )
    input_part, grad_gain_attn_own = norm_backward(x_own, inv_one, gain_attn, grad_normed_one)
    input_grad = grad_resid + input_part
    grad_a = dot_first(normed_all, grad_factor_a)
    grad_b_cols = dot_first(normed_all, factor_cols)

    features = grad_gain_attn_own.shape[0]
    gain_rows = -(-2 * features // basis_cols)
    gains = jnp.pad(
        jnp.concatenate([grad_gain_attn_own, grad_gain_ffn_own]),
        (0, gain_rows * basis_cols - 2 * features),
    ).reshape(gain_rows, basis_cols)
    tail = (
        grad_a.astype(jnp.bfloat16),
        grad_out.astype(jnp.bfloat16),
        jnp.concatenate([grad_b_cols, gains], axis=0).astype(jnp.bfloat16),
    )
    tail, (grad_gate, grad_up, grad_down) = lax.optimization_barrier(
        (tail, (grad_gate, grad_up, grad_down))
    )
    sizes = [part.size for part in tail]
    summed = dp_all_reduce_pairs(jnp.concatenate([part.reshape(-1) for part in tail]))
    grad_a, grad_out, packed = (
        summed[sum(sizes[:index]) : sum(sizes[: index + 1])].reshape(part.shape)
        for index, part in enumerate(tail)
    )
    grad_out, grad_gate, grad_up, grad_down = (
        grad_out.astype(jnp.float32),
        grad_gate.astype(jnp.float32),
        grad_up.astype(jnp.float32),
        grad_down.astype(jnp.float32),
    )
    grad_a = grad_a.astype(jnp.float32)
    packed = lax.all_gather(packed, "head", axis=1, tiled=True).astype(jnp.float32)
    grad_b = packed[: grad_b_cols.shape[0]]
    gains = jnp.sum(
        packed[grad_b_cols.shape[0] :].reshape(gain_rows, head_count, basis_cols), axis=1
    ).reshape(-1)
    grad_gain_attn, grad_gain_ffn = gains[:features], gains[features : 2 * features]
    return (
        output,
        input_grad,
        grad_gain_attn,
        grad_a,
        grad_b,
        grad_out,
        grad_gain_ffn,
        grad_gate,
        grad_up,
        grad_down,
    )


def solution(mesh):
    return jax.shard_map(
        local,
        mesh=mesh,
        in_specs=(
            P(("dp", "head"), None),
            P("dp", None),
            P(),
            P(None, "head"),
            P(),
            P("head", None),
            P(),
            P(None, "head"),
            P(None, "head"),
            P("head", None),
            P(("dp", "head"), None),
        ),
        out_specs=(
            P(("dp", "head"), None),
            P(("dp", "head"), None),
            P(),
            P(None, "head"),
            P(),
            P("head", None),
            P(),
            P(None, "head"),
            P(None, "head"),
            P("head", None),
        ),
        check_vma=False,
    )
```

```python
import math

import jax
import jax.numpy as jnp
from jax import lax
from jax.sharding import PartitionSpec as P

DH = 64
RQ = 6
RK = 2


EPSILON = 1e-06
MASKED = -1e30
PRECISE = lax.Precision.HIGHEST


def rope_tables(total_rows, length):
    half_depth = DH // 2
    position = (jnp.arange(total_rows, dtype=jnp.int32) % length).astype(jnp.float32)
    frequency = jnp.exp(jnp.arange(half_depth, dtype=jnp.float32) * (-2.0 * math.log(10000.0) / DH))
    angle = position[:, None] * frequency[None, :]
    return (jnp.cos(angle), jnp.sin(angle))


def rotate(basis, cosine, sine):
    half_depth = basis.shape[-1] // 2
    first_half = basis[..., :half_depth]
    second_half = basis[..., half_depth:]
    cosine_row = cosine[:, None, :]
    sine_row = sine[:, None, :]
    return jnp.concatenate(
        [
            first_half * cosine_row - second_half * sine_row,
            second_half * cosine_row + first_half * sine_row,
        ],
        axis=-1,
    )


def unrotate(grad_basis, cosine, sine):
    half_depth = grad_basis.shape[-1] // 2
    first_half = grad_basis[..., :half_depth]
    second_half = grad_basis[..., half_depth:]
    cosine_row = cosine[:, None, :]
    sine_row = sine[:, None, :]
    return jnp.concatenate(
        [
            first_half * cosine_row + second_half * sine_row,
            second_half * cosine_row - first_half * sine_row,
        ],
        axis=-1,
    )


def dot_last(left, right):
    return lax.dot_general(
        left, right, (((1,), (1,)), ((), ())), preferred_element_type=jnp.float32
    )


def dot_first(left, right):
    return lax.dot_general(
        left, right, (((0,), (0,)), ((), ())), preferred_element_type=jnp.float32
    )


def norm_backward(inputs, inverse, gain, grad_normed):
    scaled = gain * grad_normed
    inner = jnp.mean(scaled * inputs, axis=-1, keepdims=True)
    grad_inputs = inverse * scaled - inputs * (inverse * inverse * inverse) * inner
    grad_gain = jnp.sum(grad_normed * inputs * inverse, axis=0)
    return (grad_inputs, grad_gain)


def block_scores(queries, key_rows, doc_row, first_row, last_row):
    position = jnp.arange(last_row, dtype=jnp.int32)
    allowed = (doc_row[first_row:last_row, None] == doc_row[None, :last_row]) & (
        position[None, :] <= position[first_row:last_row, None]
    )
    score_scale = 1.0 / math.sqrt(queries.shape[2])
    scores = (
        jnp.einsum(
            "qhd,khd->hqk",
            queries[first_row:last_row],
            key_rows[:last_row],
            preferred_element_type=jnp.float32,
        )
        * score_scale
    )
    return jnp.where(allowed[None], scores, MASKED)


def attend_row(row_item):
    queries, key_rows, value_rows, doc_row = row_item
    length = queries.shape[0]
    block_rows = min(512, length)
    mixed_parts = []
    total_parts = []
    for first_row in range(0, length, block_rows):
        last_row = first_row + block_rows
        scores = block_scores(queries, key_rows, doc_row, first_row, last_row)
        row_peak = jnp.max(scores, axis=-1, keepdims=True)
        exponent = jnp.exp(scores - row_peak)
        row_total = jnp.sum(exponent, axis=-1, keepdims=True)
        weights = (exponent / row_total).astype(jnp.bfloat16)
        mixed_parts.append(
            jnp.einsum(
                "hqk,khd->qhd", weights, value_rows[:last_row], preferred_element_type=jnp.float32
            ).astype(jnp.bfloat16)
        )
        total_parts.append(row_peak[..., 0] + jnp.log(row_total[..., 0]))
    return (jnp.concatenate(mixed_parts, axis=0), jnp.concatenate(total_parts, axis=1))


def attend_back(row_item):
    queries, key_rows, value_rows, doc_row, log_total, grad_mixed = row_item
    length = queries.shape[0]
    block_rows = min(512, length)
    score_scale = 1.0 / math.sqrt(queries.shape[2])
    grad_query_parts = []
    grad_keys = jnp.zeros(key_rows.shape, jnp.float32)
    grad_values = jnp.zeros(value_rows.shape, jnp.float32)
    for first_row in range(0, length, block_rows):
        last_row = first_row + block_rows
        scores = block_scores(queries, key_rows, doc_row, first_row, last_row)
        weights = jnp.exp(scores - log_total[:, first_row:last_row, None])
        grad_weights = jnp.einsum(
            "qhd,khd->hqk",
            grad_mixed[first_row:last_row],
            value_rows[:last_row],
            preferred_element_type=jnp.float32,
        )
        inner = jnp.sum(weights * grad_weights, axis=-1, keepdims=True)
        grad_scores = (weights * (grad_weights - inner)).astype(jnp.bfloat16)
        grad_query_parts.append(
            jnp.einsum(
                "hqk,khd->qhd", grad_scores, key_rows[:last_row], preferred_element_type=jnp.float32
            )
            * score_scale
        )
        padding = ((0, length - last_row), (0, 0), (0, 0))
        key_part = (
            jnp.einsum(
                "hqk,qhd->khd",
                grad_scores,
                queries[first_row:last_row],
                preferred_element_type=jnp.float32,
            )
            * score_scale
        )
        value_part = jnp.einsum(
            "hqk,qhd->khd",
            weights.astype(jnp.bfloat16),
            grad_mixed[first_row:last_row],
            preferred_element_type=jnp.float32,
        )
        grad_keys = grad_keys + jnp.pad(key_part, padding)
        grad_values = grad_values + jnp.pad(value_part, padding)
    return (jnp.concatenate(grad_query_parts, axis=0), grad_keys, grad_values)


def rounded(values_in):
    return lax.optimization_barrier(values_in.astype(jnp.bfloat16)).astype(jnp.float32)


def head_reduce_scatter(values, axis):
    count = lax.axis_size("head")
    own = lax.axis_index("head")
    width = values.shape[axis] // count
    total = lax.dynamic_slice_in_dim(values, own * width, width, axis=axis).astype(jnp.float32)
    for shift in range(1, count):
        sent = lax.dynamic_slice_in_dim(values, ((own + shift) % count) * width, width, axis=axis)
        total = total + lax.ppermute(
            sent, "head", [(device, (device + shift) % count) for device in range(count)]
        ).astype(jnp.float32)
    return total


def head_all_gather(values, axis):
    count = lax.axis_size("head")
    own = lax.axis_index("head")
    width = values.shape[axis]
    shape = list(values.shape)
    shape[axis] = width * count
    gathered = lax.dynamic_update_slice_in_dim(
        jnp.zeros(shape, values.dtype), values, own * width, axis=axis
    )
    for shift in range(1, count):
        arrived = lax.ppermute(
            values, "head", [(device, (device + shift) % count) for device in range(count)]
        )
        gathered = lax.dynamic_update_slice_in_dim(
            gathered, arrived, ((own - shift) % count) * width, axis=axis
        )
    return gathered


def dp_all_reduce(flat):
    count = lax.axis_size("dp")
    own = lax.axis_index("dp")
    steps = count.bit_length() - 1
    assert count == 1 << steps
    width = -(-flat.shape[0] // (count * 128)) * 128
    blocks = jnp.pad(flat, (0, count * width - flat.shape[0])).reshape((2,) * steps + (width,))
    kept = blocks.astype(jnp.float32)
    for step in range(steps):
        axis = steps - 1 - step
        bit = (own >> step) & 1
        sent = lax.dynamic_index_in_dim(kept, 1 - bit, axis, keepdims=False)
        kept = lax.dynamic_index_in_dim(kept, bit, axis, keepdims=False)
        pairs = [(device, device ^ (1 << step)) for device in range(count)]
        kept = kept + lax.ppermute(sent.astype(jnp.bfloat16), "dp", pairs).astype(jnp.float32)
    whole = kept.astype(jnp.bfloat16)[None]
    for step in reversed(range(steps)):
        bit = (own >> step) & 1
        pairs = [(device, device ^ (1 << step)) for device in range(count)]
        arrived = lax.ppermute(whole, "dp", pairs)
        low_half = jnp.where(bit == 0, whole, arrived)
        high_half = jnp.where(bit == 0, arrived, whole)
        whole = jnp.stack([low_half, high_half], axis=1).reshape((-1,) + whole.shape[1:])
    return whole.reshape(-1)[: flat.shape[0]]


def head_gather_relative(values):
    count = lax.axis_size("head")
    parts = [values]
    for shift in range(1, count):
        parts.append(
            lax.ppermute(values, "head", [(device, (device + shift) % count) for device in range(count)])
        )
    return jnp.concatenate(parts, axis=0)


def head_scatter_relative(values):
    count = lax.axis_size("head")
    width = values.shape[0] // count
    total = values[:width].astype(jnp.float32)
    for shift in range(1, count):
        sent = values[(count - shift) * width : (count - shift + 1) * width]
        total = total + lax.ppermute(
            sent, "head", [(device, (device + shift) % count) for device in range(count)]
        ).astype(jnp.float32)
    return total


def map_rows(step, items):
    outs = [step(tuple(item[row] for item in items)) for row in range(items[0].shape[0])]
    return tuple(jnp.stack(parts) for parts in zip(*outs))


def turn(block, cosine, sine):
    half_depth = block.shape[-1] // 2
    first_half, second_half = block[:, :half_depth], block[:, half_depth:]
    return jnp.concatenate(
        [first_half * cosine - second_half * sine, second_half * cosine + first_half * sine], axis=1
    )


def unturn(block, cosine, sine):
    half_depth = block.shape[-1] // 2
    first_half, second_half = block[:, :half_depth], block[:, half_depth:]
    return jnp.concatenate(
        [first_half * cosine + second_half * sine, second_half * cosine - first_half * sine], axis=1
    )


def dp_all_reduce_pairs(flat):
    count = lax.axis_size("dp")
    own = lax.axis_index("dp")
    group = count // 2
    width = -(-flat.shape[0] // (count * 128)) * 128
    blocks = jnp.pad(flat, (0, count * width - flat.shape[0])).reshape(group, 2, width)
    bit = own & 1
    member = own >> 1
    partner = [(device, device ^ 1) for device in range(count)]
    sent = lax.dynamic_index_in_dim(blocks, 1 - bit, 1, keepdims=False)
    kept = lax.dynamic_index_in_dim(blocks, bit, 1, keepdims=False).astype(jnp.float32)
    kept = kept + lax.ppermute(sent, "dp", partner).astype(jnp.float32)
    shifts = [
        [(device, (device & 1) + 2 * (((device >> 1) + shift) % group)) for device in range(count)]
        for shift in range(group)
    ]
    total = lax.dynamic_index_in_dim(kept, member, 0, keepdims=False)
    for shift in range(1, group):
        sent = lax.dynamic_index_in_dim(kept, (member + shift) % group, 0, keepdims=False)
        total = total + lax.ppermute(sent.astype(jnp.bfloat16), "dp", shifts[shift]).astype(
            jnp.float32
        )
    mine = total.astype(jnp.bfloat16)
    parts = [mine] + [lax.ppermute(mine, "dp", shifts[shift]) for shift in range(1, group)]
    rows = []
    for index in range(group):
        source = (member - index) % group
        row = parts[0]
        for shift in range(1, group):
            row = jnp.where(source == shift, parts[shift], row)
        rows.append(row)
    ordered = jnp.stack(rows, axis=0)
    arrived = lax.ppermute(ordered, "dp", partner)
    low_half = jnp.where(bit == 0, ordered, arrived)
    high_half = jnp.where(bit == 0, arrived, ordered)
    return jnp.stack([low_half, high_half], axis=1).reshape(-1)[: flat.shape[0]]


def local(
    tokens,
    doc_ids,
    gain_attn,
    a_weight,
    b_weight,
    out_weight,
    gain_ffn,
    gate_weight,
    up_weight,
    down_weight,
    cotangent,
):
    rows_dev, length = doc_ids.shape
    total_rows = rows_dev * length
    own_rows = tokens.shape[0]
    local_heads = out_weight.shape[0] // DH
    rank_all = RQ + 2 * RK
    x_own = tokens.astype(jnp.float32)
    inv_one = lax.rsqrt(jnp.mean(x_own * x_own, axis=-1, keepdims=True) + EPSILON)
    normed_one = (x_own * inv_one * gain_attn).astype(jnp.bfloat16)
    normed_all = head_all_gather(normed_one, 0)
    normed_all, cotangent_late = lax.optimization_barrier((normed_all, cotangent))
    grad_out_all = head_gather_relative(cotangent_late)
    factor_a = jnp.dot(normed_all, a_weight, preferred_element_type=jnp.float32)
    factor_b = jnp.dot(normed_all, b_weight, preferred_element_type=jnp.float32)
    cosine, sine = rope_tables(total_rows, length)
    basis_query = [
        turn(factor_b[:, rank * DH : (rank + 1) * DH], cosine, sine) for rank in range(RQ)
    ]
    basis_key = [
        turn(factor_b[:, (RQ + rank) * DH : (RQ + rank + 1) * DH], cosine, sine)
        for rank in range(RK)
    ]
    basis_value = [
        factor_b[:, (RQ + RK + rank) * DH : (RQ + RK + rank + 1) * DH] for rank in range(RK)
    ]
    coef = [
        [factor_a[:, head * rank_all + column] [:, None] for column in range(rank_all)]
        for head in range(local_heads)
    ]

    def combine(bases, offset):
        return jnp.stack(
            [
                sum(coef[head][offset + rank] * bases[rank] for rank in range(len(bases)))
                / len(bases)
                for head in range(local_heads)
            ],
            axis=1,
        ).astype(jnp.bfloat16)

    queries = combine(basis_query, 0)
    key_rows = combine(basis_key, RQ)
    value_rows = combine(basis_value, RQ + RK)
    row_shape = (rows_dev, length, local_heads, DH)
    query_rows = queries.reshape(row_shape)
    keys_rows = key_rows.reshape(row_shape)
    values_rows = value_rows.reshape(row_shape)
    mixed_rows, log_total = map_rows(attend_row, (query_rows, keys_rows, values_rows, doc_ids))
    mixed = mixed_rows.reshape(total_rows, local_heads * DH)
    mixed, grad_out_all = lax.optimization_barrier((mixed, grad_out_all))
    piece = lax.slice_in_dim(mixed, 0, lax.axis_size("head") * own_rows, axis=0)
    resid_own = x_own + head_reduce_scatter(
        jnp.dot(piece, out_weight, preferred_element_type=jnp.float32).astype(jnp.bfloat16), 0
    )
    inv_two = lax.rsqrt(jnp.mean(resid_own * resid_own, axis=-1, keepdims=True) + EPSILON)
    normed_two = (resid_own * inv_two * gain_ffn).astype(jnp.bfloat16)
    normed_two_all = head_gather_relative(normed_two)
    gate_act = jnp.dot(normed_two_all, gate_weight, preferred_element_type=jnp.float32)
    up_act = jnp.dot(normed_two_all, up_weight, preferred_element_type=jnp.float32)
    sigmoid_gate = jax.nn.sigmoid(gate_act)
    silu_gate = sigmoid_gate * gate_act
    hidden = (silu_gate * up_act).astype(jnp.bfloat16)
    piece = lax.slice_in_dim(hidden, 0, lax.axis_size("head") * own_rows, axis=0)
    output = (
        resid_own
        + head_scatter_relative(
            jnp.dot(piece, down_weight, preferred_element_type=jnp.float32).astype(jnp.bfloat16)
        )
    ).astype(jnp.bfloat16)
    grad_down = dot_first(hidden, grad_out_all)
    grad_hidden = dot_last(grad_out_all, down_weight)
    grad_gate_act = (
        grad_hidden * up_act * (sigmoid_gate * (1.0 + gate_act * (1.0 - sigmoid_gate)))
    ).astype(jnp.bfloat16)
    grad_up_act = (grad_hidden * silu_gate).astype(jnp.bfloat16)
    grad_gate = dot_first(normed_two_all, grad_gate_act)
    grad_up = dot_first(normed_two_all, grad_up_act)
    gate_piece = lax.slice_in_dim(grad_gate_act, 0, lax.axis_size("head") * own_rows, axis=0)
    up_piece = lax.slice_in_dim(grad_up_act, 0, lax.axis_size("head") * own_rows, axis=0)
    grad_normed_two = head_scatter_relative(
        (dot_last(gate_piece, gate_weight) + dot_last(up_piece, up_weight)).astype(jnp.bfloat16)
    )
    ffn_grads = (grad_gate.astype(jnp.bfloat16), grad_up.astype(jnp.bfloat16), grad_down.astype(jnp.bfloat16))
    ffn_grads, grad_normed_two = lax.optimization_barrier((ffn_grads, grad_normed_two))
    grad_gate, grad_up, grad_down = lax.psum(ffn_grads, "dp")
    resid_part, grad_gain_ffn_own = norm_backward(resid_own, inv_two, gain_ffn, grad_normed_two)
    grad_resid = cotangent.astype(jnp.float32) + resid_part
    output, grad_resid = lax.optimization_barrier((output, grad_resid))
    grad_branch = head_all_gather(grad_resid.astype(jnp.bfloat16), 0)
    grad_mixed = dot_last(grad_branch, out_weight).astype(jnp.bfloat16)
    grad_out = dot_first(mixed, grad_branch)
    grad_query_rows, grad_key_rows, grad_value_rows = map_rows(
        attend_back,
        (query_rows, keys_rows, values_rows, doc_ids, log_total, grad_mixed.reshape(row_shape)),
    )
    head_shape = (total_rows, local_heads, DH)
    grad_query = rounded(grad_query_rows.reshape(head_shape))
    grad_key = rounded(grad_key_rows.reshape(head_shape))
    grad_value = rounded(grad_value_rows.reshape(head_shape))
    grads_by_part = ((grad_query, basis_query, 0), (grad_key, basis_key, RQ), (grad_value, basis_value, RQ + RK))
    coef_columns = [None] * (local_heads * rank_all)
    basis_grads = []
    for grad_part, bases, offset in grads_by_part:
        for rank, basis in enumerate(bases):
            for head in range(local_heads):
                coef_columns[head * rank_all + offset + rank] = jnp.sum(
                    grad_part[:, head, :] * basis, axis=1
                ) / len(bases)
            basis_grad = sum(
                coef[head][offset + rank] * grad_part[:, head, :] for head in range(local_heads)
            ) / len(bases)
            basis_grads.append(basis_grad if offset == RQ + RK else unturn(basis_grad, cosine, sine))
    grad_factor_a = jnp.stack(coef_columns, axis=1).astype(jnp.bfloat16)
    grad_factor_b = jnp.concatenate(basis_grads, axis=1)
    head_count = lax.axis_size("head")
    basis_cols = grad_factor_b.shape[1] // head_count
    factor_cols = head_reduce_scatter(grad_factor_b.astype(jnp.bfloat16), 1).astype(jnp.bfloat16)
    weight_cols = lax.dynamic_slice_in_dim(
        b_weight, lax.axis_index("head") * basis_cols, basis_cols, axis=1
    )
    piece = grad_factor_a
    grad_normed_one = head_reduce_scatter(
        (dot_last(piece, a_weight) + dot_last(factor_cols, weight_cols)).astype(jnp.bfloat16), 0
    )
    input_part, grad_gain_attn_own = norm_backward(x_own, inv_one, gain_attn, grad_normed_one)
    input_grad = grad_resid + input_part
    grad_a = dot_first(normed_all, grad_factor_a)
    grad_b_cols = dot_first(normed_all, factor_cols)

    features = grad_gain_attn_own.shape[0]
    gain_rows = -(-2 * features // basis_cols)
    gains = jnp.pad(
        jnp.concatenate([grad_gain_attn_own, grad_gain_ffn_own]),
        (0, gain_rows * basis_cols - 2 * features),
    ).reshape(gain_rows, basis_cols)
    tail = (
        grad_a.astype(jnp.bfloat16),
        grad_out.astype(jnp.bfloat16),
        jnp.concatenate([grad_b_cols, gains], axis=0).astype(jnp.bfloat16),
    )
    tail, (grad_gate, grad_up, grad_down) = lax.optimization_barrier(
        (tail, (grad_gate, grad_up, grad_down))
    )
    sizes = [part.size for part in tail]
    summed = dp_all_reduce_pairs(jnp.concatenate([part.reshape(-1) for part in tail]))
    grad_a, grad_out, packed = (
        summed[sum(sizes[:index]) : sum(sizes[: index + 1])].reshape(part.shape)
        for index, part in enumerate(tail)
    )
    grad_out, grad_gate, grad_up, grad_down = (
        grad_out.astype(jnp.float32),
        grad_gate.astype(jnp.float32),
        grad_up.astype(jnp.float32),
        grad_down.astype(jnp.float32),
    )
    grad_a = grad_a.astype(jnp.float32)
    packed = lax.all_gather(packed, "head", axis=1, tiled=True).astype(jnp.float32)
    grad_b = packed[: grad_b_cols.shape[0]]
    gains = jnp.sum(
        packed[grad_b_cols.shape[0] :].reshape(gain_rows, head_count, basis_cols), axis=1
    ).reshape(-1)
    grad_gain_attn, grad_gain_ffn = gains[:features], gains[features : 2 * features]
    return (
        output,
        input_grad,
        grad_gain_attn,
        grad_a,
        grad_b,
        grad_out,
        grad_gain_ffn,
        grad_gate,
        grad_up,
        grad_down,
    )


def solution(mesh):
    return jax.shard_map(
        local,
        mesh=mesh,
        in_specs=(
            P(("dp", "head"), None),
            P("dp", None),
            P(),
            P(None, "head"),
            P(),
            P("head", None),
            P(),
            P(None, "head"),
            P(None, "head"),
            P("head", None),
            P(("dp", "head"), None),
        ),
        out_specs=(
            P(("dp", "head"), None),
            P(("dp", "head"), None),
            P(),
            P(None, "head"),
            P(),
            P("head", None),
            P(),
            P(None, "head"),
            P(None, "head"),
            P("head", None),
        ),
        check_vma=False,
    )
```

```python
import math

import jax
import jax.numpy as jnp
from jax import lax
from jax.sharding import PartitionSpec as P

DH = 64
RQ = 6
RK = 2


EPSILON = 1e-06
MASKED = -1e30
PRECISE = lax.Precision.HIGHEST


def rope_tables(total_rows, length):
    half_depth = DH // 2
    position = (jnp.arange(total_rows, dtype=jnp.int32) % length).astype(jnp.float32)
    frequency = jnp.exp(jnp.arange(half_depth, dtype=jnp.float32) * (-2.0 * math.log(10000.0) / DH))
    angle = position[:, None] * frequency[None, :]
    return (jnp.cos(angle), jnp.sin(angle))


def rotate(basis, cosine, sine):
    half_depth = basis.shape[-1] // 2
    first_half = basis[..., :half_depth]
    second_half = basis[..., half_depth:]
    cosine_row = cosine[:, None, :]
    sine_row = sine[:, None, :]
    return jnp.concatenate(
        [
            first_half * cosine_row - second_half * sine_row,
            second_half * cosine_row + first_half * sine_row,
        ],
        axis=-1,
    )


def unrotate(grad_basis, cosine, sine):
    half_depth = grad_basis.shape[-1] // 2
    first_half = grad_basis[..., :half_depth]
    second_half = grad_basis[..., half_depth:]
    cosine_row = cosine[:, None, :]
    sine_row = sine[:, None, :]
    return jnp.concatenate(
        [
            first_half * cosine_row + second_half * sine_row,
            second_half * cosine_row - first_half * sine_row,
        ],
        axis=-1,
    )


def dot_last(left, right):
    return lax.dot_general(
        left, right, (((1,), (1,)), ((), ())), preferred_element_type=jnp.float32
    )


def dot_first(left, right):
    return lax.dot_general(
        left, right, (((0,), (0,)), ((), ())), preferred_element_type=jnp.float32
    )


def norm_backward(inputs, inverse, gain, grad_normed):
    scaled = gain * grad_normed
    inner = jnp.mean(scaled * inputs, axis=-1, keepdims=True)
    grad_inputs = inverse * scaled - inputs * (inverse * inverse * inverse) * inner
    grad_gain = jnp.sum(grad_normed * inputs * inverse, axis=0)
    return (grad_inputs, grad_gain)


def block_scores(queries, key_rows, doc_row, first_row, last_row):
    position = jnp.arange(last_row, dtype=jnp.int32)
    allowed = (doc_row[first_row:last_row, None] == doc_row[None, :last_row]) & (
        position[None, :] <= position[first_row:last_row, None]
    )
    score_scale = 1.0 / math.sqrt(queries.shape[2])
    scores = (
        jnp.einsum(
            "qhd,khd->hqk",
            queries[first_row:last_row],
            key_rows[:last_row],
            preferred_element_type=jnp.float32,
        )
        * score_scale
    )
    return jnp.where(allowed[None], scores, MASKED)


def attend_row(row_item):
    queries, key_rows, value_rows, doc_row = row_item
    length = queries.shape[0]
    block_rows = min(512, length)
    mixed_parts = []
    total_parts = []
    for first_row in range(0, length, block_rows):
        last_row = first_row + block_rows
        scores = block_scores(queries, key_rows, doc_row, first_row, last_row)
        row_peak = jnp.max(scores, axis=-1, keepdims=True)
        exponent = jnp.exp(scores - row_peak)
        row_total = jnp.sum(exponent, axis=-1, keepdims=True)
        weights = (exponent / row_total).astype(jnp.bfloat16)
        mixed_parts.append(
            jnp.einsum(
                "hqk,khd->qhd", weights, value_rows[:last_row], preferred_element_type=jnp.float32
            ).astype(jnp.bfloat16)
        )
        total_parts.append(row_peak[..., 0] + jnp.log(row_total[..., 0]))
    return (jnp.concatenate(mixed_parts, axis=0), jnp.concatenate(total_parts, axis=1))


def attend_back(row_item):
    queries, key_rows, value_rows, doc_row, log_total, grad_mixed = row_item
    length = queries.shape[0]
    block_rows = min(512, length)
    score_scale = 1.0 / math.sqrt(queries.shape[2])
    grad_query_parts = []
    grad_keys = jnp.zeros(key_rows.shape, jnp.float32)
    grad_values = jnp.zeros(value_rows.shape, jnp.float32)
    for first_row in range(0, length, block_rows):
        last_row = first_row + block_rows
        scores = block_scores(queries, key_rows, doc_row, first_row, last_row)
        weights = jnp.exp(scores - log_total[:, first_row:last_row, None])
        grad_weights = jnp.einsum(
            "qhd,khd->hqk",
            grad_mixed[first_row:last_row],
            value_rows[:last_row],
            preferred_element_type=jnp.float32,
        )
        inner = jnp.sum(weights * grad_weights, axis=-1, keepdims=True)
        grad_scores = (weights * (grad_weights - inner)).astype(jnp.bfloat16)
        grad_query_parts.append(
            jnp.einsum(
                "hqk,khd->qhd", grad_scores, key_rows[:last_row], preferred_element_type=jnp.float32
            )
            * score_scale
        )
        padding = ((0, length - last_row), (0, 0), (0, 0))
        key_part = (
            jnp.einsum(
                "hqk,qhd->khd",
                grad_scores,
                queries[first_row:last_row],
                preferred_element_type=jnp.float32,
            )
            * score_scale
        )
        value_part = jnp.einsum(
            "hqk,qhd->khd",
            weights.astype(jnp.bfloat16),
            grad_mixed[first_row:last_row],
            preferred_element_type=jnp.float32,
        )
        grad_keys = grad_keys + jnp.pad(key_part, padding)
        grad_values = grad_values + jnp.pad(value_part, padding)
    return (jnp.concatenate(grad_query_parts, axis=0), grad_keys, grad_values)


def rounded(values_in):
    return lax.optimization_barrier(values_in.astype(jnp.bfloat16)).astype(jnp.float32)


def head_reduce_scatter(values, axis):
    count = lax.axis_size("head")
    own = lax.axis_index("head")
    width = values.shape[axis] // count
    total = lax.dynamic_slice_in_dim(values, own * width, width, axis=axis).astype(jnp.float32)
    for shift in range(1, count):
        sent = lax.dynamic_slice_in_dim(values, ((own + shift) % count) * width, width, axis=axis)
        total = total + lax.ppermute(
            sent, "head", [(device, (device + shift) % count) for device in range(count)]
        ).astype(jnp.float32)
    return total


def head_all_gather(values, axis):
    count = lax.axis_size("head")
    own = lax.axis_index("head")
    width = values.shape[axis]
    shape = list(values.shape)
    shape[axis] = width * count
    gathered = lax.dynamic_update_slice_in_dim(
        jnp.zeros(shape, values.dtype), values, own * width, axis=axis
    )
    for shift in range(1, count):
        arrived = lax.ppermute(
            values, "head", [(device, (device + shift) % count) for device in range(count)]
        )
        gathered = lax.dynamic_update_slice_in_dim(
            gathered, arrived, ((own - shift) % count) * width, axis=axis
        )
    return gathered


def dp_all_reduce(flat):
    count = lax.axis_size("dp")
    own = lax.axis_index("dp")
    steps = count.bit_length() - 1
    assert count == 1 << steps
    width = -(-flat.shape[0] // (count * 128)) * 128
    blocks = jnp.pad(flat, (0, count * width - flat.shape[0])).reshape((2,) * steps + (width,))
    kept = blocks.astype(jnp.float32)
    for step in range(steps):
        axis = steps - 1 - step
        bit = (own >> step) & 1
        sent = lax.dynamic_index_in_dim(kept, 1 - bit, axis, keepdims=False)
        kept = lax.dynamic_index_in_dim(kept, bit, axis, keepdims=False)
        pairs = [(device, device ^ (1 << step)) for device in range(count)]
        kept = kept + lax.ppermute(sent.astype(jnp.bfloat16), "dp", pairs).astype(jnp.float32)
    whole = kept.astype(jnp.bfloat16)[None]
    for step in reversed(range(steps)):
        bit = (own >> step) & 1
        pairs = [(device, device ^ (1 << step)) for device in range(count)]
        arrived = lax.ppermute(whole, "dp", pairs)
        low_half = jnp.where(bit == 0, whole, arrived)
        high_half = jnp.where(bit == 0, arrived, whole)
        whole = jnp.stack([low_half, high_half], axis=1).reshape((-1,) + whole.shape[1:])
    return whole.reshape(-1)[: flat.shape[0]]


def head_gather_relative(values):
    count = lax.axis_size("head")
    parts = [values]
    for shift in range(1, count):
        parts.append(
            lax.ppermute(values, "head", [(device, (device + shift) % count) for device in range(count)])
        )
    return jnp.concatenate(parts, axis=0)


def head_scatter_relative(values):
    count = lax.axis_size("head")
    width = values.shape[0] // count
    total = values[:width].astype(jnp.float32)
    for shift in range(1, count):
        sent = values[(count - shift) * width : (count - shift + 1) * width]
        total = total + lax.ppermute(
            sent, "head", [(device, (device + shift) % count) for device in range(count)]
        ).astype(jnp.float32)
    return total


def map_rows(step, items):
    outs = [step(tuple(item[row] for item in items)) for row in range(items[0].shape[0])]
    return tuple(jnp.stack(parts) for parts in zip(*outs))


def turn(block, cosine, sine):
    half_depth = block.shape[-1] // 2
    first_half, second_half = block[:, :half_depth], block[:, half_depth:]
    return jnp.concatenate(
        [first_half * cosine - second_half * sine, second_half * cosine + first_half * sine], axis=1
    )


def unturn(block, cosine, sine):
    half_depth = block.shape[-1] // 2
    first_half, second_half = block[:, :half_depth], block[:, half_depth:]
    return jnp.concatenate(
        [first_half * cosine + second_half * sine, second_half * cosine - first_half * sine], axis=1
    )


def dp_all_reduce_pairs(flat):
    count = lax.axis_size("dp")
    own = lax.axis_index("dp")
    group = count // 2
    width = -(-flat.shape[0] // (count * 128)) * 128
    blocks = jnp.pad(flat, (0, count * width - flat.shape[0])).reshape(group, 2, width)
    bit = own & 1
    member = own >> 1
    partner = [(device, device ^ 1) for device in range(count)]
    sent = lax.dynamic_index_in_dim(blocks, 1 - bit, 1, keepdims=False)
    kept = lax.dynamic_index_in_dim(blocks, bit, 1, keepdims=False).astype(jnp.float32)
    kept = kept + lax.ppermute(sent, "dp", partner).astype(jnp.float32)
    shifts = [
        [(device, (device & 1) + 2 * (((device >> 1) + shift) % group)) for device in range(count)]
        for shift in range(group)
    ]
    total = lax.dynamic_index_in_dim(kept, member, 0, keepdims=False)
    for shift in range(1, group):
        sent = lax.dynamic_index_in_dim(kept, (member + shift) % group, 0, keepdims=False)
        total = total + lax.ppermute(sent.astype(jnp.bfloat16), "dp", shifts[shift]).astype(
            jnp.float32
        )
    mine = total.astype(jnp.bfloat16)
    parts = [mine] + [lax.ppermute(mine, "dp", shifts[shift]) for shift in range(1, group)]
    rows = []
    for index in range(group):
        source = (member - index) % group
        row = parts[0]
        for shift in range(1, group):
            row = jnp.where(source == shift, parts[shift], row)
        rows.append(row)
    ordered = jnp.stack(rows, axis=0)
    arrived = lax.ppermute(ordered, "dp", partner)
    low_half = jnp.where(bit == 0, ordered, arrived)
    high_half = jnp.where(bit == 0, arrived, ordered)
    return jnp.stack([low_half, high_half], axis=1).reshape(-1)[: flat.shape[0]]


def local(
    tokens,
    doc_ids,
    gain_attn,
    a_weight,
    b_weight,
    out_weight,
    gain_ffn,
    gate_weight,
    up_weight,
    down_weight,
    cotangent,
):
    rows_dev, length = doc_ids.shape
    total_rows = rows_dev * length
    own_rows = tokens.shape[0]
    local_heads = out_weight.shape[0] // DH
    rank_all = RQ + 2 * RK
    x_own = tokens.astype(jnp.float32)
    inv_one = lax.rsqrt(jnp.mean(x_own * x_own, axis=-1, keepdims=True) + EPSILON)
    normed_one = (x_own * inv_one * gain_attn).astype(jnp.bfloat16)
    normed_all = head_all_gather(normed_one, 0)
    normed_all, cotangent_late = lax.optimization_barrier((normed_all, cotangent))
    grad_out_all = head_gather_relative(cotangent_late)
    factor_a = jnp.dot(normed_all, a_weight, preferred_element_type=jnp.float32)
    factor_b = jnp.dot(normed_all, b_weight, preferred_element_type=jnp.float32)
    cosine, sine = rope_tables(total_rows, length)
    basis_query = [
        turn(factor_b[:, rank * DH : (rank + 1) * DH], cosine, sine) for rank in range(RQ)
    ]
    basis_key = [
        turn(factor_b[:, (RQ + rank) * DH : (RQ + rank + 1) * DH], cosine, sine)
        for rank in range(RK)
    ]
    basis_value = [
        factor_b[:, (RQ + RK + rank) * DH : (RQ + RK + rank + 1) * DH] for rank in range(RK)
    ]
    coef = [
        [factor_a[:, head * rank_all + column] [:, None] for column in range(rank_all)]
        for head in range(local_heads)
    ]

    def combine(bases, offset):
        return jnp.stack(
            [
                sum(coef[head][offset + rank] * bases[rank] for rank in range(len(bases)))
                / len(bases)
                for head in range(local_heads)
            ],
            axis=1,
        ).astype(jnp.bfloat16)

    queries = combine(basis_query, 0)
    key_rows = combine(basis_key, RQ)
    value_rows = combine(basis_value, RQ + RK)
    row_shape = (rows_dev, length, local_heads, DH)
    query_rows = queries.reshape(row_shape)
    keys_rows = key_rows.reshape(row_shape)
    values_rows = value_rows.reshape(row_shape)
    mixed_rows, log_total = map_rows(attend_row, (query_rows, keys_rows, values_rows, doc_ids))
    mixed = mixed_rows.reshape(total_rows, local_heads * DH)
    mixed, grad_out_all = lax.optimization_barrier((mixed, grad_out_all))
    piece = lax.slice_in_dim(mixed, 0, lax.axis_size("head") * own_rows, axis=0)
    resid_own = x_own + head_reduce_scatter(
        jnp.dot(piece, out_weight, preferred_element_type=jnp.float32).astype(jnp.bfloat16), 0
    )
    inv_two = lax.rsqrt(jnp.mean(resid_own * resid_own, axis=-1, keepdims=True) + EPSILON)
    normed_two = (resid_own * inv_two * gain_ffn).astype(jnp.bfloat16)
    normed_two_all = head_gather_relative(normed_two)
    gate_act = jnp.dot(normed_two_all, gate_weight, preferred_element_type=jnp.float32)
    up_act = jnp.dot(normed_two_all, up_weight, preferred_element_type=jnp.float32)
    sigmoid_gate = jax.nn.sigmoid(gate_act)
    silu_gate = sigmoid_gate * gate_act
    hidden = (silu_gate * up_act).astype(jnp.bfloat16)
    piece = lax.slice_in_dim(hidden, 0, lax.axis_size("head") * own_rows, axis=0)
    output = (
        resid_own
        + head_scatter_relative(
            jnp.dot(piece, down_weight, preferred_element_type=jnp.float32).astype(jnp.bfloat16)
        )
    ).astype(jnp.bfloat16)
    grad_down = dot_first(hidden, grad_out_all)
    grad_hidden = dot_last(grad_out_all, down_weight)
    grad_gate_act = (
        grad_hidden * up_act * (sigmoid_gate * (1.0 + gate_act * (1.0 - sigmoid_gate)))
    ).astype(jnp.bfloat16)
    grad_up_act = (grad_hidden * silu_gate).astype(jnp.bfloat16)
    grad_gate = dot_first(normed_two_all, grad_gate_act)
    grad_up = dot_first(normed_two_all, grad_up_act)
    gate_piece = lax.slice_in_dim(grad_gate_act, 0, lax.axis_size("head") * own_rows, axis=0)
    up_piece = lax.slice_in_dim(grad_up_act, 0, lax.axis_size("head") * own_rows, axis=0)
    grad_normed_two = head_scatter_relative(
        (dot_last(gate_piece, gate_weight) + dot_last(up_piece, up_weight)).astype(jnp.bfloat16)
    )
    ffn_grads = (grad_gate.astype(jnp.bfloat16), grad_up.astype(jnp.bfloat16), grad_down.astype(jnp.bfloat16))
    ffn_grads, grad_normed_two = lax.optimization_barrier((ffn_grads, grad_normed_two))
    grad_gate, grad_up, grad_down = lax.psum(ffn_grads, "dp")
    resid_part, grad_gain_ffn_own = norm_backward(resid_own, inv_two, gain_ffn, grad_normed_two)
    grad_resid = cotangent.astype(jnp.float32) + resid_part
    output, grad_resid = lax.optimization_barrier((output, grad_resid))
    grad_branch = head_all_gather(grad_resid.astype(jnp.bfloat16), 0)
    grad_mixed = dot_last(grad_branch, out_weight).astype(jnp.bfloat16)
    grad_out = dot_first(mixed, grad_branch)
    grad_query_rows, grad_key_rows, grad_value_rows = map_rows(
        attend_back,
        (query_rows, keys_rows, values_rows, doc_ids, log_total, grad_mixed.reshape(row_shape)),
    )
    head_shape = (total_rows, local_heads, DH)
    grad_query = rounded(grad_query_rows.reshape(head_shape))
    grad_key = rounded(grad_key_rows.reshape(head_shape))
    grad_value = rounded(grad_value_rows.reshape(head_shape))
    grads_by_part = ((grad_query, basis_query, 0), (grad_key, basis_key, RQ), (grad_value, basis_value, RQ + RK))
    coef_columns = [None] * (local_heads * rank_all)
    basis_grads = []
    for grad_part, bases, offset in grads_by_part:
        for rank, basis in enumerate(bases):
            for head in range(local_heads):
                coef_columns[head * rank_all + offset + rank] = jnp.sum(
                    grad_part[:, head, :] * basis, axis=1
                ) / len(bases)
            basis_grad = sum(
                coef[head][offset + rank] * grad_part[:, head, :] for head in range(local_heads)
            ) / len(bases)
            basis_grads.append(basis_grad if offset == RQ + RK else unturn(basis_grad, cosine, sine))
    grad_factor_a = jnp.stack(coef_columns, axis=1).astype(jnp.bfloat16)
    grad_factor_b = jnp.concatenate(basis_grads, axis=1)
    head_count = lax.axis_size("head")
    basis_cols = grad_factor_b.shape[1] // head_count
    factor_cols = head_reduce_scatter(grad_factor_b.astype(jnp.bfloat16), 1).astype(jnp.bfloat16)
    weight_cols = lax.dynamic_slice_in_dim(
        b_weight, lax.axis_index("head") * basis_cols, basis_cols, axis=1
    )
    piece = grad_factor_a
    grad_normed_one = head_reduce_scatter(
        (dot_last(piece, a_weight) + dot_last(factor_cols, weight_cols)).astype(jnp.bfloat16), 0
    )
    input_part, grad_gain_attn_own = norm_backward(x_own, inv_one, gain_attn, grad_normed_one)
    input_grad = grad_resid + input_part
    grad_a = dot_first(normed_all, grad_factor_a)
    grad_b_cols = dot_first(normed_all, factor_cols)

    features = grad_gain_attn_own.shape[0]
    gain_rows = -(-2 * features // basis_cols)
    gains = jnp.pad(
        jnp.concatenate([grad_gain_attn_own, grad_gain_ffn_own]),
        (0, gain_rows * basis_cols - 2 * features),
    ).reshape(gain_rows, basis_cols)
    tail = (
        grad_a.astype(jnp.bfloat16),
        grad_out.astype(jnp.bfloat16),
        jnp.concatenate([grad_b_cols, gains], axis=0).astype(jnp.bfloat16),
    )
    tail, (grad_gate, grad_up, grad_down) = lax.optimization_barrier(
        (tail, (grad_gate, grad_up, grad_down))
    )
    sizes = [part.size for part in tail]
    summed = dp_all_reduce_pairs(jnp.concatenate([part.reshape(-1) for part in tail]))
    grad_a, grad_out, packed = (
        summed[sum(sizes[:index]) : sum(sizes[: index + 1])].reshape(part.shape)
        for index, part in enumerate(tail)
    )
    grad_out, grad_gate, grad_up, grad_down = (
        grad_out.astype(jnp.float32),
        grad_gate.astype(jnp.float32),
        grad_up.astype(jnp.float32),
        grad_down.astype(jnp.float32),
    )
    grad_a = grad_a.astype(jnp.float32)
    own_head = lax.axis_index("head")
    arrivals = [packed] + [
        lax.ppermute(
            packed, "head", [(device, (device + shift) % head_count) for device in range(head_count)]
        )
        for shift in range(1, head_count)
    ]
    columns = []
    for index in range(head_count):
        source = (own_head - index) % head_count
        column = arrivals[0]
        for shift in range(1, head_count):
            column = jnp.where(source == shift, arrivals[shift], column)
        columns.append(column)
    packed = (
        jnp.stack(columns, axis=1).reshape(packed.shape[0], -1).astype(jnp.float32)
    )
    grad_b = packed[: grad_b_cols.shape[0]]
    gains = jnp.sum(
        packed[grad_b_cols.shape[0] :].reshape(gain_rows, head_count, basis_cols), axis=1
    ).reshape(-1)
    grad_gain_attn, grad_gain_ffn = gains[:features], gains[features : 2 * features]
    return (
        output,
        input_grad,
        grad_gain_attn,
        grad_a,
        grad_b,
        grad_out,
        grad_gain_ffn,
        grad_gate,
        grad_up,
        grad_down,
    )


def solution(mesh):
    return jax.shard_map(
        local,
        mesh=mesh,
        in_specs=(
            P(("dp", "head"), None),
            P("dp", None),
            P(),
            P(None, "head"),
            P(),
            P("head", None),
            P(),
            P(None, "head"),
            P(None, "head"),
            P("head", None),
            P(("dp", "head"), None),
        ),
        out_specs=(
            P(("dp", "head"), None),
            P(("dp", "head"), None),
            P(),
            P(None, "head"),
            P(),
            P("head", None),
            P(),
            P(None, "head"),
            P(None, "head"),
            P("head", None),
        ),
        check_vma=False,
    )
```

```python
import math

import jax
import jax.numpy as jnp
from jax import lax
from jax.sharding import PartitionSpec as P

DH = 64
RQ = 6
RK = 2


EPSILON = 1e-06
MASKED = -1e30
PRECISE = lax.Precision.HIGHEST


def rope_tables(total_rows, length):
    half_depth = DH // 2
    position = (jnp.arange(total_rows, dtype=jnp.int32) % length).astype(jnp.float32)
    frequency = jnp.exp(jnp.arange(half_depth, dtype=jnp.float32) * (-2.0 * math.log(10000.0) / DH))
    angle = position[:, None] * frequency[None, :]
    return (jnp.cos(angle), jnp.sin(angle))


def rotate(basis, cosine, sine):
    half_depth = basis.shape[-1] // 2
    first_half = basis[..., :half_depth]
    second_half = basis[..., half_depth:]
    cosine_row = cosine[:, None, :]
    sine_row = sine[:, None, :]
    return jnp.concatenate(
        [
            first_half * cosine_row - second_half * sine_row,
            second_half * cosine_row + first_half * sine_row,
        ],
        axis=-1,
    )


def unrotate(grad_basis, cosine, sine):
    half_depth = grad_basis.shape[-1] // 2
    first_half = grad_basis[..., :half_depth]
    second_half = grad_basis[..., half_depth:]
    cosine_row = cosine[:, None, :]
    sine_row = sine[:, None, :]
    return jnp.concatenate(
        [
            first_half * cosine_row + second_half * sine_row,
            second_half * cosine_row - first_half * sine_row,
        ],
        axis=-1,
    )


def dot_last(left, right):
    return lax.dot_general(
        left, right, (((1,), (1,)), ((), ())), preferred_element_type=jnp.float32
    )


def dot_first(left, right):
    return lax.dot_general(
        left, right, (((0,), (0,)), ((), ())), preferred_element_type=jnp.float32
    )


def norm_backward(inputs, inverse, gain, grad_normed):
    scaled = gain * grad_normed
    inner = jnp.mean(scaled * inputs, axis=-1, keepdims=True)
    grad_inputs = inverse * scaled - inputs * (inverse * inverse * inverse) * inner
    grad_gain = jnp.sum(grad_normed * inputs * inverse, axis=0)
    return (grad_inputs, grad_gain)


def block_scores(queries, key_rows, doc_row, first_row, last_row):
    position = jnp.arange(last_row, dtype=jnp.int32)
    allowed = (doc_row[first_row:last_row, None] == doc_row[None, :last_row]) & (
        position[None, :] <= position[first_row:last_row, None]
    )
    score_scale = 1.0 / math.sqrt(queries.shape[2])
    scores = (
        jnp.einsum(
            "qhd,khd->hqk",
            queries[first_row:last_row],
            key_rows[:last_row],
            preferred_element_type=jnp.float32,
        )
        * score_scale
    )
    return jnp.where(allowed[None], scores, MASKED)


def attend_row(row_item):
    queries, key_rows, value_rows, doc_row = row_item
    length = queries.shape[0]
    block_rows = min(512, length)
    mixed_parts = []
    total_parts = []
    for first_row in range(0, length, block_rows):
        last_row = first_row + block_rows
        scores = block_scores(queries, key_rows, doc_row, first_row, last_row)
        row_peak = jnp.max(scores, axis=-1, keepdims=True)
        exponent = jnp.exp(scores - row_peak)
        row_total = jnp.sum(exponent, axis=-1, keepdims=True)
        weights = (exponent / row_total).astype(jnp.bfloat16)
        mixed_parts.append(
            jnp.einsum(
                "hqk,khd->qhd", weights, value_rows[:last_row], preferred_element_type=jnp.float32
            ).astype(jnp.bfloat16)
        )
        total_parts.append(row_peak[..., 0] + jnp.log(row_total[..., 0]))
    return (jnp.concatenate(mixed_parts, axis=0), jnp.concatenate(total_parts, axis=1))


def attend_back(row_item):
    queries, key_rows, value_rows, doc_row, log_total, grad_mixed = row_item
    length = queries.shape[0]
    block_rows = min(512, length)
    score_scale = 1.0 / math.sqrt(queries.shape[2])
    grad_query_parts = []
    grad_keys = jnp.zeros(key_rows.shape, jnp.float32)
    grad_values = jnp.zeros(value_rows.shape, jnp.float32)
    for first_row in range(0, length, block_rows):
        last_row = first_row + block_rows
        scores = block_scores(queries, key_rows, doc_row, first_row, last_row)
        weights = jnp.exp(scores - log_total[:, first_row:last_row, None])
        grad_weights = jnp.einsum(
            "qhd,khd->hqk",
            grad_mixed[first_row:last_row],
            value_rows[:last_row],
            preferred_element_type=jnp.float32,
        )
        inner = jnp.sum(weights * grad_weights, axis=-1, keepdims=True)
        grad_scores = (weights * (grad_weights - inner)).astype(jnp.bfloat16)
        grad_query_parts.append(
            jnp.einsum(
                "hqk,khd->qhd", grad_scores, key_rows[:last_row], preferred_element_type=jnp.float32
            )
            * score_scale
        )
        padding = ((0, length - last_row), (0, 0), (0, 0))
        key_part = (
            jnp.einsum(
                "hqk,qhd->khd",
                grad_scores,
                queries[first_row:last_row],
                preferred_element_type=jnp.float32,
            )
            * score_scale
        )
        value_part = jnp.einsum(
            "hqk,qhd->khd",
            weights.astype(jnp.bfloat16),
            grad_mixed[first_row:last_row],
            preferred_element_type=jnp.float32,
        )
        grad_keys = grad_keys + jnp.pad(key_part, padding)
        grad_values = grad_values + jnp.pad(value_part, padding)
    return (jnp.concatenate(grad_query_parts, axis=0), grad_keys, grad_values)


def rounded(values_in):
    return lax.optimization_barrier(values_in.astype(jnp.bfloat16)).astype(jnp.float32)


def head_reduce_scatter(values, axis):
    count = lax.axis_size("head")
    own = lax.axis_index("head")
    width = values.shape[axis] // count
    total = lax.dynamic_slice_in_dim(values, own * width, width, axis=axis).astype(jnp.float32)
    for shift in range(1, count):
        sent = lax.dynamic_slice_in_dim(values, ((own + shift) % count) * width, width, axis=axis)
        total = total + lax.ppermute(
            sent, "head", [(device, (device + shift) % count) for device in range(count)]
        ).astype(jnp.float32)
    return total


def head_all_gather(values, axis):
    count = lax.axis_size("head")
    own = lax.axis_index("head")
    width = values.shape[axis]
    shape = list(values.shape)
    shape[axis] = width * count
    gathered = lax.dynamic_update_slice_in_dim(
        jnp.zeros(shape, values.dtype), values, own * width, axis=axis
    )
    for shift in range(1, count):
        arrived = lax.ppermute(
            values, "head", [(device, (device + shift) % count) for device in range(count)]
        )
        gathered = lax.dynamic_update_slice_in_dim(
            gathered, arrived, ((own - shift) % count) * width, axis=axis
        )
    return gathered


def dp_all_reduce(flat):
    count = lax.axis_size("dp")
    own = lax.axis_index("dp")
    steps = count.bit_length() - 1
    assert count == 1 << steps
    width = -(-flat.shape[0] // (count * 128)) * 128
    blocks = jnp.pad(flat, (0, count * width - flat.shape[0])).reshape((2,) * steps + (width,))
    kept = blocks.astype(jnp.float32)
    for step in range(steps):
        axis = steps - 1 - step
        bit = (own >> step) & 1
        sent = lax.dynamic_index_in_dim(kept, 1 - bit, axis, keepdims=False)
        kept = lax.dynamic_index_in_dim(kept, bit, axis, keepdims=False)
        pairs = [(device, device ^ (1 << step)) for device in range(count)]
        kept = kept + lax.ppermute(sent.astype(jnp.bfloat16), "dp", pairs).astype(jnp.float32)
    whole = kept.astype(jnp.bfloat16)[None]
    for step in reversed(range(steps)):
        bit = (own >> step) & 1
        pairs = [(device, device ^ (1 << step)) for device in range(count)]
        arrived = lax.ppermute(whole, "dp", pairs)
        low_half = jnp.where(bit == 0, whole, arrived)
        high_half = jnp.where(bit == 0, arrived, whole)
        whole = jnp.stack([low_half, high_half], axis=1).reshape((-1,) + whole.shape[1:])
    return whole.reshape(-1)[: flat.shape[0]]


def head_gather_relative(values):
    count = lax.axis_size("head")
    parts = [values]
    for shift in range(1, count):
        parts.append(
            lax.ppermute(values, "head", [(device, (device + shift) % count) for device in range(count)])
        )
    return jnp.concatenate(parts, axis=0)


def head_scatter_relative(values):
    count = lax.axis_size("head")
    width = values.shape[0] // count
    total = values[:width].astype(jnp.float32)
    for shift in range(1, count):
        sent = values[(count - shift) * width : (count - shift + 1) * width]
        total = total + lax.ppermute(
            sent, "head", [(device, (device + shift) % count) for device in range(count)]
        ).astype(jnp.float32)
    return total


def map_rows(step, items):
    outs = [step(tuple(item[row] for item in items)) for row in range(items[0].shape[0])]
    return tuple(jnp.stack(parts) for parts in zip(*outs))


def turn(block, cosine, sine):
    half_depth = block.shape[-1] // 2
    first_half, second_half = block[:, :half_depth], block[:, half_depth:]
    return jnp.concatenate(
        [first_half * cosine - second_half * sine, second_half * cosine + first_half * sine], axis=1
    )


def unturn(block, cosine, sine):
    half_depth = block.shape[-1] // 2
    first_half, second_half = block[:, :half_depth], block[:, half_depth:]
    return jnp.concatenate(
        [first_half * cosine + second_half * sine, second_half * cosine - first_half * sine], axis=1
    )


def dp_all_reduce_pairs(flat):
    count = lax.axis_size("dp")
    own = lax.axis_index("dp")
    group = count // 2
    width = -(-flat.shape[0] // (count * 128)) * 128
    blocks = jnp.pad(flat, (0, count * width - flat.shape[0])).reshape(group, 2, width)
    bit = own & 1
    member = own >> 1
    partner = [(device, device ^ 1) for device in range(count)]
    sent = lax.dynamic_index_in_dim(blocks, 1 - bit, 1, keepdims=False)
    kept = lax.dynamic_index_in_dim(blocks, bit, 1, keepdims=False).astype(jnp.float32)
    kept = kept + lax.ppermute(sent, "dp", partner).astype(jnp.float32)
    shifts = [
        [(device, (device & 1) + 2 * (((device >> 1) + shift) % group)) for device in range(count)]
        for shift in range(group)
    ]
    total = lax.dynamic_index_in_dim(kept, member, 0, keepdims=False)
    for shift in range(1, group):
        sent = lax.dynamic_index_in_dim(kept, (member + shift) % group, 0, keepdims=False)
        total = total + lax.ppermute(sent.astype(jnp.bfloat16), "dp", shifts[shift]).astype(
            jnp.float32
        )
    mine = total.astype(jnp.bfloat16)
    parts = [mine] + [lax.ppermute(mine, "dp", shifts[shift]) for shift in range(1, group)]
    rows = []
    for index in range(group):
        source = (member - index) % group
        row = parts[0]
        for shift in range(1, group):
            row = jnp.where(source == shift, parts[shift], row)
        rows.append(row)
    ordered = jnp.stack(rows, axis=0)
    arrived = lax.ppermute(ordered, "dp", partner)
    low_half = jnp.where(bit == 0, ordered, arrived)
    high_half = jnp.where(bit == 0, arrived, ordered)
    return jnp.stack([low_half, high_half], axis=1).reshape(-1)[: flat.shape[0]]


def local(
    tokens,
    doc_ids,
    gain_attn,
    a_weight,
    b_weight,
    out_weight,
    gain_ffn,
    gate_weight,
    up_weight,
    down_weight,
    cotangent,
):
    rows_dev, length = doc_ids.shape
    total_rows = rows_dev * length
    own_rows = tokens.shape[0]
    local_heads = out_weight.shape[0] // DH
    rank_all = RQ + 2 * RK
    x_own = tokens.astype(jnp.float32)
    inv_one = lax.rsqrt(jnp.mean(x_own * x_own, axis=-1, keepdims=True) + EPSILON)
    normed_one = (x_own * inv_one * gain_attn).astype(jnp.bfloat16)
    normed_all = head_all_gather(normed_one, 0)
    normed_all, cotangent_late = lax.optimization_barrier((normed_all, cotangent))
    grad_out_all = head_gather_relative(cotangent_late)
    factor_a = jnp.dot(normed_all, a_weight, preferred_element_type=jnp.float32)
    factor_b = jnp.dot(normed_all, b_weight, preferred_element_type=jnp.float32)
    cosine, sine = rope_tables(total_rows, length)
    basis_query = [
        turn(factor_b[:, rank * DH : (rank + 1) * DH], cosine, sine) for rank in range(RQ)
    ]
    basis_key = [
        turn(factor_b[:, (RQ + rank) * DH : (RQ + rank + 1) * DH], cosine, sine)
        for rank in range(RK)
    ]
    basis_value = [
        factor_b[:, (RQ + RK + rank) * DH : (RQ + RK + rank + 1) * DH] for rank in range(RK)
    ]
    coef = [
        [factor_a[:, head * rank_all + column] [:, None] for column in range(rank_all)]
        for head in range(local_heads)
    ]

    def combine(bases, offset):
        return jnp.stack(
            [
                sum(coef[head][offset + rank] * bases[rank] for rank in range(len(bases)))
                / len(bases)
                for head in range(local_heads)
            ],
            axis=1,
        ).astype(jnp.bfloat16)

    queries = combine(basis_query, 0)
    key_rows = combine(basis_key, RQ)
    value_rows = combine(basis_value, RQ + RK)
    row_shape = (rows_dev, length, local_heads, DH)
    query_rows = queries.reshape(row_shape)
    keys_rows = key_rows.reshape(row_shape)
    values_rows = value_rows.reshape(row_shape)
    mixed_rows, log_total = map_rows(attend_row, (query_rows, keys_rows, values_rows, doc_ids))
    mixed = mixed_rows.reshape(total_rows, local_heads * DH)
    mixed, grad_out_all = lax.optimization_barrier((mixed, grad_out_all))
    piece = lax.slice_in_dim(mixed, 0, lax.axis_size("head") * own_rows, axis=0)
    resid_own = x_own + head_reduce_scatter(
        jnp.dot(piece, out_weight, preferred_element_type=jnp.float32).astype(jnp.bfloat16), 0
    )
    inv_two = lax.rsqrt(jnp.mean(resid_own * resid_own, axis=-1, keepdims=True) + EPSILON)
    normed_two = (resid_own * inv_two * gain_ffn).astype(jnp.bfloat16)
    normed_two_all = head_gather_relative(normed_two)
    gate_act = jnp.dot(normed_two_all, gate_weight, preferred_element_type=jnp.float32)
    up_act = jnp.dot(normed_two_all, up_weight, preferred_element_type=jnp.float32)
    sigmoid_gate = jax.nn.sigmoid(gate_act)
    silu_gate = sigmoid_gate * gate_act
    hidden = (silu_gate * up_act).astype(jnp.bfloat16)
    piece = lax.slice_in_dim(hidden, 0, lax.axis_size("head") * own_rows, axis=0)
    output = (
        resid_own
        + head_scatter_relative(
            jnp.dot(piece, down_weight, preferred_element_type=jnp.float32).astype(jnp.bfloat16)
        )
    ).astype(jnp.bfloat16)
    grad_down = dot_first(hidden, grad_out_all)
    grad_hidden = dot_last(grad_out_all, down_weight)
    grad_gate_act = (
        grad_hidden * up_act * (sigmoid_gate * (1.0 + gate_act * (1.0 - sigmoid_gate)))
    ).astype(jnp.bfloat16)
    grad_up_act = (grad_hidden * silu_gate).astype(jnp.bfloat16)
    grad_gate = dot_first(normed_two_all, grad_gate_act)
    grad_up = dot_first(normed_two_all, grad_up_act)
    gate_piece = lax.slice_in_dim(grad_gate_act, 0, lax.axis_size("head") * own_rows, axis=0)
    up_piece = lax.slice_in_dim(grad_up_act, 0, lax.axis_size("head") * own_rows, axis=0)
    grad_normed_two = head_scatter_relative(
        (dot_last(gate_piece, gate_weight) + dot_last(up_piece, up_weight)).astype(jnp.bfloat16)
    )
    ffn_grads = (grad_gate.astype(jnp.bfloat16), grad_up.astype(jnp.bfloat16), grad_down.astype(jnp.bfloat16))
    ffn_grads, grad_normed_two = lax.optimization_barrier((ffn_grads, grad_normed_two))
    grad_gate, grad_up, grad_down = lax.psum(ffn_grads, "dp")
    resid_part, grad_gain_ffn_own = norm_backward(resid_own, inv_two, gain_ffn, grad_normed_two)
    grad_resid = cotangent.astype(jnp.float32) + resid_part
    output, grad_resid = lax.optimization_barrier((output, grad_resid))
    grad_branch = head_all_gather(grad_resid.astype(jnp.bfloat16), 0)
    grad_mixed = dot_last(grad_branch, out_weight).astype(jnp.bfloat16)
    grad_out = dot_first(mixed, grad_branch)
    grad_query_rows, grad_key_rows, grad_value_rows = map_rows(
        attend_back,
        (query_rows, keys_rows, values_rows, doc_ids, log_total, grad_mixed.reshape(row_shape)),
    )
    head_shape = (total_rows, local_heads, DH)
    grad_query = rounded(grad_query_rows.reshape(head_shape))
    grad_key = rounded(grad_key_rows.reshape(head_shape))
    grad_value = rounded(grad_value_rows.reshape(head_shape))
    grads_by_part = ((grad_query, basis_query, 0), (grad_key, basis_key, RQ), (grad_value, basis_value, RQ + RK))
    coef_columns = [None] * (local_heads * rank_all)
    basis_grads = []
    for grad_part, bases, offset in grads_by_part:
        for rank, basis in enumerate(bases):
            for head in range(local_heads):
                coef_columns[head * rank_all + offset + rank] = jnp.sum(
                    grad_part[:, head, :] * basis, axis=1
                ) / len(bases)
            basis_grad = sum(
                coef[head][offset + rank] * grad_part[:, head, :] for head in range(local_heads)
            ) / len(bases)
            basis_grads.append(basis_grad if offset == RQ + RK else unturn(basis_grad, cosine, sine))
    grad_factor_a = jnp.stack(coef_columns, axis=1).astype(jnp.bfloat16)
    grad_factor_b = jnp.concatenate(basis_grads, axis=1)
    head_count = lax.axis_size("head")
    basis_cols = grad_factor_b.shape[1] // head_count
    factor_cols = head_reduce_scatter(grad_factor_b.astype(jnp.bfloat16), 1).astype(jnp.bfloat16)
    weight_cols = lax.dynamic_slice_in_dim(
        b_weight, lax.axis_index("head") * basis_cols, basis_cols, axis=1
    )
    piece = grad_factor_a
    grad_normed_one = head_reduce_scatter(
        (dot_last(piece, a_weight) + dot_last(factor_cols, weight_cols)).astype(jnp.bfloat16), 0
    )
    input_part, grad_gain_attn_own = norm_backward(x_own, inv_one, gain_attn, grad_normed_one)
    input_grad = grad_resid + input_part
    grad_a = dot_first(normed_all, grad_factor_a)
    grad_b_cols = dot_first(normed_all, factor_cols)

    features = grad_gain_attn_own.shape[0]
    gain_rows = -(-2 * features // basis_cols)
    gains = jnp.pad(
        jnp.concatenate([grad_gain_attn_own, grad_gain_ffn_own]),
        (0, gain_rows * basis_cols - 2 * features),
    ).reshape(gain_rows, basis_cols)
    tail = (
        grad_a.astype(jnp.bfloat16),
        grad_out.astype(jnp.bfloat16),
        jnp.concatenate([grad_b_cols, gains], axis=0).astype(jnp.bfloat16),
    )
    tail, (grad_gate, grad_up, grad_down) = lax.optimization_barrier(
        (tail, (grad_gate, grad_up, grad_down))
    )
    sizes = [part.size for part in tail]
    summed = dp_all_reduce_pairs(jnp.concatenate([part.reshape(-1) for part in tail]))
    grad_a, grad_out, packed = (
        summed[sum(sizes[:index]) : sum(sizes[: index + 1])].reshape(part.shape)
        for index, part in enumerate(tail)
    )
    grad_out, grad_gate, grad_up, grad_down = (
        grad_out.astype(jnp.float32),
        grad_gate.astype(jnp.float32),
        grad_up.astype(jnp.float32),
        grad_down.astype(jnp.float32),
    )
    grad_a = grad_a.astype(jnp.float32)
    packed = lax.all_gather(packed, "head", axis=1, tiled=True)
    grad_b = packed[: grad_b_cols.shape[0]].astype(jnp.float32)
    gains = jnp.sum(
        packed[grad_b_cols.shape[0] :]
        .astype(jnp.float32)
        .reshape(gain_rows, head_count, basis_cols),
        axis=1,
    ).reshape(-1)
    grad_gain_attn, grad_gain_ffn = gains[:features], gains[features : 2 * features]
    return (
        output,
        input_grad,
        grad_gain_attn,
        grad_a,
        grad_b,
        grad_out,
        grad_gain_ffn,
        grad_gate,
        grad_up,
        grad_down,
    )


def solution(mesh):
    return jax.shard_map(
        local,
        mesh=mesh,
        in_specs=(
            P(("dp", "head"), None),
            P("dp", None),
            P(),
            P(None, "head"),
            P(),
            P("head", None),
            P(),
            P(None, "head"),
            P(None, "head"),
            P("head", None),
            P(("dp", "head"), None),
        ),
        out_specs=(
            P(("dp", "head"), None),
            P(("dp", "head"), None),
            P(),
            P(None, "head"),
            P(),
            P("head", None),
            P(),
            P(None, "head"),
            P(None, "head"),
            P("head", None),
        ),
        check_vma=False,
    )
```

```python
import math

import jax
import jax.numpy as jnp
from jax import lax
from jax.sharding import PartitionSpec as P

DH = 64
RQ = 6
RK = 2


EPSILON = 1e-06
MASKED = -1e30
PRECISE = lax.Precision.HIGHEST


def rope_tables(total_rows, length):
    half_depth = DH // 2
    position = (jnp.arange(total_rows, dtype=jnp.int32) % length).astype(jnp.float32)
    frequency = jnp.exp(jnp.arange(half_depth, dtype=jnp.float32) * (-2.0 * math.log(10000.0) / DH))
    angle = position[:, None] * frequency[None, :]
    return (jnp.cos(angle), jnp.sin(angle))


def rotate(basis, cosine, sine):
    half_depth = basis.shape[-1] // 2
    first_half = basis[..., :half_depth]
    second_half = basis[..., half_depth:]
    cosine_row = cosine[:, None, :]
    sine_row = sine[:, None, :]
    return jnp.concatenate(
        [
            first_half * cosine_row - second_half * sine_row,
            second_half * cosine_row + first_half * sine_row,
        ],
        axis=-1,
    )


def unrotate(grad_basis, cosine, sine):
    half_depth = grad_basis.shape[-1] // 2
    first_half = grad_basis[..., :half_depth]
    second_half = grad_basis[..., half_depth:]
    cosine_row = cosine[:, None, :]
    sine_row = sine[:, None, :]
    return jnp.concatenate(
        [
            first_half * cosine_row + second_half * sine_row,
            second_half * cosine_row - first_half * sine_row,
        ],
        axis=-1,
    )


def dot_last(left, right):
    return lax.dot_general(
        left, right, (((1,), (1,)), ((), ())), preferred_element_type=jnp.float32
    )


def dot_first(left, right):
    return lax.dot_general(
        left, right, (((0,), (0,)), ((), ())), preferred_element_type=jnp.float32
    )


def norm_backward(inputs, inverse, gain, grad_normed):
    scaled = gain * grad_normed
    inner = jnp.mean(scaled * inputs, axis=-1, keepdims=True)
    grad_inputs = inverse * scaled - inputs * (inverse * inverse * inverse) * inner
    grad_gain = jnp.sum(grad_normed * inputs * inverse, axis=0)
    return (grad_inputs, grad_gain)


def block_scores(queries, key_rows, doc_row, first_row, last_row):
    position = jnp.arange(last_row, dtype=jnp.int32)
    allowed = (doc_row[first_row:last_row, None] == doc_row[None, :last_row]) & (
        position[None, :] <= position[first_row:last_row, None]
    )
    score_scale = 1.0 / math.sqrt(queries.shape[2])
    scores = (
        jnp.einsum(
            "qhd,khd->hqk",
            queries[first_row:last_row],
            key_rows[:last_row],
            preferred_element_type=jnp.float32,
        )
        * score_scale
    )
    return jnp.where(allowed[None], scores, MASKED)


def attend_row(row_item):
    queries, key_rows, value_rows, doc_row = row_item
    length = queries.shape[0]
    block_rows = min(512, length)
    mixed_parts = []
    total_parts = []
    for first_row in range(0, length, block_rows):
        last_row = first_row + block_rows
        scores = block_scores(queries, key_rows, doc_row, first_row, last_row)
        row_peak = jnp.max(scores, axis=-1, keepdims=True)
        exponent = jnp.exp(scores - row_peak)
        row_total = jnp.sum(exponent, axis=-1, keepdims=True)
        weights = (exponent / row_total).astype(jnp.bfloat16)
        mixed_parts.append(
            jnp.einsum(
                "hqk,khd->qhd", weights, value_rows[:last_row], preferred_element_type=jnp.float32
            ).astype(jnp.bfloat16)
        )
        total_parts.append(row_peak[..., 0] + jnp.log(row_total[..., 0]))
    return (jnp.concatenate(mixed_parts, axis=0), jnp.concatenate(total_parts, axis=1))


def attend_back(row_item):
    queries, key_rows, value_rows, doc_row, log_total, grad_mixed = row_item
    length = queries.shape[0]
    block_rows = min(512, length)
    score_scale = 1.0 / math.sqrt(queries.shape[2])
    grad_query_parts = []
    grad_keys = jnp.zeros(key_rows.shape, jnp.float32)
    grad_values = jnp.zeros(value_rows.shape, jnp.float32)
    for first_row in range(0, length, block_rows):
        last_row = first_row + block_rows
        scores = block_scores(queries, key_rows, doc_row, first_row, last_row)
        weights = jnp.exp(scores - log_total[:, first_row:last_row, None])
        grad_weights = jnp.einsum(
            "qhd,khd->hqk",
            grad_mixed[first_row:last_row],
            value_rows[:last_row],
            preferred_element_type=jnp.float32,
        )
        inner = jnp.sum(weights * grad_weights, axis=-1, keepdims=True)
        grad_scores = (weights * (grad_weights - inner)).astype(jnp.bfloat16)
        grad_query_parts.append(
            jnp.einsum(
                "hqk,khd->qhd", grad_scores, key_rows[:last_row], preferred_element_type=jnp.float32
            )
            * score_scale
        )
        padding = ((0, length - last_row), (0, 0), (0, 0))
        key_part = (
            jnp.einsum(
                "hqk,qhd->khd",
                grad_scores,
                queries[first_row:last_row],
                preferred_element_type=jnp.float32,
            )
            * score_scale
        )
        value_part = jnp.einsum(
            "hqk,qhd->khd",
            weights.astype(jnp.bfloat16),
            grad_mixed[first_row:last_row],
            preferred_element_type=jnp.float32,
        )
        grad_keys = grad_keys + jnp.pad(key_part, padding)
        grad_values = grad_values + jnp.pad(value_part, padding)
    return (jnp.concatenate(grad_query_parts, axis=0), grad_keys, grad_values)


def rounded(values_in):
    return lax.optimization_barrier(values_in.astype(jnp.bfloat16)).astype(jnp.float32)


def head_reduce_scatter(values, axis):
    count = lax.axis_size("head")
    own = lax.axis_index("head")
    width = values.shape[axis] // count
    total = lax.dynamic_slice_in_dim(values, own * width, width, axis=axis).astype(jnp.float32)
    for shift in range(1, count):
        sent = lax.dynamic_slice_in_dim(values, ((own + shift) % count) * width, width, axis=axis)
        total = total + lax.ppermute(
            sent, "head", [(device, (device + shift) % count) for device in range(count)]
        ).astype(jnp.float32)
    return total


def head_all_gather(values, axis):
    count = lax.axis_size("head")
    own = lax.axis_index("head")
    width = values.shape[axis]
    shape = list(values.shape)
    shape[axis] = width * count
    gathered = lax.dynamic_update_slice_in_dim(
        jnp.zeros(shape, values.dtype), values, own * width, axis=axis
    )
    for shift in range(1, count):
        arrived = lax.ppermute(
            values, "head", [(device, (device + shift) % count) for device in range(count)]
        )
        gathered = lax.dynamic_update_slice_in_dim(
            gathered, arrived, ((own - shift) % count) * width, axis=axis
        )
    return gathered


def dp_all_reduce(flat):
    count = lax.axis_size("dp")
    own = lax.axis_index("dp")
    steps = count.bit_length() - 1
    assert count == 1 << steps
    width = -(-flat.shape[0] // (count * 128)) * 128
    blocks = jnp.pad(flat, (0, count * width - flat.shape[0])).reshape((2,) * steps + (width,))
    kept = blocks.astype(jnp.float32)
    for step in range(steps):
        axis = steps - 1 - step
        bit = (own >> step) & 1
        sent = lax.dynamic_index_in_dim(kept, 1 - bit, axis, keepdims=False)
        kept = lax.dynamic_index_in_dim(kept, bit, axis, keepdims=False)
        pairs = [(device, device ^ (1 << step)) for device in range(count)]
        kept = kept + lax.ppermute(sent.astype(jnp.bfloat16), "dp", pairs).astype(jnp.float32)
    whole = kept.astype(jnp.bfloat16)[None]
    for step in reversed(range(steps)):
        bit = (own >> step) & 1
        pairs = [(device, device ^ (1 << step)) for device in range(count)]
        arrived = lax.ppermute(whole, "dp", pairs)
        low_half = jnp.where(bit == 0, whole, arrived)
        high_half = jnp.where(bit == 0, arrived, whole)
        whole = jnp.stack([low_half, high_half], axis=1).reshape((-1,) + whole.shape[1:])
    return whole.reshape(-1)[: flat.shape[0]]


def head_gather_relative(values):
    count = lax.axis_size("head")
    parts = [values]
    for shift in range(1, count):
        parts.append(
            lax.ppermute(values, "head", [(device, (device + shift) % count) for device in range(count)])
        )
    return jnp.concatenate(parts, axis=0)


def head_scatter_relative(values):
    count = lax.axis_size("head")
    width = values.shape[0] // count
    total = values[:width].astype(jnp.float32)
    for shift in range(1, count):
        sent = values[(count - shift) * width : (count - shift + 1) * width]
        total = total + lax.ppermute(
            sent, "head", [(device, (device + shift) % count) for device in range(count)]
        ).astype(jnp.float32)
    return total


def map_rows(step, items):
    outs = [step(tuple(item[row] for item in items)) for row in range(items[0].shape[0])]
    return tuple(jnp.stack(parts) for parts in zip(*outs))


def turn(block, cosine, sine):
    half_depth = block.shape[-1] // 2
    first_half, second_half = block[:, :half_depth], block[:, half_depth:]
    return jnp.concatenate(
        [first_half * cosine - second_half * sine, second_half * cosine + first_half * sine], axis=1
    )


def unturn(block, cosine, sine):
    half_depth = block.shape[-1] // 2
    first_half, second_half = block[:, :half_depth], block[:, half_depth:]
    return jnp.concatenate(
        [first_half * cosine + second_half * sine, second_half * cosine - first_half * sine], axis=1
    )


def dp_all_reduce_pairs(flat):
    count = lax.axis_size("dp")
    own = lax.axis_index("dp")
    group = count // 2
    width = -(-flat.shape[0] // (count * 128)) * 128
    blocks = jnp.pad(flat, (0, count * width - flat.shape[0])).reshape(group, 2, width)
    bit = own & 1
    member = own >> 1
    partner = [(device, device ^ 1) for device in range(count)]
    sent = lax.dynamic_index_in_dim(blocks, 1 - bit, 1, keepdims=False)
    kept = lax.dynamic_index_in_dim(blocks, bit, 1, keepdims=False).astype(jnp.float32)
    kept = kept + lax.ppermute(sent, "dp", partner).astype(jnp.float32)
    shifts = [
        [(device, (device & 1) + 2 * (((device >> 1) + shift) % group)) for device in range(count)]
        for shift in range(group)
    ]
    total = lax.dynamic_index_in_dim(kept, member, 0, keepdims=False)
    for shift in range(1, group):
        sent = lax.dynamic_index_in_dim(kept, (member + shift) % group, 0, keepdims=False)
        total = total + lax.ppermute(sent.astype(jnp.bfloat16), "dp", shifts[shift]).astype(
            jnp.float32
        )
    mine = total.astype(jnp.bfloat16)
    parts = [mine] + [lax.ppermute(mine, "dp", shifts[shift]) for shift in range(1, group)]
    rows = []
    for index in range(group):
        source = (member - index) % group
        row = parts[0]
        for shift in range(1, group):
            row = jnp.where(source == shift, parts[shift], row)
        rows.append(row)
    ordered = jnp.stack(rows, axis=0)
    arrived = lax.ppermute(ordered, "dp", partner)
    low_half = jnp.where(bit == 0, ordered, arrived)
    high_half = jnp.where(bit == 0, arrived, ordered)
    return jnp.stack([low_half, high_half], axis=1).reshape(-1)[: flat.shape[0]]


def local(
    tokens,
    doc_ids,
    gain_attn,
    a_weight,
    b_weight,
    out_weight,
    gain_ffn,
    gate_weight,
    up_weight,
    down_weight,
    cotangent,
):
    rows_dev, length = doc_ids.shape
    total_rows = rows_dev * length
    own_rows = tokens.shape[0]
    local_heads = out_weight.shape[0] // DH
    rank_all = RQ + 2 * RK
    x_own = tokens.astype(jnp.float32)
    inv_one = lax.rsqrt(jnp.mean(x_own * x_own, axis=-1, keepdims=True) + EPSILON)
    normed_one = (x_own * inv_one * gain_attn).astype(jnp.bfloat16)
    normed_all = head_all_gather(normed_one, 0)
    normed_all, cotangent_late = lax.optimization_barrier((normed_all, cotangent))
    grad_out_all = head_gather_relative(cotangent_late)
    factor_a = jnp.dot(normed_all, a_weight, preferred_element_type=jnp.float32)
    factor_b = jnp.dot(normed_all, b_weight, preferred_element_type=jnp.float32)
    cosine, sine = rope_tables(total_rows, length)
    basis_query = [
        turn(factor_b[:, rank * DH : (rank + 1) * DH], cosine, sine) for rank in range(RQ)
    ]
    basis_key = [
        turn(factor_b[:, (RQ + rank) * DH : (RQ + rank + 1) * DH], cosine, sine)
        for rank in range(RK)
    ]
    basis_value = [
        factor_b[:, (RQ + RK + rank) * DH : (RQ + RK + rank + 1) * DH] for rank in range(RK)
    ]
    coef = [
        [factor_a[:, head * rank_all + column] [:, None] for column in range(rank_all)]
        for head in range(local_heads)
    ]

    def combine(bases, offset):
        return jnp.stack(
            [
                sum(coef[head][offset + rank] * bases[rank] for rank in range(len(bases)))
                / len(bases)
                for head in range(local_heads)
            ],
            axis=1,
        ).astype(jnp.bfloat16)

    queries = combine(basis_query, 0)
    key_rows = combine(basis_key, RQ)
    value_rows = combine(basis_value, RQ + RK)
    row_shape = (rows_dev, length, local_heads, DH)
    query_rows = queries.reshape(row_shape)
    keys_rows = key_rows.reshape(row_shape)
    values_rows = value_rows.reshape(row_shape)
    mixed_rows, log_total = map_rows(attend_row, (query_rows, keys_rows, values_rows, doc_ids))
    mixed = mixed_rows.reshape(total_rows, local_heads * DH)
    piece = lax.slice_in_dim(mixed, 0, lax.axis_size("head") * own_rows, axis=0)
    resid_own = x_own + head_reduce_scatter(
        jnp.dot(piece, out_weight, preferred_element_type=jnp.float32).astype(jnp.bfloat16), 0
    )
    resid_own, grad_out_all = lax.optimization_barrier((resid_own, grad_out_all))
    inv_two = lax.rsqrt(jnp.mean(resid_own * resid_own, axis=-1, keepdims=True) + EPSILON)
    normed_two = (resid_own * inv_two * gain_ffn).astype(jnp.bfloat16)
    normed_two_all = head_gather_relative(normed_two)
    gate_act = jnp.dot(normed_two_all, gate_weight, preferred_element_type=jnp.float32)
    up_act = jnp.dot(normed_two_all, up_weight, preferred_element_type=jnp.float32)
    sigmoid_gate = jax.nn.sigmoid(gate_act)
    silu_gate = sigmoid_gate * gate_act
    hidden = (silu_gate * up_act).astype(jnp.bfloat16)
    piece = lax.slice_in_dim(hidden, 0, lax.axis_size("head") * own_rows, axis=0)
    output = (
        resid_own
        + head_scatter_relative(
            jnp.dot(piece, down_weight, preferred_element_type=jnp.float32).astype(jnp.bfloat16)
        )
    ).astype(jnp.bfloat16)
    grad_down = dot_first(hidden, grad_out_all)
    grad_hidden = dot_last(grad_out_all, down_weight)
    grad_gate_act = (
        grad_hidden * up_act * (sigmoid_gate * (1.0 + gate_act * (1.0 - sigmoid_gate)))
    ).astype(jnp.bfloat16)
    grad_up_act = (grad_hidden * silu_gate).astype(jnp.bfloat16)
    grad_gate = dot_first(normed_two_all, grad_gate_act)
    grad_up = dot_first(normed_two_all, grad_up_act)
    gate_piece = lax.slice_in_dim(grad_gate_act, 0, lax.axis_size("head") * own_rows, axis=0)
    up_piece = lax.slice_in_dim(grad_up_act, 0, lax.axis_size("head") * own_rows, axis=0)
    grad_normed_two = head_scatter_relative(
        (dot_last(gate_piece, gate_weight) + dot_last(up_piece, up_weight)).astype(jnp.bfloat16)
    )
    ffn_grads = (grad_gate.astype(jnp.bfloat16), grad_up.astype(jnp.bfloat16), grad_down.astype(jnp.bfloat16))
    ffn_grads, grad_normed_two = lax.optimization_barrier((ffn_grads, grad_normed_two))
    grad_gate, grad_up, grad_down = lax.psum(ffn_grads, "dp")
    resid_part, grad_gain_ffn_own = norm_backward(resid_own, inv_two, gain_ffn, grad_normed_two)
    grad_resid = cotangent.astype(jnp.float32) + resid_part
    output, grad_resid = lax.optimization_barrier((output, grad_resid))
    grad_branch = head_all_gather(grad_resid.astype(jnp.bfloat16), 0)
    grad_mixed = dot_last(grad_branch, out_weight).astype(jnp.bfloat16)
    grad_out = dot_first(mixed, grad_branch)
    grad_query_rows, grad_key_rows, grad_value_rows = map_rows(
        attend_back,
        (query_rows, keys_rows, values_rows, doc_ids, log_total, grad_mixed.reshape(row_shape)),
    )
    head_shape = (total_rows, local_heads, DH)
    grad_query = rounded(grad_query_rows.reshape(head_shape))
    grad_key = rounded(grad_key_rows.reshape(head_shape))
    grad_value = rounded(grad_value_rows.reshape(head_shape))
    grads_by_part = ((grad_query, basis_query, 0), (grad_key, basis_key, RQ), (grad_value, basis_value, RQ + RK))
    coef_columns = [None] * (local_heads * rank_all)
    basis_grads = []
    for grad_part, bases, offset in grads_by_part:
        for rank, basis in enumerate(bases):
            for head in range(local_heads):
                coef_columns[head * rank_all + offset + rank] = jnp.sum(
                    grad_part[:, head, :] * basis, axis=1
                ) / len(bases)
            basis_grad = sum(
                coef[head][offset + rank] * grad_part[:, head, :] for head in range(local_heads)
            ) / len(bases)
            basis_grads.append(basis_grad if offset == RQ + RK else unturn(basis_grad, cosine, sine))
    grad_factor_a = jnp.stack(coef_columns, axis=1).astype(jnp.bfloat16)
    grad_factor_b = jnp.concatenate(basis_grads, axis=1)
    head_count = lax.axis_size("head")
    basis_cols = grad_factor_b.shape[1] // head_count
    factor_cols = head_reduce_scatter(grad_factor_b.astype(jnp.bfloat16), 1).astype(jnp.bfloat16)
    weight_cols = lax.dynamic_slice_in_dim(
        b_weight, lax.axis_index("head") * basis_cols, basis_cols, axis=1
    )
    piece = grad_factor_a
    grad_normed_one = head_reduce_scatter(
        (dot_last(piece, a_weight) + dot_last(factor_cols, weight_cols)).astype(jnp.bfloat16), 0
    )
    input_part, grad_gain_attn_own = norm_backward(x_own, inv_one, gain_attn, grad_normed_one)
    input_grad = grad_resid + input_part
    grad_a = dot_first(normed_all, grad_factor_a)
    grad_b_cols = dot_first(normed_all, factor_cols)

    features = grad_gain_attn_own.shape[0]
    gain_rows = -(-2 * features // basis_cols)
    gains = jnp.pad(
        jnp.concatenate([grad_gain_attn_own, grad_gain_ffn_own]),
        (0, gain_rows * basis_cols - 2 * features),
    ).reshape(gain_rows, basis_cols)
    tail = (
        grad_a.astype(jnp.bfloat16),
        grad_out.astype(jnp.bfloat16),
        jnp.concatenate([grad_b_cols, gains], axis=0).astype(jnp.bfloat16),
    )
    tail, (grad_gate, grad_up, grad_down) = lax.optimization_barrier(
        (tail, (grad_gate, grad_up, grad_down))
    )
    sizes = [part.size for part in tail]
    summed = dp_all_reduce_pairs(jnp.concatenate([part.reshape(-1) for part in tail]))
    grad_a, grad_out, packed = (
        summed[sum(sizes[:index]) : sum(sizes[: index + 1])].reshape(part.shape)
        for index, part in enumerate(tail)
    )
    grad_out, grad_gate, grad_up, grad_down = (
        grad_out.astype(jnp.float32),
        grad_gate.astype(jnp.float32),
        grad_up.astype(jnp.float32),
        grad_down.astype(jnp.float32),
    )
    grad_a = grad_a.astype(jnp.float32)
    packed = lax.all_gather(packed, "head", axis=1, tiled=True)
    grad_b = packed[: grad_b_cols.shape[0]].astype(jnp.float32)
    gains = jnp.sum(
        packed[grad_b_cols.shape[0] :]
        .astype(jnp.float32)
        .reshape(gain_rows, head_count, basis_cols),
        axis=1,
    ).reshape(-1)
    grad_gain_attn, grad_gain_ffn = gains[:features], gains[features : 2 * features]
    return (
        output,
        input_grad,
        grad_gain_attn,
        grad_a,
        grad_b,
        grad_out,
        grad_gain_ffn,
        grad_gate,
        grad_up,
        grad_down,
    )


def solution(mesh):
    return jax.shard_map(
        local,
        mesh=mesh,
        in_specs=(
            P(("dp", "head"), None),
            P("dp", None),
            P(),
            P(None, "head"),
            P(),
            P("head", None),
            P(),
            P(None, "head"),
            P(None, "head"),
            P("head", None),
            P(("dp", "head"), None),
        ),
        out_specs=(
            P(("dp", "head"), None),
            P(("dp", "head"), None),
            P(),
            P(None, "head"),
            P(),
            P("head", None),
            P(),
            P(None, "head"),
            P(None, "head"),
            P("head", None),
        ),
        check_vma=False,
    )
```

```python
import math

import jax
import jax.numpy as jnp
from jax import lax
from jax.sharding import PartitionSpec as P

DH = 64
RQ = 6
RK = 2


EPSILON = 1e-06
MASKED = -1e30
PRECISE = lax.Precision.HIGHEST


def rope_tables(total_rows, length):
    half_depth = DH // 2
    position = (jnp.arange(total_rows, dtype=jnp.int32) % length).astype(jnp.float32)
    frequency = jnp.exp(jnp.arange(half_depth, dtype=jnp.float32) * (-2.0 * math.log(10000.0) / DH))
    angle = position[:, None] * frequency[None, :]
    return (jnp.cos(angle), jnp.sin(angle))


def rotate(basis, cosine, sine):
    half_depth = basis.shape[-1] // 2
    first_half = basis[..., :half_depth]
    second_half = basis[..., half_depth:]
    cosine_row = cosine[:, None, :]
    sine_row = sine[:, None, :]
    return jnp.concatenate(
        [
            first_half * cosine_row - second_half * sine_row,
            second_half * cosine_row + first_half * sine_row,
        ],
        axis=-1,
    )


def unrotate(grad_basis, cosine, sine):
    half_depth = grad_basis.shape[-1] // 2
    first_half = grad_basis[..., :half_depth]
    second_half = grad_basis[..., half_depth:]
    cosine_row = cosine[:, None, :]
    sine_row = sine[:, None, :]
    return jnp.concatenate(
        [
            first_half * cosine_row + second_half * sine_row,
            second_half * cosine_row - first_half * sine_row,
        ],
        axis=-1,
    )


def dot_last(left, right):
    return lax.dot_general(
        left, right, (((1,), (1,)), ((), ())), preferred_element_type=jnp.float32
    )


def dot_first(left, right):
    return lax.dot_general(
        left, right, (((0,), (0,)), ((), ())), preferred_element_type=jnp.float32
    )


def norm_backward(inputs, inverse, gain, grad_normed):
    scaled = gain * grad_normed
    inner = jnp.mean(scaled * inputs, axis=-1, keepdims=True)
    grad_inputs = inverse * scaled - inputs * (inverse * inverse * inverse) * inner
    grad_gain = jnp.sum(grad_normed * inputs * inverse, axis=0)
    return (grad_inputs, grad_gain)


def block_scores(queries, key_rows, doc_row, first_row, last_row):
    position = jnp.arange(last_row, dtype=jnp.int32)
    allowed = (doc_row[first_row:last_row, None] == doc_row[None, :last_row]) & (
        position[None, :] <= position[first_row:last_row, None]
    )
    score_scale = 1.0 / math.sqrt(queries.shape[2])
    scores = (
        jnp.einsum(
            "qhd,khd->hqk",
            queries[first_row:last_row],
            key_rows[:last_row],
            preferred_element_type=jnp.float32,
        )
        * score_scale
    )
    return jnp.where(allowed[None], scores, MASKED)


def attend_row(row_item):
    queries, key_rows, value_rows, doc_row = row_item
    length = queries.shape[0]
    block_rows = min(512, length)
    mixed_parts = []
    total_parts = []
    for first_row in range(0, length, block_rows):
        last_row = first_row + block_rows
        scores = block_scores(queries, key_rows, doc_row, first_row, last_row)
        row_peak = jnp.max(scores, axis=-1, keepdims=True)
        exponent = jnp.exp(scores - row_peak)
        row_total = jnp.sum(exponent, axis=-1, keepdims=True)
        weights = (exponent / row_total).astype(jnp.bfloat16)
        mixed_parts.append(
            jnp.einsum(
                "hqk,khd->qhd", weights, value_rows[:last_row], preferred_element_type=jnp.float32
            ).astype(jnp.bfloat16)
        )
        total_parts.append(row_peak[..., 0] + jnp.log(row_total[..., 0]))
    return (jnp.concatenate(mixed_parts, axis=0), jnp.concatenate(total_parts, axis=1))


def attend_back(row_item):
    queries, key_rows, value_rows, doc_row, log_total, grad_mixed = row_item
    length = queries.shape[0]
    block_rows = min(512, length)
    score_scale = 1.0 / math.sqrt(queries.shape[2])
    grad_query_parts = []
    grad_keys = jnp.zeros(key_rows.shape, jnp.float32)
    grad_values = jnp.zeros(value_rows.shape, jnp.float32)
    for first_row in range(0, length, block_rows):
        last_row = first_row + block_rows
        scores = block_scores(queries, key_rows, doc_row, first_row, last_row)
        weights = jnp.exp(scores - log_total[:, first_row:last_row, None])
        grad_weights = jnp.einsum(
            "qhd,khd->hqk",
            grad_mixed[first_row:last_row],
            value_rows[:last_row],
            preferred_element_type=jnp.float32,
        )
        inner = jnp.sum(weights * grad_weights, axis=-1, keepdims=True)
        grad_scores = (weights * (grad_weights - inner)).astype(jnp.bfloat16)
        grad_query_parts.append(
            jnp.einsum(
                "hqk,khd->qhd", grad_scores, key_rows[:last_row], preferred_element_type=jnp.float32
            )
            * score_scale
        )
        padding = ((0, length - last_row), (0, 0), (0, 0))
        key_part = (
            jnp.einsum(
                "hqk,qhd->khd",
                grad_scores,
                queries[first_row:last_row],
                preferred_element_type=jnp.float32,
            )
            * score_scale
        )
        value_part = jnp.einsum(
            "hqk,qhd->khd",
            weights.astype(jnp.bfloat16),
            grad_mixed[first_row:last_row],
            preferred_element_type=jnp.float32,
        )
        grad_keys = grad_keys + jnp.pad(key_part, padding)
        grad_values = grad_values + jnp.pad(value_part, padding)
    return (jnp.concatenate(grad_query_parts, axis=0), grad_keys, grad_values)


def rounded(values_in):
    return lax.optimization_barrier(values_in.astype(jnp.bfloat16)).astype(jnp.float32)


def head_reduce_scatter(values, axis):
    count = lax.axis_size("head")
    own = lax.axis_index("head")
    width = values.shape[axis] // count
    total = lax.dynamic_slice_in_dim(values, own * width, width, axis=axis).astype(jnp.float32)
    for shift in range(1, count):
        sent = lax.dynamic_slice_in_dim(values, ((own + shift) % count) * width, width, axis=axis)
        total = total + lax.ppermute(
            sent, "head", [(device, (device + shift) % count) for device in range(count)]
        ).astype(jnp.float32)
    return total


def head_all_gather(values, axis):
    count = lax.axis_size("head")
    own = lax.axis_index("head")
    width = values.shape[axis]
    shape = list(values.shape)
    shape[axis] = width * count
    gathered = lax.dynamic_update_slice_in_dim(
        jnp.zeros(shape, values.dtype), values, own * width, axis=axis
    )
    for shift in range(1, count):
        arrived = lax.ppermute(
            values, "head", [(device, (device + shift) % count) for device in range(count)]
        )
        gathered = lax.dynamic_update_slice_in_dim(
            gathered, arrived, ((own - shift) % count) * width, axis=axis
        )
    return gathered


def dp_all_reduce(flat):
    count = lax.axis_size("dp")
    own = lax.axis_index("dp")
    steps = count.bit_length() - 1
    assert count == 1 << steps
    width = -(-flat.shape[0] // (count * 128)) * 128
    blocks = jnp.pad(flat, (0, count * width - flat.shape[0])).reshape((2,) * steps + (width,))
    kept = blocks.astype(jnp.float32)
    for step in range(steps):
        axis = steps - 1 - step
        bit = (own >> step) & 1
        sent = lax.dynamic_index_in_dim(kept, 1 - bit, axis, keepdims=False)
        kept = lax.dynamic_index_in_dim(kept, bit, axis, keepdims=False)
        pairs = [(device, device ^ (1 << step)) for device in range(count)]
        kept = kept + lax.ppermute(sent.astype(jnp.bfloat16), "dp", pairs).astype(jnp.float32)
    whole = kept.astype(jnp.bfloat16)[None]
    for step in reversed(range(steps)):
        bit = (own >> step) & 1
        pairs = [(device, device ^ (1 << step)) for device in range(count)]
        arrived = lax.ppermute(whole, "dp", pairs)
        low_half = jnp.where(bit == 0, whole, arrived)
        high_half = jnp.where(bit == 0, arrived, whole)
        whole = jnp.stack([low_half, high_half], axis=1).reshape((-1,) + whole.shape[1:])
    return whole.reshape(-1)[: flat.shape[0]]


def head_gather_relative(values):
    count = lax.axis_size("head")
    parts = [values]
    for shift in range(1, count):
        parts.append(
            lax.ppermute(values, "head", [(device, (device + shift) % count) for device in range(count)])
        )
    return jnp.concatenate(parts, axis=0)


def head_scatter_relative(values):
    count = lax.axis_size("head")
    width = values.shape[0] // count
    total = values[:width].astype(jnp.float32)
    for shift in range(1, count):
        sent = values[(count - shift) * width : (count - shift + 1) * width]
        total = total + lax.ppermute(
            sent, "head", [(device, (device + shift) % count) for device in range(count)]
        ).astype(jnp.float32)
    return total


def map_rows(step, items):
    outs = [step(tuple(item[row] for item in items)) for row in range(items[0].shape[0])]
    return tuple(jnp.stack(parts) for parts in zip(*outs))


def turn(block, cosine, sine):
    half_depth = block.shape[-1] // 2
    first_half, second_half = block[:, :half_depth], block[:, half_depth:]
    return jnp.concatenate(
        [first_half * cosine - second_half * sine, second_half * cosine + first_half * sine], axis=1
    )


def unturn(block, cosine, sine):
    half_depth = block.shape[-1] // 2
    first_half, second_half = block[:, :half_depth], block[:, half_depth:]
    return jnp.concatenate(
        [first_half * cosine + second_half * sine, second_half * cosine - first_half * sine], axis=1
    )


def dp_all_reduce_pairs(flat):
    count = lax.axis_size("dp")
    own = lax.axis_index("dp")
    group = count // 2
    width = -(-flat.shape[0] // (count * 128)) * 128
    blocks = jnp.pad(flat, (0, count * width - flat.shape[0])).reshape(group, 2, width)
    bit = own & 1
    member = own >> 1
    partner = [(device, device ^ 1) for device in range(count)]
    sent = lax.dynamic_index_in_dim(blocks, 1 - bit, 1, keepdims=False)
    kept = lax.dynamic_index_in_dim(blocks, bit, 1, keepdims=False).astype(jnp.float32)
    kept = kept + lax.ppermute(sent, "dp", partner).astype(jnp.float32)
    shifts = [
        [(device, (device & 1) + 2 * (((device >> 1) + shift) % group)) for device in range(count)]
        for shift in range(group)
    ]
    total = lax.dynamic_index_in_dim(kept, member, 0, keepdims=False)
    for shift in range(1, group):
        sent = lax.dynamic_index_in_dim(kept, (member + shift) % group, 0, keepdims=False)
        total = total + lax.ppermute(sent.astype(jnp.bfloat16), "dp", shifts[shift]).astype(
            jnp.float32
        )
    mine = total.astype(jnp.bfloat16)
    parts = [mine] + [lax.ppermute(mine, "dp", shifts[shift]) for shift in range(1, group)]
    rows = []
    for index in range(group):
        source = (member - index) % group
        row = parts[0]
        for shift in range(1, group):
            row = jnp.where(source == shift, parts[shift], row)
        rows.append(row)
    ordered = jnp.stack(rows, axis=0)
    arrived = lax.ppermute(ordered, "dp", partner)
    low_half = jnp.where(bit == 0, ordered, arrived)
    high_half = jnp.where(bit == 0, arrived, ordered)
    return jnp.stack([low_half, high_half], axis=1).reshape(-1)[: flat.shape[0]]


def local(
    tokens,
    doc_ids,
    gain_attn,
    a_weight,
    b_weight,
    out_weight,
    gain_ffn,
    gate_weight,
    up_weight,
    down_weight,
    cotangent,
):
    rows_dev, length = doc_ids.shape
    total_rows = rows_dev * length
    own_rows = tokens.shape[0]
    local_heads = out_weight.shape[0] // DH
    rank_all = RQ + 2 * RK
    x_own = tokens.astype(jnp.float32)
    inv_one = lax.rsqrt(jnp.mean(x_own * x_own, axis=-1, keepdims=True) + EPSILON)
    normed_one = (x_own * inv_one * gain_attn).astype(jnp.bfloat16)
    normed_all = head_all_gather(normed_one, 0)
    normed_all, cotangent_late = lax.optimization_barrier((normed_all, cotangent))
    grad_out_all = head_gather_relative(cotangent_late)
    factor_a = jnp.dot(normed_all, a_weight, preferred_element_type=jnp.float32)
    factor_b = jnp.dot(normed_all, b_weight, preferred_element_type=jnp.float32)
    cosine, sine = rope_tables(total_rows, length)
    basis_query = [
        turn(factor_b[:, rank * DH : (rank + 1) * DH], cosine, sine) for rank in range(RQ)
    ]
    basis_key = [
        turn(factor_b[:, (RQ + rank) * DH : (RQ + rank + 1) * DH], cosine, sine)
        for rank in range(RK)
    ]
    basis_value = [
        factor_b[:, (RQ + RK + rank) * DH : (RQ + RK + rank + 1) * DH] for rank in range(RK)
    ]
    coef = [
        [factor_a[:, head * rank_all + column] [:, None] for column in range(rank_all)]
        for head in range(local_heads)
    ]

    def combine(bases, offset):
        return jnp.stack(
            [
                sum(coef[head][offset + rank] * bases[rank] for rank in range(len(bases)))
                / len(bases)
                for head in range(local_heads)
            ],
            axis=1,
        ).astype(jnp.bfloat16)

    queries = combine(basis_query, 0)
    key_rows = combine(basis_key, RQ)
    value_rows = combine(basis_value, RQ + RK)
    row_shape = (rows_dev, length, local_heads, DH)
    query_rows = queries.reshape(row_shape)
    keys_rows = key_rows.reshape(row_shape)
    values_rows = value_rows.reshape(row_shape)
    mixed_rows, log_total = map_rows(attend_row, (query_rows, keys_rows, values_rows, doc_ids))
    mixed = mixed_rows.reshape(total_rows, local_heads * DH)
    piece = lax.slice_in_dim(mixed, 0, lax.axis_size("head") * own_rows, axis=0)
    resid_own = x_own + head_reduce_scatter(
        jnp.dot(piece, out_weight, preferred_element_type=jnp.float32).astype(jnp.bfloat16), 0
    )
    resid_own, grad_out_all = lax.optimization_barrier((resid_own, grad_out_all))
    inv_two = lax.rsqrt(jnp.mean(resid_own * resid_own, axis=-1, keepdims=True) + EPSILON)
    normed_two = (resid_own * inv_two * gain_ffn).astype(jnp.bfloat16)
    normed_two_all = head_gather_relative(normed_two)
    gate_act = jnp.dot(normed_two_all, gate_weight, preferred_element_type=jnp.float32)
    up_act = jnp.dot(normed_two_all, up_weight, preferred_element_type=jnp.float32)
    sigmoid_gate = jax.nn.sigmoid(gate_act)
    silu_gate = sigmoid_gate * gate_act
    hidden = (silu_gate * up_act).astype(jnp.bfloat16)
    piece = lax.slice_in_dim(hidden, 0, lax.axis_size("head") * own_rows, axis=0)
    output = (
        resid_own
        + head_scatter_relative(
            jnp.dot(piece, down_weight, preferred_element_type=jnp.float32).astype(jnp.bfloat16)
        )
    ).astype(jnp.bfloat16)
    grad_down = dot_first(hidden, grad_out_all)
    grad_hidden = dot_last(grad_out_all, down_weight)
    grad_gate_act = (
        grad_hidden * up_act * (sigmoid_gate * (1.0 + gate_act * (1.0 - sigmoid_gate)))
    ).astype(jnp.bfloat16)
    grad_up_act = (grad_hidden * silu_gate).astype(jnp.bfloat16)
    grad_gate = dot_first(normed_two_all, grad_gate_act)
    grad_up = dot_first(normed_two_all, grad_up_act)
    gate_piece = lax.slice_in_dim(grad_gate_act, 0, lax.axis_size("head") * own_rows, axis=0)
    up_piece = lax.slice_in_dim(grad_up_act, 0, lax.axis_size("head") * own_rows, axis=0)
    grad_normed_two = head_scatter_relative(
        (dot_last(gate_piece, gate_weight) + dot_last(up_piece, up_weight)).astype(jnp.bfloat16)
    )
    ffn_grads = (grad_gate.astype(jnp.bfloat16), grad_up.astype(jnp.bfloat16), grad_down.astype(jnp.bfloat16))
    ffn_grads, grad_normed_two = lax.optimization_barrier((ffn_grads, grad_normed_two))
    grad_gate, grad_up, grad_down = lax.psum(ffn_grads, "dp")
    resid_part, grad_gain_ffn_own = norm_backward(resid_own, inv_two, gain_ffn, grad_normed_two)
    grad_resid = cotangent.astype(jnp.float32) + resid_part
    output, grad_resid = lax.optimization_barrier((output, grad_resid))
    grad_branch = head_all_gather(grad_resid.astype(jnp.bfloat16), 0)
    grad_mixed = dot_last(grad_branch, out_weight).astype(jnp.bfloat16)
    grad_out = dot_first(mixed, grad_branch)
    grad_query_rows, grad_key_rows, grad_value_rows = map_rows(
        attend_back,
        (query_rows, keys_rows, values_rows, doc_ids, log_total, grad_mixed.reshape(row_shape)),
    )
    head_shape = (total_rows, local_heads, DH)
    grad_query = rounded(grad_query_rows.reshape(head_shape))
    grad_key = rounded(grad_key_rows.reshape(head_shape))
    grad_value = rounded(grad_value_rows.reshape(head_shape))
    grads_by_part = ((grad_query, basis_query, 0), (grad_key, basis_key, RQ), (grad_value, basis_value, RQ + RK))
    coef_columns = [None] * (local_heads * rank_all)
    basis_grads = []
    for grad_part, bases, offset in grads_by_part:
        for rank, basis in enumerate(bases):
            for head in range(local_heads):
                coef_columns[head * rank_all + offset + rank] = jnp.sum(
                    grad_part[:, head, :] * basis, axis=1
                )
            basis_grad = sum(
                coef[head][offset + rank] * grad_part[:, head, :] for head in range(local_heads)
            ) / len(bases)
            basis_grads.append(basis_grad if offset == RQ + RK else unturn(basis_grad, cosine, sine))
    rank_of = jnp.array([RQ] * RQ + [RK] * (2 * RK), jnp.float32)
    grad_factor_a = (
        jnp.stack(coef_columns, axis=1) / jnp.tile(rank_of, local_heads)[None, :]
    ).astype(jnp.bfloat16)
    grad_factor_b = jnp.concatenate(basis_grads, axis=1)
    head_count = lax.axis_size("head")
    basis_cols = grad_factor_b.shape[1] // head_count
    factor_cols = head_reduce_scatter(grad_factor_b.astype(jnp.bfloat16), 1).astype(jnp.bfloat16)
    weight_cols = lax.dynamic_slice_in_dim(
        b_weight, lax.axis_index("head") * basis_cols, basis_cols, axis=1
    )
    piece = grad_factor_a
    grad_normed_one = head_reduce_scatter(
        (dot_last(piece, a_weight) + dot_last(factor_cols, weight_cols)).astype(jnp.bfloat16), 0
    )
    input_part, grad_gain_attn_own = norm_backward(x_own, inv_one, gain_attn, grad_normed_one)
    input_grad = grad_resid + input_part
    grad_a = dot_first(normed_all, grad_factor_a)
    grad_b_cols = dot_first(normed_all, factor_cols)

    features = grad_gain_attn_own.shape[0]
    gain_rows = -(-2 * features // basis_cols)
    gains = jnp.pad(
        jnp.concatenate([grad_gain_attn_own, grad_gain_ffn_own]),
        (0, gain_rows * basis_cols - 2 * features),
    ).reshape(gain_rows, basis_cols)
    tail = (
        grad_a.astype(jnp.bfloat16),
        grad_out.astype(jnp.bfloat16),
        jnp.concatenate([grad_b_cols, gains], axis=0).astype(jnp.bfloat16),
    )
    tail, (grad_gate, grad_up, grad_down) = lax.optimization_barrier(
        (tail, (grad_gate, grad_up, grad_down))
    )
    sizes = [part.size for part in tail]
    summed = dp_all_reduce_pairs(jnp.concatenate([part.reshape(-1) for part in tail]))
    grad_a, grad_out, packed = (
        summed[sum(sizes[:index]) : sum(sizes[: index + 1])].reshape(part.shape)
        for index, part in enumerate(tail)
    )
    grad_out, grad_gate, grad_up, grad_down = (
        grad_out.astype(jnp.float32),
        grad_gate.astype(jnp.float32),
        grad_up.astype(jnp.float32),
        grad_down.astype(jnp.float32),
    )
    grad_a = grad_a.astype(jnp.float32)
    packed = lax.all_gather(packed, "head", axis=1, tiled=True)
    grad_b = packed[: grad_b_cols.shape[0]].astype(jnp.float32)
    gains = jnp.sum(
        packed[grad_b_cols.shape[0] :]
        .astype(jnp.float32)
        .reshape(gain_rows, head_count, basis_cols),
        axis=1,
    ).reshape(-1)
    grad_gain_attn, grad_gain_ffn = gains[:features], gains[features : 2 * features]
    return (
        output,
        input_grad,
        grad_gain_attn,
        grad_a,
        grad_b,
        grad_out,
        grad_gain_ffn,
        grad_gate,
        grad_up,
        grad_down,
    )


def solution(mesh):
    return jax.shard_map(
        local,
        mesh=mesh,
        in_specs=(
            P(("dp", "head"), None),
            P("dp", None),
            P(),
            P(None, "head"),
            P(),
            P("head", None),
            P(),
            P(None, "head"),
            P(None, "head"),
            P("head", None),
            P(("dp", "head"), None),
        ),
        out_specs=(
            P(("dp", "head"), None),
            P(("dp", "head"), None),
            P(),
            P(None, "head"),
            P(),
            P("head", None),
            P(),
            P(None, "head"),
            P(None, "head"),
            P("head", None),
        ),
        check_vma=False,
    )
```
